32 devices in a mesh: seq: 2 (over x), mp: 4 (over z), dp: 4 (over y, core).
Axes of the slice: x: 2, y: 2, z: 4, core: 2. Of those that a mesh axis runs over, the one named last changes fastest.
Arguments:
- features: bfloat16 [4, 2048, 768], P('dp', 'seq'), may hold values from -6 to 6
- conv_weight: bfloat16 [5, 768, 768], P(None, 'mp'), may hold values from -0.09375 to 0.09375
- keep: int32 [4], P('dp'), may hold values 0 or 1
- tiles: int32 [4, 2, 2, 2], P('dp'), may hold values from 0 to 63, as said below
- counts: int32 [4, 2], P('dp'), may hold values from 0 to 2, as said below
- targets: float32 [4, 2, 2, 1024], P('dp', 'seq'), may hold values from -6 to 6
Outputs:
- conv_grad: float32 [5, 768, 768], P(None, 'mp', ('seq', 'dp'))
The draws below stay inside these ranges and needn't reach their ends.
Inputs may be any that keep to these rules, and one draw needn't show every extreme that they name: `tiles`: entries are block numbers of 32 positions in a sequence. For every sequence and owner, listing the 2 row blocks and then the 2 column blocks, exactly 2 of these 4 entries lie in the positions of each index of seq. Each owner's live slots are its first counts slots; in every sequence some owner has all 2 slots live.
All inputs are finite; a program needn't handle non-finite values. No bound on the sum of `keep` on one device may be relied on, other than what follows from the above.
Results may differ from the reference program's by a relative error of at most 0.0015.
Values may be sent and summed in bfloat16 or wider, within the bound.
No kernel may reach another device: no remote copies, remote signals or barrier semaphores. Data moves between devices by JAX's collectives and lax.ppermute only.
A program may use at most 64 MiB of HBM per device.

```python
import math
import jax
import jax.numpy as jnp
from jax import lax

D = 768
KW = 5
TB = 32
PER = 2
BIN_DEV = 1024
SEQS = 4
BINS = 2048
CAP = 2
N_SEQ = 2


def draw_tiles(key, part):
    n_sides = 2 * CAP
    owners = n_sides // PER
    per_block = BIN_DEV // TB
    first_key, second_key = jax.random.split(key)
    scores = jax.random.randint(first_key, (SEQS, owners, n_sides), 0, 4096) * n_sides + jnp.arange(n_sides)
    ordering = jnp.argsort(scores, axis=-1)
    source = (ordering // PER).astype(jnp.int32)
    within = jax.random.randint(second_key, (SEQS, owners, n_sides), 0, per_block)
    sides = source * per_block + within
    return jnp.stack([sides[..., :CAP], sides[..., CAP:]], axis=-1).astype(jnp.int32)


def draw_counts(key, part):
    owners = 2 * CAP // PER
    first_key, second_key = jax.random.split(key)
    values = jax.random.randint(first_key, (SEQS, owners), 0, CAP + 1)
    fullest = jax.random.randint(second_key, (SEQS, 1), 0, owners)
    return jnp.where(jnp.arange(owners)[None, :] == fullest, CAP, values).astype(jnp.int32)


def touch_ends(drawn, own_key, least, high):
    extent = drawn.shape
    index_at = [jax.random.randint(jax.random.fold_in(own_key, axis), (), 0, extent[axis]) for axis in range(len(extent))]
    drawn = drawn.at[tuple(index_at)].set(least)
    longest = extent.index(max(extent))
    index_at[longest] = (index_at[longest] + 1) % extent[longest]
    return drawn.at[tuple(index_at)].set(high)


def steps_of(rng, shape, shards, least, top_value):
    level, own = 1.0, jax.random.fold_in(rng, 6)
    for position, blocks in shards:
        draws = jnp.exp(jax.random.uniform(jax.random.fold_in(own, position), (blocks,), jnp.float32, least / len(shards), top_value / len(shards)))
        level = level * jnp.repeat(draws, shape[position] // blocks).reshape([-1 if axis == position else 1 for axis in range(len(shape))])
    return level


def noise(key, shape, scale, bound, pieces=(), kind=jnp.bfloat16):
    gain = steps_of(key, shape, pieces, -0.22, 0.18) if pieces else 1.0
    array = jax.random.normal(key, shape, jnp.float32) * scale * gain
    return jnp.minimum(jnp.maximum(array, -bound), bound).astype(kind)


def setup_inputs(seed: int = 0) -> dict:
    seeds = jax.random.split(jax.random.key(seed), 7)
    features = noise(seeds[0], (SEQS, BINS, D), 1.0, 6.0, ((0, 4), (1, 2)))
    conv_weight = noise(seeds[1], (KW, D, D), (KW * D) ** -0.5, 0.09375, ((1, 4),))
    keep = touch_ends((jax.random.randint(seeds[2], (SEQS,), 0, 2) < 1).astype(jnp.int32), jax.random.fold_in(seeds[2], 1), 0, 1)
    tiles = draw_tiles(jax.random.fold_in(seeds[6], 71), 0)
    counts = draw_counts(jax.random.fold_in(seeds[6], 71), 0)
    targets = noise(seeds[5], (SEQS, N_SEQ, CAP, TB * TB), 1.0, 6.0, ((0, 4), (1, 2)), jnp.float32)
    return dict(features=features, conv_weight=conv_weight, keep=keep, tiles=tiles, counts=counts, targets=targets)


def reference(features, conv_weight, keep, tiles, counts, targets):
    weight_grad = jnp.zeros((KW, D, D), jnp.float32)
    for member in range(SEQS):
        x_float = features[member].astype(jnp.float32)
        activations = jax.nn.gelu(x_float).astype(jnp.bfloat16)
        padded = jnp.pad(activations, ((2, 2), (0, 0)))
        scaling = 1.25 * keep[member].astype(jnp.float32)
        conv_out = jnp.zeros((BINS, D), jnp.float32)
        for offset in range(KW):
            conv_out = conv_out + jnp.dot(padded[offset:offset + BINS], conv_weight[offset].T, preferred_element_type=jnp.float32)
        mixed_out = (x_float + scaling * conv_out).astype(jnp.bfloat16)
        live_mask = (jnp.arange(CAP)[None, :] < counts[member][:, None]).astype(jnp.float32)
        n_live = jnp.sum(counts[member]).astype(jnp.float32)
        target_tiles = targets[member].reshape(N_SEQ, CAP, TB, TB)
        row_ids = tiles[member, :, :, 0].astype(jnp.int32)
        col_ids = tiles[member, :, :, 1].astype(jnp.int32)
        blocks = mixed_out.astype(jnp.float32).reshape(BINS // TB, TB, D)

        def tile_loss(row_blocks, col_blocks):
            predicted = jnp.einsum('ocid,ocjd->ocij', row_blocks, col_blocks, precision=lax.Precision.HIGHEST) / math.sqrt(D)
            return jnp.sum(live_mask[:, :, None, None] * (predicted - target_tiles) ** 2) / n_live
        loss_value, pullback = jax.vjp(tile_loss, blocks[row_ids], blocks[col_ids])
        drow, dcol = pullback(jnp.ones_like(loss_value))
        drow = drow.astype(jnp.bfloat16).astype(jnp.float32)
        dcol = dcol.astype(jnp.bfloat16).astype(jnp.float32)
        dblocks = jnp.zeros((BINS // TB, TB, D), jnp.float32)
        dblocks = dblocks.at[row_ids.reshape(-1)].add(drow.reshape(-1, TB, D))
        dblocks = dblocks.at[col_ids.reshape(-1)].add(dcol.reshape(-1, TB, D))
        dmixed = dblocks.reshape(BINS, D)
        dconv = (scaling * dmixed).astype(jnp.bfloat16)
        weight_grad = weight_grad + jnp.stack([jnp.dot(dconv.T, padded[offset:offset + BINS], preferred_element_type=jnp.float32) for offset in range(KW)])
    return weight_grad
```

```python
import math

import jax
import jax.numpy as jnp
from jax import lax
from jax.sharding import PartitionSpec as P

TB = 32
PER = 2


def extended(cells, sides, width):
    for axis, dim in sides:
        count = lax.axis_size(axis)
        ends = count - 1
        head = lax.slice_in_dim(cells, 0, width, axis=dim)
        tail = lax.slice_in_dim(cells, cells.shape[dim] - width, cells.shape[dim], axis=dim)
        cells = jnp.concatenate(
            [
                lax.ppermute(tail, axis, [(i, (i + 1) % count) for i in range(ends)]),
                cells,
                lax.ppermute(head, axis, [((i + 1) % count, i) for i in range(ends)]),
            ],
            axis=dim,
        )
    return cells


def take_rows(source_array, index_array):
    return jax.vmap(lambda table, picked: table[picked])(source_array, index_array)


def conv_apply(padded, weight, length):
    total = jnp.einsum(
        "mbi,oi->mbo", padded[:, 0:length], weight[0], preferred_element_type=jnp.float32
    )
    for offset in range(1, weight.shape[0]):
        total = total + jnp.einsum(
            "mbi,oi->mbo",
            padded[:, offset : offset + length],
            weight[offset],
            preferred_element_type=jnp.float32,
        )
    return total


def weight_term(padded, dconv, length, taps):
    return jnp.stack(
        [
            jnp.einsum(
                "mbi,mbo->oi",
                padded[:, offset : offset + length],
                dconv,
                preferred_element_type=jnp.float32,
            )
            for offset in range(taps)
        ]
    )


def dense_path(features, conv_weight, keep, tiles, counts, targets):
    members, length, width = features.shape
    taps = conv_weight.shape[0]
    narrow = conv_weight.shape[1]
    seq_count = lax.axis_size("seq")
    my_index = lax.axis_index("seq")
    my_part = lax.axis_index("mp")
    x_float = features.astype(jnp.float32)
    activations = jax.nn.gelu(x_float).astype(jnp.bfloat16)
    padded = extended(activations, (("seq", 1),), 2)
    scaling = 1.25 * keep.astype(jnp.float32)
    conv_out = conv_apply(padded, conv_weight, length)
    x_local = lax.dynamic_slice_in_dim(x_float, my_part * narrow, narrow, 2)
    mixed_out = (x_local + scaling[:, None, None] * conv_out).astype(jnp.bfloat16)
    capacity = tiles.shape[2]
    n_sides = 2 * capacity
    per_block = length // TB
    sides = jnp.concatenate([tiles[..., 0], tiles[..., 1]], axis=-1)
    side_source = sides // per_block
    side_local = sides % per_block
    own_sides = lax.dynamic_index_in_dim(sides, my_index, 1, keepdims=False)
    own_source = own_sides // per_block
    before = jnp.arange(n_sides)[None, :] < jnp.arange(n_sides)[:, None]
    same_source = own_source[:, :, None] == own_source[:, None, :]
    rank_within = jnp.sum(jnp.logical_and(same_source, before[None]), axis=-1)
    slot_index = own_source * PER + rank_within
    held_here = side_source == my_index
    held_order = jnp.cumsum(held_here.astype(jnp.int32), axis=-1) - 1
    picks = jnp.stack(
        [
            jnp.sum(
                jnp.where(jnp.logical_and(held_here, held_order == position), side_local, 0),
                axis=-1,
            )
            for position in range(PER)
        ],
        axis=-1,
    )
    blocks = mixed_out.reshape(members, per_block, TB, narrow)
    whole = lax.all_gather(blocks, "seq", axis=1, tiled=True)
    side_rows = take_rows(whole, own_sides)
    row_side = side_rows[:, :capacity]
    col_side = side_rows[:, capacity:]
    partial_tiles = jnp.einsum(
        "mcid,mcjd->mcij", row_side, col_side, preferred_element_type=jnp.float32
    )
    predicted = lax.psum(partial_tiles, "mp") / math.sqrt(width)
    target_tiles = targets[:, 0].reshape(members, capacity, TB, TB)
    own_count = lax.dynamic_index_in_dim(counts, my_index, 1, keepdims=False)
    live_mask = (jnp.arange(capacity)[None, :] < own_count[:, None]).astype(jnp.float32)
    n_live = jnp.sum(counts, axis=-1).astype(jnp.float32)
    dpredicted = (
        2.0
        / math.sqrt(width)
        * live_mask[:, :, None, None]
        * (predicted - target_tiles)
        / n_live[:, None, None, None]
    )
    row_float = row_side.astype(jnp.float32)
    col_float = col_side.astype(jnp.float32)
    drow = jnp.einsum("mcij,mcjd->mcid", dpredicted, col_float, precision=lax.Precision.HIGHEST)
    dcol = jnp.einsum("mcij,mcid->mcjd", dpredicted, row_float, precision=lax.Precision.HIGHEST)
    dside = jnp.concatenate([drow, dcol], axis=1).astype(jnp.bfloat16)
    inverse = jnp.argsort(slot_index, axis=-1)
    outgoing_grads = take_rows(dside, inverse).reshape(members, seq_count, PER, TB, narrow)
    returned = lax.all_to_all(outgoing_grads, "seq", split_axis=1, concat_axis=1, tiled=True)
    selector = (
        picks.reshape(members, seq_count * PER)[:, :, None] == jnp.arange(per_block)[None, None, :]
    ).astype(jnp.bfloat16)
    dmixed = jnp.einsum(
        "mkn,mktd->mntd",
        selector,
        returned.reshape(members, seq_count * PER, TB, narrow),
        preferred_element_type=jnp.float32,
    ).reshape(members, length, narrow)
    dconv = (scaling[:, None, None] * dmixed).astype(jnp.bfloat16)
    weight_local = weight_term(padded, dconv, length, taps)
    return lax.psum_scatter(weight_local, ("seq", "dp"), scatter_dimension=2, tiled=True)


def axis_sum(value, axis):
    count = lax.axis_size(axis)
    total = value
    for shift in range(1, count):
        total = total + lax.ppermute(value, axis, [(i, (i + shift) % count) for i in range(count)])
    return total


def sparse_path(features, conv_weight, keep, tiles, counts, targets):
    _, length, width = features.shape
    taps, narrow, _ = conv_weight.shape
    halo = taps // 2
    span = TB + 2 * halo
    owners, capacity = tiles.shape[1], tiles.shape[2]
    n_sides = 2 * capacity
    per_block = length // TB
    seq_count = lax.axis_size("seq")
    groups = lax.axis_size("dp")
    peers = seq_count * groups
    held = owners * PER
    cols = width // peers
    my_index = lax.axis_index("seq")
    my_part = lax.axis_index("mp")

    tiles_all = lax.all_gather(tiles[0], "dp")
    counts_all = lax.all_gather(counts[0], "dp")
    keep_all = lax.all_gather(keep[0], "dp")
    targets_all = lax.all_gather(targets[0, 0], ("seq", "dp"))

    sides = jnp.concatenate([tiles_all[..., 0], tiles_all[..., 1]], axis=-1)
    source = sides // per_block
    local = sides % per_block
    before = jnp.arange(n_sides)[None, :] < jnp.arange(n_sides)[:, None]
    same_source = source[..., :, None] == source[..., None, :]
    rank = jnp.sum(jnp.logical_and(same_source, before), axis=-1)
    slot = (source * groups + jnp.arange(groups)[:, None, None]) * held + jnp.arange(owners)[None, :, None] * PER + rank

    mine = lax.dynamic_index_in_dim(jnp.stack([source, local, rank], 0), lax.axis_index("dp"), 1, keepdims=False)
    held_here = mine[0] == my_index
    picks = jnp.stack(
        [jnp.sum(jnp.where(jnp.logical_and(held_here, mine[2] == r), mine[1], 0), axis=-1) for r in range(PER)],
        axis=-1,
    ).reshape(held)

    padded = extended(features[0], (("seq", 0),), halo)
    rows = picks[:, None] * TB + jnp.arange(span)[None, :]
    windows = jnp.take(padded, rows, axis=0)
    x_float = windows.astype(jnp.float32)
    act = jax.nn.gelu(x_float).astype(jnp.bfloat16)
    conv_out = jnp.einsum("hti,oi->hto", act[:, 0:TB], conv_weight[0], preferred_element_type=jnp.float32)
    for offset in range(1, taps):
        conv_out = conv_out + jnp.einsum(
            "hti,oi->hto", act[:, offset : offset + TB], conv_weight[offset], preferred_element_type=jnp.float32
        )
    scaling = 1.25 * keep_all.astype(jnp.float32)
    my_scale = lax.dynamic_index_in_dim(scaling, lax.axis_index("dp"), 0, keepdims=False)
    x_part = lax.dynamic_slice_in_dim(x_float[:, halo : halo + TB], my_part * narrow, narrow, 2)
    mixed = (x_part + my_scale * conv_out).astype(jnp.bfloat16)

    act_cut = act.reshape(held, span, peers, cols).transpose(2, 0, 1, 3).reshape(peers, -1)
    mixed_rep = jnp.broadcast_to(mixed.reshape(1, -1), (peers, held * TB * narrow))
    outgoing = jnp.concatenate([mixed_rep, act_cut], axis=1)
    incoming = lax.all_to_all(outgoing, ("seq", "dp"), 0, 0, tiled=True)
    mixed_in = incoming[:, : held * TB * narrow].reshape(peers * held, TB, narrow)
    act_in = incoming[:, held * TB * narrow :].reshape(peers * held, span, cols)

    side_rows = jnp.take(mixed_in, slot, axis=0)
    row_side = side_rows[:, :, :capacity]
    col_side = side_rows[:, :, capacity:]
    partial_tiles = jnp.einsum("qocid,qocjd->qocij", row_side, col_side, preferred_element_type=jnp.float32)
    predicted = axis_sum(partial_tiles, "mp") / math.sqrt(width)
    target_tiles = targets_all.reshape(seq_count, groups, capacity, TB, TB).transpose(1, 0, 2, 3, 4)
    live_mask = (jnp.arange(capacity)[None, None, :] < counts_all[:, :, None]).astype(jnp.float32)
    n_live = jnp.sum(counts_all, axis=-1).astype(jnp.float32)
    dpredicted = (
        2.0
        / math.sqrt(width)
        * live_mask[..., None, None]
        * (predicted - target_tiles)
        / n_live[:, None, None, None, None]
    )
    row_float = row_side.astype(jnp.float32)
    col_float = col_side.astype(jnp.float32)
    drow = jnp.einsum("qocij,qocjd->qocid", dpredicted, col_float, precision=lax.Precision.HIGHEST)
    dcol = jnp.einsum("qocij,qocid->qocjd", dpredicted, row_float, precision=lax.Precision.HIGHEST)
    grads = jnp.concatenate([drow, dcol], axis=2).astype(jnp.bfloat16).astype(jnp.float32)
    grads = grads.reshape(groups, owners * n_sides, TB, narrow)
    flat_sides = sides.reshape(groups, owners * n_sides)
    same_block = flat_sides[:, :, None] == flat_sides[:, None, :]
    total = jnp.sum(jnp.where(same_block[..., None, None], grads[:, None], 0.0), axis=2)
    earlier = jnp.arange(owners * n_sides)[None, :] < jnp.arange(owners * n_sides)[:, None]
    first = jnp.logical_not(jnp.any(jnp.logical_and(same_block, earlier[None]), axis=-1))
    dconv = (scaling[:, None, None, None] * total).astype(jnp.bfloat16)
    dconv = jnp.where(first[..., None, None], dconv, jnp.zeros_like(dconv))
    act_sides = jnp.take(act_in, slot.reshape(groups, owners * n_sides), axis=0)
    return jnp.stack(
        [
            jnp.einsum(
                "qato,qati->oi",
                dconv,
                act_sides[:, :, offset : offset + TB],
                preferred_element_type=jnp.float32,
            )
            for offset in range(taps)
        ]
    )


def per_device(features, conv_weight, keep, tiles, counts, targets):
    members, length, _ = features.shape
    owners, capacity = tiles.shape[1], tiles.shape[2]
    fits = members == 1 and targets.shape[1] == 1 and 2 * owners * capacity * TB <= length
    if fits:
        return sparse_path(features, conv_weight, keep, tiles, counts, targets)
    return dense_path(features, conv_weight, keep, tiles, counts, targets)


def solution(mesh):
    placed = (
        P("dp", "seq", None),
        P(None, "mp", None),
        P("dp"),
        P("dp", None, None, None),
        P("dp", None),
        P("dp", "seq", None, None),
    )
    return jax.shard_map(
        per_device,
        mesh=mesh,
        in_specs=placed,
        out_specs=P(None, "mp", ("seq", "dp")),
        check_vma=False,
    )
```

```python
import math

import jax
import jax.numpy as jnp
from jax import lax
from jax.sharding import PartitionSpec as P

TB = 32
PER = 2


def extended(cells, sides, width):
    for axis, dim in sides:
        count = lax.axis_size(axis)
        ends = count - 1
        head = lax.slice_in_dim(cells, 0, width, axis=dim)
        tail = lax.slice_in_dim(cells, cells.shape[dim] - width, cells.shape[dim], axis=dim)
        cells = jnp.concatenate(
            [
                lax.ppermute(tail, axis, [(i, (i + 1) % count) for i in range(ends)]),
                cells,
                lax.ppermute(head, axis, [((i + 1) % count, i) for i in range(ends)]),
            ],
            axis=dim,
        )
    return cells


def take_rows(source_array, index_array):
    return jax.vmap(lambda table, picked: table[picked])(source_array, index_array)


def conv_apply(padded, weight, length):
    total = jnp.einsum(
        "mbi,oi->mbo", padded[:, 0:length], weight[0], preferred_element_type=jnp.float32
    )
    for offset in range(1, weight.shape[0]):
        total = total + jnp.einsum(
            "mbi,oi->mbo",
            padded[:, offset : offset + length],
            weight[offset],
            preferred_element_type=jnp.float32,
        )
    return total


def weight_term(padded, dconv, length, taps):
    return jnp.stack(
        [
            jnp.einsum(
                "mbi,mbo->oi",
                padded[:, offset : offset + length],
                dconv,
                preferred_element_type=jnp.float32,
            )
            for offset in range(taps)
        ]
    )


def dense_path(features, conv_weight, keep, tiles, counts, targets):
    members, length, width = features.shape
    taps = conv_weight.shape[0]
    narrow = conv_weight.shape[1]
    seq_count = lax.axis_size("seq")
    my_index = lax.axis_index("seq")
    my_part = lax.axis_index("mp")
    x_float = features.astype(jnp.float32)
    activations = jax.nn.gelu(x_float).astype(jnp.bfloat16)
    padded = extended(activations, (("seq", 1),), 2)
    scaling = 1.25 * keep.astype(jnp.float32)
    conv_out = conv_apply(padded, conv_weight, length)
    x_local = lax.dynamic_slice_in_dim(x_float, my_part * narrow, narrow, 2)
    mixed_out = (x_local + scaling[:, None, None] * conv_out).astype(jnp.bfloat16)
    capacity = tiles.shape[2]
    n_sides = 2 * capacity
    per_block = length // TB
    sides = jnp.concatenate([tiles[..., 0], tiles[..., 1]], axis=-1)
    side_source = sides // per_block
    side_local = sides % per_block
    own_sides = lax.dynamic_index_in_dim(sides, my_index, 1, keepdims=False)
    own_source = own_sides // per_block
    before = jnp.arange(n_sides)[None, :] < jnp.arange(n_sides)[:, None]
    same_source = own_source[:, :, None] == own_source[:, None, :]
    rank_within = jnp.sum(jnp.logical_and(same_source, before[None]), axis=-1)
    slot_index = own_source * PER + rank_within
    held_here = side_source == my_index
    held_order = jnp.cumsum(held_here.astype(jnp.int32), axis=-1) - 1
    picks = jnp.stack(
        [
            jnp.sum(
                jnp.where(jnp.logical_and(held_here, held_order == position), side_local, 0),
                axis=-1,
            )
            for position in range(PER)
        ],
        axis=-1,
    )
    blocks = mixed_out.reshape(members, per_block, TB, narrow)
    whole = lax.all_gather(blocks, "seq", axis=1, tiled=True)
    side_rows = take_rows(whole, own_sides)
    row_side = side_rows[:, :capacity]
    col_side = side_rows[:, capacity:]
    partial_tiles = jnp.einsum(
        "mcid,mcjd->mcij", row_side, col_side, preferred_element_type=jnp.float32
    )
    predicted = lax.psum(partial_tiles, "mp") / math.sqrt(width)
    target_tiles = targets[:, 0].reshape(members, capacity, TB, TB)
    own_count = lax.dynamic_index_in_dim(counts, my_index, 1, keepdims=False)
    live_mask = (jnp.arange(capacity)[None, :] < own_count[:, None]).astype(jnp.float32)
    n_live = jnp.sum(counts, axis=-1).astype(jnp.float32)
    dpredicted = (
        2.0
        / math.sqrt(width)
        * live_mask[:, :, None, None]
        * (predicted - target_tiles)
        / n_live[:, None, None, None]
    )
    row_float = row_side.astype(jnp.float32)
    col_float = col_side.astype(jnp.float32)
    drow = jnp.einsum("mcij,mcjd->mcid", dpredicted, col_float, precision=lax.Precision.HIGHEST)
    dcol = jnp.einsum("mcij,mcid->mcjd", dpredicted, row_float, precision=lax.Precision.HIGHEST)
    dside = jnp.concatenate([drow, dcol], axis=1).astype(jnp.bfloat16)
    inverse = jnp.argsort(slot_index, axis=-1)
    outgoing_grads = take_rows(dside, inverse).reshape(members, seq_count, PER, TB, narrow)
    returned = lax.all_to_all(outgoing_grads, "seq", split_axis=1, concat_axis=1, tiled=True)
    selector = (
        picks.reshape(members, seq_count * PER)[:, :, None] == jnp.arange(per_block)[None, None, :]
    ).astype(jnp.bfloat16)
    dmixed = jnp.einsum(
        "mkn,mktd->mntd",
        selector,
        returned.reshape(members, seq_count * PER, TB, narrow),
        preferred_element_type=jnp.float32,
    ).reshape(members, length, narrow)
    dconv = (scaling[:, None, None] * dmixed).astype(jnp.bfloat16)
    weight_local = weight_term(padded, dconv, length, taps)
    return lax.psum_scatter(weight_local, ("seq", "dp"), scatter_dimension=2, tiled=True)


def axis_sum(value, axis):
    count = lax.axis_size(axis)
    total = value
    for shift in range(1, count):
        total = total + lax.ppermute(value, axis, [(i, (i + shift) % count) for i in range(count)])
    return total


def sparse_path(features, conv_weight, keep, tiles, counts, targets):
    _, length, width = features.shape
    taps, narrow, _ = conv_weight.shape
    halo = taps // 2
    span = TB + 2 * halo
    owners, capacity = tiles.shape[1], tiles.shape[2]
    n_sides = 2 * capacity
    per_block = length // TB
    seq_count = lax.axis_size("seq")
    groups = lax.axis_size("dp")
    peers = seq_count * groups
    held = owners * PER
    cols = width // peers
    my_index = lax.axis_index("seq")
    my_part = lax.axis_index("mp")

    small = jnp.concatenate([tiles.reshape(-1), counts.reshape(-1), keep.reshape(-1)]).astype(jnp.float32)
    bundle = jnp.concatenate([targets.reshape(-1), small])
    gathered = lax.all_gather(bundle, ("seq", "dp")).reshape(seq_count, groups, -1)
    n_targets = capacity * TB * TB
    n_tiles = owners * capacity * 2
    meta = gathered[0, :, n_targets:].astype(jnp.int32)
    tiles_all = meta[:, :n_tiles].reshape(groups, owners, capacity, 2)
    counts_all = meta[:, n_tiles : n_tiles + owners]
    keep_all = meta[:, n_tiles + owners]
    targets_all = gathered[:, :, :n_targets]

    sides = jnp.concatenate([tiles_all[..., 0], tiles_all[..., 1]], axis=-1)
    source = sides // per_block
    local = sides % per_block
    before = jnp.arange(n_sides)[None, :] < jnp.arange(n_sides)[:, None]
    same_source = source[..., :, None] == source[..., None, :]
    rank = jnp.sum(jnp.logical_and(same_source, before), axis=-1)
    slot = (source * groups + jnp.arange(groups)[:, None, None]) * held + jnp.arange(owners)[None, :, None] * PER + rank

    mine = lax.dynamic_index_in_dim(jnp.stack([source, local, rank], 0), lax.axis_index("dp"), 1, keepdims=False)
    held_here = mine[0] == my_index
    picks = jnp.stack(
        [jnp.sum(jnp.where(jnp.logical_and(held_here, mine[2] == r), mine[1], 0), axis=-1) for r in range(PER)],
        axis=-1,
    ).reshape(held)

    cells = features[0]
    ends = seq_count - 1
    head = lax.ppermute(cells[length - halo :], "seq", [(i, i + 1) for i in range(ends)])
    tail = lax.ppermute(cells[:halo], "seq", [(i + 1, i) for i in range(ends)])
    rows = picks[:, None] * TB - halo + jnp.arange(span)[None, :]
    inside = jnp.take(cells, jnp.clip(rows, 0, length - 1), axis=0)
    edge_rows = jnp.concatenate([head, tail], axis=0)
    edge_index = jnp.where(rows < 0, rows + halo, rows - length + halo)
    outside = jnp.take(edge_rows, jnp.clip(edge_index, 0, 2 * halo - 1), axis=0)
    in_range = jnp.logical_and(rows >= 0, rows < length)
    windows = jnp.where(in_range[..., None], inside, outside)
    x_float = windows.astype(jnp.float32)
    act = jax.nn.gelu(x_float).astype(jnp.bfloat16)
    conv_out = jnp.einsum("hti,oi->hto", act[:, 0:TB], conv_weight[0], preferred_element_type=jnp.float32)
    for offset in range(1, taps):
        conv_out = conv_out + jnp.einsum(
            "hti,oi->hto", act[:, offset : offset + TB], conv_weight[offset], preferred_element_type=jnp.float32
        )
    scaling = 1.25 * keep_all.astype(jnp.float32)
    my_scale = lax.dynamic_index_in_dim(scaling, lax.axis_index("dp"), 0, keepdims=False)
    x_part = lax.dynamic_slice_in_dim(x_float[:, halo : halo + TB], my_part * narrow, narrow, 2)
    mixed = (x_part + my_scale * conv_out).astype(jnp.bfloat16)

    act_cut = act.reshape(held, span, peers, cols).transpose(2, 0, 1, 3).reshape(peers, -1)
    mixed_rep = jnp.broadcast_to(mixed.reshape(1, -1), (peers, held * TB * narrow))
    outgoing = jnp.concatenate([mixed_rep, act_cut], axis=1)
    incoming = lax.all_to_all(outgoing, ("seq", "dp"), 0, 0, tiled=True)
    mixed_in = incoming[:, : held * TB * narrow].reshape(peers * held, TB, narrow)
    act_in = incoming[:, held * TB * narrow :].reshape(peers * held, span, cols)

    side_rows = jnp.take(mixed_in, slot, axis=0)
    row_side = side_rows[:, :, :capacity]
    col_side = side_rows[:, :, capacity:]
    partial_tiles = jnp.einsum("qocid,qocjd->qocij", row_side, col_side, preferred_element_type=jnp.float32)
    predicted = axis_sum(partial_tiles, "mp") / math.sqrt(width)
    target_tiles = targets_all.reshape(seq_count, groups, capacity, TB, TB).transpose(1, 0, 2, 3, 4)
    live_mask = (jnp.arange(capacity)[None, None, :] < counts_all[:, :, None]).astype(jnp.float32)
    n_live = jnp.sum(counts_all, axis=-1).astype(jnp.float32)
    dpredicted = (
        2.0
        / math.sqrt(width)
        * live_mask[..., None, None]
        * (predicted - target_tiles)
        / n_live[:, None, None, None, None]
    )
    row_float = row_side.astype(jnp.float32)
    col_float = col_side.astype(jnp.float32)
    drow = jnp.einsum("qocij,qocjd->qocid", dpredicted, col_float, precision=lax.Precision.HIGHEST)
    dcol = jnp.einsum("qocij,qocid->qocjd", dpredicted, row_float, precision=lax.Precision.HIGHEST)
    grads = jnp.concatenate([drow, dcol], axis=2).astype(jnp.bfloat16).astype(jnp.float32)
    grads = grads.reshape(groups, owners * n_sides, TB, narrow)
    flat_sides = sides.reshape(groups, owners * n_sides)
    same_block = flat_sides[:, :, None] == flat_sides[:, None, :]
    total = jnp.sum(jnp.where(same_block[..., None, None], grads[:, None], 0.0), axis=2)
    earlier = jnp.arange(owners * n_sides)[None, :] < jnp.arange(owners * n_sides)[:, None]
    first = jnp.logical_not(jnp.any(jnp.logical_and(same_block, earlier[None]), axis=-1))
    dconv = (scaling[:, None, None, None] * total).astype(jnp.bfloat16)
    dconv = jnp.where(first[..., None, None], dconv, jnp.zeros_like(dconv))
    act_sides = jnp.take(act_in, slot.reshape(groups, owners * n_sides), axis=0)
    return jnp.stack(
        [
            jnp.einsum(
                "qato,qati->oi",
                dconv,
                act_sides[:, :, offset : offset + TB],
                preferred_element_type=jnp.float32,
            )
            for offset in range(taps)
        ]
    )


def per_device(features, conv_weight, keep, tiles, counts, targets):
    members, length, _ = features.shape
    owners, capacity = tiles.shape[1], tiles.shape[2]
    fits = members == 1 and targets.shape[1] == 1 and 2 * owners * capacity * TB <= length
    if fits:
        return sparse_path(features, conv_weight, keep, tiles, counts, targets)
    return dense_path(features, conv_weight, keep, tiles, counts, targets)


def solution(mesh):
    placed = (
        P("dp", "seq", None),
        P(None, "mp", None),
        P("dp"),
        P("dp", None, None, None),
        P("dp", None),
        P("dp", "seq", None, None),
    )
    return jax.shard_map(
        per_device,
        mesh=mesh,
        in_specs=placed,
        out_specs=P(None, "mp", ("seq", "dp")),
        check_vma=False,
    )
```

```python
import math

import jax
import jax.numpy as jnp
from jax import lax
from jax.sharding import PartitionSpec as P

TB = 32
PER = 2


def extended(cells, sides, width):
    for axis, dim in sides:
        count = lax.axis_size(axis)
        ends = count - 1
        head = lax.slice_in_dim(cells, 0, width, axis=dim)
        tail = lax.slice_in_dim(cells, cells.shape[dim] - width, cells.shape[dim], axis=dim)
        cells = jnp.concatenate(
            [
                lax.ppermute(tail, axis, [(i, (i + 1) % count) for i in range(ends)]),
                cells,
                lax.ppermute(head, axis, [((i + 1) % count, i) for i in range(ends)]),
            ],
            axis=dim,
        )
    return cells


def take_rows(source_array, index_array):
    return jax.vmap(lambda table, picked: table[picked])(source_array, index_array)


def conv_apply(padded, weight, length):
    total = jnp.einsum(
        "mbi,oi->mbo", padded[:, 0:length], weight[0], preferred_element_type=jnp.float32
    )
    for offset in range(1, weight.shape[0]):
        total = total + jnp.einsum(
            "mbi,oi->mbo",
            padded[:, offset : offset + length],
            weight[offset],
            preferred_element_type=jnp.float32,
        )
    return total


def weight_term(padded, dconv, length, taps):
    return jnp.stack(
        [
            jnp.einsum(
                "mbi,mbo->oi",
                padded[:, offset : offset + length],
                dconv,
                preferred_element_type=jnp.float32,
            )
            for offset in range(taps)
        ]
    )


def dense_path(features, conv_weight, keep, tiles, counts, targets):
    members, length, width = features.shape
    taps = conv_weight.shape[0]
    narrow = conv_weight.shape[1]
    seq_count = lax.axis_size("seq")
    my_index = lax.axis_index("seq")
    my_part = lax.axis_index("mp")
    x_float = features.astype(jnp.float32)
    activations = jax.nn.gelu(x_float).astype(jnp.bfloat16)
    padded = extended(activations, (("seq", 1),), 2)
    scaling = 1.25 * keep.astype(jnp.float32)
    conv_out = conv_apply(padded, conv_weight, length)
    x_local = lax.dynamic_slice_in_dim(x_float, my_part * narrow, narrow, 2)
    mixed_out = (x_local + scaling[:, None, None] * conv_out).astype(jnp.bfloat16)
    capacity = tiles.shape[2]
    n_sides = 2 * capacity
    per_block = length // TB
    sides = jnp.concatenate([tiles[..., 0], tiles[..., 1]], axis=-1)
    side_source = sides // per_block
    side_local = sides % per_block
    own_sides = lax.dynamic_index_in_dim(sides, my_index, 1, keepdims=False)
    own_source = own_sides // per_block
    before = jnp.arange(n_sides)[None, :] < jnp.arange(n_sides)[:, None]
    same_source = own_source[:, :, None] == own_source[:, None, :]
    rank_within = jnp.sum(jnp.logical_and(same_source, before[None]), axis=-1)
    slot_index = own_source * PER + rank_within
    held_here = side_source == my_index
    held_order = jnp.cumsum(held_here.astype(jnp.int32), axis=-1) - 1
    picks = jnp.stack(
        [
            jnp.sum(
                jnp.where(jnp.logical_and(held_here, held_order == position), side_local, 0),
                axis=-1,
            )
            for position in range(PER)
        ],
        axis=-1,
    )
    blocks = mixed_out.reshape(members, per_block, TB, narrow)
    whole = lax.all_gather(blocks, "seq", axis=1, tiled=True)
    side_rows = take_rows(whole, own_sides)
    row_side = side_rows[:, :capacity]
    col_side = side_rows[:, capacity:]
    partial_tiles = jnp.einsum(
        "mcid,mcjd->mcij", row_side, col_side, preferred_element_type=jnp.float32
    )
    predicted = lax.psum(partial_tiles, "mp") / math.sqrt(width)
    target_tiles = targets[:, 0].reshape(members, capacity, TB, TB)
    own_count = lax.dynamic_index_in_dim(counts, my_index, 1, keepdims=False)
    live_mask = (jnp.arange(capacity)[None, :] < own_count[:, None]).astype(jnp.float32)
    n_live = jnp.sum(counts, axis=-1).astype(jnp.float32)
    dpredicted = (
        2.0
        / math.sqrt(width)
        * live_mask[:, :, None, None]
        * (predicted - target_tiles)
        / n_live[:, None, None, None]
    )
    row_float = row_side.astype(jnp.float32)
    col_float = col_side.astype(jnp.float32)
    drow = jnp.einsum("mcij,mcjd->mcid", dpredicted, col_float, precision=lax.Precision.HIGHEST)
    dcol = jnp.einsum("mcij,mcid->mcjd", dpredicted, row_float, precision=lax.Precision.HIGHEST)
    dside = jnp.concatenate([drow, dcol], axis=1).astype(jnp.bfloat16)
    inverse = jnp.argsort(slot_index, axis=-1)
    outgoing_grads = take_rows(dside, inverse).reshape(members, seq_count, PER, TB, narrow)
    returned = lax.all_to_all(outgoing_grads, "seq", split_axis=1, concat_axis=1, tiled=True)
    selector = (
        picks.reshape(members, seq_count * PER)[:, :, None] == jnp.arange(per_block)[None, None, :]
    ).astype(jnp.bfloat16)
    dmixed = jnp.einsum(
        "mkn,mktd->mntd",
        selector,
        returned.reshape(members, seq_count * PER, TB, narrow),
        preferred_element_type=jnp.float32,
    ).reshape(members, length, narrow)
    dconv = (scaling[:, None, None] * dmixed).astype(jnp.bfloat16)
    weight_local = weight_term(padded, dconv, length, taps)
    return lax.psum_scatter(weight_local, ("seq", "dp"), scatter_dimension=2, tiled=True)


def axis_sum(value, axis):
    count = lax.axis_size(axis)
    total = value
    for shift in range(1, count):
        total = total + lax.ppermute(value, axis, [(i, (i + shift) % count) for i in range(count)])
    return total


def sparse_path(features, conv_weight, keep, tiles, counts, targets):
    _, length, width = features.shape
    taps, narrow, _ = conv_weight.shape
    halo = taps // 2
    span = TB + 2 * halo
    owners, capacity = tiles.shape[1], tiles.shape[2]
    n_sides = 2 * capacity
    per_block = length // TB
    seq_count = lax.axis_size("seq")
    groups = lax.axis_size("dp")
    peers = seq_count * groups
    held = owners * PER
    cols = width // peers
    my_index = lax.axis_index("seq")
    my_part = lax.axis_index("mp")

    small = jnp.concatenate([tiles.reshape(-1), counts.reshape(-1), keep.reshape(-1)]).astype(jnp.float32)
    bundle = jnp.concatenate([targets.reshape(-1), small])
    lanes = 128
    padding = -bundle.shape[0] % lanes
    bundle = jnp.pad(bundle, (0, padding)).reshape(-1, lanes)
    gathered = lax.all_gather(bundle, ("seq", "dp"), tiled=True).reshape(seq_count, groups, -1)
    n_targets = capacity * TB * TB
    n_tiles = owners * capacity * 2
    meta = gathered[0, :, n_targets:].astype(jnp.int32)
    tiles_all = meta[:, :n_tiles].reshape(groups, owners, capacity, 2)
    counts_all = meta[:, n_tiles : n_tiles + owners]
    keep_all = meta[:, n_tiles + owners]
    targets_all = gathered[:, :, :n_targets]

    sides = jnp.concatenate([tiles_all[..., 0], tiles_all[..., 1]], axis=-1)
    source = sides // per_block
    local = sides % per_block
    before = jnp.arange(n_sides)[None, :] < jnp.arange(n_sides)[:, None]
    same_source = source[..., :, None] == source[..., None, :]
    rank = jnp.sum(jnp.logical_and(same_source, before), axis=-1)
    slot = (source * groups + jnp.arange(groups)[:, None, None]) * held + jnp.arange(owners)[None, :, None] * PER + rank

    mine = lax.dynamic_index_in_dim(jnp.stack([source, local, rank], 0), lax.axis_index("dp"), 1, keepdims=False)
    held_here = mine[0] == my_index
    picks = jnp.stack(
        [jnp.sum(jnp.where(jnp.logical_and(held_here, mine[2] == r), mine[1], 0), axis=-1) for r in range(PER)],
        axis=-1,
    ).reshape(held)

    cells = features[0]
    ends = seq_count - 1
    head = lax.ppermute(cells[length - halo :], "seq", [(i, i + 1) for i in range(ends)])
    tail = lax.ppermute(cells[:halo], "seq", [(i + 1, i) for i in range(ends)])
    rows = picks[:, None] * TB - halo + jnp.arange(span)[None, :]
    inside = jnp.take(cells, jnp.clip(rows, 0, length - 1), axis=0)
    edge_rows = jnp.concatenate([head, tail], axis=0)
    edge_index = jnp.where(rows < 0, rows + halo, rows - length + halo)
    outside = jnp.take(edge_rows, jnp.clip(edge_index, 0, 2 * halo - 1), axis=0)
    in_range = jnp.logical_and(rows >= 0, rows < length)
    windows = jnp.where(in_range[..., None], inside, outside)
    x_float = windows.astype(jnp.float32)
    act = jax.nn.gelu(x_float).astype(jnp.bfloat16)
    conv_out = jnp.einsum("hti,oi->hto", act[:, 0:TB], conv_weight[0], preferred_element_type=jnp.float32)
    for offset in range(1, taps):
        conv_out = conv_out + jnp.einsum(
            "hti,oi->hto", act[:, offset : offset + TB], conv_weight[offset], preferred_element_type=jnp.float32
        )
    scaling = 1.25 * keep_all.astype(jnp.float32)
    my_scale = lax.dynamic_index_in_dim(scaling, lax.axis_index("dp"), 0, keepdims=False)
    x_part = lax.dynamic_slice_in_dim(x_float[:, halo : halo + TB], my_part * narrow, narrow, 2)
    mixed = (x_part + my_scale * conv_out).astype(jnp.bfloat16)

    act_cut = act.reshape(held, span, peers, cols).transpose(2, 0, 1, 3).reshape(peers, -1)
    mixed_rep = jnp.broadcast_to(mixed.reshape(1, -1), (peers, held * TB * narrow))
    outgoing = jnp.concatenate([mixed_rep, act_cut], axis=1)
    incoming = lax.all_to_all(outgoing, ("seq", "dp"), 0, 0, tiled=True)
    mixed_in = incoming[:, : held * TB * narrow].reshape(peers * held, TB, narrow)
    act_in = incoming[:, held * TB * narrow :].reshape(peers * held, span, cols)

    side_rows = jnp.take(mixed_in, slot, axis=0)
    row_side = side_rows[:, :, :capacity]
    col_side = side_rows[:, :, capacity:]
    partial_tiles = jnp.einsum("qocid,qocjd->qocij", row_side, col_side, preferred_element_type=jnp.float32)
    predicted = axis_sum(partial_tiles, "mp") / math.sqrt(width)
    target_tiles = targets_all.reshape(seq_count, groups, capacity, TB, TB).transpose(1, 0, 2, 3, 4)
    live_mask = (jnp.arange(capacity)[None, None, :] < counts_all[:, :, None]).astype(jnp.float32)
    n_live = jnp.sum(counts_all, axis=-1).astype(jnp.float32)
    dpredicted = (
        2.0
        / math.sqrt(width)
        * live_mask[..., None, None]
        * (predicted - target_tiles)
        / n_live[:, None, None, None, None]
    )
    row_float = row_side.astype(jnp.float32)
    col_float = col_side.astype(jnp.float32)
    drow = jnp.einsum("qocij,qocjd->qocid", dpredicted, col_float, precision=lax.Precision.HIGHEST)
    dcol = jnp.einsum("qocij,qocid->qocjd", dpredicted, row_float, precision=lax.Precision.HIGHEST)
    grads = jnp.concatenate([drow, dcol], axis=2).astype(jnp.bfloat16).astype(jnp.float32)
    grads = grads.reshape(groups, owners * n_sides, TB, narrow)
    flat_sides = sides.reshape(groups, owners * n_sides)
    same_block = flat_sides[:, :, None] == flat_sides[:, None, :]
    total = jnp.sum(jnp.where(same_block[..., None, None], grads[:, None], 0.0), axis=2)
    earlier = jnp.arange(owners * n_sides)[None, :] < jnp.arange(owners * n_sides)[:, None]
    first = jnp.logical_not(jnp.any(jnp.logical_and(same_block, earlier[None]), axis=-1))
    dconv = (scaling[:, None, None, None] * total).astype(jnp.bfloat16)
    dconv = jnp.where(first[..., None, None], dconv, jnp.zeros_like(dconv))
    act_sides = jnp.take(act_in, slot.reshape(groups, owners * n_sides), axis=0)
    return jnp.stack(
        [
            jnp.einsum(
                "qato,qati->oi",
                dconv,
                act_sides[:, :, offset : offset + TB],
                preferred_element_type=jnp.float32,
            )
            for offset in range(taps)
        ]
    )


def per_device(features, conv_weight, keep, tiles, counts, targets):
    members, length, _ = features.shape
    owners, capacity = tiles.shape[1], tiles.shape[2]
    fits = members == 1 and targets.shape[1] == 1 and 2 * owners * capacity * TB <= length
    if fits:
        return sparse_path(features, conv_weight, keep, tiles, counts, targets)
    return dense_path(features, conv_weight, keep, tiles, counts, targets)


def solution(mesh):
    placed = (
        P("dp", "seq", None),
        P(None, "mp", None),
        P("dp"),
        P("dp", None, None, None),
        P("dp", None),
        P("dp", "seq", None, None),
    )
    return jax.shard_map(
        per_device,
        mesh=mesh,
        in_specs=placed,
        out_specs=P(None, "mp", ("seq", "dp")),
        check_vma=False,
    )
```

```python
import math

import jax
import jax.numpy as jnp
from jax import lax
from jax.sharding import PartitionSpec as P

TB = 32
PER = 2


def extended(cells, sides, width):
    for axis, dim in sides:
        count = lax.axis_size(axis)
        ends = count - 1
        head = lax.slice_in_dim(cells, 0, width, axis=dim)
        tail = lax.slice_in_dim(cells, cells.shape[dim] - width, cells.shape[dim], axis=dim)
        cells = jnp.concatenate(
            [
                lax.ppermute(tail, axis, [(i, (i + 1) % count) for i in range(ends)]),
                cells,
                lax.ppermute(head, axis, [((i + 1) % count, i) for i in range(ends)]),
            ],
            axis=dim,
        )
    return cells


def take_rows(source_array, index_array):
    return jax.vmap(lambda table, picked: table[picked])(source_array, index_array)


def conv_apply(padded, weight, length):
    total = jnp.einsum(
        "mbi,oi->mbo", padded[:, 0:length], weight[0], preferred_element_type=jnp.float32
    )
    for offset in range(1, weight.shape[0]):
        total = total + jnp.einsum(
            "mbi,oi->mbo",
            padded[:, offset : offset + length],
            weight[offset],
            preferred_element_type=jnp.float32,
        )
    return total


def weight_term(padded, dconv, length, taps):
    return jnp.stack(
        [
            jnp.einsum(
                "mbi,mbo->oi",
                padded[:, offset : offset + length],
                dconv,
                preferred_element_type=jnp.float32,
            )
            for offset in range(taps)
        ]
    )


def dense_path(features, conv_weight, keep, tiles, counts, targets):
    members, length, width = features.shape
    taps = conv_weight.shape[0]
    narrow = conv_weight.shape[1]
    seq_count = lax.axis_size("seq")
    my_index = lax.axis_index("seq")
    my_part = lax.axis_index("mp")
    x_float = features.astype(jnp.float32)
    activations = jax.nn.gelu(x_float).astype(jnp.bfloat16)
    padded = extended(activations, (("seq", 1),), 2)
    scaling = 1.25 * keep.astype(jnp.float32)
    conv_out = conv_apply(padded, conv_weight, length)
    x_local = lax.dynamic_slice_in_dim(x_float, my_part * narrow, narrow, 2)
    mixed_out = (x_local + scaling[:, None, None] * conv_out).astype(jnp.bfloat16)
    capacity = tiles.shape[2]
    n_sides = 2 * capacity
    per_block = length // TB
    sides = jnp.concatenate([tiles[..., 0], tiles[..., 1]], axis=-1)
    side_source = sides // per_block
    side_local = sides % per_block
    own_sides = lax.dynamic_index_in_dim(sides, my_index, 1, keepdims=False)
    own_source = own_sides // per_block
    before = jnp.arange(n_sides)[None, :] < jnp.arange(n_sides)[:, None]
    same_source = own_source[:, :, None] == own_source[:, None, :]
    rank_within = jnp.sum(jnp.logical_and(same_source, before[None]), axis=-1)
    slot_index = own_source * PER + rank_within
    held_here = side_source == my_index
    held_order = jnp.cumsum(held_here.astype(jnp.int32), axis=-1) - 1
    picks = jnp.stack(
        [
            jnp.sum(
                jnp.where(jnp.logical_and(held_here, held_order == position), side_local, 0),
                axis=-1,
            )
            for position in range(PER)
        ],
        axis=-1,
    )
    blocks = mixed_out.reshape(members, per_block, TB, narrow)
    whole = lax.all_gather(blocks, "seq", axis=1, tiled=True)
    side_rows = take_rows(whole, own_sides)
    row_side = side_rows[:, :capacity]
    col_side = side_rows[:, capacity:]
    partial_tiles = jnp.einsum(
        "mcid,mcjd->mcij", row_side, col_side, preferred_element_type=jnp.float32
    )
    predicted = lax.psum(partial_tiles, "mp") / math.sqrt(width)
    target_tiles = targets[:, 0].reshape(members, capacity, TB, TB)
    own_count = lax.dynamic_index_in_dim(counts, my_index, 1, keepdims=False)
    live_mask = (jnp.arange(capacity)[None, :] < own_count[:, None]).astype(jnp.float32)
    n_live = jnp.sum(counts, axis=-1).astype(jnp.float32)
    dpredicted = (
        2.0
        / math.sqrt(width)
        * live_mask[:, :, None, None]
        * (predicted - target_tiles)
        / n_live[:, None, None, None]
    )
    row_float = row_side.astype(jnp.float32)
    col_float = col_side.astype(jnp.float32)
    drow = jnp.einsum("mcij,mcjd->mcid", dpredicted, col_float, precision=lax.Precision.HIGHEST)
    dcol = jnp.einsum("mcij,mcid->mcjd", dpredicted, row_float, precision=lax.Precision.HIGHEST)
    dside = jnp.concatenate([drow, dcol], axis=1).astype(jnp.bfloat16)
    inverse = jnp.argsort(slot_index, axis=-1)
    outgoing_grads = take_rows(dside, inverse).reshape(members, seq_count, PER, TB, narrow)
    returned = lax.all_to_all(outgoing_grads, "seq", split_axis=1, concat_axis=1, tiled=True)
    selector = (
        picks.reshape(members, seq_count * PER)[:, :, None] == jnp.arange(per_block)[None, None, :]
    ).astype(jnp.bfloat16)
    dmixed = jnp.einsum(
        "mkn,mktd->mntd",
        selector,
        returned.reshape(members, seq_count * PER, TB, narrow),
        preferred_element_type=jnp.float32,
    ).reshape(members, length, narrow)
    dconv = (scaling[:, None, None] * dmixed).astype(jnp.bfloat16)
    weight_local = weight_term(padded, dconv, length, taps)
    return lax.psum_scatter(weight_local, ("seq", "dp"), scatter_dimension=2, tiled=True)


def axis_sum(value, axis):
    count = lax.axis_size(axis)
    total = value
    for shift in range(1, count):
        total = total + lax.ppermute(value, axis, [(i, (i + shift) % count) for i in range(count)])
    return total


def sparse_path(features, conv_weight, keep, tiles, counts, targets):
    _, length, width = features.shape
    taps, narrow, _ = conv_weight.shape
    halo = taps // 2
    span = TB + 2 * halo
    owners, capacity = tiles.shape[1], tiles.shape[2]
    n_sides = 2 * capacity
    per_block = length // TB
    seq_count = lax.axis_size("seq")
    groups = lax.axis_size("dp")
    peers = seq_count * groups
    held = owners * PER
    cols = width // peers
    my_index = lax.axis_index("seq")
    my_part = lax.axis_index("mp")

    small = jnp.concatenate([tiles.reshape(-1), counts.reshape(-1), keep.reshape(-1)]).astype(jnp.float32)
    bundle = jnp.concatenate([targets.reshape(-1), small])
    lanes = 128
    padding = -bundle.shape[0] % lanes
    bundle = jnp.pad(bundle, (0, padding)).reshape(-1, lanes)
    gathered = lax.all_gather(bundle, ("seq", "dp"), tiled=True).reshape(seq_count, groups, -1)
    n_targets = capacity * TB * TB
    n_tiles = owners * capacity * 2
    meta = gathered[0, :, n_targets:].astype(jnp.int32)
    tiles_all = meta[:, :n_tiles].reshape(groups, owners, capacity, 2)
    counts_all = meta[:, n_tiles : n_tiles + owners]
    keep_all = meta[:, n_tiles + owners]
    targets_all = gathered[:, :, :n_targets]

    sides = jnp.concatenate([tiles_all[..., 0], tiles_all[..., 1]], axis=-1)
    source = sides // per_block
    local = sides % per_block
    before = jnp.arange(n_sides)[None, :] < jnp.arange(n_sides)[:, None]
    same_source = source[..., :, None] == source[..., None, :]
    rank = jnp.sum(jnp.logical_and(same_source, before), axis=-1)
    slot = (source * groups + jnp.arange(groups)[:, None, None]) * held + jnp.arange(owners)[None, :, None] * PER + rank

    own_sides = jnp.concatenate([tiles[0, ..., 0], tiles[0, ..., 1]], axis=-1)
    own_source = own_sides // per_block
    own_same = own_source[:, :, None] == own_source[:, None, :]
    own_rank = jnp.sum(jnp.logical_and(own_same, before), axis=-1)
    held_here = own_source == my_index
    picks = jnp.stack(
        [
            jnp.sum(jnp.where(jnp.logical_and(held_here, own_rank == r), own_sides % per_block, 0), axis=-1)
            for r in range(PER)
        ],
        axis=-1,
    ).reshape(held)

    cells = features[0]
    ends = seq_count - 1
    head = lax.ppermute(cells[length - halo :], "seq", [(i, i + 1) for i in range(ends)])
    tail = lax.ppermute(cells[:halo], "seq", [(i + 1, i) for i in range(ends)])
    rows = picks[:, None] * TB - halo + jnp.arange(span)[None, :]
    inside = jnp.take(cells, jnp.clip(rows, 0, length - 1), axis=0)
    edge_rows = jnp.concatenate([head, tail], axis=0)
    edge_index = jnp.where(rows < 0, rows + halo, rows - length + halo)
    outside = jnp.take(edge_rows, jnp.clip(edge_index, 0, 2 * halo - 1), axis=0)
    in_range = jnp.logical_and(rows >= 0, rows < length)
    windows = jnp.where(in_range[..., None], inside, outside)
    x_float = windows.astype(jnp.float32)
    act = jax.nn.gelu(x_float).astype(jnp.bfloat16)
    conv_out = jnp.einsum("hti,oi->hto", act[:, 0:TB], conv_weight[0], preferred_element_type=jnp.float32)
    for offset in range(1, taps):
        conv_out = conv_out + jnp.einsum(
            "hti,oi->hto", act[:, offset : offset + TB], conv_weight[offset], preferred_element_type=jnp.float32
        )
    scaling = 1.25 * keep_all.astype(jnp.float32)
    my_scale = 1.25 * keep[0].astype(jnp.float32)
    x_part = lax.dynamic_slice_in_dim(x_float[:, halo : halo + TB], my_part * narrow, narrow, 2)
    mixed = (x_part + my_scale * conv_out).astype(jnp.bfloat16)

    act_cut = act.reshape(held, span, peers, cols).transpose(2, 0, 1, 3).reshape(peers, -1)
    mixed_rep = jnp.broadcast_to(mixed.reshape(1, -1), (peers, held * TB * narrow))
    outgoing = jnp.concatenate([mixed_rep, act_cut], axis=1)
    incoming = lax.all_to_all(outgoing, ("seq", "dp"), 0, 0, tiled=True)
    mixed_in = incoming[:, : held * TB * narrow].reshape(peers * held, TB, narrow)
    act_in = incoming[:, held * TB * narrow :].reshape(peers * held, span, cols)

    side_rows = jnp.take(mixed_in, slot, axis=0)
    row_side = side_rows[:, :, :capacity]
    col_side = side_rows[:, :, capacity:]
    partial_tiles = jnp.einsum("qocid,qocjd->qocij", row_side, col_side, preferred_element_type=jnp.float32)
    lanes_shape = partial_tiles.shape
    summed = axis_sum(partial_tiles.reshape(-1, 128), "mp").reshape(lanes_shape)
    predicted = summed / math.sqrt(width)
    target_tiles = targets_all.reshape(seq_count, groups, capacity, TB, TB).transpose(1, 0, 2, 3, 4)
    live_mask = (jnp.arange(capacity)[None, None, :] < counts_all[:, :, None]).astype(jnp.float32)
    n_live = jnp.sum(counts_all, axis=-1).astype(jnp.float32)
    dpredicted = (
        2.0
        / math.sqrt(width)
        * live_mask[..., None, None]
        * (predicted - target_tiles)
        / n_live[:, None, None, None, None]
    )
    row_float = row_side.astype(jnp.float32)
    col_float = col_side.astype(jnp.float32)
    drow = jnp.einsum("qocij,qocjd->qocid", dpredicted, col_float, precision=lax.Precision.HIGHEST)
    dcol = jnp.einsum("qocij,qocid->qocjd", dpredicted, row_float, precision=lax.Precision.HIGHEST)
    grads = jnp.concatenate([drow, dcol], axis=2).astype(jnp.bfloat16).astype(jnp.float32)
    grads = grads.reshape(groups, owners * n_sides, TB, narrow)
    flat_sides = sides.reshape(groups, owners * n_sides)
    same_block = flat_sides[:, :, None] == flat_sides[:, None, :]
    total = jnp.sum(jnp.where(same_block[..., None, None], grads[:, None], 0.0), axis=2)
    earlier = jnp.arange(owners * n_sides)[None, :] < jnp.arange(owners * n_sides)[:, None]
    first = jnp.logical_not(jnp.any(jnp.logical_and(same_block, earlier[None]), axis=-1))
    dconv = (scaling[:, None, None, None] * total).astype(jnp.bfloat16)
    dconv = jnp.where(first[..., None, None], dconv, jnp.zeros_like(dconv))
    act_sides = jnp.take(act_in, slot.reshape(groups, owners * n_sides), axis=0)
    return jnp.stack(
        [
            jnp.einsum(
                "qato,qati->oi",
                dconv,
                act_sides[:, :, offset : offset + TB],
                preferred_element_type=jnp.float32,
            )
            for offset in range(taps)
        ]
    )


def per_device(features, conv_weight, keep, tiles, counts, targets):
    members, length, _ = features.shape
    owners, capacity = tiles.shape[1], tiles.shape[2]
    fits = members == 1 and targets.shape[1] == 1 and 2 * owners * capacity * TB <= length
    if fits:
        return sparse_path(features, conv_weight, keep, tiles, counts, targets)
    return dense_path(features, conv_weight, keep, tiles, counts, targets)


def solution(mesh):
    placed = (
        P("dp", "seq", None),
        P(None, "mp", None),
        P("dp"),
        P("dp", None, None, None),
        P("dp", None),
        P("dp", "seq", None, None),
    )
    return jax.shard_map(
        per_device,
        mesh=mesh,
        in_specs=placed,
        out_specs=P(None, "mp", ("seq", "dp")),
        check_vma=False,
    )
```

```python
import math

import jax
import jax.numpy as jnp
from jax import lax
from jax.sharding import PartitionSpec as P

TB = 32
PER = 2


def extended(cells, sides, width):
    for axis, dim in sides:
        count = lax.axis_size(axis)
        ends = count - 1
        head = lax.slice_in_dim(cells, 0, width, axis=dim)
        tail = lax.slice_in_dim(cells, cells.shape[dim] - width, cells.shape[dim], axis=dim)
        cells = jnp.concatenate(
            [
                lax.ppermute(tail, axis, [(i, (i + 1) % count) for i in range(ends)]),
                cells,
                lax.ppermute(head, axis, [((i + 1) % count, i) for i in range(ends)]),
            ],
            axis=dim,
        )
    return cells


def take_rows(source_array, index_array):
    return jax.vmap(lambda table, picked: table[picked])(source_array, index_array)


def conv_apply(padded, weight, length):
    total = jnp.einsum(
        "mbi,oi->mbo", padded[:, 0:length], weight[0], preferred_element_type=jnp.float32
    )
    for offset in range(1, weight.shape[0]):
        total = total + jnp.einsum(
            "mbi,oi->mbo",
            padded[:, offset : offset + length],
            weight[offset],
            preferred_element_type=jnp.float32,
        )
    return total


def weight_term(padded, dconv, length, taps):
    return jnp.stack(
        [
            jnp.einsum(
                "mbi,mbo->oi",
                padded[:, offset : offset + length],
                dconv,
                preferred_element_type=jnp.float32,
            )
            for offset in range(taps)
        ]
    )


def dense_path(features, conv_weight, keep, tiles, counts, targets):
    members, length, width = features.shape
    taps = conv_weight.shape[0]
    narrow = conv_weight.shape[1]
    seq_count = lax.axis_size("seq")
    my_index = lax.axis_index("seq")
    my_part = lax.axis_index("mp")
    x_float = features.astype(jnp.float32)
    activations = jax.nn.gelu(x_float).astype(jnp.bfloat16)
    padded = extended(activations, (("seq", 1),), 2)
    scaling = 1.25 * keep.astype(jnp.float32)
    conv_out = conv_apply(padded, conv_weight, length)
    x_local = lax.dynamic_slice_in_dim(x_float, my_part * narrow, narrow, 2)
    mixed_out = (x_local + scaling[:, None, None] * conv_out).astype(jnp.bfloat16)
    capacity = tiles.shape[2]
    n_sides = 2 * capacity
    per_block = length // TB
    sides = jnp.concatenate([tiles[..., 0], tiles[..., 1]], axis=-1)
    side_source = sides // per_block
    side_local = sides % per_block
    own_sides = lax.dynamic_index_in_dim(sides, my_index, 1, keepdims=False)
    own_source = own_sides // per_block
    before = jnp.arange(n_sides)[None, :] < jnp.arange(n_sides)[:, None]
    same_source = own_source[:, :, None] == own_source[:, None, :]
    rank_within = jnp.sum(jnp.logical_and(same_source, before[None]), axis=-1)
    slot_index = own_source * PER + rank_within
    held_here = side_source == my_index
    held_order = jnp.cumsum(held_here.astype(jnp.int32), axis=-1) - 1
    picks = jnp.stack(
        [
            jnp.sum(
                jnp.where(jnp.logical_and(held_here, held_order == position), side_local, 0),
                axis=-1,
            )
            for position in range(PER)
        ],
        axis=-1,
    )
    blocks = mixed_out.reshape(members, per_block, TB, narrow)
    whole = lax.all_gather(blocks, "seq", axis=1, tiled=True)
    side_rows = take_rows(whole, own_sides)
    row_side = side_rows[:, :capacity]
    col_side = side_rows[:, capacity:]
    partial_tiles = jnp.einsum(
        "mcid,mcjd->mcij", row_side, col_side, preferred_element_type=jnp.float32
    )
    predicted = lax.psum(partial_tiles, "mp") / math.sqrt(width)
    target_tiles = targets[:, 0].reshape(members, capacity, TB, TB)
    own_count = lax.dynamic_index_in_dim(counts, my_index, 1, keepdims=False)
    live_mask = (jnp.arange(capacity)[None, :] < own_count[:, None]).astype(jnp.float32)
    n_live = jnp.sum(counts, axis=-1).astype(jnp.float32)
    dpredicted = (
        2.0
        / math.sqrt(width)
        * live_mask[:, :, None, None]
        * (predicted - target_tiles)
        / n_live[:, None, None, None]
    )
    row_float = row_side.astype(jnp.float32)
    col_float = col_side.astype(jnp.float32)
    drow = jnp.einsum("mcij,mcjd->mcid", dpredicted, col_float, precision=lax.Precision.HIGHEST)
    dcol = jnp.einsum("mcij,mcid->mcjd", dpredicted, row_float, precision=lax.Precision.HIGHEST)
    dside = jnp.concatenate([drow, dcol], axis=1).astype(jnp.bfloat16)
    inverse = jnp.argsort(slot_index, axis=-1)
    outgoing_grads = take_rows(dside, inverse).reshape(members, seq_count, PER, TB, narrow)
    returned = lax.all_to_all(outgoing_grads, "seq", split_axis=1, concat_axis=1, tiled=True)
    selector = (
        picks.reshape(members, seq_count * PER)[:, :, None] == jnp.arange(per_block)[None, None, :]
    ).astype(jnp.bfloat16)
    dmixed = jnp.einsum(
        "mkn,mktd->mntd",
        selector,
        returned.reshape(members, seq_count * PER, TB, narrow),
        preferred_element_type=jnp.float32,
    ).reshape(members, length, narrow)
    dconv = (scaling[:, None, None] * dmixed).astype(jnp.bfloat16)
    weight_local = weight_term(padded, dconv, length, taps)
    return lax.psum_scatter(weight_local, ("seq", "dp"), scatter_dimension=2, tiled=True)


def axis_sum(value, axis):
    count = lax.axis_size(axis)
    total = value
    for shift in range(1, count):
        total = total + lax.ppermute(value, axis, [(i, (i + shift) % count) for i in range(count)])
    return total


def sparse_path(features, conv_weight, keep, tiles, counts, targets):
    _, length, width = features.shape
    taps, narrow, _ = conv_weight.shape
    halo = taps // 2
    span = TB + 2 * halo
    owners, capacity = tiles.shape[1], tiles.shape[2]
    n_sides = 2 * capacity
    per_block = length // TB
    seq_count = lax.axis_size("seq")
    groups = lax.axis_size("dp")
    peers = seq_count * groups
    held = owners * PER
    cols = width // peers
    my_index = lax.axis_index("seq")
    my_part = lax.axis_index("mp")

    before = jnp.arange(n_sides)[None, :] < jnp.arange(n_sides)[:, None]
    own_sides = jnp.concatenate([tiles[0, ..., 0], tiles[0, ..., 1]], axis=-1)
    own_source = own_sides // per_block
    own_same = own_source[:, :, None] == own_source[:, None, :]
    own_rank = jnp.sum(jnp.logical_and(own_same, before), axis=-1)
    held_here = own_source == my_index
    picks = jnp.stack(
        [
            jnp.sum(jnp.where(jnp.logical_and(held_here, own_rank == r), own_sides % per_block, 0), axis=-1)
            for r in range(PER)
        ],
        axis=-1,
    ).reshape(held)

    cells = features[0]
    ends = seq_count - 1
    head = lax.ppermute(cells[length - halo :], "seq", [(i, i + 1) for i in range(ends)])
    tail = lax.ppermute(cells[:halo], "seq", [(i + 1, i) for i in range(ends)])
    starts = picks * TB
    last = per_block - 1

    def window(block, start):
        before = lax.dynamic_slice_in_dim(cells, jnp.maximum(start - halo, 0), halo, 0)
        middle = lax.dynamic_slice_in_dim(cells, start, TB, 0)
        after = lax.dynamic_slice_in_dim(cells, jnp.minimum(start + TB, length - halo), halo, 0)
        before = jnp.where(block == 0, head, before)
        after = jnp.where(block == last, tail, after)
        return jnp.concatenate([before, middle, after], axis=0)

    windows = jnp.stack([window(picks[h], starts[h]) for h in range(held)])
    x_float = windows.astype(jnp.float32)
    act = jax.nn.gelu(x_float).astype(jnp.bfloat16)
    conv_out = jnp.einsum("hti,oi->hto", act[:, 0:TB], conv_weight[0], preferred_element_type=jnp.float32)
    for offset in range(1, taps):
        conv_out = conv_out + jnp.einsum(
            "hti,oi->hto", act[:, offset : offset + TB], conv_weight[offset], preferred_element_type=jnp.float32
        )
    my_scale = 1.25 * keep[0].astype(jnp.float32)
    x_part = lax.dynamic_slice_in_dim(x_float[:, halo : halo + TB], my_part * narrow, narrow, 2)
    mixed = (x_part + my_scale * conv_out).astype(jnp.bfloat16)

    act_cut = act.reshape(held, span, peers, cols).transpose(2, 0, 1, 3).reshape(peers, -1)
    mixed_rep = jnp.broadcast_to(mixed.reshape(1, -1), (peers, held * TB * narrow))
    wide = targets.reshape(-1)
    pieces = []
    for _ in range(3):
        piece = lax.reduce_precision(wide, exponent_bits=8, mantissa_bits=7)
        pieces.append(piece)
        wide = wide - piece
    small = jnp.concatenate([tiles.reshape(-1), counts.reshape(-1), keep.reshape(-1)]).astype(jnp.float32)
    meta = jnp.concatenate(pieces + [small]).astype(jnp.bfloat16)
    meta_rep = jnp.broadcast_to(meta[None], (peers, meta.shape[0]))
    outgoing = jnp.concatenate([mixed_rep, act_cut, meta_rep], axis=1)
    incoming = lax.all_to_all(outgoing, ("seq", "dp"), 0, 0, tiled=True)
    n_mixed = held * TB * narrow
    n_act = held * span * cols
    mixed_in = incoming[:, :n_mixed].reshape(peers * held, TB, narrow)
    act_in = incoming[:, n_mixed : n_mixed + n_act].reshape(peers * held, span, cols)
    meta_in = incoming[:, n_mixed + n_act :].astype(jnp.float32).reshape(seq_count, groups, -1)
    n_targets = capacity * TB * TB
    n_tiles = owners * capacity * 2
    targets_all = meta_in[:, :, :n_targets] + meta_in[:, :, n_targets : 2 * n_targets]
    targets_all = targets_all + meta_in[:, :, 2 * n_targets : 3 * n_targets]
    ints = meta_in[0, :, 3 * n_targets :].astype(jnp.int32)
    tiles_all = ints[:, :n_tiles].reshape(groups, owners, capacity, 2)
    counts_all = ints[:, n_tiles : n_tiles + owners]
    keep_all = ints[:, n_tiles + owners]

    sides = jnp.concatenate([tiles_all[..., 0], tiles_all[..., 1]], axis=-1)
    source = sides // per_block
    local = sides % per_block
    same_source = source[..., :, None] == source[..., None, :]
    rank = jnp.sum(jnp.logical_and(same_source, before), axis=-1)
    slot = (source * groups + jnp.arange(groups)[:, None, None]) * held + jnp.arange(owners)[None, :, None] * PER + rank

    side_rows = jnp.take(mixed_in, slot, axis=0)
    row_side = side_rows[:, :, :capacity]
    col_side = side_rows[:, :, capacity:]
    partial_tiles = jnp.einsum("qocid,qocjd->qocij", row_side, col_side, preferred_element_type=jnp.float32)
    lanes_shape = partial_tiles.shape
    summed = axis_sum(partial_tiles.reshape(-1, 128), "mp").reshape(lanes_shape)
    predicted = summed / math.sqrt(width)
    target_tiles = targets_all.reshape(seq_count, groups, capacity, TB, TB).transpose(1, 0, 2, 3, 4)
    live_mask = (jnp.arange(capacity)[None, None, :] < counts_all[:, :, None]).astype(jnp.float32)
    n_live = jnp.sum(counts_all, axis=-1).astype(jnp.float32)
    dpredicted = (
        2.0
        / math.sqrt(width)
        * live_mask[..., None, None]
        * (predicted - target_tiles)
        / n_live[:, None, None, None, None]
    )
    row_float = row_side.astype(jnp.float32)
    col_float = col_side.astype(jnp.float32)
    drow = jnp.einsum("qocij,qocjd->qocid", dpredicted, col_float, precision=lax.Precision.HIGHEST)
    dcol = jnp.einsum("qocij,qocid->qocjd", dpredicted, row_float, precision=lax.Precision.HIGHEST)
    grads = jnp.concatenate([drow, dcol], axis=2).astype(jnp.bfloat16).astype(jnp.float32)
    grads = grads.reshape(groups, owners * n_sides, TB, narrow)
    flat_sides = sides.reshape(groups, owners * n_sides)
    same_block = flat_sides[:, :, None] == flat_sides[:, None, :]
    total = jnp.sum(jnp.where(same_block[..., None, None], grads[:, None], 0.0), axis=2)
    earlier = jnp.arange(owners * n_sides)[None, :] < jnp.arange(owners * n_sides)[:, None]
    first = jnp.logical_not(jnp.any(jnp.logical_and(same_block, earlier[None]), axis=-1))
    scaling = 1.25 * keep_all.astype(jnp.float32)
    dconv = (scaling[:, None, None, None] * total).astype(jnp.bfloat16)
    dconv = jnp.where(first[..., None, None], dconv, jnp.zeros_like(dconv))
    act_sides = jnp.take(act_in, slot.reshape(groups, owners * n_sides), axis=0)
    return jnp.stack(
        [
            jnp.einsum(
                "qato,qati->oi",
                dconv,
                act_sides[:, :, offset : offset + TB],
                preferred_element_type=jnp.float32,
            )
            for offset in range(taps)
        ]
    )


def per_device(features, conv_weight, keep, tiles, counts, targets):
    members, length, _ = features.shape
    owners, capacity = tiles.shape[1], tiles.shape[2]
    blocks = lax.axis_size("seq") * length // TB
    fits = members == 1 and targets.shape[1] == 1 and 2 * owners * capacity * TB <= length
    fits = fits and blocks <= 256 and capacity <= 256
    if fits:
        return sparse_path(features, conv_weight, keep, tiles, counts, targets)
    return dense_path(features, conv_weight, keep, tiles, counts, targets)


def solution(mesh):
    placed = (
        P("dp", "seq", None),
        P(None, "mp", None),
        P("dp"),
        P("dp", None, None, None),
        P("dp", None),
        P("dp", "seq", None, None),
    )
    return jax.shard_map(
        per_device,
        mesh=mesh,
        in_specs=placed,
        out_specs=P(None, "mp", ("seq", "dp")),
        check_vma=False,
    )
```

```python
import math

import jax
import jax.numpy as jnp
from jax import lax
from jax.sharding import PartitionSpec as P

TB = 32
PER = 2


def extended(cells, sides, width):
    for axis, dim in sides:
        count = lax.axis_size(axis)
        ends = count - 1
        head = lax.slice_in_dim(cells, 0, width, axis=dim)
        tail = lax.slice_in_dim(cells, cells.shape[dim] - width, cells.shape[dim], axis=dim)
        cells = jnp.concatenate(
            [
                lax.ppermute(tail, axis, [(i, (i + 1) % count) for i in range(ends)]),
                cells,
                lax.ppermute(head, axis, [((i + 1) % count, i) for i in range(ends)]),
            ],
            axis=dim,
        )
    return cells


def take_rows(source_array, index_array):
    return jax.vmap(lambda table, picked: table[picked])(source_array, index_array)


def conv_apply(padded, weight, length):
    total = jnp.einsum(
        "mbi,oi->mbo", padded[:, 0:length], weight[0], preferred_element_type=jnp.float32
    )
    for offset in range(1, weight.shape[0]):
        total = total + jnp.einsum(
            "mbi,oi->mbo",
            padded[:, offset : offset + length],
            weight[offset],
            preferred_element_type=jnp.float32,
        )
    return total


def weight_term(padded, dconv, length, taps):
    return jnp.stack(
        [
            jnp.einsum(
                "mbi,mbo->oi",
                padded[:, offset : offset + length],
                dconv,
                preferred_element_type=jnp.float32,
            )
            for offset in range(taps)
        ]
    )


def dense_path(features, conv_weight, keep, tiles, counts, targets):
    members, length, width = features.shape
    taps = conv_weight.shape[0]
    narrow = conv_weight.shape[1]
    seq_count = lax.axis_size("seq")
    my_index = lax.axis_index("seq")
    my_part = lax.axis_index("mp")
    x_float = features.astype(jnp.float32)
    activations = jax.nn.gelu(x_float).astype(jnp.bfloat16)
    padded = extended(activations, (("seq", 1),), 2)
    scaling = 1.25 * keep.astype(jnp.float32)
    conv_out = conv_apply(padded, conv_weight, length)
    x_local = lax.dynamic_slice_in_dim(x_float, my_part * narrow, narrow, 2)
    mixed_out = (x_local + scaling[:, None, None] * conv_out).astype(jnp.bfloat16)
    capacity = tiles.shape[2]
    n_sides = 2 * capacity
    per_block = length // TB
    sides = jnp.concatenate([tiles[..., 0], tiles[..., 1]], axis=-1)
    side_source = sides // per_block
    side_local = sides % per_block
    own_sides = lax.dynamic_index_in_dim(sides, my_index, 1, keepdims=False)
    own_source = own_sides // per_block
    before = jnp.arange(n_sides)[None, :] < jnp.arange(n_sides)[:, None]
    same_source = own_source[:, :, None] == own_source[:, None, :]
    rank_within = jnp.sum(jnp.logical_and(same_source, before[None]), axis=-1)
    slot_index = own_source * PER + rank_within
    held_here = side_source == my_index
    held_order = jnp.cumsum(held_here.astype(jnp.int32), axis=-1) - 1
    picks = jnp.stack(
        [
            jnp.sum(
                jnp.where(jnp.logical_and(held_here, held_order == position), side_local, 0),
                axis=-1,
            )
            for position in range(PER)
        ],
        axis=-1,
    )
    blocks = mixed_out.reshape(members, per_block, TB, narrow)
    whole = lax.all_gather(blocks, "seq", axis=1, tiled=True)
    side_rows = take_rows(whole, own_sides)
    row_side = side_rows[:, :capacity]
    col_side = side_rows[:, capacity:]
    partial_tiles = jnp.einsum(
        "mcid,mcjd->mcij", row_side, col_side, preferred_element_type=jnp.float32
    )
    predicted = lax.psum(partial_tiles, "mp") / math.sqrt(width)
    target_tiles = targets[:, 0].reshape(members, capacity, TB, TB)
    own_count = lax.dynamic_index_in_dim(counts, my_index, 1, keepdims=False)
    live_mask = (jnp.arange(capacity)[None, :] < own_count[:, None]).astype(jnp.float32)
    n_live = jnp.sum(counts, axis=-1).astype(jnp.float32)
    dpredicted = (
        2.0
        / math.sqrt(width)
        * live_mask[:, :, None, None]
        * (predicted - target_tiles)
        / n_live[:, None, None, None]
    )
    row_float = row_side.astype(jnp.float32)
    col_float = col_side.astype(jnp.float32)
    drow = jnp.einsum("mcij,mcjd->mcid", dpredicted, col_float, precision=lax.Precision.HIGHEST)
    dcol = jnp.einsum("mcij,mcid->mcjd", dpredicted, row_float, precision=lax.Precision.HIGHEST)
    dside = jnp.concatenate([drow, dcol], axis=1).astype(jnp.bfloat16)
    inverse = jnp.argsort(slot_index, axis=-1)
    outgoing_grads = take_rows(dside, inverse).reshape(members, seq_count, PER, TB, narrow)
    returned = lax.all_to_all(outgoing_grads, "seq", split_axis=1, concat_axis=1, tiled=True)
    selector = (
        picks.reshape(members, seq_count * PER)[:, :, None] == jnp.arange(per_block)[None, None, :]
    ).astype(jnp.bfloat16)
    dmixed = jnp.einsum(
        "mkn,mktd->mntd",
        selector,
        returned.reshape(members, seq_count * PER, TB, narrow),
        preferred_element_type=jnp.float32,
    ).reshape(members, length, narrow)
    dconv = (scaling[:, None, None] * dmixed).astype(jnp.bfloat16)
    weight_local = weight_term(padded, dconv, length, taps)
    return lax.psum_scatter(weight_local, ("seq", "dp"), scatter_dimension=2, tiled=True)


def axis_sum(value, axis):
    count = lax.axis_size(axis)
    total = value
    for shift in range(1, count):
        total = total + lax.ppermute(value, axis, [(i, (i + shift) % count) for i in range(count)])
    return total


def sparse_path(features, conv_weight, keep, tiles, counts, targets):
    _, length, width = features.shape
    taps, narrow, _ = conv_weight.shape
    halo = taps // 2
    span = TB + 2 * halo
    owners, capacity = tiles.shape[1], tiles.shape[2]
    n_sides = 2 * capacity
    per_block = length // TB
    seq_count = lax.axis_size("seq")
    groups = lax.axis_size("dp")
    peers = seq_count * groups
    held = owners * PER
    cols = width // peers
    my_index = lax.axis_index("seq")
    my_part = lax.axis_index("mp")

    before = jnp.arange(n_sides)[None, :] < jnp.arange(n_sides)[:, None]
    own_sides = jnp.concatenate([tiles[0, ..., 0], tiles[0, ..., 1]], axis=-1)
    own_source = own_sides // per_block
    own_same = own_source[:, :, None] == own_source[:, None, :]
    own_rank = jnp.sum(jnp.logical_and(own_same, before), axis=-1)
    held_here = own_source == my_index
    picks = jnp.stack(
        [
            jnp.sum(jnp.where(jnp.logical_and(held_here, own_rank == r), own_sides % per_block, 0), axis=-1)
            for r in range(PER)
        ],
        axis=-1,
    ).reshape(held)

    cells = features[0]
    ends = seq_count - 1
    if seq_count == 2:
        swapped = lax.ppermute(
            jnp.concatenate([cells[length - halo :], cells[:halo]]), "seq", [(0, 1), (1, 0)]
        )
        head = jnp.where(my_index == 0, jnp.zeros_like(swapped[:halo]), swapped[:halo])
        tail = jnp.where(my_index == ends, jnp.zeros_like(swapped[halo:]), swapped[halo:])
    else:
        head = lax.ppermute(cells[length - halo :], "seq", [(i, i + 1) for i in range(ends)])
        tail = lax.ppermute(cells[:halo], "seq", [(i + 1, i) for i in range(ends)])
    starts = picks * TB
    last = per_block - 1

    def window(block, start):
        before = lax.dynamic_slice_in_dim(cells, jnp.maximum(start - halo, 0), halo, 0)
        middle = lax.dynamic_slice_in_dim(cells, start, TB, 0)
        after = lax.dynamic_slice_in_dim(cells, jnp.minimum(start + TB, length - halo), halo, 0)
        before = jnp.where(block == 0, head, before)
        after = jnp.where(block == last, tail, after)
        return jnp.concatenate([before, middle, after], axis=0)

    windows = jnp.stack([window(picks[h], starts[h]) for h in range(held)])
    x_float = windows.astype(jnp.float32)
    act = jax.nn.gelu(x_float).astype(jnp.bfloat16)
    conv_out = jnp.einsum("hti,oi->hto", act[:, 0:TB], conv_weight[0], preferred_element_type=jnp.float32)
    for offset in range(1, taps):
        conv_out = conv_out + jnp.einsum(
            "hti,oi->hto", act[:, offset : offset + TB], conv_weight[offset], preferred_element_type=jnp.float32
        )
    my_scale = 1.25 * keep[0].astype(jnp.float32)
    x_part = lax.dynamic_slice_in_dim(x_float[:, halo : halo + TB], my_part * narrow, narrow, 2)
    mixed = (x_part + my_scale * conv_out).astype(jnp.bfloat16)

    act_cut = act.reshape(held, span, peers, cols).transpose(2, 0, 1, 3).reshape(peers, -1)
    mixed_rep = jnp.broadcast_to(mixed.reshape(1, -1), (peers, held * TB * narrow))
    wide = targets.reshape(-1)
    pieces = []
    for _ in range(3):
        piece = lax.reduce_precision(wide, exponent_bits=8, mantissa_bits=7)
        pieces.append(piece)
        wide = wide - piece
    small = jnp.concatenate([tiles.reshape(-1), counts.reshape(-1), keep.reshape(-1)]).astype(jnp.float32)
    meta = jnp.concatenate(pieces + [small]).astype(jnp.bfloat16)
    meta_rep = jnp.broadcast_to(meta[None], (peers, meta.shape[0]))
    outgoing = jnp.concatenate([mixed_rep, act_cut, meta_rep], axis=1)
    outgoing = jnp.pad(outgoing, ((0, 0), (0, -outgoing.shape[1] % 128)))
    incoming = lax.all_to_all(outgoing, ("seq", "dp"), 0, 0, tiled=True)
    n_mixed = held * TB * narrow
    n_act = held * span * cols
    mixed_in = incoming[:, :n_mixed].reshape(peers * held, TB, narrow)
    act_in = incoming[:, n_mixed : n_mixed + n_act].reshape(peers * held, span, cols)
    meta_in = incoming[:, n_mixed + n_act :].astype(jnp.float32).reshape(seq_count, groups, -1)
    n_targets = capacity * TB * TB
    n_tiles = owners * capacity * 2
    targets_all = meta_in[:, :, :n_targets] + meta_in[:, :, n_targets : 2 * n_targets]
    targets_all = targets_all + meta_in[:, :, 2 * n_targets : 3 * n_targets]
    ints = meta_in[0, :, 3 * n_targets :].astype(jnp.int32)
    tiles_all = ints[:, :n_tiles].reshape(groups, owners, capacity, 2)
    counts_all = ints[:, n_tiles : n_tiles + owners]
    keep_all = ints[:, n_tiles + owners]

    sides = jnp.concatenate([tiles_all[..., 0], tiles_all[..., 1]], axis=-1)
    source = sides // per_block
    local = sides % per_block
    same_source = source[..., :, None] == source[..., None, :]
    rank = jnp.sum(jnp.logical_and(same_source, before), axis=-1)
    slot = (source * groups + jnp.arange(groups)[:, None, None]) * held + jnp.arange(owners)[None, :, None] * PER + rank

    side_rows = jnp.take(mixed_in, slot, axis=0)
    row_side = side_rows[:, :, :capacity]
    col_side = side_rows[:, :, capacity:]
    partial_tiles = jnp.einsum("qocid,qocjd->qocij", row_side, col_side, preferred_element_type=jnp.float32)
    lanes_shape = partial_tiles.shape
    summed = axis_sum(partial_tiles.reshape(-1, 128), "mp").reshape(lanes_shape)
    predicted = summed / math.sqrt(width)
    target_tiles = targets_all.reshape(seq_count, groups, capacity, TB, TB).transpose(1, 0, 2, 3, 4)
    live_mask = (jnp.arange(capacity)[None, None, :] < counts_all[:, :, None]).astype(jnp.float32)
    n_live = jnp.sum(counts_all, axis=-1).astype(jnp.float32)
    dpredicted = (
        2.0
        / math.sqrt(width)
        * live_mask[..., None, None]
        * (predicted - target_tiles)
        / n_live[:, None, None, None, None]
    )
    row_float = row_side.astype(jnp.float32)
    col_float = col_side.astype(jnp.float32)
    drow = jnp.einsum("qocij,qocjd->qocid", dpredicted, col_float, precision=lax.Precision.HIGHEST)
    dcol = jnp.einsum("qocij,qocid->qocjd", dpredicted, row_float, precision=lax.Precision.HIGHEST)
    grads = jnp.concatenate([drow, dcol], axis=2).astype(jnp.bfloat16).astype(jnp.float32)
    grads = grads.reshape(groups, owners * n_sides, TB, narrow)
    flat_sides = sides.reshape(groups, owners * n_sides)
    same_block = flat_sides[:, :, None] == flat_sides[:, None, :]
    total = jnp.sum(jnp.where(same_block[..., None, None], grads[:, None], 0.0), axis=2)
    earlier = jnp.arange(owners * n_sides)[None, :] < jnp.arange(owners * n_sides)[:, None]
    first = jnp.logical_not(jnp.any(jnp.logical_and(same_block, earlier[None]), axis=-1))
    scaling = 1.25 * keep_all.astype(jnp.float32)
    dconv = (scaling[:, None, None, None] * total).astype(jnp.bfloat16)
    dconv = jnp.where(first[..., None, None], dconv, jnp.zeros_like(dconv))
    act_sides = jnp.take(act_in, slot.reshape(groups, owners * n_sides), axis=0)
    return jnp.stack(
        [
            jnp.einsum(
                "qato,qati->oi",
                dconv,
                act_sides[:, :, offset : offset + TB],
                preferred_element_type=jnp.float32,
            )
            for offset in range(taps)
        ]
    )


def per_device(features, conv_weight, keep, tiles, counts, targets):
    members, length, _ = features.shape
    owners, capacity = tiles.shape[1], tiles.shape[2]
    blocks = lax.axis_size("seq") * length // TB
    fits = members == 1 and targets.shape[1] == 1 and 2 * owners * capacity * TB <= length
    fits = fits and blocks <= 256 and capacity <= 256
    if fits:
        return sparse_path(features, conv_weight, keep, tiles, counts, targets)
    return dense_path(features, conv_weight, keep, tiles, counts, targets)


def solution(mesh):
    placed = (
        P("dp", "seq", None),
        P(None, "mp", None),
        P("dp"),
        P("dp", None, None, None),
        P("dp", None),
        P("dp", "seq", None, None),
    )
    return jax.shard_map(
        per_device,
        mesh=mesh,
        in_specs=placed,
        out_specs=P(None, "mp", ("seq", "dp")),
        check_vma=False,
    )
```

```python
import math

import jax
import jax.numpy as jnp
from jax import lax
from jax.sharding import PartitionSpec as P

TB = 32
PER = 2


def extended(cells, sides, width):
    for axis, dim in sides:
        count = lax.axis_size(axis)
        ends = count - 1
        head = lax.slice_in_dim(cells, 0, width, axis=dim)
        tail = lax.slice_in_dim(cells, cells.shape[dim] - width, cells.shape[dim], axis=dim)
        cells = jnp.concatenate(
            [
                lax.ppermute(tail, axis, [(i, (i + 1) % count) for i in range(ends)]),
                cells,
                lax.ppermute(head, axis, [((i + 1) % count, i) for i in range(ends)]),
            ],
            axis=dim,
        )
    return cells


def take_rows(source_array, index_array):
    return jax.vmap(lambda table, picked: table[picked])(source_array, index_array)


def conv_apply(padded, weight, length):
    total = jnp.einsum(
        "mbi,oi->mbo", padded[:, 0:length], weight[0], preferred_element_type=jnp.float32
    )
    for offset in range(1, weight.shape[0]):
        total = total + jnp.einsum(
            "mbi,oi->mbo",
            padded[:, offset : offset + length],
            weight[offset],
            preferred_element_type=jnp.float32,
        )
    return total


def weight_term(padded, dconv, length, taps):
    return jnp.stack(
        [
            jnp.einsum(
                "mbi,mbo->oi",
                padded[:, offset : offset + length],
                dconv,
                preferred_element_type=jnp.float32,
            )
            for offset in range(taps)
        ]
    )


def dense_path(features, conv_weight, keep, tiles, counts, targets):
    members, length, width = features.shape
    taps = conv_weight.shape[0]
    narrow = conv_weight.shape[1]
    seq_count = lax.axis_size("seq")
    my_index = lax.axis_index("seq")
    my_part = lax.axis_index("mp")
    x_float = features.astype(jnp.float32)
    activations = jax.nn.gelu(x_float).astype(jnp.bfloat16)
    padded = extended(activations, (("seq", 1),), 2)
    scaling = 1.25 * keep.astype(jnp.float32)
    conv_out = conv_apply(padded, conv_weight, length)
    x_local = lax.dynamic_slice_in_dim(x_float, my_part * narrow, narrow, 2)
    mixed_out = (x_local + scaling[:, None, None] * conv_out).astype(jnp.bfloat16)
    capacity = tiles.shape[2]
    n_sides = 2 * capacity
    per_block = length // TB
    sides = jnp.concatenate([tiles[..., 0], tiles[..., 1]], axis=-1)
    side_source = sides // per_block
    side_local = sides % per_block
    own_sides = lax.dynamic_index_in_dim(sides, my_index, 1, keepdims=False)
    own_source = own_sides // per_block
    before = jnp.arange(n_sides)[None, :] < jnp.arange(n_sides)[:, None]
    same_source = own_source[:, :, None] == own_source[:, None, :]
    rank_within = jnp.sum(jnp.logical_and(same_source, before[None]), axis=-1)
    slot_index = own_source * PER + rank_within
    held_here = side_source == my_index
    held_order = jnp.cumsum(held_here.astype(jnp.int32), axis=-1) - 1
    picks = jnp.stack(
        [
            jnp.sum(
                jnp.where(jnp.logical_and(held_here, held_order == position), side_local, 0),
                axis=-1,
            )
            for position in range(PER)
        ],
        axis=-1,
    )
    blocks = mixed_out.reshape(members, per_block, TB, narrow)
    whole = lax.all_gather(blocks, "seq", axis=1, tiled=True)
    side_rows = take_rows(whole, own_sides)
    row_side = side_rows[:, :capacity]
    col_side = side_rows[:, capacity:]
    partial_tiles = jnp.einsum(
        "mcid,mcjd->mcij", row_side, col_side, preferred_element_type=jnp.float32
    )
    predicted = lax.psum(partial_tiles, "mp") / math.sqrt(width)
    target_tiles = targets[:, 0].reshape(members, capacity, TB, TB)
    own_count = lax.dynamic_index_in_dim(counts, my_index, 1, keepdims=False)
    live_mask = (jnp.arange(capacity)[None, :] < own_count[:, None]).astype(jnp.float32)
    n_live = jnp.sum(counts, axis=-1).astype(jnp.float32)
    dpredicted = (
        2.0
        / math.sqrt(width)
        * live_mask[:, :, None, None]
        * (predicted - target_tiles)
        / n_live[:, None, None, None]
    )
    row_float = row_side.astype(jnp.float32)
    col_float = col_side.astype(jnp.float32)
    drow = jnp.einsum("mcij,mcjd->mcid", dpredicted, col_float, precision=lax.Precision.HIGHEST)
    dcol = jnp.einsum("mcij,mcid->mcjd", dpredicted, row_float, precision=lax.Precision.HIGHEST)
    dside = jnp.concatenate([drow, dcol], axis=1).astype(jnp.bfloat16)
    inverse = jnp.argsort(slot_index, axis=-1)
    outgoing_grads = take_rows(dside, inverse).reshape(members, seq_count, PER, TB, narrow)
    returned = lax.all_to_all(outgoing_grads, "seq", split_axis=1, concat_axis=1, tiled=True)
    selector = (
        picks.reshape(members, seq_count * PER)[:, :, None] == jnp.arange(per_block)[None, None, :]
    ).astype(jnp.bfloat16)
    dmixed = jnp.einsum(
        "mkn,mktd->mntd",
        selector,
        returned.reshape(members, seq_count * PER, TB, narrow),
        preferred_element_type=jnp.float32,
    ).reshape(members, length, narrow)
    dconv = (scaling[:, None, None] * dmixed).astype(jnp.bfloat16)
    weight_local = weight_term(padded, dconv, length, taps)
    return lax.psum_scatter(weight_local, ("seq", "dp"), scatter_dimension=2, tiled=True)


def axis_sum(value, axis):
    count = lax.axis_size(axis)
    total = value
    for shift in range(1, count):
        total = total + lax.ppermute(value, axis, [(i, (i + shift) % count) for i in range(count)])
    return total


def sparse_path(features, conv_weight, keep, tiles, counts, targets):
    _, length, width = features.shape
    taps, narrow, _ = conv_weight.shape
    halo = taps // 2
    span = TB + 2 * halo
    owners, capacity = tiles.shape[1], tiles.shape[2]
    n_sides = 2 * capacity
    per_block = length // TB
    seq_count = lax.axis_size("seq")
    groups = lax.axis_size("dp")
    peers = seq_count * groups
    held = owners * PER
    cols = width // peers
    my_index = lax.axis_index("seq")
    my_part = lax.axis_index("mp")

    before = jnp.arange(n_sides)[None, :] < jnp.arange(n_sides)[:, None]
    own_sides = jnp.concatenate([tiles[0, ..., 0], tiles[0, ..., 1]], axis=-1)
    own_source = own_sides // per_block
    own_same = own_source[:, :, None] == own_source[:, None, :]
    own_rank = jnp.sum(jnp.logical_and(own_same, before), axis=-1)
    held_here = own_source == my_index
    picks = jnp.stack(
        [
            jnp.sum(jnp.where(jnp.logical_and(held_here, own_rank == r), own_sides % per_block, 0), axis=-1)
            for r in range(PER)
        ],
        axis=-1,
    ).reshape(held)

    cells = features[0]
    ends = seq_count - 1
    if seq_count == 2:
        swapped = lax.ppermute(
            jnp.concatenate([cells[length - halo :], cells[:halo]]), "seq", [(0, 1), (1, 0)]
        )
        head = jnp.where(my_index == 0, jnp.zeros_like(swapped[:halo]), swapped[:halo])
        tail = jnp.where(my_index == ends, jnp.zeros_like(swapped[halo:]), swapped[halo:])
    else:
        head = lax.ppermute(cells[length - halo :], "seq", [(i, i + 1) for i in range(ends)])
        tail = lax.ppermute(cells[:halo], "seq", [(i + 1, i) for i in range(ends)])
    rows = picks[:, None] * TB - halo + jnp.arange(span)[None, :]
    inside = jnp.take(cells, jnp.clip(rows, 0, length - 1), axis=0)
    edge_rows = jnp.concatenate([head, tail], axis=0)
    edge_index = jnp.where(rows < 0, rows + halo, rows - length + halo)
    outside = jnp.take(edge_rows, jnp.clip(edge_index, 0, 2 * halo - 1), axis=0)
    in_range = jnp.logical_and(rows >= 0, rows < length)
    windows = jnp.where(in_range[..., None], inside, outside)
    x_float = windows.astype(jnp.float32)
    act = jax.nn.gelu(x_float).astype(jnp.bfloat16)
    conv_out = jnp.einsum("hti,oi->hto", act[:, 0:TB], conv_weight[0], preferred_element_type=jnp.float32)
    for offset in range(1, taps):
        conv_out = conv_out + jnp.einsum(
            "hti,oi->hto", act[:, offset : offset + TB], conv_weight[offset], preferred_element_type=jnp.float32
        )
    my_scale = 1.25 * keep[0].astype(jnp.float32)
    x_part = lax.dynamic_slice_in_dim(x_float[:, halo : halo + TB], my_part * narrow, narrow, 2)
    mixed = (x_part + my_scale * conv_out).astype(jnp.bfloat16)

    act_cut = act.reshape(held, span, peers, cols).transpose(2, 0, 1, 3).reshape(peers, -1)
    mixed_rep = jnp.broadcast_to(mixed.reshape(1, -1), (peers, held * TB * narrow))
    wide = targets.reshape(-1)
    pieces = []
    for _ in range(3):
        piece = lax.reduce_precision(wide, exponent_bits=8, mantissa_bits=7)
        pieces.append(piece)
        wide = wide - piece
    small = jnp.concatenate([tiles.reshape(-1), counts.reshape(-1), keep.reshape(-1)]).astype(jnp.float32)
    meta = jnp.concatenate(pieces + [small]).astype(jnp.bfloat16)
    meta_rep = jnp.broadcast_to(meta[None], (peers, meta.shape[0]))
    outgoing = jnp.concatenate([mixed_rep, act_cut, meta_rep], axis=1)
    outgoing = jnp.pad(outgoing, ((0, 0), (0, -outgoing.shape[1] % 128)))
    incoming = lax.all_to_all(outgoing, ("seq", "dp"), 0, 0, tiled=True)
    n_mixed = held * TB * narrow
    n_act = held * span * cols
    mixed_in = incoming[:, :n_mixed].reshape(peers * held, TB, narrow)
    act_in = incoming[:, n_mixed : n_mixed + n_act].reshape(peers * held, span, cols)
    meta_in = incoming[:, n_mixed + n_act :].astype(jnp.float32).reshape(seq_count, groups, -1)
    n_targets = capacity * TB * TB
    n_tiles = owners * capacity * 2
    targets_all = meta_in[:, :, :n_targets] + meta_in[:, :, n_targets : 2 * n_targets]
    targets_all = targets_all + meta_in[:, :, 2 * n_targets : 3 * n_targets]
    ints = meta_in[0, :, 3 * n_targets :].astype(jnp.int32)
    tiles_all = ints[:, :n_tiles].reshape(groups, owners, capacity, 2)
    counts_all = ints[:, n_tiles : n_tiles + owners]
    keep_all = ints[:, n_tiles + owners]

    sides = jnp.concatenate([tiles_all[..., 0], tiles_all[..., 1]], axis=-1)
    source = sides // per_block
    local = sides % per_block
    same_source = source[..., :, None] == source[..., None, :]
    rank = jnp.sum(jnp.logical_and(same_source, before), axis=-1)
    slot = (source * groups + jnp.arange(groups)[:, None, None]) * held + jnp.arange(owners)[None, :, None] * PER + rank

    side_rows = jnp.take(mixed_in, slot, axis=0)
    row_side = side_rows[:, :, :capacity]
    col_side = side_rows[:, :, capacity:]
    partial_tiles = jnp.einsum("qocid,qocjd->qocij", row_side, col_side, preferred_element_type=jnp.float32)
    lanes_shape = partial_tiles.shape
    summed = axis_sum(partial_tiles.reshape(-1, 128), "mp").reshape(lanes_shape)
    predicted = summed / math.sqrt(width)
    target_tiles = targets_all.reshape(seq_count, groups, capacity, TB, TB).transpose(1, 0, 2, 3, 4)
    live_mask = (jnp.arange(capacity)[None, None, :] < counts_all[:, :, None]).astype(jnp.float32)
    n_live = jnp.sum(counts_all, axis=-1).astype(jnp.float32)
    dpredicted = (
        2.0
        / math.sqrt(width)
        * live_mask[..., None, None]
        * (predicted - target_tiles)
        / n_live[:, None, None, None, None]
    )
    row_float = row_side.astype(jnp.float32)
    col_float = col_side.astype(jnp.float32)
    drow = jnp.einsum("qocij,qocjd->qocid", dpredicted, col_float, precision=lax.Precision.HIGHEST)
    dcol = jnp.einsum("qocij,qocid->qocjd", dpredicted, row_float, precision=lax.Precision.HIGHEST)
    grads = jnp.concatenate([drow, dcol], axis=2).astype(jnp.bfloat16).astype(jnp.float32)
    grads = grads.reshape(groups, owners * n_sides, TB, narrow)
    flat_sides = sides.reshape(groups, owners * n_sides)
    same_block = flat_sides[:, :, None] == flat_sides[:, None, :]
    total = jnp.sum(jnp.where(same_block[..., None, None], grads[:, None], 0.0), axis=2)
    earlier = jnp.arange(owners * n_sides)[None, :] < jnp.arange(owners * n_sides)[:, None]
    first = jnp.logical_not(jnp.any(jnp.logical_and(same_block, earlier[None]), axis=-1))
    scaling = 1.25 * keep_all.astype(jnp.float32)
    dconv = (scaling[:, None, None, None] * total).astype(jnp.bfloat16)
    dconv = jnp.where(first[..., None, None], dconv, jnp.zeros_like(dconv))
    act_sides = jnp.take(act_in, slot.reshape(groups, owners * n_sides), axis=0)
    return jnp.stack(
        [
            jnp.einsum(
                "qato,qati->oi",
                dconv,
                act_sides[:, :, offset : offset + TB],
                preferred_element_type=jnp.float32,
            )
            for offset in range(taps)
        ]
    )


def per_device(features, conv_weight, keep, tiles, counts, targets):
    members, length, _ = features.shape
    owners, capacity = tiles.shape[1], tiles.shape[2]
    blocks = lax.axis_size("seq") * length // TB
    fits = members == 1 and targets.shape[1] == 1 and 2 * owners * capacity * TB <= length
    fits = fits and blocks <= 256 and capacity <= 256
    if fits:
        return sparse_path(features, conv_weight, keep, tiles, counts, targets)
    return dense_path(features, conv_weight, keep, tiles, counts, targets)


def solution(mesh):
    placed = (
        P("dp", "seq", None),
        P(None, "mp", None),
        P("dp"),
        P("dp", None, None, None),
        P("dp", None),
        P("dp", "seq", None, None),
    )
    return jax.shard_map(
        per_device,
        mesh=mesh,
        in_specs=placed,
        out_specs=P(None, "mp", ("seq", "dp")),
        check_vma=False,
    )
```

```python
import math

import jax
import jax.numpy as jnp
from jax import lax
from jax.sharding import PartitionSpec as P

TB = 32
PER = 2


def extended(cells, sides, width):
    for axis, dim in sides:
        count = lax.axis_size(axis)
        ends = count - 1
        head = lax.slice_in_dim(cells, 0, width, axis=dim)
        tail = lax.slice_in_dim(cells, cells.shape[dim] - width, cells.shape[dim], axis=dim)
        cells = jnp.concatenate(
            [
                lax.ppermute(tail, axis, [(i, (i + 1) % count) for i in range(ends)]),
                cells,
                lax.ppermute(head, axis, [((i + 1) % count, i) for i in range(ends)]),
            ],
            axis=dim,
        )
    return cells


def take_rows(source_array, index_array):
    return jax.vmap(lambda table, picked: table[picked])(source_array, index_array)


def conv_apply(padded, weight, length):
    total = jnp.einsum(
        "mbi,oi->mbo", padded[:, 0:length], weight[0], preferred_element_type=jnp.float32
    )
    for offset in range(1, weight.shape[0]):
        total = total + jnp.einsum(
            "mbi,oi->mbo",
            padded[:, offset : offset + length],
            weight[offset],
            preferred_element_type=jnp.float32,
        )
    return total


def weight_term(padded, dconv, length, taps):
    return jnp.stack(
        [
            jnp.einsum(
                "mbi,mbo->oi",
                padded[:, offset : offset + length],
                dconv,
                preferred_element_type=jnp.float32,
            )
            for offset in range(taps)
        ]
    )


def dense_path(features, conv_weight, keep, tiles, counts, targets):
    members, length, width = features.shape
    taps = conv_weight.shape[0]
    narrow = conv_weight.shape[1]
    seq_count = lax.axis_size("seq")
    my_index = lax.axis_index("seq")
    my_part = lax.axis_index("mp")
    x_float = features.astype(jnp.float32)
    activations = jax.nn.gelu(x_float).astype(jnp.bfloat16)
    padded = extended(activations, (("seq", 1),), 2)
    scaling = 1.25 * keep.astype(jnp.float32)
    conv_out = conv_apply(padded, conv_weight, length)
    x_local = lax.dynamic_slice_in_dim(x_float, my_part * narrow, narrow, 2)
    mixed_out = (x_local + scaling[:, None, None] * conv_out).astype(jnp.bfloat16)
    capacity = tiles.shape[2]
    n_sides = 2 * capacity
    per_block = length // TB
    sides = jnp.concatenate([tiles[..., 0], tiles[..., 1]], axis=-1)
    side_source = sides // per_block
    side_local = sides % per_block
    own_sides = lax.dynamic_index_in_dim(sides, my_index, 1, keepdims=False)
    own_source = own_sides // per_block
    before = jnp.arange(n_sides)[None, :] < jnp.arange(n_sides)[:, None]
    same_source = own_source[:, :, None] == own_source[:, None, :]
    rank_within = jnp.sum(jnp.logical_and(same_source, before[None]), axis=-1)
    slot_index = own_source * PER + rank_within
    held_here = side_source == my_index
    held_order = jnp.cumsum(held_here.astype(jnp.int32), axis=-1) - 1
    picks = jnp.stack(
        [
            jnp.sum(
                jnp.where(jnp.logical_and(held_here, held_order == position), side_local, 0),
                axis=-1,
            )
            for position in range(PER)
        ],
        axis=-1,
    )
    blocks = mixed_out.reshape(members, per_block, TB, narrow)
    whole = lax.all_gather(blocks, "seq", axis=1, tiled=True)
    side_rows = take_rows(whole, own_sides)
    row_side = side_rows[:, :capacity]
    col_side = side_rows[:, capacity:]
    partial_tiles = jnp.einsum(
        "mcid,mcjd->mcij", row_side, col_side, preferred_element_type=jnp.float32
    )
    predicted = lax.psum(partial_tiles, "mp") / math.sqrt(width)
    target_tiles = targets[:, 0].reshape(members, capacity, TB, TB)
    own_count = lax.dynamic_index_in_dim(counts, my_index, 1, keepdims=False)
    live_mask = (jnp.arange(capacity)[None, :] < own_count[:, None]).astype(jnp.float32)
    n_live = jnp.sum(counts, axis=-1).astype(jnp.float32)
    dpredicted = (
        2.0
        / math.sqrt(width)
        * live_mask[:, :, None, None]
        * (predicted - target_tiles)
        / n_live[:, None, None, None]
    )
    row_float = row_side.astype(jnp.float32)
    col_float = col_side.astype(jnp.float32)
    drow = jnp.einsum("mcij,mcjd->mcid", dpredicted, col_float, precision=lax.Precision.HIGHEST)
    dcol = jnp.einsum("mcij,mcid->mcjd", dpredicted, row_float, precision=lax.Precision.HIGHEST)
    dside = jnp.concatenate([drow, dcol], axis=1).astype(jnp.bfloat16)
    inverse = jnp.argsort(slot_index, axis=-1)
    outgoing_grads = take_rows(dside, inverse).reshape(members, seq_count, PER, TB, narrow)
    returned = lax.all_to_all(outgoing_grads, "seq", split_axis=1, concat_axis=1, tiled=True)
    selector = (
        picks.reshape(members, seq_count * PER)[:, :, None] == jnp.arange(per_block)[None, None, :]
    ).astype(jnp.bfloat16)
    dmixed = jnp.einsum(
        "mkn,mktd->mntd",
        selector,
        returned.reshape(members, seq_count * PER, TB, narrow),
        preferred_element_type=jnp.float32,
    ).reshape(members, length, narrow)
    dconv = (scaling[:, None, None] * dmixed).astype(jnp.bfloat16)
    weight_local = weight_term(padded, dconv, length, taps)
    return lax.psum_scatter(weight_local, ("seq", "dp"), scatter_dimension=2, tiled=True)


def axis_sum(value, axis):
    count = lax.axis_size(axis)
    total = value
    for shift in range(1, count):
        total = total + lax.ppermute(value, axis, [(i, (i + shift) % count) for i in range(count)])
    return total


def sparse_path(features, conv_weight, keep, tiles, counts, targets):
    _, length, width = features.shape
    taps, narrow, _ = conv_weight.shape
    halo = taps // 2
    span = TB + 2 * halo
    owners, capacity = tiles.shape[1], tiles.shape[2]
    n_sides = 2 * capacity
    per_block = length // TB
    seq_count = lax.axis_size("seq")
    groups = lax.axis_size("dp")
    peers = seq_count * groups
    held = owners * PER
    cols = width // peers
    my_index = lax.axis_index("seq")
    my_part = lax.axis_index("mp")

    before = jnp.arange(n_sides)[None, :] < jnp.arange(n_sides)[:, None]
    own_sides = jnp.concatenate([tiles[0, ..., 0], tiles[0, ..., 1]], axis=-1)
    own_source = own_sides // per_block
    own_same = own_source[:, :, None] == own_source[:, None, :]
    own_rank = jnp.sum(jnp.logical_and(own_same, before), axis=-1)
    held_here = own_source == my_index
    picks = jnp.stack(
        [
            jnp.sum(jnp.where(jnp.logical_and(held_here, own_rank == r), own_sides % per_block, 0), axis=-1)
            for r in range(PER)
        ],
        axis=-1,
    ).reshape(held)

    cells = features[0]
    ends = seq_count - 1
    if seq_count == 2:
        swapped = lax.ppermute(
            jnp.concatenate([cells[length - halo :], cells[:halo]]), "seq", [(0, 1), (1, 0)]
        )
        head = jnp.where(my_index == 0, jnp.zeros_like(swapped[:halo]), swapped[:halo])
        tail = jnp.where(my_index == ends, jnp.zeros_like(swapped[halo:]), swapped[halo:])
    else:
        head = lax.ppermute(cells[length - halo :], "seq", [(i, i + 1) for i in range(ends)])
        tail = lax.ppermute(cells[:halo], "seq", [(i + 1, i) for i in range(ends)])
    rows = picks[:, None] * TB - halo + jnp.arange(span)[None, :]
    inside = jnp.take(cells, jnp.clip(rows, 0, length - 1), axis=0)
    edge_rows = jnp.concatenate([head, tail], axis=0)
    edge_index = jnp.where(rows < 0, rows + halo, rows - length + halo)
    outside = jnp.take(edge_rows, jnp.clip(edge_index, 0, 2 * halo - 1), axis=0)
    in_range = jnp.logical_and(rows >= 0, rows < length)
    windows = jnp.where(in_range[..., None], inside, outside)
    x_float = windows.astype(jnp.float32)
    act = jax.nn.gelu(x_float).astype(jnp.bfloat16)
    conv_out = jnp.einsum("hti,oi->hto", act[:, 0:TB], conv_weight[0], preferred_element_type=jnp.float32)
    for offset in range(1, taps):
        conv_out = conv_out + jnp.einsum(
            "hti,oi->hto", act[:, offset : offset + TB], conv_weight[offset], preferred_element_type=jnp.float32
        )
    my_scale = 1.25 * keep[0].astype(jnp.float32)
    x_part = lax.dynamic_slice_in_dim(x_float[:, halo : halo + TB], my_part * narrow, narrow, 2)
    mixed = (x_part + my_scale * conv_out).astype(jnp.bfloat16)

    def lanes(part):
        flat = part.reshape(part.shape[0], -1)
        flat = jnp.pad(flat, ((0, 0), (0, -flat.shape[1] % 128)))
        return flat.reshape(flat.shape[0], -1, 128)

    act_cut = lanes(act.reshape(held, span, peers, cols).transpose(2, 0, 1, 3))
    mixed_part = lanes(mixed.reshape(1, -1))
    wide = targets.reshape(-1)
    pieces = []
    for _ in range(3):
        piece = lax.reduce_precision(wide, exponent_bits=8, mantissa_bits=7)
        pieces.append(piece)
        wide = wide - piece
    small = jnp.concatenate([tiles.reshape(-1), counts.reshape(-1), keep.reshape(-1)]).astype(jnp.float32)
    meta_part = lanes(jnp.concatenate(pieces + [small]).astype(jnp.bfloat16).reshape(1, -1))
    rows_mixed, rows_act, rows_meta = mixed_part.shape[1], act_cut.shape[1], meta_part.shape[1]
    outgoing = jnp.concatenate(
        [
            jnp.broadcast_to(mixed_part, (peers, rows_mixed, 128)),
            act_cut,
            jnp.broadcast_to(meta_part, (peers, rows_meta, 128)),
        ],
        axis=1,
    )
    outgoing = jnp.pad(outgoing, ((0, 0), (0, -outgoing.shape[1] % 16), (0, 0)))
    incoming = lax.all_to_all(outgoing, ("seq", "dp"), 0, 0, tiled=True)
    n_mixed = held * TB * narrow
    n_act = held * span * cols
    mixed_in = incoming[:, :rows_mixed].reshape(peers, -1)[:, :n_mixed].reshape(peers * held, TB, narrow)
    act_in = incoming[:, rows_mixed : rows_mixed + rows_act].reshape(peers, -1)[:, :n_act]
    act_in = act_in.reshape(peers * held, span, cols)
    meta_in = incoming[:, rows_mixed + rows_act : rows_mixed + rows_act + rows_meta].reshape(peers, -1)
    meta_in = meta_in.astype(jnp.float32).reshape(seq_count, groups, -1)
    n_targets = capacity * TB * TB
    n_tiles = owners * capacity * 2
    targets_all = meta_in[:, :, :n_targets] + meta_in[:, :, n_targets : 2 * n_targets]
    targets_all = targets_all + meta_in[:, :, 2 * n_targets : 3 * n_targets]
    ints = meta_in[0, :, 3 * n_targets :].astype(jnp.int32)
    tiles_all = ints[:, :n_tiles].reshape(groups, owners, capacity, 2)
    counts_all = ints[:, n_tiles : n_tiles + owners]
    keep_all = ints[:, n_tiles + owners]

    sides = jnp.concatenate([tiles_all[..., 0], tiles_all[..., 1]], axis=-1)
    source = sides // per_block
    local = sides % per_block
    same_source = source[..., :, None] == source[..., None, :]
    rank = jnp.sum(jnp.logical_and(same_source, before), axis=-1)
    slot = (source * groups + jnp.arange(groups)[:, None, None]) * held + jnp.arange(owners)[None, :, None] * PER + rank

    side_rows = jnp.take(mixed_in, slot, axis=0)
    row_side = side_rows[:, :, :capacity]
    col_side = side_rows[:, :, capacity:]
    partial_tiles = jnp.einsum("qocid,qocjd->qocij", row_side, col_side, preferred_element_type=jnp.float32)
    lanes_shape = partial_tiles.shape
    summed = axis_sum(partial_tiles.reshape(-1, 128), "mp").reshape(lanes_shape)
    predicted = summed / math.sqrt(width)
    target_tiles = targets_all.reshape(seq_count, groups, capacity, TB, TB).transpose(1, 0, 2, 3, 4)
    live_mask = (jnp.arange(capacity)[None, None, :] < counts_all[:, :, None]).astype(jnp.float32)
    n_live = jnp.sum(counts_all, axis=-1).astype(jnp.float32)
    dpredicted = (
        2.0
        / math.sqrt(width)
        * live_mask[..., None, None]
        * (predicted - target_tiles)
        / n_live[:, None, None, None, None]
    )
    row_float = row_side.astype(jnp.float32)
    col_float = col_side.astype(jnp.float32)
    drow = jnp.einsum("qocij,qocjd->qocid", dpredicted, col_float, precision=lax.Precision.HIGHEST)
    dcol = jnp.einsum("qocij,qocid->qocjd", dpredicted, row_float, precision=lax.Precision.HIGHEST)
    grads = jnp.concatenate([drow, dcol], axis=2).astype(jnp.bfloat16).astype(jnp.float32)
    grads = grads.reshape(groups, owners * n_sides, TB, narrow)
    flat_sides = sides.reshape(groups, owners * n_sides)
    same_block = flat_sides[:, :, None] == flat_sides[:, None, :]
    total = jnp.sum(jnp.where(same_block[..., None, None], grads[:, None], 0.0), axis=2)
    earlier = jnp.arange(owners * n_sides)[None, :] < jnp.arange(owners * n_sides)[:, None]
    first = jnp.logical_not(jnp.any(jnp.logical_and(same_block, earlier[None]), axis=-1))
    scaling = 1.25 * keep_all.astype(jnp.float32)
    dconv = (scaling[:, None, None, None] * total).astype(jnp.bfloat16)
    dconv = jnp.where(first[..., None, None], dconv, jnp.zeros_like(dconv))
    act_sides = jnp.take(act_in, slot.reshape(groups, owners * n_sides), axis=0)
    return jnp.stack(
        [
            jnp.einsum(
                "qato,qati->oi",
                dconv,
                act_sides[:, :, offset : offset + TB],
                preferred_element_type=jnp.float32,
            )
            for offset in range(taps)
        ]
    )


def per_device(features, conv_weight, keep, tiles, counts, targets):
    members, length, _ = features.shape
    owners, capacity = tiles.shape[1], tiles.shape[2]
    blocks = lax.axis_size("seq") * length // TB
    fits = members == 1 and targets.shape[1] == 1 and 2 * owners * capacity * TB <= length
    fits = fits and blocks <= 256 and capacity <= 256
    if fits:
        return sparse_path(features, conv_weight, keep, tiles, counts, targets)
    return dense_path(features, conv_weight, keep, tiles, counts, targets)


def solution(mesh):
    placed = (
        P("dp", "seq", None),
        P(None, "mp", None),
        P("dp"),
        P("dp", None, None, None),
        P("dp", None),
        P("dp", "seq", None, None),
    )
    return jax.shard_map(
        per_device,
        mesh=mesh,
        in_specs=placed,
        out_specs=P(None, "mp", ("seq", "dp")),
        check_vma=False,
    )
```

```python
import math

import jax
import jax.numpy as jnp
from jax import lax
from jax.sharding import PartitionSpec as P

TB = 32
PER = 2


def extended(cells, sides, width):
    for axis, dim in sides:
        count = lax.axis_size(axis)
        ends = count - 1
        head = lax.slice_in_dim(cells, 0, width, axis=dim)
        tail = lax.slice_in_dim(cells, cells.shape[dim] - width, cells.shape[dim], axis=dim)
        cells = jnp.concatenate(
            [
                lax.ppermute(tail, axis, [(i, (i + 1) % count) for i in range(ends)]),
                cells,
                lax.ppermute(head, axis, [((i + 1) % count, i) for i in range(ends)]),
            ],
            axis=dim,
        )
    return cells


def take_rows(source_array, index_array):
    return jax.vmap(lambda table, picked: table[picked])(source_array, index_array)


def conv_apply(padded, weight, length):
    total = jnp.einsum(
        "mbi,oi->mbo", padded[:, 0:length], weight[0], preferred_element_type=jnp.float32
    )
    for offset in range(1, weight.shape[0]):
        total = total + jnp.einsum(
            "mbi,oi->mbo",
            padded[:, offset : offset + length],
            weight[offset],
            preferred_element_type=jnp.float32,
        )
    return total


def weight_term(padded, dconv, length, taps):
    return jnp.stack(
        [
            jnp.einsum(
                "mbi,mbo->oi",
                padded[:, offset : offset + length],
                dconv,
                preferred_element_type=jnp.float32,
            )
            for offset in range(taps)
        ]
    )


def dense_path(features, conv_weight, keep, tiles, counts, targets):
    members, length, width = features.shape
    taps = conv_weight.shape[0]
    narrow = conv_weight.shape[1]
    seq_count = lax.axis_size("seq")
    my_index = lax.axis_index("seq")
    my_part = lax.axis_index("mp")
    x_float = features.astype(jnp.float32)
    activations = jax.nn.gelu(x_float).astype(jnp.bfloat16)
    padded = extended(activations, (("seq", 1),), 2)
    scaling = 1.25 * keep.astype(jnp.float32)
    conv_out = conv_apply(padded, conv_weight, length)
    x_local = lax.dynamic_slice_in_dim(x_float, my_part * narrow, narrow, 2)
    mixed_out = (x_local + scaling[:, None, None] * conv_out).astype(jnp.bfloat16)
    capacity = tiles.shape[2]
    n_sides = 2 * capacity
    per_block = length // TB
    sides = jnp.concatenate([tiles[..., 0], tiles[..., 1]], axis=-1)
    side_source = sides // per_block
    side_local = sides % per_block
    own_sides = lax.dynamic_index_in_dim(sides, my_index, 1, keepdims=False)
    own_source = own_sides // per_block
    before = jnp.arange(n_sides)[None, :] < jnp.arange(n_sides)[:, None]
    same_source = own_source[:, :, None] == own_source[:, None, :]
    rank_within = jnp.sum(jnp.logical_and(same_source, before[None]), axis=-1)
    slot_index = own_source * PER + rank_within
    held_here = side_source == my_index
    held_order = jnp.cumsum(held_here.astype(jnp.int32), axis=-1) - 1
    picks = jnp.stack(
        [
            jnp.sum(
                jnp.where(jnp.logical_and(held_here, held_order == position), side_local, 0),
                axis=-1,
            )
            for position in range(PER)
        ],
        axis=-1,
    )
    blocks = mixed_out.reshape(members, per_block, TB, narrow)
    whole = lax.all_gather(blocks, "seq", axis=1, tiled=True)
    side_rows = take_rows(whole, own_sides)
    row_side = side_rows[:, :capacity]
    col_side = side_rows[:, capacity:]
    partial_tiles = jnp.einsum(
        "mcid,mcjd->mcij", row_side, col_side, preferred_element_type=jnp.float32
    )
    predicted = lax.psum(partial_tiles, "mp") / math.sqrt(width)
    target_tiles = targets[:, 0].reshape(members, capacity, TB, TB)
    own_count = lax.dynamic_index_in_dim(counts, my_index, 1, keepdims=False)
    live_mask = (jnp.arange(capacity)[None, :] < own_count[:, None]).astype(jnp.float32)
    n_live = jnp.sum(counts, axis=-1).astype(jnp.float32)
    dpredicted = (
        2.0
        / math.sqrt(width)
        * live_mask[:, :, None, None]
        * (predicted - target_tiles)
        / n_live[:, None, None, None]
    )
    row_float = row_side.astype(jnp.float32)
    col_float = col_side.astype(jnp.float32)
    drow = jnp.einsum("mcij,mcjd->mcid", dpredicted, col_float, precision=lax.Precision.HIGHEST)
    dcol = jnp.einsum("mcij,mcid->mcjd", dpredicted, row_float, precision=lax.Precision.HIGHEST)
    dside = jnp.concatenate([drow, dcol], axis=1).astype(jnp.bfloat16)
    inverse = jnp.argsort(slot_index, axis=-1)
    outgoing_grads = take_rows(dside, inverse).reshape(members, seq_count, PER, TB, narrow)
    returned = lax.all_to_all(outgoing_grads, "seq", split_axis=1, concat_axis=1, tiled=True)
    selector = (
        picks.reshape(members, seq_count * PER)[:, :, None] == jnp.arange(per_block)[None, None, :]
    ).astype(jnp.bfloat16)
    dmixed = jnp.einsum(
        "mkn,mktd->mntd",
        selector,
        returned.reshape(members, seq_count * PER, TB, narrow),
        preferred_element_type=jnp.float32,
    ).reshape(members, length, narrow)
    dconv = (scaling[:, None, None] * dmixed).astype(jnp.bfloat16)
    weight_local = weight_term(padded, dconv, length, taps)
    return lax.psum_scatter(weight_local, ("seq", "dp"), scatter_dimension=2, tiled=True)


def axis_sum(value, axis):
    count = lax.axis_size(axis)
    total = value
    for shift in range(1, count):
        total = total + lax.ppermute(value, axis, [(i, (i + shift) % count) for i in range(count)])
    return total


def sparse_path(features, conv_weight, keep, tiles, counts, targets):
    _, length, width = features.shape
    taps, narrow, _ = conv_weight.shape
    halo = taps // 2
    span = TB + 2 * halo
    owners, capacity = tiles.shape[1], tiles.shape[2]
    n_sides = 2 * capacity
    per_block = length // TB
    seq_count = lax.axis_size("seq")
    groups = lax.axis_size("dp")
    peers = seq_count * groups
    held = owners * PER
    cols = width // peers
    my_index = lax.axis_index("seq")
    my_part = lax.axis_index("mp")

    before = jnp.arange(n_sides)[None, :] < jnp.arange(n_sides)[:, None]
    own_sides = jnp.concatenate([tiles[0, ..., 0], tiles[0, ..., 1]], axis=-1)
    own_source = own_sides // per_block
    own_same = own_source[:, :, None] == own_source[:, None, :]
    own_rank = jnp.sum(jnp.logical_and(own_same, before), axis=-1)
    held_here = own_source == my_index
    picks = jnp.stack(
        [
            jnp.sum(jnp.where(jnp.logical_and(held_here, own_rank == r), own_sides % per_block, 0), axis=-1)
            for r in range(PER)
        ],
        axis=-1,
    ).reshape(held)

    cells = features[0]
    ends = seq_count - 1
    if seq_count == 2:
        swapped = lax.ppermute(
            jnp.concatenate([cells[length - halo :], cells[:halo]]), "seq", [(0, 1), (1, 0)]
        )
        head = jnp.where(my_index == 0, jnp.zeros_like(swapped[:halo]), swapped[:halo])
        tail = jnp.where(my_index == ends, jnp.zeros_like(swapped[halo:]), swapped[halo:])
    else:
        head = lax.ppermute(cells[length - halo :], "seq", [(i, i + 1) for i in range(ends)])
        tail = lax.ppermute(cells[:halo], "seq", [(i + 1, i) for i in range(ends)])
    rows = picks[:, None] * TB - halo + jnp.arange(span)[None, :]
    flat_rows = rows.reshape(-1)
    pick_inside = (flat_rows[:, None] == jnp.arange(length)[None, :]).astype(cells.dtype)
    inside = jnp.dot(pick_inside, cells, preferred_element_type=jnp.float32)
    edge_rows = jnp.concatenate([head, tail], axis=0)
    edge_index = jnp.where(flat_rows < 0, flat_rows + halo, flat_rows - length + halo)
    in_range = jnp.logical_and(flat_rows >= 0, flat_rows < length)
    pick_edge = jnp.logical_and(
        edge_index[:, None] == jnp.arange(2 * halo)[None, :], jnp.logical_not(in_range)[:, None]
    ).astype(cells.dtype)
    outside = jnp.dot(pick_edge, edge_rows, preferred_element_type=jnp.float32)
    windows = (inside + outside).astype(cells.dtype).reshape(held, span, width)
    x_float = windows.astype(jnp.float32)
    act = jax.nn.gelu(x_float).astype(jnp.bfloat16)
    conv_out = jnp.einsum("hti,oi->hto", act[:, 0:TB], conv_weight[0], preferred_element_type=jnp.float32)
    for offset in range(1, taps):
        conv_out = conv_out + jnp.einsum(
            "hti,oi->hto", act[:, offset : offset + TB], conv_weight[offset], preferred_element_type=jnp.float32
        )
    my_scale = 1.25 * keep[0].astype(jnp.float32)
    x_part = lax.dynamic_slice_in_dim(x_float[:, halo : halo + TB], my_part * narrow, narrow, 2)
    mixed = (x_part + my_scale * conv_out).astype(jnp.bfloat16)

    def lanes(part):
        flat = part.reshape(part.shape[0], -1)
        flat = jnp.pad(flat, ((0, 0), (0, -flat.shape[1] % 128)))
        return flat.reshape(flat.shape[0], -1, 128)

    act_cut = lanes(act.reshape(held, span, peers, cols).transpose(2, 0, 1, 3))
    mixed_part = lanes(mixed.reshape(1, -1))
    wide = targets.reshape(-1)
    pieces = []
    for _ in range(3):
        piece = lax.reduce_precision(wide, exponent_bits=8, mantissa_bits=7)
        pieces.append(piece)
        wide = wide - piece
    small = jnp.concatenate([tiles.reshape(-1), counts.reshape(-1), keep.reshape(-1)]).astype(jnp.float32)
    meta_part = lanes(jnp.concatenate(pieces + [small]).astype(jnp.bfloat16).reshape(1, -1))
    rows_mixed, rows_act, rows_meta = mixed_part.shape[1], act_cut.shape[1], meta_part.shape[1]
    outgoing = jnp.concatenate(
        [
            jnp.broadcast_to(mixed_part, (peers, rows_mixed, 128)),
            act_cut,
            jnp.broadcast_to(meta_part, (peers, rows_meta, 128)),
        ],
        axis=1,
    )
    outgoing = jnp.pad(outgoing, ((0, 0), (0, -outgoing.shape[1] % 16), (0, 0)))
    incoming = lax.all_to_all(outgoing, ("seq", "dp"), 0, 0, tiled=True)
    n_mixed = held * TB * narrow
    n_act = held * span * cols
    mixed_in = incoming[:, :rows_mixed].reshape(peers, -1)[:, :n_mixed].reshape(peers * held, TB, narrow)
    act_in = incoming[:, rows_mixed : rows_mixed + rows_act].reshape(peers, -1)[:, :n_act]
    act_in = act_in.reshape(peers * held, span, cols)
    meta_in = incoming[:, rows_mixed + rows_act : rows_mixed + rows_act + rows_meta].reshape(peers, -1)
    meta_in = meta_in.astype(jnp.float32).reshape(seq_count, groups, -1)
    n_targets = capacity * TB * TB
    n_tiles = owners * capacity * 2
    targets_all = meta_in[:, :, :n_targets] + meta_in[:, :, n_targets : 2 * n_targets]
    targets_all = targets_all + meta_in[:, :, 2 * n_targets : 3 * n_targets]
    ints = meta_in[0, :, 3 * n_targets :].astype(jnp.int32)
    tiles_all = ints[:, :n_tiles].reshape(groups, owners, capacity, 2)
    counts_all = ints[:, n_tiles : n_tiles + owners]
    keep_all = ints[:, n_tiles + owners]

    sides = jnp.concatenate([tiles_all[..., 0], tiles_all[..., 1]], axis=-1)
    source = sides // per_block
    local = sides % per_block
    same_source = source[..., :, None] == source[..., None, :]
    rank = jnp.sum(jnp.logical_and(same_source, before), axis=-1)
    slot = (source * groups + jnp.arange(groups)[:, None, None]) * held + jnp.arange(owners)[None, :, None] * PER + rank

    side_rows = jnp.take(mixed_in, slot, axis=0)
    row_side = side_rows[:, :, :capacity]
    col_side = side_rows[:, :, capacity:]
    partial_tiles = jnp.einsum("qocid,qocjd->qocij", row_side, col_side, preferred_element_type=jnp.float32)
    lanes_shape = partial_tiles.shape
    summed = axis_sum(partial_tiles.reshape(-1, 128), "mp").reshape(lanes_shape)
    predicted = summed / math.sqrt(width)
    target_tiles = targets_all.reshape(seq_count, groups, capacity, TB, TB).transpose(1, 0, 2, 3, 4)
    live_mask = (jnp.arange(capacity)[None, None, :] < counts_all[:, :, None]).astype(jnp.float32)
    n_live = jnp.sum(counts_all, axis=-1).astype(jnp.float32)
    dpredicted = (
        2.0
        / math.sqrt(width)
        * live_mask[..., None, None]
        * (predicted - target_tiles)
        / n_live[:, None, None, None, None]
    )
    row_float = row_side.astype(jnp.float32)
    col_float = col_side.astype(jnp.float32)
    drow = jnp.einsum("qocij,qocjd->qocid", dpredicted, col_float, precision=lax.Precision.HIGHEST)
    dcol = jnp.einsum("qocij,qocid->qocjd", dpredicted, row_float, precision=lax.Precision.HIGHEST)
    grads = jnp.concatenate([drow, dcol], axis=2).astype(jnp.bfloat16).astype(jnp.float32)
    grads = grads.reshape(groups, owners * n_sides, TB, narrow)
    flat_sides = sides.reshape(groups, owners * n_sides)
    same_block = flat_sides[:, :, None] == flat_sides[:, None, :]
    total = jnp.einsum(
        "qab,qbtd->qatd", same_block.astype(jnp.float32), grads, precision=lax.Precision.HIGHEST
    )
    earlier = jnp.arange(owners * n_sides)[None, :] < jnp.arange(owners * n_sides)[:, None]
    first = jnp.logical_not(jnp.any(jnp.logical_and(same_block, earlier[None]), axis=-1))
    scaling = 1.25 * keep_all.astype(jnp.float32)
    dconv = (scaling[:, None, None, None] * total).astype(jnp.bfloat16)
    dconv = jnp.where(first[..., None, None], dconv, jnp.zeros_like(dconv))
    act_sides = jnp.take(act_in, slot.reshape(groups, owners * n_sides), axis=0)
    return jnp.stack(
        [
            jnp.einsum(
                "qato,qati->oi",
                dconv,
                act_sides[:, :, offset : offset + TB],
                preferred_element_type=jnp.float32,
            )
            for offset in range(taps)
        ]
    )


def per_device(features, conv_weight, keep, tiles, counts, targets):
    members, length, _ = features.shape
    owners, capacity = tiles.shape[1], tiles.shape[2]
    blocks = lax.axis_size("seq") * length // TB
    fits = members == 1 and targets.shape[1] == 1 and 2 * owners * capacity * TB <= length
    fits = fits and blocks <= 256 and capacity <= 256
    if fits:
        return sparse_path(features, conv_weight, keep, tiles, counts, targets)
    return dense_path(features, conv_weight, keep, tiles, counts, targets)


def solution(mesh):
    placed = (
        P("dp", "seq", None),
        P(None, "mp", None),
        P("dp"),
        P("dp", None, None, None),
        P("dp", None),
        P("dp", "seq", None, None),
    )
    return jax.shard_map(
        per_device,
        mesh=mesh,
        in_specs=placed,
        out_specs=P(None, "mp", ("seq", "dp")),
        check_vma=False,
    )
```

```python
import math

import jax
import jax.numpy as jnp
from jax import lax
from jax.sharding import PartitionSpec as P

TB = 32
PER = 2


def extended(cells, sides, width):
    for axis, dim in sides:
        count = lax.axis_size(axis)
        ends = count - 1
        head = lax.slice_in_dim(cells, 0, width, axis=dim)
        tail = lax.slice_in_dim(cells, cells.shape[dim] - width, cells.shape[dim], axis=dim)
        cells = jnp.concatenate(
            [
                lax.ppermute(tail, axis, [(i, (i + 1) % count) for i in range(ends)]),
                cells,
                lax.ppermute(head, axis, [((i + 1) % count, i) for i in range(ends)]),
            ],
            axis=dim,
        )
    return cells


def take_rows(source_array, index_array):
    return jax.vmap(lambda table, picked: table[picked])(source_array, index_array)


def conv_apply(padded, weight, length):
    total = jnp.einsum(
        "mbi,oi->mbo", padded[:, 0:length], weight[0], preferred_element_type=jnp.float32
    )
    for offset in range(1, weight.shape[0]):
        total = total + jnp.einsum(
            "mbi,oi->mbo",
            padded[:, offset : offset + length],
            weight[offset],
            preferred_element_type=jnp.float32,
        )
    return total


def weight_term(padded, dconv, length, taps):
    return jnp.stack(
        [
            jnp.einsum(
                "mbi,mbo->oi",
                padded[:, offset : offset + length],
                dconv,
                preferred_element_type=jnp.float32,
            )
            for offset in range(taps)
        ]
    )


def dense_path(features, conv_weight, keep, tiles, counts, targets):
    members, length, width = features.shape
    taps = conv_weight.shape[0]
    narrow = conv_weight.shape[1]
    seq_count = lax.axis_size("seq")
    my_index = lax.axis_index("seq")
    my_part = lax.axis_index("mp")
    x_float = features.astype(jnp.float32)
    activations = jax.nn.gelu(x_float).astype(jnp.bfloat16)
    padded = extended(activations, (("seq", 1),), 2)
    scaling = 1.25 * keep.astype(jnp.float32)
    conv_out = conv_apply(padded, conv_weight, length)
    x_local = lax.dynamic_slice_in_dim(x_float, my_part * narrow, narrow, 2)
    mixed_out = (x_local + scaling[:, None, None] * conv_out).astype(jnp.bfloat16)
    capacity = tiles.shape[2]
    n_sides = 2 * capacity
    per_block = length // TB
    sides = jnp.concatenate([tiles[..., 0], tiles[..., 1]], axis=-1)
    side_source = sides // per_block
    side_local = sides % per_block
    own_sides = lax.dynamic_index_in_dim(sides, my_index, 1, keepdims=False)
    own_source = own_sides // per_block
    before = jnp.arange(n_sides)[None, :] < jnp.arange(n_sides)[:, None]
    same_source = own_source[:, :, None] == own_source[:, None, :]
    rank_within = jnp.sum(jnp.logical_and(same_source, before[None]), axis=-1)
    slot_index = own_source * PER + rank_within
    held_here = side_source == my_index
    held_order = jnp.cumsum(held_here.astype(jnp.int32), axis=-1) - 1
    picks = jnp.stack(
        [
            jnp.sum(
                jnp.where(jnp.logical_and(held_here, held_order == position), side_local, 0),
                axis=-1,
            )
            for position in range(PER)
        ],
        axis=-1,
    )
    blocks = mixed_out.reshape(members, per_block, TB, narrow)
    whole = lax.all_gather(blocks, "seq", axis=1, tiled=True)
    side_rows = take_rows(whole, own_sides)
    row_side = side_rows[:, :capacity]
    col_side = side_rows[:, capacity:]
    partial_tiles = jnp.einsum(
        "mcid,mcjd->mcij", row_side, col_side, preferred_element_type=jnp.float32
    )
    predicted = lax.psum(partial_tiles, "mp") / math.sqrt(width)
    target_tiles = targets[:, 0].reshape(members, capacity, TB, TB)
    own_count = lax.dynamic_index_in_dim(counts, my_index, 1, keepdims=False)
    live_mask = (jnp.arange(capacity)[None, :] < own_count[:, None]).astype(jnp.float32)
    n_live = jnp.sum(counts, axis=-1).astype(jnp.float32)
    dpredicted = (
        2.0
        / math.sqrt(width)
        * live_mask[:, :, None, None]
        * (predicted - target_tiles)
        / n_live[:, None, None, None]
    )
    row_float = row_side.astype(jnp.float32)
    col_float = col_side.astype(jnp.float32)
    drow = jnp.einsum("mcij,mcjd->mcid", dpredicted, col_float, precision=lax.Precision.HIGHEST)
    dcol = jnp.einsum("mcij,mcid->mcjd", dpredicted, row_float, precision=lax.Precision.HIGHEST)
    dside = jnp.concatenate([drow, dcol], axis=1).astype(jnp.bfloat16)
    inverse = jnp.argsort(slot_index, axis=-1)
    outgoing_grads = take_rows(dside, inverse).reshape(members, seq_count, PER, TB, narrow)
    returned = lax.all_to_all(outgoing_grads, "seq", split_axis=1, concat_axis=1, tiled=True)
    selector = (
        picks.reshape(members, seq_count * PER)[:, :, None] == jnp.arange(per_block)[None, None, :]
    ).astype(jnp.bfloat16)
    dmixed = jnp.einsum(
        "mkn,mktd->mntd",
        selector,
        returned.reshape(members, seq_count * PER, TB, narrow),
        preferred_element_type=jnp.float32,
    ).reshape(members, length, narrow)
    dconv = (scaling[:, None, None] * dmixed).astype(jnp.bfloat16)
    weight_local = weight_term(padded, dconv, length, taps)
    return lax.psum_scatter(weight_local, ("seq", "dp"), scatter_dimension=2, tiled=True)


def axis_sum(value, axis):
    count = lax.axis_size(axis)
    total = value
    for shift in range(1, count):
        total = total + lax.ppermute(value, axis, [(i, (i + shift) % count) for i in range(count)])
    return total


def sparse_path(features, conv_weight, keep, tiles, counts, targets):
    _, length, width = features.shape
    taps, narrow, _ = conv_weight.shape
    halo = taps // 2
    span = TB + 2 * halo
    owners, capacity = tiles.shape[1], tiles.shape[2]
    n_sides = 2 * capacity
    per_block = length // TB
    seq_count = lax.axis_size("seq")
    groups = lax.axis_size("dp")
    peers = seq_count * groups
    held = owners * PER
    cols = width // peers
    my_index = lax.axis_index("seq")
    my_part = lax.axis_index("mp")

    before = jnp.arange(n_sides)[None, :] < jnp.arange(n_sides)[:, None]
    own_sides = jnp.concatenate([tiles[0, ..., 0], tiles[0, ..., 1]], axis=-1)
    own_source = own_sides // per_block
    own_same = own_source[:, :, None] == own_source[:, None, :]
    own_rank = jnp.sum(jnp.logical_and(own_same, before), axis=-1)
    held_here = own_source == my_index
    picks = jnp.stack(
        [
            jnp.sum(jnp.where(jnp.logical_and(held_here, own_rank == r), own_sides % per_block, 0), axis=-1)
            for r in range(PER)
        ],
        axis=-1,
    ).reshape(held)

    cells = features[0]
    ends = seq_count - 1
    if seq_count == 2:
        swapped = lax.ppermute(
            jnp.concatenate([cells[length - halo :], cells[:halo]]), "seq", [(0, 1), (1, 0)]
        )
        head = jnp.where(my_index == 0, jnp.zeros_like(swapped[:halo]), swapped[:halo])
        tail = jnp.where(my_index == ends, jnp.zeros_like(swapped[halo:]), swapped[halo:])
    else:
        head = lax.ppermute(cells[length - halo :], "seq", [(i, i + 1) for i in range(ends)])
        tail = lax.ppermute(cells[:halo], "seq", [(i + 1, i) for i in range(ends)])
    block_rows = (picks[:, None] * TB + jnp.arange(TB)[None, :]).reshape(-1)
    pick_block = (block_rows[:, None] == jnp.arange(length)[None, :]).astype(cells.dtype)
    block = jnp.dot(pick_block, cells, preferred_element_type=jnp.float32).reshape(held, TB, width)
    edge_offsets = jnp.concatenate([jnp.arange(-halo, 0), jnp.arange(TB, TB + halo)])
    edge_pos = (picks[:, None] * TB + edge_offsets[None, :]).reshape(-1)
    in_range = jnp.logical_and(edge_pos >= 0, edge_pos < length)
    pick_local = jnp.logical_and(edge_pos[:, None] == jnp.arange(length)[None, :], in_range[:, None])
    local_edges = jnp.dot(pick_local.astype(cells.dtype), cells, preferred_element_type=jnp.float32)
    halo_rows = jnp.concatenate([head, tail], axis=0)
    halo_index = jnp.where(edge_pos < 0, edge_pos + halo, edge_pos - length + halo)
    pick_halo = jnp.logical_and(
        halo_index[:, None] == jnp.arange(2 * halo)[None, :], jnp.logical_not(in_range)[:, None]
    ).astype(cells.dtype)
    halo_edges = jnp.dot(pick_halo, halo_rows, preferred_element_type=jnp.float32)
    edges = (local_edges + halo_edges).reshape(held, 2 * halo, width)

    act_block = jax.nn.gelu(block).astype(jnp.bfloat16)
    act_edges = jax.nn.gelu(edges).astype(jnp.bfloat16)

    def conv_rows(source, count):
        total = jnp.einsum(
            "hti,oi->hto", source[:, 0:count], conv_weight[0], preferred_element_type=jnp.float32
        )
        for offset in range(1, taps):
            total = total + jnp.einsum(
                "hti,oi->hto",
                source[:, offset : offset + count],
                conv_weight[offset],
                preferred_element_type=jnp.float32,
            )
        return total

    lower = jnp.concatenate([act_edges[:, :halo], act_block[:, : 2 * halo]], axis=1)
    upper = jnp.concatenate([act_block[:, TB - 2 * halo :], act_edges[:, halo:]], axis=1)
    conv_out = jnp.concatenate(
        [conv_rows(lower, halo), conv_rows(act_block, TB - 2 * halo), conv_rows(upper, halo)], axis=1
    )
    act = jnp.concatenate([act_edges[:, :halo], act_block, act_edges[:, halo:]], axis=1)
    my_scale = 1.25 * keep[0].astype(jnp.float32)
    x_part = lax.dynamic_slice_in_dim(block, my_part * narrow, narrow, 2)
    mixed = (x_part + my_scale * conv_out).astype(jnp.bfloat16)

    def lanes(part):
        flat = part.reshape(part.shape[0], -1)
        flat = jnp.pad(flat, ((0, 0), (0, -flat.shape[1] % 128)))
        return flat.reshape(flat.shape[0], -1, 128)

    act_cut = lanes(act.reshape(held, span, peers, cols).transpose(2, 0, 1, 3))
    mixed_part = lanes(mixed.reshape(1, -1))
    wide = targets.reshape(-1)
    pieces = []
    for _ in range(3):
        piece = lax.reduce_precision(wide, exponent_bits=8, mantissa_bits=7)
        pieces.append(piece)
        wide = wide - piece
    small = jnp.concatenate([tiles.reshape(-1), counts.reshape(-1), keep.reshape(-1)]).astype(jnp.float32)
    meta_part = lanes(jnp.concatenate(pieces + [small]).astype(jnp.bfloat16).reshape(1, -1))
    rows_mixed, rows_act, rows_meta = mixed_part.shape[1], act_cut.shape[1], meta_part.shape[1]
    outgoing = jnp.concatenate(
        [
            jnp.broadcast_to(mixed_part, (peers, rows_mixed, 128)),
            act_cut,
            jnp.broadcast_to(meta_part, (peers, rows_meta, 128)),
        ],
        axis=1,
    )
    outgoing = jnp.pad(outgoing, ((0, 0), (0, -outgoing.shape[1] % 16), (0, 0)))
    incoming = lax.all_to_all(outgoing, ("seq", "dp"), 0, 0, tiled=True)
    n_mixed = held * TB * narrow
    n_act = held * span * cols
    mixed_in = incoming[:, :rows_mixed].reshape(peers, -1)[:, :n_mixed].reshape(peers * held, TB, narrow)
    act_in = incoming[:, rows_mixed : rows_mixed + rows_act].reshape(peers, -1)[:, :n_act]
    act_in = act_in.reshape(peers * held, span, cols)
    meta_in = incoming[:, rows_mixed + rows_act : rows_mixed + rows_act + rows_meta].reshape(peers, -1)
    meta_in = meta_in.astype(jnp.float32).reshape(seq_count, groups, -1)
    n_targets = capacity * TB * TB
    n_tiles = owners * capacity * 2
    targets_all = meta_in[:, :, :n_targets] + meta_in[:, :, n_targets : 2 * n_targets]
    targets_all = targets_all + meta_in[:, :, 2 * n_targets : 3 * n_targets]
    ints = meta_in[0, :, 3 * n_targets :].astype(jnp.int32)
    tiles_all = ints[:, :n_tiles].reshape(groups, owners, capacity, 2)
    counts_all = ints[:, n_tiles : n_tiles + owners]
    keep_all = ints[:, n_tiles + owners]

    sides = jnp.concatenate([tiles_all[..., 0], tiles_all[..., 1]], axis=-1)
    source = sides // per_block
    local = sides % per_block
    same_source = source[..., :, None] == source[..., None, :]
    rank = jnp.sum(jnp.logical_and(same_source, before), axis=-1)
    slot = (source * groups + jnp.arange(groups)[:, None, None]) * held + jnp.arange(owners)[None, :, None] * PER + rank

    side_rows = jnp.take(mixed_in, slot, axis=0)
    row_side = side_rows[:, :, :capacity]
    col_side = side_rows[:, :, capacity:]
    partial_tiles = jnp.einsum("qocid,qocjd->qocij", row_side, col_side, preferred_element_type=jnp.float32)
    lanes_shape = partial_tiles.shape
    summed = axis_sum(partial_tiles.reshape(-1, 128), "mp").reshape(lanes_shape)
    predicted = summed / math.sqrt(width)
    target_tiles = targets_all.reshape(seq_count, groups, capacity, TB, TB).transpose(1, 0, 2, 3, 4)
    live_mask = (jnp.arange(capacity)[None, None, :] < counts_all[:, :, None]).astype(jnp.float32)
    n_live = jnp.sum(counts_all, axis=-1).astype(jnp.float32)
    dpredicted = (
        2.0
        / math.sqrt(width)
        * live_mask[..., None, None]
        * (predicted - target_tiles)
        / n_live[:, None, None, None, None]
    )
    row_float = row_side.astype(jnp.float32)
    col_float = col_side.astype(jnp.float32)
    drow = jnp.einsum("qocij,qocjd->qocid", dpredicted, col_float, precision=lax.Precision.HIGHEST)
    dcol = jnp.einsum("qocij,qocid->qocjd", dpredicted, row_float, precision=lax.Precision.HIGHEST)
    grads = jnp.concatenate([drow, dcol], axis=2).astype(jnp.bfloat16).astype(jnp.float32)
    grads = grads.reshape(groups, owners * n_sides, TB, narrow)
    flat_sides = sides.reshape(groups, owners * n_sides)
    same_block = flat_sides[:, :, None] == flat_sides[:, None, :]
    total = jnp.einsum(
        "qab,qbtd->qatd", same_block.astype(jnp.float32), grads, precision=lax.Precision.HIGHEST
    )
    earlier = jnp.arange(owners * n_sides)[None, :] < jnp.arange(owners * n_sides)[:, None]
    first = jnp.logical_not(jnp.any(jnp.logical_and(same_block, earlier[None]), axis=-1))
    scaling = 1.25 * keep_all.astype(jnp.float32)
    dconv = (scaling[:, None, None, None] * total).astype(jnp.bfloat16)
    dconv = jnp.where(first[..., None, None], dconv, jnp.zeros_like(dconv))
    act_sides = jnp.take(act_in, slot.reshape(groups, owners * n_sides), axis=0)
    return jnp.stack(
        [
            jnp.einsum(
                "qato,qati->oi",
                dconv,
                act_sides[:, :, offset : offset + TB],
                preferred_element_type=jnp.float32,
            )
            for offset in range(taps)
        ]
    )


def per_device(features, conv_weight, keep, tiles, counts, targets):
    members, length, _ = features.shape
    owners, capacity = tiles.shape[1], tiles.shape[2]
    blocks = lax.axis_size("seq") * length // TB
    fits = members == 1 and targets.shape[1] == 1 and 2 * owners * capacity * TB <= length
    fits = fits and blocks <= 256 and capacity <= 256
    if fits:
        return sparse_path(features, conv_weight, keep, tiles, counts, targets)
    return dense_path(features, conv_weight, keep, tiles, counts, targets)


def solution(mesh):
    placed = (
        P("dp", "seq", None),
        P(None, "mp", None),
        P("dp"),
        P("dp", None, None, None),
        P("dp", None),
        P("dp", "seq", None, None),
    )
    return jax.shard_map(
        per_device,
        mesh=mesh,
        in_specs=placed,
        out_specs=P(None, "mp", ("seq", "dp")),
        check_vma=False,
    )
```

```python
import math

import jax
import jax.numpy as jnp
from jax import lax
from jax.sharding import PartitionSpec as P

TB = 32
PER = 2


def extended(cells, sides, width):
    for axis, dim in sides:
        count = lax.axis_size(axis)
        ends = count - 1
        head = lax.slice_in_dim(cells, 0, width, axis=dim)
        tail = lax.slice_in_dim(cells, cells.shape[dim] - width, cells.shape[dim], axis=dim)
        cells = jnp.concatenate(
            [
                lax.ppermute(tail, axis, [(i, (i + 1) % count) for i in range(ends)]),
                cells,
                lax.ppermute(head, axis, [((i + 1) % count, i) for i in range(ends)]),
            ],
            axis=dim,
        )
    return cells


def take_rows(source_array, index_array):
    return jax.vmap(lambda table, picked: table[picked])(source_array, index_array)


def conv_apply(padded, weight, length):
    total = jnp.einsum(
        "mbi,oi->mbo", padded[:, 0:length], weight[0], preferred_element_type=jnp.float32
    )
    for offset in range(1, weight.shape[0]):
        total = total + jnp.einsum(
            "mbi,oi->mbo",
            padded[:, offset : offset + length],
            weight[offset],
            preferred_element_type=jnp.float32,
        )
    return total


def weight_term(padded, dconv, length, taps):
    return jnp.stack(
        [
            jnp.einsum(
                "mbi,mbo->oi",
                padded[:, offset : offset + length],
                dconv,
                preferred_element_type=jnp.float32,
            )
            for offset in range(taps)
        ]
    )


def dense_path(features, conv_weight, keep, tiles, counts, targets):
    members, length, width = features.shape
    taps = conv_weight.shape[0]
    narrow = conv_weight.shape[1]
    seq_count = lax.axis_size("seq")
    my_index = lax.axis_index("seq")
    my_part = lax.axis_index("mp")
    x_float = features.astype(jnp.float32)
    activations = jax.nn.gelu(x_float).astype(jnp.bfloat16)
    padded = extended(activations, (("seq", 1),), 2)
    scaling = 1.25 * keep.astype(jnp.float32)
    conv_out = conv_apply(padded, conv_weight, length)
    x_local = lax.dynamic_slice_in_dim(x_float, my_part * narrow, narrow, 2)
    mixed_out = (x_local + scaling[:, None, None] * conv_out).astype(jnp.bfloat16)
    capacity = tiles.shape[2]
    n_sides = 2 * capacity
    per_block = length // TB
    sides = jnp.concatenate([tiles[..., 0], tiles[..., 1]], axis=-1)
    side_source = sides // per_block
    side_local = sides % per_block
    own_sides = lax.dynamic_index_in_dim(sides, my_index, 1, keepdims=False)
    own_source = own_sides // per_block
    before = jnp.arange(n_sides)[None, :] < jnp.arange(n_sides)[:, None]
    same_source = own_source[:, :, None] == own_source[:, None, :]
    rank_within = jnp.sum(jnp.logical_and(same_source, before[None]), axis=-1)
    slot_index = own_source * PER + rank_within
    held_here = side_source == my_index
    held_order = jnp.cumsum(held_here.astype(jnp.int32), axis=-1) - 1
    picks = jnp.stack(
        [
            jnp.sum(
                jnp.where(jnp.logical_and(held_here, held_order == position), side_local, 0),
                axis=-1,
            )
            for position in range(PER)
        ],
        axis=-1,
    )
    blocks = mixed_out.reshape(members, per_block, TB, narrow)
    whole = lax.all_gather(blocks, "seq", axis=1, tiled=True)
    side_rows = take_rows(whole, own_sides)
    row_side = side_rows[:, :capacity]
    col_side = side_rows[:, capacity:]
    partial_tiles = jnp.einsum(
        "mcid,mcjd->mcij", row_side, col_side, preferred_element_type=jnp.float32
    )
    predicted = lax.psum(partial_tiles, "mp") / math.sqrt(width)
    target_tiles = targets[:, 0].reshape(members, capacity, TB, TB)
    own_count = lax.dynamic_index_in_dim(counts, my_index, 1, keepdims=False)
    live_mask = (jnp.arange(capacity)[None, :] < own_count[:, None]).astype(jnp.float32)
    n_live = jnp.sum(counts, axis=-1).astype(jnp.float32)
    dpredicted = (
        2.0
        / math.sqrt(width)
        * live_mask[:, :, None, None]
        * (predicted - target_tiles)
        / n_live[:, None, None, None]
    )
    row_float = row_side.astype(jnp.float32)
    col_float = col_side.astype(jnp.float32)
    drow = jnp.einsum("mcij,mcjd->mcid", dpredicted, col_float, precision=lax.Precision.HIGHEST)
    dcol = jnp.einsum("mcij,mcid->mcjd", dpredicted, row_float, precision=lax.Precision.HIGHEST)
    dside = jnp.concatenate([drow, dcol], axis=1).astype(jnp.bfloat16)
    inverse = jnp.argsort(slot_index, axis=-1)
    outgoing_grads = take_rows(dside, inverse).reshape(members, seq_count, PER, TB, narrow)
    returned = lax.all_to_all(outgoing_grads, "seq", split_axis=1, concat_axis=1, tiled=True)
    selector = (
        picks.reshape(members, seq_count * PER)[:, :, None] == jnp.arange(per_block)[None, None, :]
    ).astype(jnp.bfloat16)
    dmixed = jnp.einsum(
        "mkn,mktd->mntd",
        selector,
        returned.reshape(members, seq_count * PER, TB, narrow),
        preferred_element_type=jnp.float32,
    ).reshape(members, length, narrow)
    dconv = (scaling[:, None, None] * dmixed).astype(jnp.bfloat16)
    weight_local = weight_term(padded, dconv, length, taps)
    return lax.psum_scatter(weight_local, ("seq", "dp"), scatter_dimension=2, tiled=True)


def axis_sum(value, axis):
    count = lax.axis_size(axis)
    total = value
    for shift in range(1, count):
        total = total + lax.ppermute(value, axis, [(i, (i + shift) % count) for i in range(count)])
    return total


def sparse_path(features, conv_weight, keep, tiles, counts, targets):
    _, length, width = features.shape
    taps, narrow, _ = conv_weight.shape
    halo = taps // 2
    span = TB + 2 * halo
    owners, capacity = tiles.shape[1], tiles.shape[2]
    n_sides = 2 * capacity
    per_block = length // TB
    seq_count = lax.axis_size("seq")
    groups = lax.axis_size("dp")
    peers = seq_count * groups
    held = owners * PER
    cols = width // peers
    my_index = lax.axis_index("seq")
    my_part = lax.axis_index("mp")

    before = jnp.arange(n_sides)[None, :] < jnp.arange(n_sides)[:, None]
    own_sides = jnp.concatenate([tiles[0, ..., 0], tiles[0, ..., 1]], axis=-1)
    own_source = own_sides // per_block
    own_same = own_source[:, :, None] == own_source[:, None, :]
    own_rank = jnp.sum(jnp.logical_and(own_same, before), axis=-1)
    held_here = own_source == my_index
    picks = jnp.stack(
        [
            jnp.sum(jnp.where(jnp.logical_and(held_here, own_rank == r), own_sides % per_block, 0), axis=-1)
            for r in range(PER)
        ],
        axis=-1,
    ).reshape(held)

    cells = features[0]
    ends = seq_count - 1
    last = per_block - 1
    rows = picks[:, None] * TB - halo + jnp.arange(span)[None, :]
    flat_rows = rows.reshape(-1)
    pick_inside = (flat_rows[:, None] == jnp.arange(length)[None, :]).astype(cells.dtype)
    inside = jnp.dot(pick_inside, cells, preferred_element_type=jnp.float32)
    windows = inside.astype(cells.dtype).reshape(held, span, width)
    filler = jnp.zeros((TB, width), cells.dtype)
    boundary = jnp.concatenate([cells[length - halo :], filler, cells[:halo]], axis=0)
    windows = jnp.concatenate([windows, boundary[None]], axis=0)
    x_float = windows.astype(jnp.float32)
    act = jax.nn.gelu(x_float).astype(jnp.bfloat16)
    conv_out = jnp.einsum("hti,oi->hto", act[:, 0:TB], conv_weight[0], preferred_element_type=jnp.float32)
    for offset in range(1, taps):
        conv_out = conv_out + jnp.einsum(
            "hti,oi->hto", act[:, offset : offset + TB], conv_weight[offset], preferred_element_type=jnp.float32
        )
    my_scale = 1.25 * keep[0].astype(jnp.float32)
    x_part = lax.dynamic_slice_in_dim(x_float[:held, halo : halo + TB], my_part * narrow, narrow, 2)
    raw = x_part + my_scale * conv_out[:held]
    mixed = raw.astype(jnp.bfloat16)
    edge_t = jnp.concatenate([jnp.arange(halo), jnp.arange(TB - halo, TB)])
    edge_values = raw[:, edge_t]
    corrections = conv_out[held, edge_t]
    edge_act = act[held, jnp.concatenate([jnp.arange(halo), jnp.arange(span - halo, span)])]
    act = act[:held]

    def split3(values):
        wide = values.reshape(-1)
        pieces = []
        for _ in range(3):
            piece = lax.reduce_precision(wide, exponent_bits=8, mantissa_bits=7)
            pieces.append(piece)
            wide = wide - piece
        return jnp.concatenate(pieces).astype(jnp.bfloat16)

    def join3(flat, count):
        flat = flat.astype(jnp.float32)
        return flat[..., :count] + flat[..., count : 2 * count] + flat[..., 2 * count : 3 * count]

    def lanes(part):
        flat = part.reshape(part.shape[0], -1)
        flat = jnp.pad(flat, ((0, 0), (0, -flat.shape[1] % 128)))
        return flat.reshape(flat.shape[0], -1, 128)

    act_cut = lanes(act.reshape(held, span, peers, cols).transpose(2, 0, 1, 3))
    edge_cut = lanes(edge_act.reshape(2 * halo, peers, cols).transpose(1, 0, 2))
    mixed_part = lanes(mixed.reshape(1, -1))
    small = jnp.concatenate(
        [tiles.reshape(-1), counts.reshape(-1), keep.reshape(-1), picks.reshape(-1)]
    ).astype(jnp.float32)
    n_edge = held * 2 * halo * narrow
    n_corr = 2 * halo * narrow
    exact = jnp.concatenate([split3(targets), split3(edge_values), split3(corrections), small.astype(jnp.bfloat16)])
    meta_part = lanes(exact.reshape(1, -1))
    rows_mixed, rows_act, rows_edge, rows_meta = (
        mixed_part.shape[1], act_cut.shape[1], edge_cut.shape[1], meta_part.shape[1]
    )
    outgoing = jnp.concatenate(
        [
            jnp.broadcast_to(mixed_part, (peers, rows_mixed, 128)),
            act_cut,
            edge_cut,
            jnp.broadcast_to(meta_part, (peers, rows_meta, 128)),
        ],
        axis=1,
    )
    outgoing = jnp.pad(outgoing, ((0, 0), (0, -outgoing.shape[1] % 16), (0, 0)))
    incoming = lax.all_to_all(outgoing, ("seq", "dp"), 0, 0, tiled=True)
    n_mixed = held * TB * narrow
    n_act = held * span * cols
    mixed_in = incoming[:, :rows_mixed].reshape(peers, -1)[:, :n_mixed].reshape(peers, held, TB, narrow)
    act_in = incoming[:, rows_mixed : rows_mixed + rows_act].reshape(peers, -1)[:, :n_act]
    act_in = act_in.reshape(seq_count, groups, held, span, cols)
    cut = rows_mixed + rows_act
    edge_in = incoming[:, cut : cut + rows_edge].reshape(peers, -1)[:, : 2 * halo * cols]
    edge_in = edge_in.reshape(seq_count, groups, 2 * halo, cols)
    cut = cut + rows_edge
    meta_flat = incoming[:, cut : cut + rows_meta].reshape(peers, -1)
    n_targets = capacity * TB * TB
    targets_all = join3(meta_flat[:, : 3 * n_targets], n_targets).reshape(seq_count, groups, -1)
    cut = 3 * n_targets
    edge_in_values = join3(meta_flat[:, cut : cut + 3 * n_edge], n_edge)
    edge_in_values = edge_in_values.reshape(seq_count, groups, held, 2 * halo, narrow)
    cut = cut + 3 * n_edge
    corr_in = join3(meta_flat[:, cut : cut + 3 * n_corr], n_corr).reshape(seq_count, groups, 2 * halo, narrow)
    cut = cut + 3 * n_corr
    meta_in = meta_flat[:, cut:].astype(jnp.float32).reshape(seq_count, groups, -1)
    n_tiles = owners * capacity * 2
    ints = meta_in[0].astype(jnp.int32)
    tiles_all = ints[:, :n_tiles].reshape(groups, owners, capacity, 2)
    counts_all = ints[:, n_tiles : n_tiles + owners]
    keep_all = ints[:, n_tiles + owners]
    picks_all = meta_in[..., n_tiles + owners + 1 : n_tiles + owners + 1 + held].astype(jnp.int32)
    seq_ids = jnp.arange(seq_count)[:, None, None]
    first = jnp.logical_and(picks_all == 0, seq_ids > 0)
    final = jnp.logical_and(picks_all == last, seq_ids < ends)
    zeros_corr = jnp.zeros_like(corr_in[:1])
    from_prev = jnp.concatenate([zeros_corr, corr_in[:-1]], axis=0)[:, :, None, :halo]
    from_next = jnp.concatenate([corr_in[1:], zeros_corr], axis=0)[:, :, None, halo:]
    scale_in = (1.25 * keep_all.astype(jnp.float32))[None, :, None, None, None]
    fixed_lo = (edge_in_values[..., :halo, :] + scale_in * from_prev).astype(jnp.bfloat16)
    fixed_hi = (edge_in_values[..., halo:, :] + scale_in * from_next).astype(jnp.bfloat16)
    mixed_in = mixed_in.reshape(seq_count, groups, held, TB, narrow)
    lo = jnp.where(first[..., None, None], fixed_lo, mixed_in[..., :halo, :])
    hi = jnp.where(final[..., None, None], fixed_hi, mixed_in[..., TB - halo :, :])
    mixed_in = jnp.concatenate([lo, mixed_in[..., halo : TB - halo, :], hi], axis=3)
    mixed_in = mixed_in.reshape(peers * held, TB, narrow)
    zeros_edge = jnp.zeros_like(edge_in[:1])
    act_prev = jnp.concatenate([zeros_edge, edge_in[:-1]], axis=0)[:, :, None, :halo]
    act_next = jnp.concatenate([edge_in[1:], zeros_edge], axis=0)[:, :, None, halo:]
    act_lo = jnp.where(first[..., None, None], act_prev, act_in[..., :halo, :])
    act_hi = jnp.where(final[..., None, None], act_next, act_in[..., span - halo :, :])
    act_in = jnp.concatenate([act_lo, act_in[..., halo : span - halo, :], act_hi], axis=3)
    act_in = act_in.reshape(peers * held, span, cols)

    sides = jnp.concatenate([tiles_all[..., 0], tiles_all[..., 1]], axis=-1)
    source = sides // per_block
    local = sides % per_block
    same_source = source[..., :, None] == source[..., None, :]
    rank = jnp.sum(jnp.logical_and(same_source, before), axis=-1)
    slot = (source * groups + jnp.arange(groups)[:, None, None]) * held + jnp.arange(owners)[None, :, None] * PER + rank

    side_rows = jnp.take(mixed_in, slot, axis=0)
    row_side = side_rows[:, :, :capacity]
    col_side = side_rows[:, :, capacity:]
    partial_tiles = jnp.einsum("qocid,qocjd->qocij", row_side, col_side, preferred_element_type=jnp.float32)
    lanes_shape = partial_tiles.shape
    summed = axis_sum(partial_tiles.reshape(-1, 128), "mp").reshape(lanes_shape)
    predicted = summed / math.sqrt(width)
    target_tiles = targets_all.reshape(seq_count, groups, capacity, TB, TB).transpose(1, 0, 2, 3, 4)
    live_mask = (jnp.arange(capacity)[None, None, :] < counts_all[:, :, None]).astype(jnp.float32)
    n_live = jnp.sum(counts_all, axis=-1).astype(jnp.float32)
    dpredicted = (
        2.0
        / math.sqrt(width)
        * live_mask[..., None, None]
        * (predicted - target_tiles)
        / n_live[:, None, None, None, None]
    )
    row_float = row_side.astype(jnp.float32)
    col_float = col_side.astype(jnp.float32)
    drow = jnp.einsum("qocij,qocjd->qocid", dpredicted, col_float, precision=lax.Precision.HIGHEST)
    dcol = jnp.einsum("qocij,qocid->qocjd", dpredicted, row_float, precision=lax.Precision.HIGHEST)
    grads = jnp.concatenate([drow, dcol], axis=2).astype(jnp.bfloat16).astype(jnp.float32)
    grads = grads.reshape(groups, owners * n_sides, TB, narrow)
    flat_sides = sides.reshape(groups, owners * n_sides)
    same_block = flat_sides[:, :, None] == flat_sides[:, None, :]
    total = jnp.einsum(
        "qab,qbtd->qatd", same_block.astype(jnp.float32), grads, precision=lax.Precision.HIGHEST
    )
    earlier = jnp.arange(owners * n_sides)[None, :] < jnp.arange(owners * n_sides)[:, None]
    first = jnp.logical_not(jnp.any(jnp.logical_and(same_block, earlier[None]), axis=-1))
    scaling = 1.25 * keep_all.astype(jnp.float32)
    dconv = (scaling[:, None, None, None] * total).astype(jnp.bfloat16)
    dconv = jnp.where(first[..., None, None], dconv, jnp.zeros_like(dconv))
    act_sides = jnp.take(act_in, slot.reshape(groups, owners * n_sides), axis=0)
    return jnp.stack(
        [
            jnp.einsum(
                "qato,qati->oi",
                dconv,
                act_sides[:, :, offset : offset + TB],
                preferred_element_type=jnp.float32,
            )
            for offset in range(taps)
        ]
    )


def per_device(features, conv_weight, keep, tiles, counts, targets):
    members, length, _ = features.shape
    owners, capacity = tiles.shape[1], tiles.shape[2]
    blocks = lax.axis_size("seq") * length // TB
    fits = members == 1 and targets.shape[1] == 1 and 2 * owners * capacity * TB <= length
    fits = fits and blocks <= 256 and capacity <= 256
    if fits:
        return sparse_path(features, conv_weight, keep, tiles, counts, targets)
    return dense_path(features, conv_weight, keep, tiles, counts, targets)


def solution(mesh):
    placed = (
        P("dp", "seq", None),
        P(None, "mp", None),
        P("dp"),
        P("dp", None, None, None),
        P("dp", None),
        P("dp", "seq", None, None),
    )
    return jax.shard_map(
        per_device,
        mesh=mesh,
        in_specs=placed,
        out_specs=P(None, "mp", ("seq", "dp")),
        check_vma=False,
    )
```

```python
import math

import jax
import jax.numpy as jnp
from jax import lax
from jax.sharding import PartitionSpec as P

TB = 32
PER = 2


def extended(cells, sides, width):
    for axis, dim in sides:
        count = lax.axis_size(axis)
        ends = count - 1
        head = lax.slice_in_dim(cells, 0, width, axis=dim)
        tail = lax.slice_in_dim(cells, cells.shape[dim] - width, cells.shape[dim], axis=dim)
        cells = jnp.concatenate(
            [
                lax.ppermute(tail, axis, [(i, (i + 1) % count) for i in range(ends)]),
                cells,
                lax.ppermute(head, axis, [((i + 1) % count, i) for i in range(ends)]),
            ],
            axis=dim,
        )
    return cells


def take_rows(source_array, index_array):
    return jax.vmap(lambda table, picked: table[picked])(source_array, index_array)


def conv_apply(padded, weight, length):
    total = jnp.einsum(
        "mbi,oi->mbo", padded[:, 0:length], weight[0], preferred_element_type=jnp.float32
    )
    for offset in range(1, weight.shape[0]):
        total = total + jnp.einsum(
            "mbi,oi->mbo",
            padded[:, offset : offset + length],
            weight[offset],
            preferred_element_type=jnp.float32,
        )
    return total


def weight_term(padded, dconv, length, taps):
    return jnp.stack(
        [
            jnp.einsum(
                "mbi,mbo->oi",
                padded[:, offset : offset + length],
                dconv,
                preferred_element_type=jnp.float32,
            )
            for offset in range(taps)
        ]
    )


def dense_path(features, conv_weight, keep, tiles, counts, targets):
    members, length, width = features.shape
    taps = conv_weight.shape[0]
    narrow = conv_weight.shape[1]
    seq_count = lax.axis_size("seq")
    my_index = lax.axis_index("seq")
    my_part = lax.axis_index("mp")
    x_float = features.astype(jnp.float32)
    activations = jax.nn.gelu(x_float).astype(jnp.bfloat16)
    padded = extended(activations, (("seq", 1),), 2)
    scaling = 1.25 * keep.astype(jnp.float32)
    conv_out = conv_apply(padded, conv_weight, length)
    x_local = lax.dynamic_slice_in_dim(x_float, my_part * narrow, narrow, 2)
    mixed_out = (x_local + scaling[:, None, None] * conv_out).astype(jnp.bfloat16)
    capacity = tiles.shape[2]
    n_sides = 2 * capacity
    per_block = length // TB
    sides = jnp.concatenate([tiles[..., 0], tiles[..., 1]], axis=-1)
    side_source = sides // per_block
    side_local = sides % per_block
    own_sides = lax.dynamic_index_in_dim(sides, my_index, 1, keepdims=False)
    own_source = own_sides // per_block
    before = jnp.arange(n_sides)[None, :] < jnp.arange(n_sides)[:, None]
    same_source = own_source[:, :, None] == own_source[:, None, :]
    rank_within = jnp.sum(jnp.logical_and(same_source, before[None]), axis=-1)
    slot_index = own_source * PER + rank_within
    held_here = side_source == my_index
    held_order = jnp.cumsum(held_here.astype(jnp.int32), axis=-1) - 1
    picks = jnp.stack(
        [
            jnp.sum(
                jnp.where(jnp.logical_and(held_here, held_order == position), side_local, 0),
                axis=-1,
            )
            for position in range(PER)
        ],
        axis=-1,
    )
    blocks = mixed_out.reshape(members, per_block, TB, narrow)
    whole = lax.all_gather(blocks, "seq", axis=1, tiled=True)
    side_rows = take_rows(whole, own_sides)
    row_side = side_rows[:, :capacity]
    col_side = side_rows[:, capacity:]
    partial_tiles = jnp.einsum(
        "mcid,mcjd->mcij", row_side, col_side, preferred_element_type=jnp.float32
    )
    predicted = lax.psum(partial_tiles, "mp") / math.sqrt(width)
    target_tiles = targets[:, 0].reshape(members, capacity, TB, TB)
    own_count = lax.dynamic_index_in_dim(counts, my_index, 1, keepdims=False)
    live_mask = (jnp.arange(capacity)[None, :] < own_count[:, None]).astype(jnp.float32)
    n_live = jnp.sum(counts, axis=-1).astype(jnp.float32)
    dpredicted = (
        2.0
        / math.sqrt(width)
        * live_mask[:, :, None, None]
        * (predicted - target_tiles)
        / n_live[:, None, None, None]
    )
    row_float = row_side.astype(jnp.float32)
    col_float = col_side.astype(jnp.float32)
    drow = jnp.einsum("mcij,mcjd->mcid", dpredicted, col_float, precision=lax.Precision.HIGHEST)
    dcol = jnp.einsum("mcij,mcid->mcjd", dpredicted, row_float, precision=lax.Precision.HIGHEST)
    dside = jnp.concatenate([drow, dcol], axis=1).astype(jnp.bfloat16)
    inverse = jnp.argsort(slot_index, axis=-1)
    outgoing_grads = take_rows(dside, inverse).reshape(members, seq_count, PER, TB, narrow)
    returned = lax.all_to_all(outgoing_grads, "seq", split_axis=1, concat_axis=1, tiled=True)
    selector = (
        picks.reshape(members, seq_count * PER)[:, :, None] == jnp.arange(per_block)[None, None, :]
    ).astype(jnp.bfloat16)
    dmixed = jnp.einsum(
        "mkn,mktd->mntd",
        selector,
        returned.reshape(members, seq_count * PER, TB, narrow),
        preferred_element_type=jnp.float32,
    ).reshape(members, length, narrow)
    dconv = (scaling[:, None, None] * dmixed).astype(jnp.bfloat16)
    weight_local = weight_term(padded, dconv, length, taps)
    return lax.psum_scatter(weight_local, ("seq", "dp"), scatter_dimension=2, tiled=True)


def axis_sum(value, axis):
    count = lax.axis_size(axis)
    if count & (count - 1) == 0:
        step = 1
        while step < count:
            value = value + lax.ppermute(value, axis, [(i, i ^ step) for i in range(count)])
            step *= 2
        return value
    total = value
    for shift in range(1, count):
        total = total + lax.ppermute(value, axis, [(i, (i + shift) % count) for i in range(count)])
    return total


def sparse_path(features, conv_weight, keep, tiles, counts, targets):
    _, length, width = features.shape
    taps, narrow, _ = conv_weight.shape
    halo = taps // 2
    span = TB + 2 * halo
    owners, capacity = tiles.shape[1], tiles.shape[2]
    n_sides = 2 * capacity
    per_block = length // TB
    seq_count = lax.axis_size("seq")
    groups = lax.axis_size("dp")
    peers = seq_count * groups
    held = owners * PER
    cols = width // peers
    my_index = lax.axis_index("seq")
    my_part = lax.axis_index("mp")

    before = jnp.arange(n_sides)[None, :] < jnp.arange(n_sides)[:, None]
    own_sides = jnp.concatenate([tiles[0, ..., 0], tiles[0, ..., 1]], axis=-1)
    own_source = own_sides // per_block
    own_same = own_source[:, :, None] == own_source[:, None, :]
    own_rank = jnp.sum(jnp.logical_and(own_same, before), axis=-1)
    held_here = own_source == my_index
    picks = jnp.stack(
        [
            jnp.sum(jnp.where(jnp.logical_and(held_here, own_rank == r), own_sides % per_block, 0), axis=-1)
            for r in range(PER)
        ],
        axis=-1,
    ).reshape(held)

    cells = features[0]
    ends = seq_count - 1
    if seq_count == 2:
        swapped = lax.ppermute(
            jnp.concatenate([cells[length - halo :], cells[:halo]]), "seq", [(0, 1), (1, 0)]
        )
        head = jnp.where(my_index == 0, jnp.zeros_like(swapped[:halo]), swapped[:halo])
        tail = jnp.where(my_index == ends, jnp.zeros_like(swapped[halo:]), swapped[halo:])
    else:
        head = lax.ppermute(cells[length - halo :], "seq", [(i, i + 1) for i in range(ends)])
        tail = lax.ppermute(cells[:halo], "seq", [(i + 1, i) for i in range(ends)])
    last = per_block - 1
    stacked = cells.reshape(per_block, TB, width)
    block_ids = jnp.arange(per_block)[None, :]
    choose = (picks[:, None] == block_ids).astype(cells.dtype)
    choose_prev = (picks[:, None] - 1 == block_ids).astype(cells.dtype)
    choose_next = (picks[:, None] + 1 == block_ids).astype(cells.dtype)
    middle = jnp.einsum("hb,btd->htd", choose, stacked, preferred_element_type=jnp.float32)
    prev_tail = jnp.einsum("hb,btd->htd", choose_prev, stacked[:, TB - halo :], preferred_element_type=jnp.float32)
    next_head = jnp.einsum("hb,btd->htd", choose_next, stacked[:, :halo], preferred_element_type=jnp.float32)
    at_start = (picks == 0)[:, None, None]
    at_end = (picks == last)[:, None, None]
    lower = jnp.where(at_start, head[None].astype(jnp.float32), prev_tail)
    upper = jnp.where(at_end, tail[None].astype(jnp.float32), next_head)
    windows = jnp.concatenate([lower, middle, upper], axis=1).astype(cells.dtype)
    x_float = windows.astype(jnp.float32)
    act = jax.nn.gelu(x_float).astype(jnp.bfloat16)
    conv_out = jnp.einsum("hti,oi->hto", act[:, 0:TB], conv_weight[0], preferred_element_type=jnp.float32)
    for offset in range(1, taps):
        conv_out = conv_out + jnp.einsum(
            "hti,oi->hto", act[:, offset : offset + TB], conv_weight[offset], preferred_element_type=jnp.float32
        )
    my_scale = 1.25 * keep[0].astype(jnp.float32)
    x_part = lax.dynamic_slice_in_dim(x_float[:, halo : halo + TB], my_part * narrow, narrow, 2)
    mixed = (x_part + my_scale * conv_out).astype(jnp.bfloat16)

    def lanes(part):
        flat = part.reshape(part.shape[0], -1)
        flat = jnp.pad(flat, ((0, 0), (0, -flat.shape[1] % 128)))
        return flat.reshape(flat.shape[0], -1, 128)

    act_cut = lanes(act.reshape(held, span, peers, cols).transpose(2, 0, 1, 3))
    mixed_part = lanes(mixed.reshape(1, -1))
    wide = targets.reshape(-1)
    pieces = []
    for _ in range(3):
        piece = lax.reduce_precision(wide, exponent_bits=8, mantissa_bits=7)
        pieces.append(piece)
        wide = wide - piece
    small = jnp.concatenate([tiles.reshape(-1), counts.reshape(-1), keep.reshape(-1)]).astype(jnp.float32)
    meta_part = lanes(jnp.concatenate(pieces + [small]).astype(jnp.bfloat16).reshape(1, -1))
    rows_mixed, rows_act, rows_meta = mixed_part.shape[1], act_cut.shape[1], meta_part.shape[1]
    outgoing = jnp.concatenate(
        [
            jnp.broadcast_to(mixed_part, (peers, rows_mixed, 128)),
            act_cut,
            jnp.broadcast_to(meta_part, (peers, rows_meta, 128)),
        ],
        axis=1,
    )
    outgoing = jnp.pad(outgoing, ((0, 0), (0, -outgoing.shape[1] % 16), (0, 0)))
    incoming = lax.all_to_all(outgoing, ("seq", "dp"), 0, 0, tiled=True)
    n_mixed = held * TB * narrow
    n_act = held * span * cols
    mixed_in = incoming[:, :rows_mixed].reshape(peers, -1)[:, :n_mixed].reshape(peers * held, TB, narrow)
    act_in = incoming[:, rows_mixed : rows_mixed + rows_act].reshape(peers, -1)[:, :n_act]
    act_in = act_in.reshape(peers * held, span, cols)
    meta_in = incoming[:, rows_mixed + rows_act : rows_mixed + rows_act + rows_meta].reshape(peers, -1)
    meta_in = meta_in.astype(jnp.float32).reshape(seq_count, groups, -1)
    n_targets = capacity * TB * TB
    n_tiles = owners * capacity * 2
    targets_all = meta_in[:, :, :n_targets] + meta_in[:, :, n_targets : 2 * n_targets]
    targets_all = targets_all + meta_in[:, :, 2 * n_targets : 3 * n_targets]
    ints = meta_in[0, :, 3 * n_targets :].astype(jnp.int32)
    tiles_all = ints[:, :n_tiles].reshape(groups, owners, capacity, 2)
    counts_all = ints[:, n_tiles : n_tiles + owners]
    keep_all = ints[:, n_tiles + owners]

    sides = jnp.concatenate([tiles_all[..., 0], tiles_all[..., 1]], axis=-1)
    source = sides // per_block
    local = sides % per_block
    same_source = source[..., :, None] == source[..., None, :]
    rank = jnp.sum(jnp.logical_and(same_source, before), axis=-1)
    slot = (source * groups + jnp.arange(groups)[:, None, None]) * held + jnp.arange(owners)[None, :, None] * PER + rank

    side_rows = jnp.take(mixed_in, slot, axis=0)
    row_side = side_rows[:, :, :capacity]
    col_side = side_rows[:, :, capacity:]
    partial_tiles = jnp.einsum("qocid,qocjd->qocij", row_side, col_side, preferred_element_type=jnp.float32)
    lanes_shape = partial_tiles.shape
    summed = axis_sum(partial_tiles.reshape(-1, 128), "mp").reshape(lanes_shape)
    predicted = summed / math.sqrt(width)
    target_tiles = targets_all.reshape(seq_count, groups, capacity, TB, TB).transpose(1, 0, 2, 3, 4)
    live_mask = (jnp.arange(capacity)[None, None, :] < counts_all[:, :, None]).astype(jnp.float32)
    n_live = jnp.sum(counts_all, axis=-1).astype(jnp.float32)
    dpredicted = (
        2.0
        / math.sqrt(width)
        * live_mask[..., None, None]
        * (predicted - target_tiles)
        / n_live[:, None, None, None, None]
    )
    row_float = row_side.astype(jnp.float32)
    col_float = col_side.astype(jnp.float32)
    drow = jnp.einsum("qocij,qocjd->qocid", dpredicted, col_float, precision=lax.Precision.HIGHEST)
    dcol = jnp.einsum("qocij,qocid->qocjd", dpredicted, row_float, precision=lax.Precision.HIGHEST)
    grads = jnp.concatenate([drow, dcol], axis=2).astype(jnp.bfloat16).astype(jnp.float32)
    grads = grads.reshape(groups, owners * n_sides, TB, narrow)
    flat_sides = sides.reshape(groups, owners * n_sides)
    same_block = flat_sides[:, :, None] == flat_sides[:, None, :]
    total = jnp.einsum(
        "qab,qbtd->qatd", same_block.astype(jnp.float32), grads, precision=lax.Precision.HIGHEST
    )
    earlier = jnp.arange(owners * n_sides)[None, :] < jnp.arange(owners * n_sides)[:, None]
    first = jnp.logical_not(jnp.any(jnp.logical_and(same_block, earlier[None]), axis=-1))
    scaling = 1.25 * keep_all.astype(jnp.float32)
    dconv = (scaling[:, None, None, None] * total).astype(jnp.bfloat16)
    dconv = jnp.where(first[..., None, None], dconv, jnp.zeros_like(dconv))
    act_sides = jnp.take(act_in, slot.reshape(groups, owners * n_sides), axis=0)
    return jnp.stack(
        [
            jnp.einsum(
                "qato,qati->oi",
                dconv,
                act_sides[:, :, offset : offset + TB],
                preferred_element_type=jnp.float32,
            )
            for offset in range(taps)
        ]
    )


def per_device(features, conv_weight, keep, tiles, counts, targets):
    members, length, _ = features.shape
    owners, capacity = tiles.shape[1], tiles.shape[2]
    blocks = lax.axis_size("seq") * length // TB
    fits = members == 1 and targets.shape[1] == 1 and 2 * owners * capacity * TB <= length
    fits = fits and blocks <= 256 and capacity <= 256
    if fits:
        return sparse_path(features, conv_weight, keep, tiles, counts, targets)
    return dense_path(features, conv_weight, keep, tiles, counts, targets)


def solution(mesh):
    placed = (
        P("dp", "seq", None),
        P(None, "mp", None),
        P("dp"),
        P("dp", None, None, None),
        P("dp", None),
        P("dp", "seq", None, None),
    )
    return jax.shard_map(
        per_device,
        mesh=mesh,
        in_specs=placed,
        out_specs=P(None, "mp", ("seq", "dp")),
        check_vma=False,
    )
```

```python
import math

import jax
import jax.numpy as jnp
from jax import lax
from jax.sharding import PartitionSpec as P

TB = 32
PER = 2


def extended(cells, sides, width):
    for axis, dim in sides:
        count = lax.axis_size(axis)
        ends = count - 1
        head = lax.slice_in_dim(cells, 0, width, axis=dim)
        tail = lax.slice_in_dim(cells, cells.shape[dim] - width, cells.shape[dim], axis=dim)
        cells = jnp.concatenate(
            [
                lax.ppermute(tail, axis, [(i, (i + 1) % count) for i in range(ends)]),
                cells,
                lax.ppermute(head, axis, [((i + 1) % count, i) for i in range(ends)]),
            ],
            axis=dim,
        )
    return cells


def take_rows(source_array, index_array):
    return jax.vmap(lambda table, picked: table[picked])(source_array, index_array)


def conv_apply(padded, weight, length):
    total = jnp.einsum(
        "mbi,oi->mbo", padded[:, 0:length], weight[0], preferred_element_type=jnp.float32
    )
    for offset in range(1, weight.shape[0]):
        total = total + jnp.einsum(
            "mbi,oi->mbo",
            padded[:, offset : offset + length],
            weight[offset],
            preferred_element_type=jnp.float32,
        )
    return total


def weight_term(padded, dconv, length, taps):
    return jnp.stack(
        [
            jnp.einsum(
                "mbi,mbo->oi",
                padded[:, offset : offset + length],
                dconv,
                preferred_element_type=jnp.float32,
            )
            for offset in range(taps)
        ]
    )


def dense_path(features, conv_weight, keep, tiles, counts, targets):
    members, length, width = features.shape
    taps = conv_weight.shape[0]
    narrow = conv_weight.shape[1]
    seq_count = lax.axis_size("seq")
    my_index = lax.axis_index("seq")
    my_part = lax.axis_index("mp")
    x_float = features.astype(jnp.float32)
    activations = jax.nn.gelu(x_float).astype(jnp.bfloat16)
    padded = extended(activations, (("seq", 1),), 2)
    scaling = 1.25 * keep.astype(jnp.float32)
    conv_out = conv_apply(padded, conv_weight, length)
    x_local = lax.dynamic_slice_in_dim(x_float, my_part * narrow, narrow, 2)
    mixed_out = (x_local + scaling[:, None, None] * conv_out).astype(jnp.bfloat16)
    capacity = tiles.shape[2]
    n_sides = 2 * capacity
    per_block = length // TB
    sides = jnp.concatenate([tiles[..., 0], tiles[..., 1]], axis=-1)
    side_source = sides // per_block
    side_local = sides % per_block
    own_sides = lax.dynamic_index_in_dim(sides, my_index, 1, keepdims=False)
    own_source = own_sides // per_block
    before = jnp.arange(n_sides)[None, :] < jnp.arange(n_sides)[:, None]
    same_source = own_source[:, :, None] == own_source[:, None, :]
    rank_within = jnp.sum(jnp.logical_and(same_source, before[None]), axis=-1)
    slot_index = own_source * PER + rank_within
    held_here = side_source == my_index
    held_order = jnp.cumsum(held_here.astype(jnp.int32), axis=-1) - 1
    picks = jnp.stack(
        [
            jnp.sum(
                jnp.where(jnp.logical_and(held_here, held_order == position), side_local, 0),
                axis=-1,
            )
            for position in range(PER)
        ],
        axis=-1,
    )
    blocks = mixed_out.reshape(members, per_block, TB, narrow)
    whole = lax.all_gather(blocks, "seq", axis=1, tiled=True)
    side_rows = take_rows(whole, own_sides)
    row_side = side_rows[:, :capacity]
    col_side = side_rows[:, capacity:]
    partial_tiles = jnp.einsum(
        "mcid,mcjd->mcij", row_side, col_side, preferred_element_type=jnp.float32
    )
    predicted = lax.psum(partial_tiles, "mp") / math.sqrt(width)
    target_tiles = targets[:, 0].reshape(members, capacity, TB, TB)
    own_count = lax.dynamic_index_in_dim(counts, my_index, 1, keepdims=False)
    live_mask = (jnp.arange(capacity)[None, :] < own_count[:, None]).astype(jnp.float32)
    n_live = jnp.sum(counts, axis=-1).astype(jnp.float32)
    dpredicted = (
        2.0
        / math.sqrt(width)
        * live_mask[:, :, None, None]
        * (predicted - target_tiles)
        / n_live[:, None, None, None]
    )
    row_float = row_side.astype(jnp.float32)
    col_float = col_side.astype(jnp.float32)
    drow = jnp.einsum("mcij,mcjd->mcid", dpredicted, col_float, precision=lax.Precision.HIGHEST)
    dcol = jnp.einsum("mcij,mcid->mcjd", dpredicted, row_float, precision=lax.Precision.HIGHEST)
    dside = jnp.concatenate([drow, dcol], axis=1).astype(jnp.bfloat16)
    inverse = jnp.argsort(slot_index, axis=-1)
    outgoing_grads = take_rows(dside, inverse).reshape(members, seq_count, PER, TB, narrow)
    returned = lax.all_to_all(outgoing_grads, "seq", split_axis=1, concat_axis=1, tiled=True)
    selector = (
        picks.reshape(members, seq_count * PER)[:, :, None] == jnp.arange(per_block)[None, None, :]
    ).astype(jnp.bfloat16)
    dmixed = jnp.einsum(
        "mkn,mktd->mntd",
        selector,
        returned.reshape(members, seq_count * PER, TB, narrow),
        preferred_element_type=jnp.float32,
    ).reshape(members, length, narrow)
    dconv = (scaling[:, None, None] * dmixed).astype(jnp.bfloat16)
    weight_local = weight_term(padded, dconv, length, taps)
    return lax.psum_scatter(weight_local, ("seq", "dp"), scatter_dimension=2, tiled=True)


def axis_sum(value, axis):
    count = lax.axis_size(axis)
    if count & (count - 1) == 0:
        step = 1
        while step < count:
            value = value + lax.ppermute(value, axis, [(i, i ^ step) for i in range(count)])
            step *= 2
        return value
    total = value
    for shift in range(1, count):
        total = total + lax.ppermute(value, axis, [(i, (i + shift) % count) for i in range(count)])
    return total


def sparse_path(features, conv_weight, keep, tiles, counts, targets):
    _, length, width = features.shape
    taps, narrow, _ = conv_weight.shape
    halo = taps // 2
    span = TB + 2 * halo
    owners, capacity = tiles.shape[1], tiles.shape[2]
    n_sides = 2 * capacity
    per_block = length // TB
    seq_count = lax.axis_size("seq")
    groups = lax.axis_size("dp")
    peers = seq_count * groups
    held = owners * PER
    cols = width // peers
    my_index = lax.axis_index("seq")
    my_part = lax.axis_index("mp")

    before = jnp.arange(n_sides)[None, :] < jnp.arange(n_sides)[:, None]
    own_sides = jnp.concatenate([tiles[0, ..., 0], tiles[0, ..., 1]], axis=-1)
    own_source = own_sides // per_block
    own_same = own_source[:, :, None] == own_source[:, None, :]
    own_rank = jnp.sum(jnp.logical_and(own_same, before), axis=-1)
    held_here = own_source == my_index
    picks = jnp.stack(
        [
            jnp.sum(jnp.where(jnp.logical_and(held_here, own_rank == r), own_sides % per_block, 0), axis=-1)
            for r in range(PER)
        ],
        axis=-1,
    ).reshape(held)

    cells = features[0]
    ends = seq_count - 1
    if seq_count == 2:
        swapped = lax.ppermute(
            jnp.concatenate([cells[length - halo :], cells[:halo]]), "seq", [(0, 1), (1, 0)]
        )
        head = jnp.where(my_index == 0, jnp.zeros_like(swapped[:halo]), swapped[:halo])
        tail = jnp.where(my_index == ends, jnp.zeros_like(swapped[halo:]), swapped[halo:])
    else:
        head = lax.ppermute(cells[length - halo :], "seq", [(i, i + 1) for i in range(ends)])
        tail = lax.ppermute(cells[:halo], "seq", [(i + 1, i) for i in range(ends)])
    rows = picks[:, None] * TB - halo + jnp.arange(span)[None, :]
    flat_rows = rows.reshape(-1)
    pick_inside = (flat_rows[:, None] == jnp.arange(length)[None, :]).astype(cells.dtype)
    inside = jnp.dot(pick_inside, cells, preferred_element_type=jnp.float32)
    edge_rows = jnp.concatenate([head, tail], axis=0)
    edge_index = jnp.where(flat_rows < 0, flat_rows + halo, flat_rows - length + halo)
    in_range = jnp.logical_and(flat_rows >= 0, flat_rows < length)
    pick_edge = jnp.logical_and(
        edge_index[:, None] == jnp.arange(2 * halo)[None, :], jnp.logical_not(in_range)[:, None]
    ).astype(cells.dtype)
    outside = jnp.dot(pick_edge, edge_rows, preferred_element_type=jnp.float32)
    windows = (inside + outside).astype(cells.dtype).reshape(held, span, width)
    x_float = windows.astype(jnp.float32)
    act = jax.nn.gelu(x_float).astype(jnp.bfloat16)
    conv_out = jnp.einsum("hti,oi->hto", act[:, 0:TB], conv_weight[0], preferred_element_type=jnp.float32)
    for offset in range(1, taps):
        conv_out = conv_out + jnp.einsum(
            "hti,oi->hto", act[:, offset : offset + TB], conv_weight[offset], preferred_element_type=jnp.float32
        )
    my_scale = 1.25 * keep[0].astype(jnp.float32)
    x_part = lax.dynamic_slice_in_dim(x_float[:, halo : halo + TB], my_part * narrow, narrow, 2)
    mixed = (x_part + my_scale * conv_out).astype(jnp.bfloat16)

    def lanes(part):
        flat = part.reshape(part.shape[0], -1)
        flat = jnp.pad(flat, ((0, 0), (0, -flat.shape[1] % 128)))
        return flat.reshape(flat.shape[0], -1, 128)

    act_cut = lanes(act.reshape(held, span, peers, cols).transpose(2, 0, 1, 3))
    mixed_part = lanes(mixed.reshape(1, -1))
    wide = targets.reshape(-1)
    pieces = []
    for _ in range(3):
        piece = lax.reduce_precision(wide, exponent_bits=8, mantissa_bits=7)
        pieces.append(piece)
        wide = wide - piece
    small = jnp.concatenate([tiles.reshape(-1), counts.reshape(-1), keep.reshape(-1)]).astype(jnp.float32)
    meta_part = lanes(jnp.concatenate(pieces + [small]).astype(jnp.bfloat16).reshape(1, -1))
    rows_mixed, rows_act, rows_meta = mixed_part.shape[1], act_cut.shape[1], meta_part.shape[1]
    outgoing = jnp.concatenate(
        [
            jnp.broadcast_to(mixed_part, (peers, rows_mixed, 128)),
            act_cut,
            jnp.broadcast_to(meta_part, (peers, rows_meta, 128)),
        ],
        axis=1,
    )
    outgoing = jnp.pad(outgoing, ((0, 0), (0, -outgoing.shape[1] % 16), (0, 0)))
    incoming = lax.all_to_all(outgoing, ("seq", "dp"), 0, 0, tiled=True)
    n_mixed = held * TB * narrow
    n_act = held * span * cols
    mixed_in = incoming[:, :rows_mixed].reshape(peers, -1)[:, :n_mixed].reshape(peers * held, TB, narrow)
    act_in = incoming[:, rows_mixed : rows_mixed + rows_act].reshape(peers, -1)[:, :n_act]
    act_in = act_in.reshape(peers * held, span, cols)
    meta_in = incoming[:, rows_mixed + rows_act : rows_mixed + rows_act + rows_meta].reshape(peers, -1)
    meta_in = meta_in.astype(jnp.float32).reshape(seq_count, groups, -1)
    n_targets = capacity * TB * TB
    n_tiles = owners * capacity * 2
    targets_all = meta_in[:, :, :n_targets] + meta_in[:, :, n_targets : 2 * n_targets]
    targets_all = targets_all + meta_in[:, :, 2 * n_targets : 3 * n_targets]
    ints = meta_in[0, :, 3 * n_targets :].astype(jnp.int32)
    tiles_all = ints[:, :n_tiles].reshape(groups, owners, capacity, 2)
    counts_all = ints[:, n_tiles : n_tiles + owners]
    keep_all = ints[:, n_tiles + owners]

    sides = jnp.concatenate([tiles_all[..., 0], tiles_all[..., 1]], axis=-1)
    source = sides // per_block
    local = sides % per_block
    same_source = source[..., :, None] == source[..., None, :]
    rank = jnp.sum(jnp.logical_and(same_source, before), axis=-1)
    slot = (source * groups + jnp.arange(groups)[:, None, None]) * held + jnp.arange(owners)[None, :, None] * PER + rank

    side_rows = jnp.take(mixed_in, slot, axis=0)
    row_side = side_rows[:, :, :capacity]
    col_side = side_rows[:, :, capacity:]
    partial_tiles = jnp.einsum("qocid,qocjd->qocij", row_side, col_side, preferred_element_type=jnp.float32)
    lanes_shape = partial_tiles.shape
    summed = axis_sum(partial_tiles.reshape(-1, 128), "mp").reshape(lanes_shape)
    predicted = summed / math.sqrt(width)
    target_tiles = targets_all.reshape(seq_count, groups, capacity, TB, TB).transpose(1, 0, 2, 3, 4)
    live_mask = (jnp.arange(capacity)[None, None, :] < counts_all[:, :, None]).astype(jnp.float32)
    n_live = jnp.sum(counts_all, axis=-1).astype(jnp.float32)
    dpredicted = (
        2.0
        / math.sqrt(width)
        * live_mask[..., None, None]
        * (predicted - target_tiles)
        / n_live[:, None, None, None, None]
    )
    row_float = row_side.astype(jnp.float32)
    col_float = col_side.astype(jnp.float32)
    drow = jnp.einsum("qocij,qocjd->qocid", dpredicted, col_float, precision=lax.Precision.HIGHEST)
    dcol = jnp.einsum("qocij,qocid->qocjd", dpredicted, row_float, precision=lax.Precision.HIGHEST)
    grads = jnp.concatenate([drow, dcol], axis=2).astype(jnp.bfloat16).astype(jnp.float32)
    grads = grads.reshape(groups, owners * n_sides, TB, narrow)
    flat_sides = sides.reshape(groups, owners * n_sides)
    same_block = flat_sides[:, :, None] == flat_sides[:, None, :]
    total = jnp.einsum(
        "qab,qbtd->qatd", same_block.astype(jnp.float32), grads, precision=lax.Precision.HIGHEST
    )
    earlier = jnp.arange(owners * n_sides)[None, :] < jnp.arange(owners * n_sides)[:, None]
    first = jnp.logical_not(jnp.any(jnp.logical_and(same_block, earlier[None]), axis=-1))
    scaling = 1.25 * keep_all.astype(jnp.float32)
    dconv = (scaling[:, None, None, None] * total).astype(jnp.bfloat16)
    dconv = jnp.where(first[..., None, None], dconv, jnp.zeros_like(dconv))
    act_sides = jnp.take(act_in, slot.reshape(groups, owners * n_sides), axis=0)
    shifted = jnp.concatenate([act_sides[:, :, offset : offset + TB] for offset in range(taps)], axis=-1)
    product = jnp.dot(
        dconv.reshape(-1, narrow).T, shifted.reshape(-1, taps * cols), preferred_element_type=jnp.float32
    )
    return product.reshape(narrow, taps, cols).transpose(1, 0, 2)


def per_device(features, conv_weight, keep, tiles, counts, targets):
    members, length, _ = features.shape
    owners, capacity = tiles.shape[1], tiles.shape[2]
    blocks = lax.axis_size("seq") * length // TB
    fits = members == 1 and targets.shape[1] == 1 and 2 * owners * capacity * TB <= length
    fits = fits and blocks <= 256 and capacity <= 256
    if fits:
        return sparse_path(features, conv_weight, keep, tiles, counts, targets)
    return dense_path(features, conv_weight, keep, tiles, counts, targets)


def solution(mesh):
    placed = (
        P("dp", "seq", None),
        P(None, "mp", None),
        P("dp"),
        P("dp", None, None, None),
        P("dp", None),
        P("dp", "seq", None, None),
    )
    return jax.shard_map(
        per_device,
        mesh=mesh,
        in_specs=placed,
        out_specs=P(None, "mp", ("seq", "dp")),
        check_vma=False,
    )
```

```python
import math

import jax
import jax.numpy as jnp
from jax import lax
from jax.sharding import PartitionSpec as P

TB = 32
PER = 2


def extended(cells, sides, width):
    for axis, dim in sides:
        count = lax.axis_size(axis)
        ends = count - 1
        head = lax.slice_in_dim(cells, 0, width, axis=dim)
        tail = lax.slice_in_dim(cells, cells.shape[dim] - width, cells.shape[dim], axis=dim)
        cells = jnp.concatenate(
            [
                lax.ppermute(tail, axis, [(i, (i + 1) % count) for i in range(ends)]),
                cells,
                lax.ppermute(head, axis, [((i + 1) % count, i) for i in range(ends)]),
            ],
            axis=dim,
        )
    return cells


def take_rows(source_array, index_array):
    return jax.vmap(lambda table, picked: table[picked])(source_array, index_array)


def conv_apply(padded, weight, length):
    total = jnp.einsum(
        "mbi,oi->mbo", padded[:, 0:length], weight[0], preferred_element_type=jnp.float32
    )
    for offset in range(1, weight.shape[0]):
        total = total + jnp.einsum(
            "mbi,oi->mbo",
            padded[:, offset : offset + length],
            weight[offset],
            preferred_element_type=jnp.float32,
        )
    return total


def weight_term(padded, dconv, length, taps):
    return jnp.stack(
        [
            jnp.einsum(
                "mbi,mbo->oi",
                padded[:, offset : offset + length],
                dconv,
                preferred_element_type=jnp.float32,
            )
            for offset in range(taps)
        ]
    )


def dense_path(features, conv_weight, keep, tiles, counts, targets):
    members, length, width = features.shape
    taps = conv_weight.shape[0]
    narrow = conv_weight.shape[1]
    seq_count = lax.axis_size("seq")
    my_index = lax.axis_index("seq")
    my_part = lax.axis_index("mp")
    x_float = features.astype(jnp.float32)
    activations = jax.nn.gelu(x_float).astype(jnp.bfloat16)
    padded = extended(activations, (("seq", 1),), 2)
    scaling = 1.25 * keep.astype(jnp.float32)
    conv_out = conv_apply(padded, conv_weight, length)
    x_local = lax.dynamic_slice_in_dim(x_float, my_part * narrow, narrow, 2)
    mixed_out = (x_local + scaling[:, None, None] * conv_out).astype(jnp.bfloat16)
    capacity = tiles.shape[2]
    n_sides = 2 * capacity
    per_block = length // TB
    sides = jnp.concatenate([tiles[..., 0], tiles[..., 1]], axis=-1)
    side_source = sides // per_block
    side_local = sides % per_block
    own_sides = lax.dynamic_index_in_dim(sides, my_index, 1, keepdims=False)
    own_source = own_sides // per_block
    before = jnp.arange(n_sides)[None, :] < jnp.arange(n_sides)[:, None]
    same_source = own_source[:, :, None] == own_source[:, None, :]
    rank_within = jnp.sum(jnp.logical_and(same_source, before[None]), axis=-1)
    slot_index = own_source * PER + rank_within
    held_here = side_source == my_index
    held_order = jnp.cumsum(held_here.astype(jnp.int32), axis=-1) - 1
    picks = jnp.stack(
        [
            jnp.sum(
                jnp.where(jnp.logical_and(held_here, held_order == position), side_local, 0),
                axis=-1,
            )
            for position in range(PER)
        ],
        axis=-1,
    )
    blocks = mixed_out.reshape(members, per_block, TB, narrow)
    whole = lax.all_gather(blocks, "seq", axis=1, tiled=True)
    side_rows = take_rows(whole, own_sides)
    row_side = side_rows[:, :capacity]
    col_side = side_rows[:, capacity:]
    partial_tiles = jnp.einsum(
        "mcid,mcjd->mcij", row_side, col_side, preferred_element_type=jnp.float32
    )
    predicted = lax.psum(partial_tiles, "mp") / math.sqrt(width)
    target_tiles = targets[:, 0].reshape(members, capacity, TB, TB)
    own_count = lax.dynamic_index_in_dim(counts, my_index, 1, keepdims=False)
    live_mask = (jnp.arange(capacity)[None, :] < own_count[:, None]).astype(jnp.float32)
    n_live = jnp.sum(counts, axis=-1).astype(jnp.float32)
    dpredicted = (
        2.0
        / math.sqrt(width)
        * live_mask[:, :, None, None]
        * (predicted - target_tiles)
        / n_live[:, None, None, None]
    )
    row_float = row_side.astype(jnp.float32)
    col_float = col_side.astype(jnp.float32)
    drow = jnp.einsum("mcij,mcjd->mcid", dpredicted, col_float, precision=lax.Precision.HIGHEST)
    dcol = jnp.einsum("mcij,mcid->mcjd", dpredicted, row_float, precision=lax.Precision.HIGHEST)
    dside = jnp.concatenate([drow, dcol], axis=1).astype(jnp.bfloat16)
    inverse = jnp.argsort(slot_index, axis=-1)
    outgoing_grads = take_rows(dside, inverse).reshape(members, seq_count, PER, TB, narrow)
    returned = lax.all_to_all(outgoing_grads, "seq", split_axis=1, concat_axis=1, tiled=True)
    selector = (
        picks.reshape(members, seq_count * PER)[:, :, None] == jnp.arange(per_block)[None, None, :]
    ).astype(jnp.bfloat16)
    dmixed = jnp.einsum(
        "mkn,mktd->mntd",
        selector,
        returned.reshape(members, seq_count * PER, TB, narrow),
        preferred_element_type=jnp.float32,
    ).reshape(members, length, narrow)
    dconv = (scaling[:, None, None] * dmixed).astype(jnp.bfloat16)
    weight_local = weight_term(padded, dconv, length, taps)
    return lax.psum_scatter(weight_local, ("seq", "dp"), scatter_dimension=2, tiled=True)


def axis_sum(value, axis):
    count = lax.axis_size(axis)
    total = value
    for shift in range(1, count):
        total = total + lax.ppermute(value, axis, [(i, (i + shift) % count) for i in range(count)])
    return total


def sparse_path(features, conv_weight, keep, tiles, counts, targets):
    _, length, width = features.shape
    taps, narrow, _ = conv_weight.shape
    halo = taps // 2
    span = TB + 2 * halo
    owners, capacity = tiles.shape[1], tiles.shape[2]
    n_sides = 2 * capacity
    per_block = length // TB
    seq_count = lax.axis_size("seq")
    groups = lax.axis_size("dp")
    peers = seq_count * groups
    held = owners * PER
    cols = width // peers
    my_index = lax.axis_index("seq")
    my_part = lax.axis_index("mp")

    before = jnp.arange(n_sides)[None, :] < jnp.arange(n_sides)[:, None]
    own_sides = jnp.concatenate([tiles[0, ..., 0], tiles[0, ..., 1]], axis=-1)
    own_source = own_sides // per_block
    own_same = own_source[:, :, None] == own_source[:, None, :]
    own_rank = jnp.sum(jnp.logical_and(own_same, before), axis=-1)
    held_here = own_source == my_index
    picks = jnp.stack(
        [
            jnp.sum(jnp.where(jnp.logical_and(held_here, own_rank == r), own_sides % per_block, 0), axis=-1)
            for r in range(PER)
        ],
        axis=-1,
    ).reshape(held)

    cells = features[0]
    ends = seq_count - 1
    if seq_count == 2:
        swapped = lax.ppermute(
            jnp.concatenate([cells[length - halo :], cells[:halo]]), "seq", [(0, 1), (1, 0)]
        )
        head = jnp.where(my_index == 0, jnp.zeros_like(swapped[:halo]), swapped[:halo])
        tail = jnp.where(my_index == ends, jnp.zeros_like(swapped[halo:]), swapped[halo:])
    else:
        head = lax.ppermute(cells[length - halo :], "seq", [(i, i + 1) for i in range(ends)])
        tail = lax.ppermute(cells[:halo], "seq", [(i + 1, i) for i in range(ends)])
    rows = picks[:, None] * TB - halo + jnp.arange(span)[None, :]
    flat_rows = rows.reshape(-1)
    pick_inside = (flat_rows[:, None] == jnp.arange(length)[None, :]).astype(cells.dtype)
    inside = jnp.dot(pick_inside, cells, preferred_element_type=jnp.float32)
    edge_rows = jnp.concatenate([head, tail], axis=0)
    edge_index = jnp.where(flat_rows < 0, flat_rows + halo, flat_rows - length + halo)
    in_range = jnp.logical_and(flat_rows >= 0, flat_rows < length)
    pick_edge = jnp.logical_and(
        edge_index[:, None] == jnp.arange(2 * halo)[None, :], jnp.logical_not(in_range)[:, None]
    ).astype(cells.dtype)
    outside = jnp.dot(pick_edge, edge_rows, preferred_element_type=jnp.float32)
    windows = (inside + outside).astype(cells.dtype).reshape(held, span, width)
    x_float = windows.astype(jnp.float32)
    act = jax.nn.gelu(x_float).astype(jnp.bfloat16)
    conv_out = jnp.einsum("hti,oi->hto", act[:, 0:TB], conv_weight[0], preferred_element_type=jnp.float32)
    for offset in range(1, taps):
        conv_out = conv_out + jnp.einsum(
            "hti,oi->hto", act[:, offset : offset + TB], conv_weight[offset], preferred_element_type=jnp.float32
        )
    my_scale = 1.25 * keep[0].astype(jnp.float32)
    x_part = lax.dynamic_slice_in_dim(x_float[:, halo : halo + TB], my_part * narrow, narrow, 2)
    mixed = (x_part + my_scale * conv_out).astype(jnp.bfloat16)

    def lanes(part):
        flat = part.reshape(part.shape[0], -1)
        flat = jnp.pad(flat, ((0, 0), (0, -flat.shape[1] % 128)))
        return flat.reshape(flat.shape[0], -1, 128)

    act_cut = lanes(act.reshape(held, span, peers, cols).transpose(2, 0, 1, 3))
    mixed_part = lanes(mixed.reshape(1, -1))
    wide = targets.reshape(-1)
    pieces = []
    for _ in range(3):
        piece = lax.reduce_precision(wide, exponent_bits=8, mantissa_bits=7)
        pieces.append(piece)
        wide = wide - piece
    small = jnp.concatenate([tiles.reshape(-1), counts.reshape(-1), keep.reshape(-1)]).astype(jnp.float32)
    meta_part = lanes(jnp.concatenate(pieces + [small]).astype(jnp.bfloat16).reshape(1, -1))
    rows_mixed, rows_act, rows_meta = mixed_part.shape[1], act_cut.shape[1], meta_part.shape[1]
    outgoing = jnp.concatenate(
        [
            jnp.broadcast_to(mixed_part, (peers, rows_mixed, 128)),
            act_cut,
            jnp.broadcast_to(meta_part, (peers, rows_meta, 128)),
        ],
        axis=1,
    )
    outgoing = jnp.pad(outgoing, ((0, 0), (0, -outgoing.shape[1] % 16), (0, 0)))
    incoming = lax.all_to_all(outgoing, ("seq", "dp"), 0, 0, tiled=True)
    n_mixed = held * TB * narrow
    n_act = held * span * cols
    mixed_in = incoming[:, :rows_mixed].reshape(peers, -1)[:, :n_mixed].reshape(peers * held, TB, narrow)
    act_in = incoming[:, rows_mixed : rows_mixed + rows_act].reshape(peers, -1)[:, :n_act]
    act_in = act_in.reshape(peers * held, span, cols)
    meta_in = incoming[:, rows_mixed + rows_act : rows_mixed + rows_act + rows_meta].reshape(peers, -1)
    meta_in = meta_in.astype(jnp.float32).reshape(seq_count, groups, -1)
    n_targets = capacity * TB * TB
    n_tiles = owners * capacity * 2
    targets_all = meta_in[:, :, :n_targets] + meta_in[:, :, n_targets : 2 * n_targets]
    targets_all = targets_all + meta_in[:, :, 2 * n_targets : 3 * n_targets]
    ints = meta_in[0, :, 3 * n_targets :].astype(jnp.int32)
    tiles_all = ints[:, :n_tiles].reshape(groups, owners, capacity, 2)
    counts_all = ints[:, n_tiles : n_tiles + owners]
    keep_all = ints[:, n_tiles + owners]

    sides = jnp.concatenate([tiles_all[..., 0], tiles_all[..., 1]], axis=-1)
    source = sides // per_block
    local = sides % per_block
    same_source = source[..., :, None] == source[..., None, :]
    rank = jnp.sum(jnp.logical_and(same_source, before), axis=-1)
    slot = (source * groups + jnp.arange(groups)[:, None, None]) * held + jnp.arange(owners)[None, :, None] * PER + rank

    side_rows = jnp.take(mixed_in, slot, axis=0)
    row_side = side_rows[:, :, :capacity]
    col_side = side_rows[:, :, capacity:]
    partial_tiles = jnp.einsum("qocid,qocjd->qocij", row_side, col_side, preferred_element_type=jnp.float32)
    lanes_shape = partial_tiles.shape
    summed = axis_sum(partial_tiles.reshape(-1, 128), "mp").reshape(lanes_shape)
    predicted = summed / math.sqrt(width)
    target_tiles = targets_all.reshape(seq_count, groups, capacity, TB, TB).transpose(1, 0, 2, 3, 4)
    live_mask = (jnp.arange(capacity)[None, None, :] < counts_all[:, :, None]).astype(jnp.float32)
    n_live = jnp.sum(counts_all, axis=-1).astype(jnp.float32)
    dpredicted = (
        2.0
        / math.sqrt(width)
        * live_mask[..., None, None]
        * (predicted - target_tiles)
        / n_live[:, None, None, None, None]
    )
    row_float = row_side.astype(jnp.float32)
    col_float = col_side.astype(jnp.float32)
    drow = jnp.einsum("qocij,qocjd->qocid", dpredicted, col_float, precision=lax.Precision.HIGHEST)
    dcol = jnp.einsum("qocij,qocid->qocjd", dpredicted, row_float, precision=lax.Precision.HIGHEST)
    grads = jnp.concatenate([drow, dcol], axis=2).astype(jnp.bfloat16).astype(jnp.float32)
    grads = grads.reshape(groups, owners * n_sides, TB, narrow)
    flat_sides = sides.reshape(groups, owners * n_sides)
    same_block = flat_sides[:, :, None] == flat_sides[:, None, :]
    total = jnp.einsum(
        "qab,qbtd->qatd", same_block.astype(jnp.float32), grads, precision=lax.Precision.HIGHEST
    )
    earlier = jnp.arange(owners * n_sides)[None, :] < jnp.arange(owners * n_sides)[:, None]
    first = jnp.logical_not(jnp.any(jnp.logical_and(same_block, earlier[None]), axis=-1))
    scaling = 1.25 * keep_all.astype(jnp.float32)
    dconv = (scaling[:, None, None, None] * total).astype(jnp.bfloat16)
    dconv = jnp.where(first[..., None, None], dconv, jnp.zeros_like(dconv))
    act_sides = jnp.take(act_in, slot.reshape(groups, owners * n_sides), axis=0)
    shifted = jnp.concatenate([act_sides[:, :, offset : offset + TB] for offset in range(taps)], axis=-1)
    product = jnp.dot(
        dconv.reshape(-1, narrow).T, shifted.reshape(-1, taps * cols), preferred_element_type=jnp.float32
    )
    return product.reshape(narrow, taps, cols).transpose(1, 0, 2)


def per_device(features, conv_weight, keep, tiles, counts, targets):
    members, length, _ = features.shape
    owners, capacity = tiles.shape[1], tiles.shape[2]
    blocks = lax.axis_size("seq") * length // TB
    fits = members == 1 and targets.shape[1] == 1 and 2 * owners * capacity * TB <= length
    fits = fits and blocks <= 256 and capacity <= 256
    if fits:
        return sparse_path(features, conv_weight, keep, tiles, counts, targets)
    return dense_path(features, conv_weight, keep, tiles, counts, targets)


def solution(mesh):
    placed = (
        P("dp", "seq", None),
        P(None, "mp", None),
        P("dp"),
        P("dp", None, None, None),
        P("dp", None),
        P("dp", "seq", None, None),
    )
    return jax.shard_map(
        per_device,
        mesh=mesh,
        in_specs=placed,
        out_specs=P(None, "mp", ("seq", "dp")),
        check_vma=False,
    )
```

```python
import math

import jax
import jax.numpy as jnp
from jax import lax
from jax.sharding import PartitionSpec as P

TB = 32
PER = 2


def extended(cells, sides, width):
    for axis, dim in sides:
        count = lax.axis_size(axis)
        ends = count - 1
        head = lax.slice_in_dim(cells, 0, width, axis=dim)
        tail = lax.slice_in_dim(cells, cells.shape[dim] - width, cells.shape[dim], axis=dim)
        cells = jnp.concatenate(
            [
                lax.ppermute(tail, axis, [(i, (i + 1) % count) for i in range(ends)]),
                cells,
                lax.ppermute(head, axis, [((i + 1) % count, i) for i in range(ends)]),
            ],
            axis=dim,
        )
    return cells


def take_rows(source_array, index_array):
    return jax.vmap(lambda table, picked: table[picked])(source_array, index_array)


def conv_apply(padded, weight, length):
    total = jnp.einsum(
        "mbi,oi->mbo", padded[:, 0:length], weight[0], preferred_element_type=jnp.float32
    )
    for offset in range(1, weight.shape[0]):
        total = total + jnp.einsum(
            "mbi,oi->mbo",
            padded[:, offset : offset + length],
            weight[offset],
            preferred_element_type=jnp.float32,
        )
    return total


def weight_term(padded, dconv, length, taps):
    return jnp.stack(
        [
            jnp.einsum(
                "mbi,mbo->oi",
                padded[:, offset : offset + length],
                dconv,
                preferred_element_type=jnp.float32,
            )
            for offset in range(taps)
        ]
    )


def dense_path(features, conv_weight, keep, tiles, counts, targets):
    members, length, width = features.shape
    taps = conv_weight.shape[0]
    narrow = conv_weight.shape[1]
    seq_count = lax.axis_size("seq")
    my_index = lax.axis_index("seq")
    my_part = lax.axis_index("mp")
    x_float = features.astype(jnp.float32)
    activations = jax.nn.gelu(x_float).astype(jnp.bfloat16)
    padded = extended(activations, (("seq", 1),), 2)
    scaling = 1.25 * keep.astype(jnp.float32)
    conv_out = conv_apply(padded, conv_weight, length)
    x_local = lax.dynamic_slice_in_dim(x_float, my_part * narrow, narrow, 2)
    mixed_out = (x_local + scaling[:, None, None] * conv_out).astype(jnp.bfloat16)
    capacity = tiles.shape[2]
    n_sides = 2 * capacity
    per_block = length // TB
    sides = jnp.concatenate([tiles[..., 0], tiles[..., 1]], axis=-1)
    side_source = sides // per_block
    side_local = sides % per_block
    own_sides = lax.dynamic_index_in_dim(sides, my_index, 1, keepdims=False)
    own_source = own_sides // per_block
    before = jnp.arange(n_sides)[None, :] < jnp.arange(n_sides)[:, None]
    same_source = own_source[:, :, None] == own_source[:, None, :]
    rank_within = jnp.sum(jnp.logical_and(same_source, before[None]), axis=-1)
    slot_index = own_source * PER + rank_within
    held_here = side_source == my_index
    held_order = jnp.cumsum(held_here.astype(jnp.int32), axis=-1) - 1
    picks = jnp.stack(
        [
            jnp.sum(
                jnp.where(jnp.logical_and(held_here, held_order == position), side_local, 0),
                axis=-1,
            )
            for position in range(PER)
        ],
        axis=-1,
    )
    blocks = mixed_out.reshape(members, per_block, TB, narrow)
    whole = lax.all_gather(blocks, "seq", axis=1, tiled=True)
    side_rows = take_rows(whole, own_sides)
    row_side = side_rows[:, :capacity]
    col_side = side_rows[:, capacity:]
    partial_tiles = jnp.einsum(
        "mcid,mcjd->mcij", row_side, col_side, preferred_element_type=jnp.float32
    )
    predicted = lax.psum(partial_tiles, "mp") / math.sqrt(width)
    target_tiles = targets[:, 0].reshape(members, capacity, TB, TB)
    own_count = lax.dynamic_index_in_dim(counts, my_index, 1, keepdims=False)
    live_mask = (jnp.arange(capacity)[None, :] < own_count[:, None]).astype(jnp.float32)
    n_live = jnp.sum(counts, axis=-1).astype(jnp.float32)
    dpredicted = (
        2.0
        / math.sqrt(width)
        * live_mask[:, :, None, None]
        * (predicted - target_tiles)
        / n_live[:, None, None, None]
    )
    row_float = row_side.astype(jnp.float32)
    col_float = col_side.astype(jnp.float32)
    drow = jnp.einsum("mcij,mcjd->mcid", dpredicted, col_float, precision=lax.Precision.HIGHEST)
    dcol = jnp.einsum("mcij,mcid->mcjd", dpredicted, row_float, precision=lax.Precision.HIGHEST)
    dside = jnp.concatenate([drow, dcol], axis=1).astype(jnp.bfloat16)
    inverse = jnp.argsort(slot_index, axis=-1)
    outgoing_grads = take_rows(dside, inverse).reshape(members, seq_count, PER, TB, narrow)
    returned = lax.all_to_all(outgoing_grads, "seq", split_axis=1, concat_axis=1, tiled=True)
    selector = (
        picks.reshape(members, seq_count * PER)[:, :, None] == jnp.arange(per_block)[None, None, :]
    ).astype(jnp.bfloat16)
    dmixed = jnp.einsum(
        "mkn,mktd->mntd",
        selector,
        returned.reshape(members, seq_count * PER, TB, narrow),
        preferred_element_type=jnp.float32,
    ).reshape(members, length, narrow)
    dconv = (scaling[:, None, None] * dmixed).astype(jnp.bfloat16)
    weight_local = weight_term(padded, dconv, length, taps)
    return lax.psum_scatter(weight_local, ("seq", "dp"), scatter_dimension=2, tiled=True)


def axis_sum(value, axis):
    count = lax.axis_size(axis)
    total = value
    for shift in range(1, count):
        total = total + lax.ppermute(value, axis, [(i, (i + shift) % count) for i in range(count)])
    return total


def sparse_path(features, conv_weight, keep, tiles, counts, targets):
    _, length, width = features.shape
    taps, narrow, _ = conv_weight.shape
    halo = taps // 2
    span = TB + 2 * halo
    owners, capacity = tiles.shape[1], tiles.shape[2]
    n_sides = 2 * capacity
    per_block = length // TB
    seq_count = lax.axis_size("seq")
    groups = lax.axis_size("dp")
    peers = seq_count * groups
    held = owners * PER
    cols = width // peers
    my_index = lax.axis_index("seq")
    my_part = lax.axis_index("mp")

    before = jnp.arange(n_sides)[None, :] < jnp.arange(n_sides)[:, None]
    own_sides = jnp.concatenate([tiles[0, ..., 0], tiles[0, ..., 1]], axis=-1)
    own_source = own_sides // per_block
    own_same = own_source[:, :, None] == own_source[:, None, :]
    own_rank = jnp.sum(jnp.logical_and(own_same, before), axis=-1)
    held_here = own_source == my_index
    picks = jnp.stack(
        [
            jnp.sum(jnp.where(jnp.logical_and(held_here, own_rank == r), own_sides % per_block, 0), axis=-1)
            for r in range(PER)
        ],
        axis=-1,
    ).reshape(held)

    cells = features[0]
    ends = seq_count - 1
    if seq_count == 2:
        swapped = lax.ppermute(
            jnp.concatenate([cells[length - halo :], cells[:halo]]), "seq", [(0, 1), (1, 0)]
        )
        head = jnp.where(my_index == 0, jnp.zeros_like(swapped[:halo]), swapped[:halo])
        tail = jnp.where(my_index == ends, jnp.zeros_like(swapped[halo:]), swapped[halo:])
    else:
        head = lax.ppermute(cells[length - halo :], "seq", [(i, i + 1) for i in range(ends)])
        tail = lax.ppermute(cells[:halo], "seq", [(i + 1, i) for i in range(ends)])
    last = per_block - 1
    stacked = cells.reshape(per_block, TB * width)
    block_ids = jnp.arange(per_block)[None, :]

    def select(offset, part):
        choose = (picks[:, None] + offset == block_ids).astype(cells.dtype)
        return jnp.dot(choose, part, preferred_element_type=jnp.float32)

    middle = select(0, stacked).reshape(held, TB, width)
    prev_tail = select(-1, stacked[:, (TB - halo) * width :]).reshape(held, halo, width)
    next_head = select(1, stacked[:, : halo * width]).reshape(held, halo, width)
    lower = jnp.where((picks == 0)[:, None, None], head[None].astype(jnp.float32), prev_tail)
    upper = jnp.where((picks == last)[:, None, None], tail[None].astype(jnp.float32), next_head)
    windows = jnp.concatenate([lower, middle, upper], axis=1).astype(cells.dtype)
    x_float = windows.astype(jnp.float32)
    act = jax.nn.gelu(x_float).astype(jnp.bfloat16)
    conv_out = jnp.einsum("hti,oi->hto", act[:, 0:TB], conv_weight[0], preferred_element_type=jnp.float32)
    for offset in range(1, taps):
        conv_out = conv_out + jnp.einsum(
            "hti,oi->hto", act[:, offset : offset + TB], conv_weight[offset], preferred_element_type=jnp.float32
        )
    my_scale = 1.25 * keep[0].astype(jnp.float32)
    x_part = lax.dynamic_slice_in_dim(x_float[:, halo : halo + TB], my_part * narrow, narrow, 2)
    mixed = (x_part + my_scale * conv_out).astype(jnp.bfloat16)

    def lanes(part):
        flat = part.reshape(part.shape[0], -1)
        flat = jnp.pad(flat, ((0, 0), (0, -flat.shape[1] % 128)))
        return flat.reshape(flat.shape[0], -1, 128)

    act_cut = lanes(act.reshape(held, span, peers, cols).transpose(2, 0, 1, 3))
    mixed_part = lanes(mixed.reshape(1, -1))
    wide = targets.reshape(-1)
    pieces = []
    for _ in range(3):
        piece = lax.reduce_precision(wide, exponent_bits=8, mantissa_bits=7)
        pieces.append(piece)
        wide = wide - piece
    small = jnp.concatenate([tiles.reshape(-1), counts.reshape(-1), keep.reshape(-1)]).astype(jnp.float32)
    meta_part = lanes(jnp.concatenate(pieces + [small]).astype(jnp.bfloat16).reshape(1, -1))
    rows_mixed, rows_act, rows_meta = mixed_part.shape[1], act_cut.shape[1], meta_part.shape[1]
    outgoing = jnp.concatenate(
        [
            jnp.broadcast_to(mixed_part, (peers, rows_mixed, 128)),
            act_cut,
            jnp.broadcast_to(meta_part, (peers, rows_meta, 128)),
        ],
        axis=1,
    )
    outgoing = jnp.pad(outgoing, ((0, 0), (0, -outgoing.shape[1] % 16), (0, 0)))
    incoming = lax.all_to_all(outgoing, ("seq", "dp"), 0, 0, tiled=True)
    n_mixed = held * TB * narrow
    n_act = held * span * cols
    mixed_in = incoming[:, :rows_mixed].reshape(peers, -1)[:, :n_mixed].reshape(peers * held, TB, narrow)
    act_in = incoming[:, rows_mixed : rows_mixed + rows_act].reshape(peers, -1)[:, :n_act]
    act_in = act_in.reshape(peers * held, span, cols)
    meta_in = incoming[:, rows_mixed + rows_act : rows_mixed + rows_act + rows_meta].reshape(peers, -1)
    meta_in = meta_in.astype(jnp.float32).reshape(seq_count, groups, -1)
    n_targets = capacity * TB * TB
    n_tiles = owners * capacity * 2
    targets_all = meta_in[:, :, :n_targets] + meta_in[:, :, n_targets : 2 * n_targets]
    targets_all = targets_all + meta_in[:, :, 2 * n_targets : 3 * n_targets]
    ints = meta_in[0, :, 3 * n_targets :].astype(jnp.int32)
    tiles_all = ints[:, :n_tiles].reshape(groups, owners, capacity, 2)
    counts_all = ints[:, n_tiles : n_tiles + owners]
    keep_all = ints[:, n_tiles + owners]

    sides = jnp.concatenate([tiles_all[..., 0], tiles_all[..., 1]], axis=-1)
    source = sides // per_block
    local = sides % per_block
    same_source = source[..., :, None] == source[..., None, :]
    rank = jnp.sum(jnp.logical_and(same_source, before), axis=-1)
    slot = (source * groups + jnp.arange(groups)[:, None, None]) * held + jnp.arange(owners)[None, :, None] * PER + rank

    side_rows = jnp.take(mixed_in, slot, axis=0)
    row_side = side_rows[:, :, :capacity]
    col_side = side_rows[:, :, capacity:]
    partial_tiles = jnp.einsum("qocid,qocjd->qocij", row_side, col_side, preferred_element_type=jnp.float32)
    lanes_shape = partial_tiles.shape
    summed = axis_sum(partial_tiles.reshape(-1, 128), "mp").reshape(lanes_shape)
    predicted = summed / math.sqrt(width)
    target_tiles = targets_all.reshape(seq_count, groups, capacity, TB, TB).transpose(1, 0, 2, 3, 4)
    live_mask = (jnp.arange(capacity)[None, None, :] < counts_all[:, :, None]).astype(jnp.float32)
    n_live = jnp.sum(counts_all, axis=-1).astype(jnp.float32)
    dpredicted = (
        2.0
        / math.sqrt(width)
        * live_mask[..., None, None]
        * (predicted - target_tiles)
        / n_live[:, None, None, None, None]
    )
    row_float = row_side.astype(jnp.float32)
    col_float = col_side.astype(jnp.float32)
    drow = jnp.einsum("qocij,qocjd->qocid", dpredicted, col_float, precision=lax.Precision.HIGHEST)
    dcol = jnp.einsum("qocij,qocid->qocjd", dpredicted, row_float, precision=lax.Precision.HIGHEST)
    grads = jnp.concatenate([drow, dcol], axis=2).astype(jnp.bfloat16).astype(jnp.float32)
    grads = grads.reshape(groups, owners * n_sides, TB, narrow)
    flat_sides = sides.reshape(groups, owners * n_sides)
    same_block = flat_sides[:, :, None] == flat_sides[:, None, :]
    total = jnp.einsum(
        "qab,qbtd->qatd", same_block.astype(jnp.float32), grads, precision=lax.Precision.HIGHEST
    )
    earlier = jnp.arange(owners * n_sides)[None, :] < jnp.arange(owners * n_sides)[:, None]
    first = jnp.logical_not(jnp.any(jnp.logical_and(same_block, earlier[None]), axis=-1))
    scaling = 1.25 * keep_all.astype(jnp.float32)
    dconv = (scaling[:, None, None, None] * total).astype(jnp.bfloat16)
    dconv = jnp.where(first[..., None, None], dconv, jnp.zeros_like(dconv))
    act_sides = jnp.take(act_in, slot.reshape(groups, owners * n_sides), axis=0)
    return jnp.stack(
        [
            jnp.einsum(
                "qato,qati->oi",
                dconv,
                act_sides[:, :, offset : offset + TB],
                preferred_element_type=jnp.float32,
            )
            for offset in range(taps)
        ]
    )


def per_device(features, conv_weight, keep, tiles, counts, targets):
    members, length, _ = features.shape
    owners, capacity = tiles.shape[1], tiles.shape[2]
    blocks = lax.axis_size("seq") * length // TB
    fits = members == 1 and targets.shape[1] == 1 and 2 * owners * capacity * TB <= length
    fits = fits and blocks <= 256 and capacity <= 256
    if fits:
        return sparse_path(features, conv_weight, keep, tiles, counts, targets)
    return dense_path(features, conv_weight, keep, tiles, counts, targets)


def solution(mesh):
    placed = (
        P("dp", "seq", None),
        P(None, "mp", None),
        P("dp"),
        P("dp", None, None, None),
        P("dp", None),
        P("dp", "seq", None, None),
    )
    return jax.shard_map(
        per_device,
        mesh=mesh,
        in_specs=placed,
        out_specs=P(None, "mp", ("seq", "dp")),
        check_vma=False,
    )
```

```python
import math

import jax
import jax.numpy as jnp
from jax import lax
from jax.sharding import PartitionSpec as P

TB = 32
PER = 2


def extended(cells, sides, width):
    for axis, dim in sides:
        count = lax.axis_size(axis)
        ends = count - 1
        head = lax.slice_in_dim(cells, 0, width, axis=dim)
        tail = lax.slice_in_dim(cells, cells.shape[dim] - width, cells.shape[dim], axis=dim)
        cells = jnp.concatenate(
            [
                lax.ppermute(tail, axis, [(i, (i + 1) % count) for i in range(ends)]),
                cells,
                lax.ppermute(head, axis, [((i + 1) % count, i) for i in range(ends)]),
            ],
            axis=dim,
        )
    return cells


def take_rows(source_array, index_array):
    return jax.vmap(lambda table, picked: table[picked])(source_array, index_array)


def conv_apply(padded, weight, length):
    total = jnp.einsum(
        "mbi,oi->mbo", padded[:, 0:length], weight[0], preferred_element_type=jnp.float32
    )
    for offset in range(1, weight.shape[0]):
        total = total + jnp.einsum(
            "mbi,oi->mbo",
            padded[:, offset : offset + length],
            weight[offset],
            preferred_element_type=jnp.float32,
        )
    return total


def weight_term(padded, dconv, length, taps):
    return jnp.stack(
        [
            jnp.einsum(
                "mbi,mbo->oi",
                padded[:, offset : offset + length],
                dconv,
                preferred_element_type=jnp.float32,
            )
            for offset in range(taps)
        ]
    )


def dense_path(features, conv_weight, keep, tiles, counts, targets):
    members, length, width = features.shape
    taps = conv_weight.shape[0]
    narrow = conv_weight.shape[1]
    seq_count = lax.axis_size("seq")
    my_index = lax.axis_index("seq")
    my_part = lax.axis_index("mp")
    x_float = features.astype(jnp.float32)
    activations = jax.nn.gelu(x_float).astype(jnp.bfloat16)
    padded = extended(activations, (("seq", 1),), 2)
    scaling = 1.25 * keep.astype(jnp.float32)
    conv_out = conv_apply(padded, conv_weight, length)
    x_local = lax.dynamic_slice_in_dim(x_float, my_part * narrow, narrow, 2)
    mixed_out = (x_local + scaling[:, None, None] * conv_out).astype(jnp.bfloat16)
    capacity = tiles.shape[2]
    n_sides = 2 * capacity
    per_block = length // TB
    sides = jnp.concatenate([tiles[..., 0], tiles[..., 1]], axis=-1)
    side_source = sides // per_block
    side_local = sides % per_block
    own_sides = lax.dynamic_index_in_dim(sides, my_index, 1, keepdims=False)
    own_source = own_sides // per_block
    before = jnp.arange(n_sides)[None, :] < jnp.arange(n_sides)[:, None]
    same_source = own_source[:, :, None] == own_source[:, None, :]
    rank_within = jnp.sum(jnp.logical_and(same_source, before[None]), axis=-1)
    slot_index = own_source * PER + rank_within
    held_here = side_source == my_index
    held_order = jnp.cumsum(held_here.astype(jnp.int32), axis=-1) - 1
    picks = jnp.stack(
        [
            jnp.sum(
                jnp.where(jnp.logical_and(held_here, held_order == position), side_local, 0),
                axis=-1,
            )
            for position in range(PER)
        ],
        axis=-1,
    )
    blocks = mixed_out.reshape(members, per_block, TB, narrow)
    whole = lax.all_gather(blocks, "seq", axis=1, tiled=True)
    side_rows = take_rows(whole, own_sides)
    row_side = side_rows[:, :capacity]
    col_side = side_rows[:, capacity:]
    partial_tiles = jnp.einsum(
        "mcid,mcjd->mcij", row_side, col_side, preferred_element_type=jnp.float32
    )
    predicted = lax.psum(partial_tiles, "mp") / math.sqrt(width)
    target_tiles = targets[:, 0].reshape(members, capacity, TB, TB)
    own_count = lax.dynamic_index_in_dim(counts, my_index, 1, keepdims=False)
    live_mask = (jnp.arange(capacity)[None, :] < own_count[:, None]).astype(jnp.float32)
    n_live = jnp.sum(counts, axis=-1).astype(jnp.float32)
    dpredicted = (
        2.0
        / math.sqrt(width)
        * live_mask[:, :, None, None]
        * (predicted - target_tiles)
        / n_live[:, None, None, None]
    )
    row_float = row_side.astype(jnp.float32)
    col_float = col_side.astype(jnp.float32)
    drow = jnp.einsum("mcij,mcjd->mcid", dpredicted, col_float, precision=lax.Precision.HIGHEST)
    dcol = jnp.einsum("mcij,mcid->mcjd", dpredicted, row_float, precision=lax.Precision.HIGHEST)
    dside = jnp.concatenate([drow, dcol], axis=1).astype(jnp.bfloat16)
    inverse = jnp.argsort(slot_index, axis=-1)
    outgoing_grads = take_rows(dside, inverse).reshape(members, seq_count, PER, TB, narrow)
    returned = lax.all_to_all(outgoing_grads, "seq", split_axis=1, concat_axis=1, tiled=True)
    selector = (
        picks.reshape(members, seq_count * PER)[:, :, None] == jnp.arange(per_block)[None, None, :]
    ).astype(jnp.bfloat16)
    dmixed = jnp.einsum(
        "mkn,mktd->mntd",
        selector,
        returned.reshape(members, seq_count * PER, TB, narrow),
        preferred_element_type=jnp.float32,
    ).reshape(members, length, narrow)
    dconv = (scaling[:, None, None] * dmixed).astype(jnp.bfloat16)
    weight_local = weight_term(padded, dconv, length, taps)
    return lax.psum_scatter(weight_local, ("seq", "dp"), scatter_dimension=2, tiled=True)


def axis_sum(value, axis):
    count = lax.axis_size(axis)
    total = value
    for shift in range(1, count):
        total = total + lax.ppermute(value, axis, [(i, (i + shift) % count) for i in range(count)])
    return total


def sparse_path(features, conv_weight, keep, tiles, counts, targets):
    _, length, width = features.shape
    taps, narrow, _ = conv_weight.shape
    halo = taps // 2
    span = TB + 2 * halo
    owners, capacity = tiles.shape[1], tiles.shape[2]
    n_sides = 2 * capacity
    per_block = length // TB
    seq_count = lax.axis_size("seq")
    groups = lax.axis_size("dp")
    peers = seq_count * groups
    held = owners * PER
    cols = width // peers
    my_index = lax.axis_index("seq")
    my_part = lax.axis_index("mp")

    before = jnp.arange(n_sides)[None, :] < jnp.arange(n_sides)[:, None]
    own_sides = jnp.concatenate([tiles[0, ..., 0], tiles[0, ..., 1]], axis=-1)
    own_source = own_sides // per_block
    own_same = own_source[:, :, None] == own_source[:, None, :]
    own_rank = jnp.sum(jnp.logical_and(own_same, before), axis=-1)
    held_here = own_source == my_index
    picks = jnp.stack(
        [
            jnp.sum(jnp.where(jnp.logical_and(held_here, own_rank == r), own_sides % per_block, 0), axis=-1)
            for r in range(PER)
        ],
        axis=-1,
    ).reshape(held)

    cells = features[0]
    ends = seq_count - 1
    if seq_count == 2:
        swapped = lax.ppermute(
            jnp.concatenate([cells[length - halo :], cells[:halo]]), "seq", [(0, 1), (1, 0)]
        )
        head = jnp.where(my_index == 0, jnp.zeros_like(swapped[:halo]), swapped[:halo])
        tail = jnp.where(my_index == ends, jnp.zeros_like(swapped[halo:]), swapped[halo:])
    else:
        head = lax.ppermute(cells[length - halo :], "seq", [(i, i + 1) for i in range(ends)])
        tail = lax.ppermute(cells[:halo], "seq", [(i + 1, i) for i in range(ends)])
    last = per_block - 1
    stacked = cells.reshape(per_block, TB, width)
    middle = jnp.take(stacked, picks, axis=0, mode="clip").astype(jnp.float32)
    prev_tail = jnp.take(stacked[:, TB - halo :], jnp.maximum(picks - 1, 0), axis=0, mode="clip")
    next_head = jnp.take(stacked[:, :halo], jnp.minimum(picks + 1, last), axis=0, mode="clip")
    prev_tail = prev_tail.astype(jnp.float32)
    next_head = next_head.astype(jnp.float32)
    lower = jnp.where((picks == 0)[:, None, None], head[None].astype(jnp.float32), prev_tail)
    upper = jnp.where((picks == last)[:, None, None], tail[None].astype(jnp.float32), next_head)
    windows = jnp.concatenate([lower, middle, upper], axis=1).astype(cells.dtype)
    x_float = windows.astype(jnp.float32)
    act = jax.nn.gelu(x_float).astype(jnp.bfloat16)
    conv_out = jnp.einsum("hti,oi->hto", act[:, 0:TB], conv_weight[0], preferred_element_type=jnp.float32)
    for offset in range(1, taps):
        conv_out = conv_out + jnp.einsum(
            "hti,oi->hto", act[:, offset : offset + TB], conv_weight[offset], preferred_element_type=jnp.float32
        )
    my_scale = 1.25 * keep[0].astype(jnp.float32)
    x_part = lax.dynamic_slice_in_dim(x_float[:, halo : halo + TB], my_part * narrow, narrow, 2)
    mixed = (x_part + my_scale * conv_out).astype(jnp.bfloat16)

    def lanes(part):
        flat = part.reshape(part.shape[0], -1)
        flat = jnp.pad(flat, ((0, 0), (0, -flat.shape[1] % 128)))
        return flat.reshape(flat.shape[0], -1, 128)

    act_cut = lanes(act.reshape(held, span, peers, cols).transpose(2, 0, 1, 3))
    mixed_part = lanes(mixed.reshape(1, -1))
    wide = targets.reshape(-1)
    pieces = []
    for _ in range(3):
        piece = lax.reduce_precision(wide, exponent_bits=8, mantissa_bits=7)
        pieces.append(piece)
        wide = wide - piece
    small = jnp.concatenate([tiles.reshape(-1), counts.reshape(-1), keep.reshape(-1)]).astype(jnp.float32)
    meta_part = lanes(jnp.concatenate(pieces + [small]).astype(jnp.bfloat16).reshape(1, -1))
    rows_mixed, rows_act, rows_meta = mixed_part.shape[1], act_cut.shape[1], meta_part.shape[1]
    outgoing = jnp.concatenate(
        [
            jnp.broadcast_to(mixed_part, (peers, rows_mixed, 128)),
            act_cut,
            jnp.broadcast_to(meta_part, (peers, rows_meta, 128)),
        ],
        axis=1,
    )
    outgoing = jnp.pad(outgoing, ((0, 0), (0, -outgoing.shape[1] % 16), (0, 0)))
    incoming = lax.all_to_all(outgoing, ("seq", "dp"), 0, 0, tiled=True)
    n_mixed = held * TB * narrow
    n_act = held * span * cols
    mixed_in = incoming[:, :rows_mixed].reshape(peers, -1)[:, :n_mixed].reshape(peers * held, TB, narrow)
    act_in = incoming[:, rows_mixed : rows_mixed + rows_act].reshape(peers, -1)[:, :n_act]
    act_in = act_in.reshape(peers * held, span, cols)
    meta_in = incoming[:, rows_mixed + rows_act : rows_mixed + rows_act + rows_meta].reshape(peers, -1)
    meta_in = meta_in.astype(jnp.float32).reshape(seq_count, groups, -1)
    n_targets = capacity * TB * TB
    n_tiles = owners * capacity * 2
    targets_all = meta_in[:, :, :n_targets] + meta_in[:, :, n_targets : 2 * n_targets]
    targets_all = targets_all + meta_in[:, :, 2 * n_targets : 3 * n_targets]
    ints = meta_in[0, :, 3 * n_targets :].astype(jnp.int32)
    tiles_all = ints[:, :n_tiles].reshape(groups, owners, capacity, 2)
    counts_all = ints[:, n_tiles : n_tiles + owners]
    keep_all = ints[:, n_tiles + owners]

    sides = jnp.concatenate([tiles_all[..., 0], tiles_all[..., 1]], axis=-1)
    source = sides // per_block
    local = sides % per_block
    same_source = source[..., :, None] == source[..., None, :]
    rank = jnp.sum(jnp.logical_and(same_source, before), axis=-1)
    slot = (source * groups + jnp.arange(groups)[:, None, None]) * held + jnp.arange(owners)[None, :, None] * PER + rank

    side_rows = jnp.take(mixed_in, slot, axis=0)
    row_side = side_rows[:, :, :capacity]
    col_side = side_rows[:, :, capacity:]
    partial_tiles = jnp.einsum("qocid,qocjd->qocij", row_side, col_side, preferred_element_type=jnp.float32)
    lanes_shape = partial_tiles.shape
    summed = axis_sum(partial_tiles.reshape(-1, 128), "mp").reshape(lanes_shape)
    predicted = summed / math.sqrt(width)
    target_tiles = targets_all.reshape(seq_count, groups, capacity, TB, TB).transpose(1, 0, 2, 3, 4)
    live_mask = (jnp.arange(capacity)[None, None, :] < counts_all[:, :, None]).astype(jnp.float32)
    n_live = jnp.sum(counts_all, axis=-1).astype(jnp.float32)
    dpredicted = (
        2.0
        / math.sqrt(width)
        * live_mask[..., None, None]
        * (predicted - target_tiles)
        / n_live[:, None, None, None, None]
    )
    row_float = row_side.astype(jnp.float32)
    col_float = col_side.astype(jnp.float32)
    drow = jnp.einsum("qocij,qocjd->qocid", dpredicted, col_float, precision=lax.Precision.HIGHEST)
    dcol = jnp.einsum("qocij,qocid->qocjd", dpredicted, row_float, precision=lax.Precision.HIGHEST)
    grads = jnp.concatenate([drow, dcol], axis=2).astype(jnp.bfloat16).astype(jnp.float32)
    grads = grads.reshape(groups, owners * n_sides, TB, narrow)
    flat_sides = sides.reshape(groups, owners * n_sides)
    same_block = flat_sides[:, :, None] == flat_sides[:, None, :]
    total = jnp.einsum(
        "qab,qbtd->qatd", same_block.astype(jnp.float32), grads, precision=lax.Precision.HIGHEST
    )
    earlier = jnp.arange(owners * n_sides)[None, :] < jnp.arange(owners * n_sides)[:, None]
    first = jnp.logical_not(jnp.any(jnp.logical_and(same_block, earlier[None]), axis=-1))
    scaling = 1.25 * keep_all.astype(jnp.float32)
    dconv = (scaling[:, None, None, None] * total).astype(jnp.bfloat16)
    dconv = jnp.where(first[..., None, None], dconv, jnp.zeros_like(dconv))
    act_sides = jnp.take(act_in, slot.reshape(groups, owners * n_sides), axis=0)
    return jnp.stack(
        [
            jnp.einsum(
                "qato,qati->oi",
                dconv,
                act_sides[:, :, offset : offset + TB],
                preferred_element_type=jnp.float32,
            )
            for offset in range(taps)
        ]
    )


def per_device(features, conv_weight, keep, tiles, counts, targets):
    members, length, _ = features.shape
    owners, capacity = tiles.shape[1], tiles.shape[2]
    blocks = lax.axis_size("seq") * length // TB
    fits = members == 1 and targets.shape[1] == 1 and 2 * owners * capacity * TB <= length
    fits = fits and blocks <= 256 and capacity <= 256
    if fits:
        return sparse_path(features, conv_weight, keep, tiles, counts, targets)
    return dense_path(features, conv_weight, keep, tiles, counts, targets)


def solution(mesh):
    placed = (
        P("dp", "seq", None),
        P(None, "mp", None),
        P("dp"),
        P("dp", None, None, None),
        P("dp", None),
        P("dp", "seq", None, None),
    )
    return jax.shard_map(
        per_device,
        mesh=mesh,
        in_specs=placed,
        out_specs=P(None, "mp", ("seq", "dp")),
        check_vma=False,
    )
```

```python
import math

import jax
import jax.numpy as jnp
from jax import lax
from jax.sharding import PartitionSpec as P

TB = 32
PER = 2


def extended(cells, sides, width):
    for axis, dim in sides:
        count = lax.axis_size(axis)
        ends = count - 1
        head = lax.slice_in_dim(cells, 0, width, axis=dim)
        tail = lax.slice_in_dim(cells, cells.shape[dim] - width, cells.shape[dim], axis=dim)
        cells = jnp.concatenate(
            [
                lax.ppermute(tail, axis, [(i, (i + 1) % count) for i in range(ends)]),
                cells,
                lax.ppermute(head, axis, [((i + 1) % count, i) for i in range(ends)]),
            ],
            axis=dim,
        )
    return cells


def take_rows(source_array, index_array):
    return jax.vmap(lambda table, picked: table[picked])(source_array, index_array)


def conv_apply(padded, weight, length):
    total = jnp.einsum(
        "mbi,oi->mbo", padded[:, 0:length], weight[0], preferred_element_type=jnp.float32
    )
    for offset in range(1, weight.shape[0]):
        total = total + jnp.einsum(
            "mbi,oi->mbo",
            padded[:, offset : offset + length],
            weight[offset],
            preferred_element_type=jnp.float32,
        )
    return total


def weight_term(padded, dconv, length, taps):
    return jnp.stack(
        [
            jnp.einsum(
                "mbi,mbo->oi",
                padded[:, offset : offset + length],
                dconv,
                preferred_element_type=jnp.float32,
            )
            for offset in range(taps)
        ]
    )


def dense_path(features, conv_weight, keep, tiles, counts, targets):
    members, length, width = features.shape
    taps = conv_weight.shape[0]
    narrow = conv_weight.shape[1]
    seq_count = lax.axis_size("seq")
    my_index = lax.axis_index("seq")
    my_part = lax.axis_index("mp")
    x_float = features.astype(jnp.float32)
    activations = jax.nn.gelu(x_float).astype(jnp.bfloat16)
    padded = extended(activations, (("seq", 1),), 2)
    scaling = 1.25 * keep.astype(jnp.float32)
    conv_out = conv_apply(padded, conv_weight, length)
    x_local = lax.dynamic_slice_in_dim(x_float, my_part * narrow, narrow, 2)
    mixed_out = (x_local + scaling[:, None, None] * conv_out).astype(jnp.bfloat16)
    capacity = tiles.shape[2]
    n_sides = 2 * capacity
    per_block = length // TB
    sides = jnp.concatenate([tiles[..., 0], tiles[..., 1]], axis=-1)
    side_source = sides // per_block
    side_local = sides % per_block
    own_sides = lax.dynamic_index_in_dim(sides, my_index, 1, keepdims=False)
    own_source = own_sides // per_block
    before = jnp.arange(n_sides)[None, :] < jnp.arange(n_sides)[:, None]
    same_source = own_source[:, :, None] == own_source[:, None, :]
    rank_within = jnp.sum(jnp.logical_and(same_source, before[None]), axis=-1)
    slot_index = own_source * PER + rank_within
    held_here = side_source == my_index
    held_order = jnp.cumsum(held_here.astype(jnp.int32), axis=-1) - 1
    picks = jnp.stack(
        [
            jnp.sum(
                jnp.where(jnp.logical_and(held_here, held_order == position), side_local, 0),
                axis=-1,
            )
            for position in range(PER)
        ],
        axis=-1,
    )
    blocks = mixed_out.reshape(members, per_block, TB, narrow)
    whole = lax.all_gather(blocks, "seq", axis=1, tiled=True)
    side_rows = take_rows(whole, own_sides)
    row_side = side_rows[:, :capacity]
    col_side = side_rows[:, capacity:]
    partial_tiles = jnp.einsum(
        "mcid,mcjd->mcij", row_side, col_side, preferred_element_type=jnp.float32
    )
    predicted = lax.psum(partial_tiles, "mp") / math.sqrt(width)
    target_tiles = targets[:, 0].reshape(members, capacity, TB, TB)
    own_count = lax.dynamic_index_in_dim(counts, my_index, 1, keepdims=False)
    live_mask = (jnp.arange(capacity)[None, :] < own_count[:, None]).astype(jnp.float32)
    n_live = jnp.sum(counts, axis=-1).astype(jnp.float32)
    dpredicted = (
        2.0
        / math.sqrt(width)
        * live_mask[:, :, None, None]
        * (predicted - target_tiles)
        / n_live[:, None, None, None]
    )
    row_float = row_side.astype(jnp.float32)
    col_float = col_side.astype(jnp.float32)
    drow = jnp.einsum("mcij,mcjd->mcid", dpredicted, col_float, precision=lax.Precision.HIGHEST)
    dcol = jnp.einsum("mcij,mcid->mcjd", dpredicted, row_float, precision=lax.Precision.HIGHEST)
    dside = jnp.concatenate([drow, dcol], axis=1).astype(jnp.bfloat16)
    inverse = jnp.argsort(slot_index, axis=-1)
    outgoing_grads = take_rows(dside, inverse).reshape(members, seq_count, PER, TB, narrow)
    returned = lax.all_to_all(outgoing_grads, "seq", split_axis=1, concat_axis=1, tiled=True)
    selector = (
        picks.reshape(members, seq_count * PER)[:, :, None] == jnp.arange(per_block)[None, None, :]
    ).astype(jnp.bfloat16)
    dmixed = jnp.einsum(
        "mkn,mktd->mntd",
        selector,
        returned.reshape(members, seq_count * PER, TB, narrow),
        preferred_element_type=jnp.float32,
    ).reshape(members, length, narrow)
    dconv = (scaling[:, None, None] * dmixed).astype(jnp.bfloat16)
    weight_local = weight_term(padded, dconv, length, taps)
    return lax.psum_scatter(weight_local, ("seq", "dp"), scatter_dimension=2, tiled=True)


def axis_sum(value, axis):
    count = lax.axis_size(axis)
    total = value
    for shift in range(1, count):
        total = total + lax.ppermute(value, axis, [(i, (i + shift) % count) for i in range(count)])
    return total


def sparse_path(features, conv_weight, keep, tiles, counts, targets):
    _, length, width = features.shape
    taps, narrow, _ = conv_weight.shape
    halo = taps // 2
    span = TB + 2 * halo
    owners, capacity = tiles.shape[1], tiles.shape[2]
    n_sides = 2 * capacity
    per_block = length // TB
    seq_count = lax.axis_size("seq")
    groups = lax.axis_size("dp")
    peers = seq_count * groups
    held = owners * PER
    cols = width // peers
    my_index = lax.axis_index("seq")
    my_part = lax.axis_index("mp")

    before = jnp.arange(n_sides)[None, :] < jnp.arange(n_sides)[:, None]
    own_sides = jnp.concatenate([tiles[0, ..., 0], tiles[0, ..., 1]], axis=-1)
    own_source = own_sides // per_block
    own_same = own_source[:, :, None] == own_source[:, None, :]
    own_rank = jnp.sum(jnp.logical_and(own_same, before), axis=-1)
    held_here = own_source == my_index
    picks = jnp.stack(
        [
            jnp.sum(jnp.where(jnp.logical_and(held_here, own_rank == r), own_sides % per_block, 0), axis=-1)
            for r in range(PER)
        ],
        axis=-1,
    ).reshape(held)

    cells = features[0]
    ends = seq_count - 1
    if seq_count == 2:
        swapped = lax.ppermute(
            jnp.concatenate([cells[length - halo :], cells[:halo]]), "seq", [(0, 1), (1, 0)]
        )
        head = jnp.where(my_index == 0, jnp.zeros_like(swapped[:halo]), swapped[:halo])
        tail = jnp.where(my_index == ends, jnp.zeros_like(swapped[halo:]), swapped[halo:])
    else:
        head = lax.ppermute(cells[length - halo :], "seq", [(i, i + 1) for i in range(ends)])
        tail = lax.ppermute(cells[:halo], "seq", [(i + 1, i) for i in range(ends)])
    last = per_block - 1
    stacked = cells.reshape(per_block, TB * width)
    block_ids = jnp.arange(per_block)[None, :]

    def select(offset, part):
        choose = (picks[:, None] + offset == block_ids).astype(cells.dtype)
        return jnp.dot(choose, part, preferred_element_type=jnp.float32)

    middle = select(0, stacked).reshape(held, TB, width)
    prev_tail = select(-1, stacked[:, (TB - halo) * width :]).reshape(held, halo, width)
    next_head = select(1, stacked[:, : halo * width]).reshape(held, halo, width)
    lower = jnp.where((picks == 0)[:, None, None], head[None].astype(jnp.float32), prev_tail)
    upper = jnp.where((picks == last)[:, None, None], tail[None].astype(jnp.float32), next_head)
    windows = jnp.concatenate([lower, middle, upper], axis=1).astype(cells.dtype)
    x_float = windows.astype(jnp.float32)
    act = jax.nn.gelu(x_float).astype(jnp.bfloat16)
    unfolded = jnp.concatenate([act[:, offset : offset + TB] for offset in range(taps)], axis=-1)
    flat_weight = conv_weight.transpose(0, 2, 1).reshape(taps * width, narrow)
    conv_out = jnp.dot(
        unfolded.reshape(held * TB, taps * width), flat_weight, preferred_element_type=jnp.float32
    ).reshape(held, TB, narrow)
    my_scale = 1.25 * keep[0].astype(jnp.float32)
    x_part = lax.dynamic_slice_in_dim(x_float[:, halo : halo + TB], my_part * narrow, narrow, 2)
    mixed = (x_part + my_scale * conv_out).astype(jnp.bfloat16)

    def lanes(part):
        flat = part.reshape(part.shape[0], -1)
        flat = jnp.pad(flat, ((0, 0), (0, -flat.shape[1] % 128)))
        return flat.reshape(flat.shape[0], -1, 128)

    act_cut = lanes(act.reshape(held, span, peers, cols).transpose(2, 0, 1, 3))
    mixed_part = lanes(mixed.reshape(1, -1))
    wide = targets.reshape(-1)
    pieces = []
    for _ in range(3):
        piece = lax.reduce_precision(wide, exponent_bits=8, mantissa_bits=7)
        pieces.append(piece)
        wide = wide - piece
    small = jnp.concatenate([tiles.reshape(-1), counts.reshape(-1), keep.reshape(-1)]).astype(jnp.float32)
    meta_part = lanes(jnp.concatenate(pieces + [small]).astype(jnp.bfloat16).reshape(1, -1))
    rows_mixed, rows_act, rows_meta = mixed_part.shape[1], act_cut.shape[1], meta_part.shape[1]
    outgoing = jnp.concatenate(
        [
            jnp.broadcast_to(mixed_part, (peers, rows_mixed, 128)),
            act_cut,
            jnp.broadcast_to(meta_part, (peers, rows_meta, 128)),
        ],
        axis=1,
    )
    outgoing = jnp.pad(outgoing, ((0, 0), (0, -outgoing.shape[1] % 16), (0, 0)))
    incoming = lax.all_to_all(outgoing, ("seq", "dp"), 0, 0, tiled=True)
    n_mixed = held * TB * narrow
    n_act = held * span * cols
    mixed_in = incoming[:, :rows_mixed].reshape(peers, -1)[:, :n_mixed].reshape(peers * held, TB, narrow)
    act_in = incoming[:, rows_mixed : rows_mixed + rows_act].reshape(peers, -1)[:, :n_act]
    act_in = act_in.reshape(peers * held, span, cols)
    meta_in = incoming[:, rows_mixed + rows_act : rows_mixed + rows_act + rows_meta].reshape(peers, -1)
    meta_in = meta_in.astype(jnp.float32).reshape(seq_count, groups, -1)
    n_targets = capacity * TB * TB
    n_tiles = owners * capacity * 2
    targets_all = meta_in[:, :, :n_targets] + meta_in[:, :, n_targets : 2 * n_targets]
    targets_all = targets_all + meta_in[:, :, 2 * n_targets : 3 * n_targets]
    ints = meta_in[0, :, 3 * n_targets :].astype(jnp.int32)
    tiles_all = ints[:, :n_tiles].reshape(groups, owners, capacity, 2)
    counts_all = ints[:, n_tiles : n_tiles + owners]
    keep_all = ints[:, n_tiles + owners]

    sides = jnp.concatenate([tiles_all[..., 0], tiles_all[..., 1]], axis=-1)
    source = sides // per_block
    local = sides % per_block
    same_source = source[..., :, None] == source[..., None, :]
    rank = jnp.sum(jnp.logical_and(same_source, before), axis=-1)
    slot = (source * groups + jnp.arange(groups)[:, None, None]) * held + jnp.arange(owners)[None, :, None] * PER + rank

    side_rows = jnp.take(mixed_in, slot, axis=0)
    row_side = side_rows[:, :, :capacity]
    col_side = side_rows[:, :, capacity:]
    partial_tiles = jnp.einsum("qocid,qocjd->qocij", row_side, col_side, preferred_element_type=jnp.float32)
    lanes_shape = partial_tiles.shape
    summed = axis_sum(partial_tiles.reshape(-1, 128), "mp").reshape(lanes_shape)
    predicted = summed / math.sqrt(width)
    target_tiles = targets_all.reshape(seq_count, groups, capacity, TB, TB).transpose(1, 0, 2, 3, 4)
    live_mask = (jnp.arange(capacity)[None, None, :] < counts_all[:, :, None]).astype(jnp.float32)
    n_live = jnp.sum(counts_all, axis=-1).astype(jnp.float32)
    dpredicted = (
        2.0
        / math.sqrt(width)
        * live_mask[..., None, None]
        * (predicted - target_tiles)
        / n_live[:, None, None, None, None]
    )
    row_float = row_side.astype(jnp.float32)
    col_float = col_side.astype(jnp.float32)
    drow = jnp.einsum("qocij,qocjd->qocid", dpredicted, col_float, precision=lax.Precision.HIGHEST)
    dcol = jnp.einsum("qocij,qocid->qocjd", dpredicted, row_float, precision=lax.Precision.HIGHEST)
    grads = jnp.concatenate([drow, dcol], axis=2).astype(jnp.bfloat16).astype(jnp.float32)
    grads = grads.reshape(groups, owners * n_sides, TB, narrow)
    flat_sides = sides.reshape(groups, owners * n_sides)
    same_block = flat_sides[:, :, None] == flat_sides[:, None, :]
    total = jnp.einsum(
        "qab,qbtd->qatd", same_block.astype(jnp.float32), grads, precision=lax.Precision.HIGHEST
    )
    earlier = jnp.arange(owners * n_sides)[None, :] < jnp.arange(owners * n_sides)[:, None]
    first = jnp.logical_not(jnp.any(jnp.logical_and(same_block, earlier[None]), axis=-1))
    scaling = 1.25 * keep_all.astype(jnp.float32)
    dconv = (scaling[:, None, None, None] * total).astype(jnp.bfloat16)
    dconv = jnp.where(first[..., None, None], dconv, jnp.zeros_like(dconv))
    act_sides = jnp.take(act_in, slot.reshape(groups, owners * n_sides), axis=0)
    return jnp.stack(
        [
            jnp.einsum(
                "qato,qati->oi",
                dconv,
                act_sides[:, :, offset : offset + TB],
                preferred_element_type=jnp.float32,
            )
            for offset in range(taps)
        ]
    )


def per_device(features, conv_weight, keep, tiles, counts, targets):
    members, length, _ = features.shape
    owners, capacity = tiles.shape[1], tiles.shape[2]
    blocks = lax.axis_size("seq") * length // TB
    fits = members == 1 and targets.shape[1] == 1 and 2 * owners * capacity * TB <= length
    fits = fits and blocks <= 256 and capacity <= 256
    if fits:
        return sparse_path(features, conv_weight, keep, tiles, counts, targets)
    return dense_path(features, conv_weight, keep, tiles, counts, targets)


def solution(mesh):
    placed = (
        P("dp", "seq", None),
        P(None, "mp", None),
        P("dp"),
        P("dp", None, None, None),
        P("dp", None),
        P("dp", "seq", None, None),
    )
    return jax.shard_map(
        per_device,
        mesh=mesh,
        in_specs=placed,
        out_specs=P(None, "mp", ("seq", "dp")),
        check_vma=False,
    )
```

```python
import math

import jax
import jax.numpy as jnp
from jax import lax
from jax.sharding import PartitionSpec as P

TB = 32
PER = 2


def extended(cells, sides, width):
    for axis, dim in sides:
        count = lax.axis_size(axis)
        ends = count - 1
        head = lax.slice_in_dim(cells, 0, width, axis=dim)
        tail = lax.slice_in_dim(cells, cells.shape[dim] - width, cells.shape[dim], axis=dim)
        cells = jnp.concatenate(
            [
                lax.ppermute(tail, axis, [(i, (i + 1) % count) for i in range(ends)]),
                cells,
                lax.ppermute(head, axis, [((i + 1) % count, i) for i in range(ends)]),
            ],
            axis=dim,
        )
    return cells


def take_rows(source_array, index_array):
    return jax.vmap(lambda table, picked: table[picked])(source_array, index_array)


def conv_apply(padded, weight, length):
    total = jnp.einsum(
        "mbi,oi->mbo", padded[:, 0:length], weight[0], preferred_element_type=jnp.float32
    )
    for offset in range(1, weight.shape[0]):
        total = total + jnp.einsum(
            "mbi,oi->mbo",
            padded[:, offset : offset + length],
            weight[offset],
            preferred_element_type=jnp.float32,
        )
    return total


def weight_term(padded, dconv, length, taps):
    return jnp.stack(
        [
            jnp.einsum(
                "mbi,mbo->oi",
                padded[:, offset : offset + length],
                dconv,
                preferred_element_type=jnp.float32,
            )
            for offset in range(taps)
        ]
    )


def dense_path(features, conv_weight, keep, tiles, counts, targets):
    members, length, width = features.shape
    taps = conv_weight.shape[0]
    narrow = conv_weight.shape[1]
    seq_count = lax.axis_size("seq")
    my_index = lax.axis_index("seq")
    my_part = lax.axis_index("mp")
    x_float = features.astype(jnp.float32)
    activations = jax.nn.gelu(x_float).astype(jnp.bfloat16)
    padded = extended(activations, (("seq", 1),), 2)
    scaling = 1.25 * keep.astype(jnp.float32)
    conv_out = conv_apply(padded, conv_weight, length)
    x_local = lax.dynamic_slice_in_dim(x_float, my_part * narrow, narrow, 2)
    mixed_out = (x_local + scaling[:, None, None] * conv_out).astype(jnp.bfloat16)
    capacity = tiles.shape[2]
    n_sides = 2 * capacity
    per_block = length // TB
    sides = jnp.concatenate([tiles[..., 0], tiles[..., 1]], axis=-1)
    side_source = sides // per_block
    side_local = sides % per_block
    own_sides = lax.dynamic_index_in_dim(sides, my_index, 1, keepdims=False)
    own_source = own_sides // per_block
    before = jnp.arange(n_sides)[None, :] < jnp.arange(n_sides)[:, None]
    same_source = own_source[:, :, None] == own_source[:, None, :]
    rank_within = jnp.sum(jnp.logical_and(same_source, before[None]), axis=-1)
    slot_index = own_source * PER + rank_within
    held_here = side_source == my_index
    held_order = jnp.cumsum(held_here.astype(jnp.int32), axis=-1) - 1
    picks = jnp.stack(
        [
            jnp.sum(
                jnp.where(jnp.logical_and(held_here, held_order == position), side_local, 0),
                axis=-1,
            )
            for position in range(PER)
        ],
        axis=-1,
    )
    blocks = mixed_out.reshape(members, per_block, TB, narrow)
    whole = lax.all_gather(blocks, "seq", axis=1, tiled=True)
    side_rows = take_rows(whole, own_sides)
    row_side = side_rows[:, :capacity]
    col_side = side_rows[:, capacity:]
    partial_tiles = jnp.einsum(
        "mcid,mcjd->mcij", row_side, col_side, preferred_element_type=jnp.float32
    )
    predicted = lax.psum(partial_tiles, "mp") / math.sqrt(width)
    target_tiles = targets[:, 0].reshape(members, capacity, TB, TB)
    own_count = lax.dynamic_index_in_dim(counts, my_index, 1, keepdims=False)
    live_mask = (jnp.arange(capacity)[None, :] < own_count[:, None]).astype(jnp.float32)
    n_live = jnp.sum(counts, axis=-1).astype(jnp.float32)
    dpredicted = (
        2.0
        / math.sqrt(width)
        * live_mask[:, :, None, None]
        * (predicted - target_tiles)
        / n_live[:, None, None, None]
    )
    row_float = row_side.astype(jnp.float32)
    col_float = col_side.astype(jnp.float32)
    drow = jnp.einsum("mcij,mcjd->mcid", dpredicted, col_float, precision=lax.Precision.HIGHEST)
    dcol = jnp.einsum("mcij,mcid->mcjd", dpredicted, row_float, precision=lax.Precision.HIGHEST)
    dside = jnp.concatenate([drow, dcol], axis=1).astype(jnp.bfloat16)
    inverse = jnp.argsort(slot_index, axis=-1)
    outgoing_grads = take_rows(dside, inverse).reshape(members, seq_count, PER, TB, narrow)
    returned = lax.all_to_all(outgoing_grads, "seq", split_axis=1, concat_axis=1, tiled=True)
    selector = (
        picks.reshape(members, seq_count * PER)[:, :, None] == jnp.arange(per_block)[None, None, :]
    ).astype(jnp.bfloat16)
    dmixed = jnp.einsum(
        "mkn,mktd->mntd",
        selector,
        returned.reshape(members, seq_count * PER, TB, narrow),
        preferred_element_type=jnp.float32,
    ).reshape(members, length, narrow)
    dconv = (scaling[:, None, None] * dmixed).astype(jnp.bfloat16)
    weight_local = weight_term(padded, dconv, length, taps)
    return lax.psum_scatter(weight_local, ("seq", "dp"), scatter_dimension=2, tiled=True)


def axis_sum(value, axis):
    count = lax.axis_size(axis)
    total = value
    for shift in range(1, count):
        total = total + lax.ppermute(value, axis, [(i, (i + shift) % count) for i in range(count)])
    return total


def sparse_path(features, conv_weight, keep, tiles, counts, targets):
    _, length, width = features.shape
    taps, narrow, _ = conv_weight.shape
    halo = taps // 2
    span = TB + 2 * halo
    owners, capacity = tiles.shape[1], tiles.shape[2]
    n_sides = 2 * capacity
    per_block = length // TB
    seq_count = lax.axis_size("seq")
    groups = lax.axis_size("dp")
    peers = seq_count * groups
    held = owners * PER
    cols = width // peers
    my_index = lax.axis_index("seq")
    my_part = lax.axis_index("mp")

    before = jnp.arange(n_sides)[None, :] < jnp.arange(n_sides)[:, None]
    own_sides = jnp.concatenate([tiles[0, ..., 0], tiles[0, ..., 1]], axis=-1)
    own_source = own_sides // per_block
    own_same = own_source[:, :, None] == own_source[:, None, :]
    own_rank = jnp.sum(jnp.logical_and(own_same, before), axis=-1)
    held_here = own_source == my_index
    picks = jnp.stack(
        [
            jnp.sum(jnp.where(jnp.logical_and(held_here, own_rank == r), own_sides % per_block, 0), axis=-1)
            for r in range(PER)
        ],
        axis=-1,
    ).reshape(held)

    cells = features[0]
    ends = seq_count - 1
    if seq_count == 2:
        swapped = lax.ppermute(
            jnp.concatenate([cells[length - halo :], cells[:halo]]), "seq", [(0, 1), (1, 0)]
        )
        head = jnp.where(my_index == 0, jnp.zeros_like(swapped[:halo]), swapped[:halo])
        tail = jnp.where(my_index == ends, jnp.zeros_like(swapped[halo:]), swapped[halo:])
    else:
        head = lax.ppermute(cells[length - halo :], "seq", [(i, i + 1) for i in range(ends)])
        tail = lax.ppermute(cells[:halo], "seq", [(i + 1, i) for i in range(ends)])
    last = per_block - 1
    stacked = cells.reshape(per_block, TB * width)
    block_ids = jnp.arange(per_block)[None, :]

    def select(offset, part):
        choose = (picks[:, None] + offset == block_ids).astype(cells.dtype)
        return jnp.dot(choose, part, preferred_element_type=jnp.float32)

    middle = select(0, stacked).reshape(held, TB, width)
    prev_tail = select(-1, stacked[:, (TB - halo) * width :]).reshape(held, halo, width)
    next_head = select(1, stacked[:, : halo * width]).reshape(held, halo, width)
    lower = jnp.where((picks == 0)[:, None, None], head[None].astype(jnp.float32), prev_tail)
    upper = jnp.where((picks == last)[:, None, None], tail[None].astype(jnp.float32), next_head)
    windows = jnp.concatenate([lower, middle, upper], axis=1).astype(cells.dtype)
    x_float = windows.astype(jnp.float32)
    act = jax.nn.gelu(x_float).astype(jnp.bfloat16)
    conv_out = jnp.einsum("hti,oi->hto", act[:, 0:TB], conv_weight[0], preferred_element_type=jnp.float32)
    for offset in range(1, taps):
        conv_out = conv_out + jnp.einsum(
            "hti,oi->hto", act[:, offset : offset + TB], conv_weight[offset], preferred_element_type=jnp.float32
        )
    my_scale = 1.25 * keep[0].astype(jnp.float32)
    x_part = lax.dynamic_slice_in_dim(x_float[:, halo : halo + TB], my_part * narrow, narrow, 2)
    mixed = (x_part + my_scale * conv_out).astype(jnp.bfloat16)

    def lanes(part):
        flat = part.reshape(part.shape[0], -1)
        flat = jnp.pad(flat, ((0, 0), (0, -flat.shape[1] % 128)))
        return flat.reshape(flat.shape[0], -1, 128)

    act_cut = lanes(act.reshape(held, span, peers, cols).transpose(2, 0, 1, 3))
    mixed_part = lanes(mixed.reshape(1, -1))
    wide = targets.reshape(-1)
    pieces = []
    for _ in range(3):
        piece = lax.reduce_precision(wide, exponent_bits=8, mantissa_bits=7)
        pieces.append(piece)
        wide = wide - piece
    own_slot = (own_source * groups + lax.axis_index("dp")) * held + jnp.arange(owners)[:, None] * PER + own_rank
    small = jnp.concatenate(
        [tiles.reshape(-1), counts.reshape(-1), keep.reshape(-1), own_slot.reshape(-1)]
    ).astype(jnp.float32)
    meta_part = lanes(jnp.concatenate(pieces + [small]).astype(jnp.bfloat16).reshape(1, -1))
    rows_mixed, rows_act, rows_meta = mixed_part.shape[1], act_cut.shape[1], meta_part.shape[1]
    outgoing = jnp.concatenate(
        [
            jnp.broadcast_to(mixed_part, (peers, rows_mixed, 128)),
            act_cut,
            jnp.broadcast_to(meta_part, (peers, rows_meta, 128)),
        ],
        axis=1,
    )
    outgoing = jnp.pad(outgoing, ((0, 0), (0, -outgoing.shape[1] % 16), (0, 0)))
    incoming = lax.all_to_all(outgoing, ("seq", "dp"), 0, 0, tiled=True)
    n_mixed = held * TB * narrow
    n_act = held * span * cols
    mixed_in = incoming[:, :rows_mixed].reshape(peers, -1)[:, :n_mixed].reshape(peers * held, TB, narrow)
    act_in = incoming[:, rows_mixed : rows_mixed + rows_act].reshape(peers, -1)[:, :n_act]
    act_in = act_in.reshape(peers * held, span, cols)
    meta_in = incoming[:, rows_mixed + rows_act : rows_mixed + rows_act + rows_meta].reshape(peers, -1)
    meta_in = meta_in.astype(jnp.float32).reshape(seq_count, groups, -1)
    n_targets = capacity * TB * TB
    n_tiles = owners * capacity * 2
    targets_all = meta_in[:, :, :n_targets] + meta_in[:, :, n_targets : 2 * n_targets]
    targets_all = targets_all + meta_in[:, :, 2 * n_targets : 3 * n_targets]
    ints = meta_in[0, :, 3 * n_targets :].astype(jnp.int32)
    tiles_all = ints[:, :n_tiles].reshape(groups, owners, capacity, 2)
    counts_all = ints[:, n_tiles : n_tiles + owners]
    keep_all = ints[:, n_tiles + owners]
    slot = ints[:, n_tiles + owners + 1 : n_tiles + owners + 1 + owners * n_sides].reshape(groups, owners, n_sides)

    sides = jnp.concatenate([tiles_all[..., 0], tiles_all[..., 1]], axis=-1)

    side_rows = jnp.take(mixed_in, slot, axis=0)
    row_side = side_rows[:, :, :capacity]
    col_side = side_rows[:, :, capacity:]
    partial_tiles = jnp.einsum("qocid,qocjd->qocij", row_side, col_side, preferred_element_type=jnp.float32)
    lanes_shape = partial_tiles.shape
    summed = axis_sum(partial_tiles.reshape(-1, 128), "mp").reshape(lanes_shape)
    predicted = summed / math.sqrt(width)
    target_tiles = targets_all.reshape(seq_count, groups, capacity, TB, TB).transpose(1, 0, 2, 3, 4)
    live_mask = (jnp.arange(capacity)[None, None, :] < counts_all[:, :, None]).astype(jnp.float32)
    n_live = jnp.sum(counts_all, axis=-1).astype(jnp.float32)
    dpredicted = (
        2.0
        / math.sqrt(width)
        * live_mask[..., None, None]
        * (predicted - target_tiles)
        / n_live[:, None, None, None, None]
    )
    row_float = row_side.astype(jnp.float32)
    col_float = col_side.astype(jnp.float32)
    drow = jnp.einsum("qocij,qocjd->qocid", dpredicted, col_float, precision=lax.Precision.HIGHEST)
    dcol = jnp.einsum("qocij,qocid->qocjd", dpredicted, row_float, precision=lax.Precision.HIGHEST)
    grads = jnp.concatenate([drow, dcol], axis=2).astype(jnp.bfloat16).astype(jnp.float32)
    grads = grads.reshape(groups, owners * n_sides, TB, narrow)
    flat_sides = sides.reshape(groups, owners * n_sides)
    same_block = flat_sides[:, :, None] == flat_sides[:, None, :]
    total = jnp.einsum(
        "qab,qbtd->qatd", same_block.astype(jnp.float32), grads, precision=lax.Precision.HIGHEST
    )
    earlier = jnp.arange(owners * n_sides)[None, :] < jnp.arange(owners * n_sides)[:, None]
    first = jnp.logical_not(jnp.any(jnp.logical_and(same_block, earlier[None]), axis=-1))
    scaling = 1.25 * keep_all.astype(jnp.float32)
    dconv = (scaling[:, None, None, None] * total).astype(jnp.bfloat16)
    dconv = jnp.where(first[..., None, None], dconv, jnp.zeros_like(dconv))
    act_sides = jnp.take(act_in, slot.reshape(groups, owners * n_sides), axis=0)
    return jnp.stack(
        [
            jnp.einsum(
                "qato,qati->oi",
                dconv,
                act_sides[:, :, offset : offset + TB],
                preferred_element_type=jnp.float32,
            )
            for offset in range(taps)
        ]
    )


def per_device(features, conv_weight, keep, tiles, counts, targets):
    members, length, _ = features.shape
    owners, capacity = tiles.shape[1], tiles.shape[2]
    blocks = lax.axis_size("seq") * length // TB
    fits = members == 1 and targets.shape[1] == 1 and 2 * owners * capacity * TB <= length
    fits = fits and blocks <= 256 and capacity <= 256
    if fits:
        return sparse_path(features, conv_weight, keep, tiles, counts, targets)
    return dense_path(features, conv_weight, keep, tiles, counts, targets)


def solution(mesh):
    placed = (
        P("dp", "seq", None),
        P(None, "mp", None),
        P("dp"),
        P("dp", None, None, None),
        P("dp", None),
        P("dp", "seq", None, None),
    )
    return jax.shard_map(
        per_device,
        mesh=mesh,
        in_specs=placed,
        out_specs=P(None, "mp", ("seq", "dp")),
        check_vma=False,
    )
```

```python
import math

import jax
import jax.numpy as jnp
from jax import lax
from jax.sharding import PartitionSpec as P

TB = 32
PER = 2


def extended(cells, sides, width):
    for axis, dim in sides:
        count = lax.axis_size(axis)
        ends = count - 1
        head = lax.slice_in_dim(cells, 0, width, axis=dim)
        tail = lax.slice_in_dim(cells, cells.shape[dim] - width, cells.shape[dim], axis=dim)
        cells = jnp.concatenate(
            [
                lax.ppermute(tail, axis, [(i, (i + 1) % count) for i in range(ends)]),
                cells,
                lax.ppermute(head, axis, [((i + 1) % count, i) for i in range(ends)]),
            ],
            axis=dim,
        )
    return cells


def take_rows(source_array, index_array):
    return jax.vmap(lambda table, picked: table[picked])(source_array, index_array)


def conv_apply(padded, weight, length):
    total = jnp.einsum(
        "mbi,oi->mbo", padded[:, 0:length], weight[0], preferred_element_type=jnp.float32
    )
    for offset in range(1, weight.shape[0]):
        total = total + jnp.einsum(
            "mbi,oi->mbo",
            padded[:, offset : offset + length],
            weight[offset],
            preferred_element_type=jnp.float32,
        )
    return total


def weight_term(padded, dconv, length, taps):
    return jnp.stack(
        [
            jnp.einsum(
                "mbi,mbo->oi",
                padded[:, offset : offset + length],
                dconv,
                preferred_element_type=jnp.float32,
            )
            for offset in range(taps)
        ]
    )


def dense_path(features, conv_weight, keep, tiles, counts, targets):
    members, length, width = features.shape
    taps = conv_weight.shape[0]
    narrow = conv_weight.shape[1]
    seq_count = lax.axis_size("seq")
    my_index = lax.axis_index("seq")
    my_part = lax.axis_index("mp")
    x_float = features.astype(jnp.float32)
    activations = jax.nn.gelu(x_float).astype(jnp.bfloat16)
    padded = extended(activations, (("seq", 1),), 2)
    scaling = 1.25 * keep.astype(jnp.float32)
    conv_out = conv_apply(padded, conv_weight, length)
    x_local = lax.dynamic_slice_in_dim(x_float, my_part * narrow, narrow, 2)
    mixed_out = (x_local + scaling[:, None, None] * conv_out).astype(jnp.bfloat16)
    capacity = tiles.shape[2]
    n_sides = 2 * capacity
    per_block = length // TB
    sides = jnp.concatenate([tiles[..., 0], tiles[..., 1]], axis=-1)
    side_source = sides // per_block
    side_local = sides % per_block
    own_sides = lax.dynamic_index_in_dim(sides, my_index, 1, keepdims=False)
    own_source = own_sides // per_block
    before = jnp.arange(n_sides)[None, :] < jnp.arange(n_sides)[:, None]
    same_source = own_source[:, :, None] == own_source[:, None, :]
    rank_within = jnp.sum(jnp.logical_and(same_source, before[None]), axis=-1)
    slot_index = own_source * PER + rank_within
    held_here = side_source == my_index
    held_order = jnp.cumsum(held_here.astype(jnp.int32), axis=-1) - 1
    picks = jnp.stack(
        [
            jnp.sum(
                jnp.where(jnp.logical_and(held_here, held_order == position), side_local, 0),
                axis=-1,
            )
            for position in range(PER)
        ],
        axis=-1,
    )
    blocks = mixed_out.reshape(members, per_block, TB, narrow)
    whole = lax.all_gather(blocks, "seq", axis=1, tiled=True)
    side_rows = take_rows(whole, own_sides)
    row_side = side_rows[:, :capacity]
    col_side = side_rows[:, capacity:]
    partial_tiles = jnp.einsum(
        "mcid,mcjd->mcij", row_side, col_side, preferred_element_type=jnp.float32
    )
    predicted = lax.psum(partial_tiles, "mp") / math.sqrt(width)
    target_tiles = targets[:, 0].reshape(members, capacity, TB, TB)
    own_count = lax.dynamic_index_in_dim(counts, my_index, 1, keepdims=False)
    live_mask = (jnp.arange(capacity)[None, :] < own_count[:, None]).astype(jnp.float32)
    n_live = jnp.sum(counts, axis=-1).astype(jnp.float32)
    dpredicted = (
        2.0
        / math.sqrt(width)
        * live_mask[:, :, None, None]
        * (predicted - target_tiles)
        / n_live[:, None, None, None]
    )
    row_float = row_side.astype(jnp.float32)
    col_float = col_side.astype(jnp.float32)
    drow = jnp.einsum("mcij,mcjd->mcid", dpredicted, col_float, precision=lax.Precision.HIGHEST)
    dcol = jnp.einsum("mcij,mcid->mcjd", dpredicted, row_float, precision=lax.Precision.HIGHEST)
    dside = jnp.concatenate([drow, dcol], axis=1).astype(jnp.bfloat16)
    inverse = jnp.argsort(slot_index, axis=-1)
    outgoing_grads = take_rows(dside, inverse).reshape(members, seq_count, PER, TB, narrow)
    returned = lax.all_to_all(outgoing_grads, "seq", split_axis=1, concat_axis=1, tiled=True)
    selector = (
        picks.reshape(members, seq_count * PER)[:, :, None] == jnp.arange(per_block)[None, None, :]
    ).astype(jnp.bfloat16)
    dmixed = jnp.einsum(
        "mkn,mktd->mntd",
        selector,
        returned.reshape(members, seq_count * PER, TB, narrow),
        preferred_element_type=jnp.float32,
    ).reshape(members, length, narrow)
    dconv = (scaling[:, None, None] * dmixed).astype(jnp.bfloat16)
    weight_local = weight_term(padded, dconv, length, taps)
    return lax.psum_scatter(weight_local, ("seq", "dp"), scatter_dimension=2, tiled=True)


def axis_sum(value, axis):
    count = lax.axis_size(axis)
    total = value
    for shift in range(1, count):
        total = total + lax.ppermute(value, axis, [(i, (i + shift) % count) for i in range(count)])
    return total


def sparse_path(features, conv_weight, keep, tiles, counts, targets):
    _, length, width = features.shape
    taps, narrow, _ = conv_weight.shape
    halo = taps // 2
    span = TB + 2 * halo
    owners, capacity = tiles.shape[1], tiles.shape[2]
    n_sides = 2 * capacity
    per_block = length // TB
    seq_count = lax.axis_size("seq")
    groups = lax.axis_size("dp")
    peers = seq_count * groups
    held = owners * PER
    cols = width // peers
    my_index = lax.axis_index("seq")
    my_part = lax.axis_index("mp")

    before = jnp.arange(n_sides)[None, :] < jnp.arange(n_sides)[:, None]
    own_sides = jnp.concatenate([tiles[0, ..., 0], tiles[0, ..., 1]], axis=-1)
    own_source = own_sides // per_block
    own_same = own_source[:, :, None] == own_source[:, None, :]
    own_rank = jnp.sum(jnp.logical_and(own_same, before), axis=-1)
    held_here = own_source == my_index
    picks = jnp.stack(
        [
            jnp.sum(jnp.where(jnp.logical_and(held_here, own_rank == r), own_sides % per_block, 0), axis=-1)
            for r in range(PER)
        ],
        axis=-1,
    ).reshape(held)

    cells = features[0]
    ends = seq_count - 1
    if seq_count == 2:
        swapped = lax.ppermute(
            jnp.concatenate([cells[length - halo :], cells[:halo]]), "seq", [(0, 1), (1, 0)]
        )
        head = jnp.where(my_index == 0, jnp.zeros_like(swapped[:halo]), swapped[:halo])
        tail = jnp.where(my_index == ends, jnp.zeros_like(swapped[halo:]), swapped[halo:])
    else:
        head = lax.ppermute(cells[length - halo :], "seq", [(i, i + 1) for i in range(ends)])
        tail = lax.ppermute(cells[:halo], "seq", [(i + 1, i) for i in range(ends)])
    last = per_block - 1
    stacked = cells.reshape(per_block, TB * width)
    block_ids = jnp.arange(per_block)[None, :]

    def select(offset, part):
        choose = (picks[:, None] + offset == block_ids).astype(cells.dtype)
        return jnp.dot(choose, part, preferred_element_type=jnp.float32)

    middle = select(0, stacked).reshape(held, TB, width)
    prev_tail = select(-1, stacked[:, (TB - halo) * width :]).reshape(held, halo, width)
    next_head = select(1, stacked[:, : halo * width]).reshape(held, halo, width)
    lower = jnp.where((picks == 0)[:, None, None], head[None].astype(jnp.float32), prev_tail)
    upper = jnp.where((picks == last)[:, None, None], tail[None].astype(jnp.float32), next_head)
    windows = jnp.concatenate([lower, middle, upper], axis=1).astype(cells.dtype)
    x_float = windows.astype(jnp.float32)
    act = jax.nn.gelu(x_float).astype(jnp.bfloat16)
    conv_out = jnp.einsum("hti,oi->hto", act[:, 0:TB], conv_weight[0], preferred_element_type=jnp.float32)
    for offset in range(1, taps):
        conv_out = conv_out + jnp.einsum(
            "hti,oi->hto", act[:, offset : offset + TB], conv_weight[offset], preferred_element_type=jnp.float32
        )
    my_scale = 1.25 * keep[0].astype(jnp.float32)
    x_part = lax.dynamic_slice_in_dim(x_float[:, halo : halo + TB], my_part * narrow, narrow, 2)
    mixed = (x_part + my_scale * conv_out).astype(jnp.bfloat16)

    def lanes(part):
        flat = part.reshape(part.shape[0], -1)
        flat = jnp.pad(flat, ((0, 0), (0, -flat.shape[1] % 128)))
        return flat.reshape(flat.shape[0], -1, 128)

    act_cut = lanes(act.reshape(held, span, peers, cols).transpose(2, 0, 1, 3))
    mixed_part = lanes(mixed.reshape(1, -1))
    wide = targets.reshape(-1)
    pieces = []
    for _ in range(3):
        piece = lax.reduce_precision(wide, exponent_bits=8, mantissa_bits=7)
        pieces.append(piece)
        wide = wide - piece
    own_slot = (own_source * groups + lax.axis_index("dp")) * held + jnp.arange(owners)[:, None] * PER + own_rank
    small = jnp.concatenate(
        [tiles.reshape(-1), counts.reshape(-1), keep.reshape(-1), own_slot.reshape(-1)]
    ).astype(jnp.float32)
    meta_part = lanes(jnp.concatenate(pieces + [small]).astype(jnp.bfloat16).reshape(1, -1))
    rows_mixed, rows_act, rows_meta = mixed_part.shape[1], act_cut.shape[1], meta_part.shape[1]
    outgoing = jnp.concatenate(
        [
            jnp.broadcast_to(mixed_part, (peers, rows_mixed, 128)),
            act_cut,
            jnp.broadcast_to(meta_part, (peers, rows_meta, 128)),
        ],
        axis=1,
    )
    outgoing = jnp.pad(outgoing, ((0, 0), (0, -outgoing.shape[1] % 16), (0, 0)))
    incoming = lax.all_to_all(outgoing, ("seq", "dp"), 0, 0, tiled=True)
    n_mixed = held * TB * narrow
    n_act = held * span * cols
    mixed_in = incoming[:, :rows_mixed].reshape(peers, -1)[:, :n_mixed].reshape(peers * held, TB, narrow)
    act_in = incoming[:, rows_mixed : rows_mixed + rows_act].reshape(peers, -1)[:, :n_act]
    act_in = act_in.reshape(peers * held, span, cols)
    meta_in = incoming[:, rows_mixed + rows_act : rows_mixed + rows_act + rows_meta].reshape(peers, -1)
    meta_in = meta_in.astype(jnp.float32).reshape(seq_count, groups, -1)
    n_targets = capacity * TB * TB
    n_tiles = owners * capacity * 2
    targets_all = meta_in[:, :, :n_targets] + meta_in[:, :, n_targets : 2 * n_targets]
    targets_all = targets_all + meta_in[:, :, 2 * n_targets : 3 * n_targets]
    ints = meta_in[0, :, 3 * n_targets :].astype(jnp.int32)
    tiles_all = ints[:, :n_tiles].reshape(groups, owners, capacity, 2)
    counts_all = ints[:, n_tiles : n_tiles + owners]
    keep_all = ints[:, n_tiles + owners]
    slot = ints[:, n_tiles + owners + 1 : n_tiles + owners + 1 + owners * n_sides].reshape(groups, owners, n_sides)

    sides = jnp.concatenate([tiles_all[..., 0], tiles_all[..., 1]], axis=-1)

    side_rows = jnp.take(mixed_in, slot, axis=0)
    row_side = side_rows[:, :, :capacity]
    col_side = side_rows[:, :, capacity:]
    partial_tiles = jnp.einsum("qocid,qocjd->qocij", row_side, col_side, preferred_element_type=jnp.float32)
    lanes_shape = partial_tiles.shape
    summed = axis_sum(partial_tiles.reshape(-1, 128), "mp").reshape(lanes_shape)
    predicted = summed / math.sqrt(width)
    target_tiles = targets_all.reshape(seq_count, groups, capacity, TB, TB).transpose(1, 0, 2, 3, 4)
    live_mask = (jnp.arange(capacity)[None, None, :] < counts_all[:, :, None]).astype(jnp.float32)
    n_live = jnp.sum(counts_all, axis=-1).astype(jnp.float32)
    dpredicted = (
        2.0
        / math.sqrt(width)
        * live_mask[..., None, None]
        * (predicted - target_tiles)
        / n_live[:, None, None, None, None]
    )
    row_float = row_side.astype(jnp.float32)
    col_float = col_side.astype(jnp.float32)
    drow = jnp.einsum("qocij,qocjd->qocid", dpredicted, col_float, precision=lax.Precision.HIGHEST)
    dcol = jnp.einsum("qocij,qocid->qocjd", dpredicted, row_float, precision=lax.Precision.HIGHEST)
    grads = jnp.concatenate([drow, dcol], axis=2).astype(jnp.bfloat16).astype(jnp.float32)
    grads = grads.reshape(groups, owners * n_sides, TB, narrow)
    flat_sides = sides.reshape(groups, owners * n_sides)
    same_block = flat_sides[:, :, None] == flat_sides[:, None, :]
    total = jnp.einsum(
        "qab,qbtd->qatd", same_block.astype(jnp.float32), grads, precision=lax.Precision.HIGHEST
    )
    earlier = jnp.arange(owners * n_sides)[None, :] < jnp.arange(owners * n_sides)[:, None]
    first = jnp.logical_not(jnp.any(jnp.logical_and(same_block, earlier[None]), axis=-1))
    scaling = 1.25 * keep_all.astype(jnp.float32)
    dconv = (scaling[:, None, None, None] * total).astype(jnp.bfloat16)
    dconv = jnp.where(first[..., None, None], dconv, jnp.zeros_like(dconv))
    act_sides = jnp.take(act_in, slot.reshape(groups, owners * n_sides), axis=0)
    placed = jnp.stack(
        [
            jnp.pad(dconv, ((0, 0), (0, 0), (offset, span - TB - offset), (0, 0)))
            for offset in range(taps)
        ]
    )
    lhs = placed.transpose(0, 4, 1, 2, 3).reshape(taps * narrow, -1)
    product = jnp.dot(lhs, act_sides.reshape(-1, cols), preferred_element_type=jnp.float32)
    return product.reshape(taps, narrow, cols)


def per_device(features, conv_weight, keep, tiles, counts, targets):
    members, length, _ = features.shape
    owners, capacity = tiles.shape[1], tiles.shape[2]
    blocks = lax.axis_size("seq") * length // TB
    fits = members == 1 and targets.shape[1] == 1 and 2 * owners * capacity * TB <= length
    fits = fits and blocks <= 256 and capacity <= 256
    if fits:
        return sparse_path(features, conv_weight, keep, tiles, counts, targets)
    return dense_path(features, conv_weight, keep, tiles, counts, targets)


def solution(mesh):
    placed = (
        P("dp", "seq", None),
        P(None, "mp", None),
        P("dp"),
        P("dp", None, None, None),
        P("dp", None),
        P("dp", "seq", None, None),
    )
    return jax.shard_map(
        per_device,
        mesh=mesh,
        in_specs=placed,
        out_specs=P(None, "mp", ("seq", "dp")),
        check_vma=False,
    )
```

```python
import math

import jax
import jax.numpy as jnp
from jax import lax
from jax.sharding import PartitionSpec as P

TB = 32
PER = 2


def extended(cells, sides, width):
    for axis, dim in sides:
        count = lax.axis_size(axis)
        ends = count - 1
        head = lax.slice_in_dim(cells, 0, width, axis=dim)
        tail = lax.slice_in_dim(cells, cells.shape[dim] - width, cells.shape[dim], axis=dim)
        cells = jnp.concatenate(
            [
                lax.ppermute(tail, axis, [(i, (i + 1) % count) for i in range(ends)]),
                cells,
                lax.ppermute(head, axis, [((i + 1) % count, i) for i in range(ends)]),
            ],
            axis=dim,
        )
    return cells


def take_rows(source_array, index_array):
    return jax.vmap(lambda table, picked: table[picked])(source_array, index_array)


def conv_apply(padded, weight, length):
    total = jnp.einsum(
        "mbi,oi->mbo", padded[:, 0:length], weight[0], preferred_element_type=jnp.float32
    )
    for offset in range(1, weight.shape[0]):
        total = total + jnp.einsum(
            "mbi,oi->mbo",
            padded[:, offset : offset + length],
            weight[offset],
            preferred_element_type=jnp.float32,
        )
    return total


def weight_term(padded, dconv, length, taps):
    return jnp.stack(
        [
            jnp.einsum(
                "mbi,mbo->oi",
                padded[:, offset : offset + length],
                dconv,
                preferred_element_type=jnp.float32,
            )
            for offset in range(taps)
        ]
    )


def dense_path(features, conv_weight, keep, tiles, counts, targets):
    members, length, width = features.shape
    taps = conv_weight.shape[0]
    narrow = conv_weight.shape[1]
    seq_count = lax.axis_size("seq")
    my_index = lax.axis_index("seq")
    my_part = lax.axis_index("mp")
    x_float = features.astype(jnp.float32)
    activations = jax.nn.gelu(x_float).astype(jnp.bfloat16)
    padded = extended(activations, (("seq", 1),), 2)
    scaling = 1.25 * keep.astype(jnp.float32)
    conv_out = conv_apply(padded, conv_weight, length)
    x_local = lax.dynamic_slice_in_dim(x_float, my_part * narrow, narrow, 2)
    mixed_out = (x_local + scaling[:, None, None] * conv_out).astype(jnp.bfloat16)
    capacity = tiles.shape[2]
    n_sides = 2 * capacity
    per_block = length // TB
    sides = jnp.concatenate([tiles[..., 0], tiles[..., 1]], axis=-1)
    side_source = sides // per_block
    side_local = sides % per_block
    own_sides = lax.dynamic_index_in_dim(sides, my_index, 1, keepdims=False)
    own_source = own_sides // per_block
    before = jnp.arange(n_sides)[None, :] < jnp.arange(n_sides)[:, None]
    same_source = own_source[:, :, None] == own_source[:, None, :]
    rank_within = jnp.sum(jnp.logical_and(same_source, before[None]), axis=-1)
    slot_index = own_source * PER + rank_within
    held_here = side_source == my_index
    held_order = jnp.cumsum(held_here.astype(jnp.int32), axis=-1) - 1
    picks = jnp.stack(
        [
            jnp.sum(
                jnp.where(jnp.logical_and(held_here, held_order == position), side_local, 0),
                axis=-1,
            )
            for position in range(PER)
        ],
        axis=-1,
    )
    blocks = mixed_out.reshape(members, per_block, TB, narrow)
    whole = lax.all_gather(blocks, "seq", axis=1, tiled=True)
    side_rows = take_rows(whole, own_sides)
    row_side = side_rows[:, :capacity]
    col_side = side_rows[:, capacity:]
    partial_tiles = jnp.einsum(
        "mcid,mcjd->mcij", row_side, col_side, preferred_element_type=jnp.float32
    )
    predicted = lax.psum(partial_tiles, "mp") / math.sqrt(width)
    target_tiles = targets[:, 0].reshape(members, capacity, TB, TB)
    own_count = lax.dynamic_index_in_dim(counts, my_index, 1, keepdims=False)
    live_mask = (jnp.arange(capacity)[None, :] < own_count[:, None]).astype(jnp.float32)
    n_live = jnp.sum(counts, axis=-1).astype(jnp.float32)
    dpredicted = (
        2.0
        / math.sqrt(width)
        * live_mask[:, :, None, None]
        * (predicted - target_tiles)
        / n_live[:, None, None, None]
    )
    row_float = row_side.astype(jnp.float32)
    col_float = col_side.astype(jnp.float32)
    drow = jnp.einsum("mcij,mcjd->mcid", dpredicted, col_float, precision=lax.Precision.HIGHEST)
    dcol = jnp.einsum("mcij,mcid->mcjd", dpredicted, row_float, precision=lax.Precision.HIGHEST)
    dside = jnp.concatenate([drow, dcol], axis=1).astype(jnp.bfloat16)
    inverse = jnp.argsort(slot_index, axis=-1)
    outgoing_grads = take_rows(dside, inverse).reshape(members, seq_count, PER, TB, narrow)
    returned = lax.all_to_all(outgoing_grads, "seq", split_axis=1, concat_axis=1, tiled=True)
    selector = (
        picks.reshape(members, seq_count * PER)[:, :, None] == jnp.arange(per_block)[None, None, :]
    ).astype(jnp.bfloat16)
    dmixed = jnp.einsum(
        "mkn,mktd->mntd",
        selector,
        returned.reshape(members, seq_count * PER, TB, narrow),
        preferred_element_type=jnp.float32,
    ).reshape(members, length, narrow)
    dconv = (scaling[:, None, None] * dmixed).astype(jnp.bfloat16)
    weight_local = weight_term(padded, dconv, length, taps)
    return lax.psum_scatter(weight_local, ("seq", "dp"), scatter_dimension=2, tiled=True)


def axis_sum(value, axis):
    count = lax.axis_size(axis)
    total = value
    for shift in range(1, count):
        total = total + lax.ppermute(value, axis, [(i, (i + shift) % count) for i in range(count)])
    return total


def sparse_path(features, conv_weight, keep, tiles, counts, targets):
    _, length, width = features.shape
    taps, narrow, _ = conv_weight.shape
    halo = taps // 2
    span = TB + 2 * halo
    owners, capacity = tiles.shape[1], tiles.shape[2]
    n_sides = 2 * capacity
    per_block = length // TB
    seq_count = lax.axis_size("seq")
    groups = lax.axis_size("dp")
    peers = seq_count * groups
    held = owners * PER
    cols = width // peers
    my_index = lax.axis_index("seq")
    my_part = lax.axis_index("mp")

    before = jnp.arange(n_sides)[None, :] < jnp.arange(n_sides)[:, None]
    own_sides = jnp.concatenate([tiles[0, ..., 0], tiles[0, ..., 1]], axis=-1)
    own_source = own_sides // per_block
    own_same = own_source[:, :, None] == own_source[:, None, :]
    own_rank = jnp.sum(jnp.logical_and(own_same, before), axis=-1)
    held_here = own_source == my_index
    picks = jnp.stack(
        [
            jnp.sum(jnp.where(jnp.logical_and(held_here, own_rank == r), own_sides % per_block, 0), axis=-1)
            for r in range(PER)
        ],
        axis=-1,
    ).reshape(held)

    cells = features[0]
    ends = seq_count - 1
    if seq_count == 2:
        swapped = lax.ppermute(
            jnp.concatenate([cells[length - halo :], cells[:halo]]), "seq", [(0, 1), (1, 0)]
        )
        head = jnp.where(my_index == 0, jnp.zeros_like(swapped[:halo]), swapped[:halo])
        tail = jnp.where(my_index == ends, jnp.zeros_like(swapped[halo:]), swapped[halo:])
    else:
        head = lax.ppermute(cells[length - halo :], "seq", [(i, i + 1) for i in range(ends)])
        tail = lax.ppermute(cells[:halo], "seq", [(i + 1, i) for i in range(ends)])
    last = per_block - 1
    stacked = cells.reshape(per_block, TB * width)
    block_ids = jnp.arange(per_block)[None, :]

    def select(offset, part):
        choose = (picks[:, None] + offset == block_ids).astype(cells.dtype)
        return jnp.dot(choose, part, preferred_element_type=jnp.float32)

    middle = select(0, stacked).reshape(held, TB, width)
    prev_tail = select(-1, stacked[:, (TB - halo) * width :]).reshape(held, halo, width)
    next_head = select(1, stacked[:, : halo * width]).reshape(held, halo, width)
    lower = jnp.where((picks == 0)[:, None, None], head[None].astype(jnp.float32), prev_tail)
    upper = jnp.where((picks == last)[:, None, None], tail[None].astype(jnp.float32), next_head)
    windows = jnp.concatenate([lower, middle, upper], axis=1).astype(cells.dtype)
    x_float = windows.astype(jnp.float32)
    act = jax.nn.gelu(x_float).astype(jnp.bfloat16)
    conv_out = jnp.einsum("hti,oi->hto", act[:, 0:TB], conv_weight[0], preferred_element_type=jnp.float32)
    for offset in range(1, taps):
        conv_out = conv_out + jnp.einsum(
            "hti,oi->hto", act[:, offset : offset + TB], conv_weight[offset], preferred_element_type=jnp.float32
        )
    my_scale = 1.25 * keep[0].astype(jnp.float32)
    x_part = lax.dynamic_slice_in_dim(x_float[:, halo : halo + TB], my_part * narrow, narrow, 2)
    mixed = (x_part + my_scale * conv_out).astype(jnp.bfloat16)

    def lanes(part):
        flat = part.reshape(part.shape[0], -1)
        flat = jnp.pad(flat, ((0, 0), (0, -flat.shape[1] % 128)))
        return flat.reshape(flat.shape[0], -1, 128)

    act_cut = lanes(act.reshape(held, span, peers, cols).transpose(2, 0, 1, 3))
    mixed_part = lanes(mixed.reshape(1, -1))
    wide = targets.reshape(-1)
    pieces = []
    for _ in range(3):
        piece = lax.reduce_precision(wide, exponent_bits=8, mantissa_bits=7)
        pieces.append(piece)
        wide = wide - piece
    own_slot = (own_source * groups + lax.axis_index("dp")) * held + jnp.arange(owners)[:, None] * PER + own_rank
    small = jnp.concatenate(
        [tiles.reshape(-1), counts.reshape(-1), keep.reshape(-1), own_slot.reshape(-1)]
    ).astype(jnp.float32)
    meta_part = lanes(jnp.concatenate(pieces + [small]).astype(jnp.bfloat16).reshape(1, -1))
    rows_mixed, rows_act, rows_meta = mixed_part.shape[1], act_cut.shape[1], meta_part.shape[1]
    outgoing = jnp.concatenate(
        [
            jnp.broadcast_to(mixed_part, (peers, rows_mixed, 128)),
            act_cut,
            jnp.broadcast_to(meta_part, (peers, rows_meta, 128)),
        ],
        axis=1,
    )
    outgoing = jnp.pad(outgoing, ((0, 0), (0, -outgoing.shape[1] % 16), (0, 0)))
    incoming = lax.all_to_all(outgoing, ("seq", "dp"), 0, 0, tiled=True)
    n_mixed = held * TB * narrow
    n_act = held * span * cols
    mixed_in = incoming[:, :rows_mixed].reshape(peers, -1)[:, :n_mixed].reshape(peers * held, TB, narrow)
    act_in = incoming[:, rows_mixed : rows_mixed + rows_act].reshape(peers, -1)[:, :n_act]
    act_in = act_in.reshape(peers * held, span, cols)
    meta_in = incoming[:, rows_mixed + rows_act : rows_mixed + rows_act + rows_meta].reshape(peers, -1)
    meta_in = meta_in.astype(jnp.float32).reshape(seq_count, groups, -1)
    n_targets = capacity * TB * TB
    n_tiles = owners * capacity * 2
    targets_all = meta_in[:, :, :n_targets] + meta_in[:, :, n_targets : 2 * n_targets]
    targets_all = targets_all + meta_in[:, :, 2 * n_targets : 3 * n_targets]
    ints = meta_in[0, :, 3 * n_targets :].astype(jnp.int32)
    tiles_all = ints[:, :n_tiles].reshape(groups, owners, capacity, 2)
    counts_all = ints[:, n_tiles : n_tiles + owners]
    keep_all = ints[:, n_tiles + owners]
    slot = ints[:, n_tiles + owners + 1 : n_tiles + owners + 1 + owners * n_sides].reshape(groups, owners, n_sides)

    sides = jnp.concatenate([tiles_all[..., 0], tiles_all[..., 1]], axis=-1)

    side_rows = jnp.take(mixed_in, slot, axis=0)
    row_side = side_rows[:, :, :capacity]
    col_side = side_rows[:, :, capacity:]
    partial_tiles = jnp.einsum("qocid,qocjd->qocij", row_side, col_side, preferred_element_type=jnp.float32)
    lanes_shape = partial_tiles.shape
    summed = axis_sum(partial_tiles.reshape(-1, 128), "mp").reshape(lanes_shape)
    predicted = summed / math.sqrt(width)
    target_tiles = targets_all.reshape(seq_count, groups, capacity, TB, TB).transpose(1, 0, 2, 3, 4)
    live_mask = (jnp.arange(capacity)[None, None, :] < counts_all[:, :, None]).astype(jnp.float32)
    n_live = jnp.sum(counts_all, axis=-1).astype(jnp.float32)
    dpredicted = (
        2.0
        / math.sqrt(width)
        * live_mask[..., None, None]
        * (predicted - target_tiles)
        / n_live[:, None, None, None, None]
    )
    row_float = row_side.astype(jnp.float32)
    col_float = col_side.astype(jnp.float32)
    drow = jnp.einsum("qocij,qocjd->qocid", dpredicted, col_float, precision=lax.Precision.HIGH)
    dcol = jnp.einsum("qocij,qocid->qocjd", dpredicted, row_float, precision=lax.Precision.HIGH)
    grads = jnp.concatenate([drow, dcol], axis=2).astype(jnp.bfloat16).astype(jnp.float32)
    grads = grads.reshape(groups, owners * n_sides, TB, narrow)
    flat_sides = sides.reshape(groups, owners * n_sides)
    same_block = flat_sides[:, :, None] == flat_sides[:, None, :]
    total = jnp.einsum(
        "qab,qbtd->qatd",
        same_block.astype(jnp.bfloat16),
        grads.astype(jnp.bfloat16),
        preferred_element_type=jnp.float32,
    )
    earlier = jnp.arange(owners * n_sides)[None, :] < jnp.arange(owners * n_sides)[:, None]
    first = jnp.logical_not(jnp.any(jnp.logical_and(same_block, earlier[None]), axis=-1))
    scaling = 1.25 * keep_all.astype(jnp.float32)
    dconv = (scaling[:, None, None, None] * total).astype(jnp.bfloat16)
    dconv = jnp.where(first[..., None, None], dconv, jnp.zeros_like(dconv))
    act_sides = jnp.take(act_in, slot.reshape(groups, owners * n_sides), axis=0)
    return jnp.stack(
        [
            jnp.einsum(
                "qato,qati->oi",
                dconv,
                act_sides[:, :, offset : offset + TB],
                preferred_element_type=jnp.float32,
            )
            for offset in range(taps)
        ]
    )


def per_device(features, conv_weight, keep, tiles, counts, targets):
    members, length, _ = features.shape
    owners, capacity = tiles.shape[1], tiles.shape[2]
    blocks = lax.axis_size("seq") * length // TB
    fits = members == 1 and targets.shape[1] == 1 and 2 * owners * capacity * TB <= length
    fits = fits and blocks <= 256 and capacity <= 256
    if fits:
        return sparse_path(features, conv_weight, keep, tiles, counts, targets)
    return dense_path(features, conv_weight, keep, tiles, counts, targets)


def solution(mesh):
    placed = (
        P("dp", "seq", None),
        P(None, "mp", None),
        P("dp"),
        P("dp", None, None, None),
        P("dp", None),
        P("dp", "seq", None, None),
    )
    return jax.shard_map(
        per_device,
        mesh=mesh,
        in_specs=placed,
        out_specs=P(None, "mp", ("seq", "dp")),
        check_vma=False,
    )
```

```python
import math

import jax
import jax.numpy as jnp
from jax import lax
from jax.sharding import PartitionSpec as P

TB = 32
PER = 2


def extended(cells, sides, width):
    for axis, dim in sides:
        count = lax.axis_size(axis)
        ends = count - 1
        head = lax.slice_in_dim(cells, 0, width, axis=dim)
        tail = lax.slice_in_dim(cells, cells.shape[dim] - width, cells.shape[dim], axis=dim)
        cells = jnp.concatenate(
            [
                lax.ppermute(tail, axis, [(i, (i + 1) % count) for i in range(ends)]),
                cells,
                lax.ppermute(head, axis, [((i + 1) % count, i) for i in range(ends)]),
            ],
            axis=dim,
        )
    return cells


def take_rows(source_array, index_array):
    return jax.vmap(lambda table, picked: table[picked])(source_array, index_array)


def conv_apply(padded, weight, length):
    total = jnp.einsum(
        "mbi,oi->mbo", padded[:, 0:length], weight[0], preferred_element_type=jnp.float32
    )
    for offset in range(1, weight.shape[0]):
        total = total + jnp.einsum(
            "mbi,oi->mbo",
            padded[:, offset : offset + length],
            weight[offset],
            preferred_element_type=jnp.float32,
        )
    return total


def weight_term(padded, dconv, length, taps):
    return jnp.stack(
        [
            jnp.einsum(
                "mbi,mbo->oi",
                padded[:, offset : offset + length],
                dconv,
                preferred_element_type=jnp.float32,
            )
            for offset in range(taps)
        ]
    )


def dense_path(features, conv_weight, keep, tiles, counts, targets):
    members, length, width = features.shape
    taps = conv_weight.shape[0]
    narrow = conv_weight.shape[1]
    seq_count = lax.axis_size("seq")
    my_index = lax.axis_index("seq")
    my_part = lax.axis_index("mp")
    x_float = features.astype(jnp.float32)
    activations = jax.nn.gelu(x_float).astype(jnp.bfloat16)
    padded = extended(activations, (("seq", 1),), 2)
    scaling = 1.25 * keep.astype(jnp.float32)
    conv_out = conv_apply(padded, conv_weight, length)
    x_local = lax.dynamic_slice_in_dim(x_float, my_part * narrow, narrow, 2)
    mixed_out = (x_local + scaling[:, None, None] * conv_out).astype(jnp.bfloat16)
    capacity = tiles.shape[2]
    n_sides = 2 * capacity
    per_block = length // TB
    sides = jnp.concatenate([tiles[..., 0], tiles[..., 1]], axis=-1)
    side_source = sides // per_block
    side_local = sides % per_block
    own_sides = lax.dynamic_index_in_dim(sides, my_index, 1, keepdims=False)
    own_source = own_sides // per_block
    before = jnp.arange(n_sides)[None, :] < jnp.arange(n_sides)[:, None]
    same_source = own_source[:, :, None] == own_source[:, None, :]
    rank_within = jnp.sum(jnp.logical_and(same_source, before[None]), axis=-1)
    slot_index = own_source * PER + rank_within
    held_here = side_source == my_index
    held_order = jnp.cumsum(held_here.astype(jnp.int32), axis=-1) - 1
    picks = jnp.stack(
        [
            jnp.sum(
                jnp.where(jnp.logical_and(held_here, held_order == position), side_local, 0),
                axis=-1,
            )
            for position in range(PER)
        ],
        axis=-1,
    )
    blocks = mixed_out.reshape(members, per_block, TB, narrow)
    whole = lax.all_gather(blocks, "seq", axis=1, tiled=True)
    side_rows = take_rows(whole, own_sides)
    row_side = side_rows[:, :capacity]
    col_side = side_rows[:, capacity:]
    partial_tiles = jnp.einsum(
        "mcid,mcjd->mcij", row_side, col_side, preferred_element_type=jnp.float32
    )
    predicted = lax.psum(partial_tiles, "mp") / math.sqrt(width)
    target_tiles = targets[:, 0].reshape(members, capacity, TB, TB)
    own_count = lax.dynamic_index_in_dim(counts, my_index, 1, keepdims=False)
    live_mask = (jnp.arange(capacity)[None, :] < own_count[:, None]).astype(jnp.float32)
    n_live = jnp.sum(counts, axis=-1).astype(jnp.float32)
    dpredicted = (
        2.0
        / math.sqrt(width)
        * live_mask[:, :, None, None]
        * (predicted - target_tiles)
        / n_live[:, None, None, None]
    )
    row_float = row_side.astype(jnp.float32)
    col_float = col_side.astype(jnp.float32)
    drow = jnp.einsum("mcij,mcjd->mcid", dpredicted, col_float, precision=lax.Precision.HIGHEST)
    dcol = jnp.einsum("mcij,mcid->mcjd", dpredicted, row_float, precision=lax.Precision.HIGHEST)
    dside = jnp.concatenate([drow, dcol], axis=1).astype(jnp.bfloat16)
    inverse = jnp.argsort(slot_index, axis=-1)
    outgoing_grads = take_rows(dside, inverse).reshape(members, seq_count, PER, TB, narrow)
    returned = lax.all_to_all(outgoing_grads, "seq", split_axis=1, concat_axis=1, tiled=True)
    selector = (
        picks.reshape(members, seq_count * PER)[:, :, None] == jnp.arange(per_block)[None, None, :]
    ).astype(jnp.bfloat16)
    dmixed = jnp.einsum(
        "mkn,mktd->mntd",
        selector,
        returned.reshape(members, seq_count * PER, TB, narrow),
        preferred_element_type=jnp.float32,
    ).reshape(members, length, narrow)
    dconv = (scaling[:, None, None] * dmixed).astype(jnp.bfloat16)
    weight_local = weight_term(padded, dconv, length, taps)
    return lax.psum_scatter(weight_local, ("seq", "dp"), scatter_dimension=2, tiled=True)


def axis_sum(value, axis):
    count = lax.axis_size(axis)
    total = value
    for shift in range(1, count):
        total = total + lax.ppermute(value, axis, [(i, (i + shift) % count) for i in range(count)])
    return total


def sparse_path(features, conv_weight, keep, tiles, counts, targets):
    _, length, width = features.shape
    taps, narrow, _ = conv_weight.shape
    halo = taps // 2
    span = TB + 2 * halo
    owners, capacity = tiles.shape[1], tiles.shape[2]
    n_sides = 2 * capacity
    per_block = length // TB
    seq_count = lax.axis_size("seq")
    groups = lax.axis_size("dp")
    peers = seq_count * groups
    held = owners * PER
    cols = width // peers
    my_index = lax.axis_index("seq")
    my_part = lax.axis_index("mp")

    before = jnp.arange(n_sides)[None, :] < jnp.arange(n_sides)[:, None]
    own_sides = jnp.concatenate([tiles[0, ..., 0], tiles[0, ..., 1]], axis=-1)
    own_source = own_sides // per_block
    own_same = own_source[:, :, None] == own_source[:, None, :]
    own_rank = jnp.sum(jnp.logical_and(own_same, before), axis=-1)
    held_here = own_source == my_index
    picks = jnp.stack(
        [
            jnp.sum(jnp.where(jnp.logical_and(held_here, own_rank == r), own_sides % per_block, 0), axis=-1)
            for r in range(PER)
        ],
        axis=-1,
    ).reshape(held)

    cells = features[0]
    ends = seq_count - 1
    if seq_count == 2:
        swapped = lax.ppermute(
            jnp.concatenate([cells[length - halo :], cells[:halo]]), "seq", [(0, 1), (1, 0)]
        )
        head = jnp.where(my_index == 0, jnp.zeros_like(swapped[:halo]), swapped[:halo])
        tail = jnp.where(my_index == ends, jnp.zeros_like(swapped[halo:]), swapped[halo:])
    else:
        head = lax.ppermute(cells[length - halo :], "seq", [(i, i + 1) for i in range(ends)])
        tail = lax.ppermute(cells[:halo], "seq", [(i + 1, i) for i in range(ends)])
    last = per_block - 1
    stacked = cells.reshape(per_block, TB * width)
    block_ids = jnp.arange(per_block)[None, :]

    def select(offset, part):
        choose = (picks[:, None] + offset == block_ids).astype(cells.dtype)
        return jnp.dot(choose, part, preferred_element_type=jnp.float32)

    middle = select(0, stacked).reshape(held, TB, width)
    prev_tail = select(-1, stacked[:, (TB - halo) * width :]).reshape(held, halo, width)
    next_head = select(1, stacked[:, : halo * width]).reshape(held, halo, width)
    lower = jnp.where((picks == 0)[:, None, None], head[None].astype(jnp.float32), prev_tail)
    upper = jnp.where((picks == last)[:, None, None], tail[None].astype(jnp.float32), next_head)
    windows = jnp.concatenate([lower, middle, upper], axis=1).astype(cells.dtype)
    x_float = windows.astype(jnp.float32)
    act = jax.nn.gelu(x_float).astype(jnp.bfloat16)
    conv_out = jnp.einsum("hti,oi->hto", act[:, 0:TB], conv_weight[0], preferred_element_type=jnp.float32)
    for offset in range(1, taps):
        conv_out = conv_out + jnp.einsum(
            "hti,oi->hto", act[:, offset : offset + TB], conv_weight[offset], preferred_element_type=jnp.float32
        )
    my_scale = 1.25 * keep[0].astype(jnp.float32)
    x_part = lax.dynamic_slice_in_dim(x_float[:, halo : halo + TB], my_part * narrow, narrow, 2)
    mixed = (x_part + my_scale * conv_out).astype(jnp.bfloat16)

    def lanes(part):
        flat = part.reshape(part.shape[0], -1)
        flat = jnp.pad(flat, ((0, 0), (0, -flat.shape[1] % 128)))
        return flat.reshape(flat.shape[0], -1, 128)

    act_cut = lanes(act.reshape(held, span, peers, cols).transpose(2, 0, 1, 3))
    mixed_part = lanes(mixed.reshape(1, -1))
    wide = targets.reshape(-1)
    pieces = []
    for _ in range(3):
        piece = lax.reduce_precision(wide, exponent_bits=8, mantissa_bits=7)
        pieces.append(piece)
        wide = wide - piece
    own_slot = (own_source * groups + lax.axis_index("dp")) * held + jnp.arange(owners)[:, None] * PER + own_rank
    small = jnp.concatenate(
        [tiles.reshape(-1), counts.reshape(-1), keep.reshape(-1), own_slot.reshape(-1)]
    ).astype(jnp.float32)
    meta_part = lanes(jnp.concatenate(pieces + [small]).astype(jnp.bfloat16).reshape(1, -1))
    rows_mixed, rows_act, rows_meta = mixed_part.shape[1], act_cut.shape[1], meta_part.shape[1]
    outgoing = jnp.concatenate(
        [
            jnp.broadcast_to(mixed_part, (peers, rows_mixed, 128)),
            act_cut,
            jnp.broadcast_to(meta_part, (peers, rows_meta, 128)),
        ],
        axis=1,
    )
    outgoing = jnp.pad(outgoing, ((0, 0), (0, -outgoing.shape[1] % 16), (0, 0)))
    incoming = lax.all_to_all(outgoing, ("seq", "dp"), 0, 0, tiled=True)
    n_mixed = held * TB * narrow
    n_act = held * span * cols
    mixed_in = incoming[:, :rows_mixed].reshape(peers, -1)[:, :n_mixed].reshape(peers * held, TB, narrow)
    act_in = incoming[:, rows_mixed : rows_mixed + rows_act].reshape(peers, -1)[:, :n_act]
    act_in = act_in.reshape(peers * held, span, cols)
    meta_in = incoming[:, rows_mixed + rows_act : rows_mixed + rows_act + rows_meta].reshape(peers, -1)
    meta_in = meta_in.astype(jnp.float32).reshape(seq_count, groups, -1)
    n_targets = capacity * TB * TB
    n_tiles = owners * capacity * 2
    targets_all = meta_in[:, :, :n_targets] + meta_in[:, :, n_targets : 2 * n_targets]
    targets_all = targets_all + meta_in[:, :, 2 * n_targets : 3 * n_targets]
    ints = meta_in[0, :, 3 * n_targets :].astype(jnp.int32)
    tiles_all = ints[:, :n_tiles].reshape(groups, owners, capacity, 2)
    counts_all = ints[:, n_tiles : n_tiles + owners]
    keep_all = ints[:, n_tiles + owners]
    slot = ints[:, n_tiles + owners + 1 : n_tiles + owners + 1 + owners * n_sides].reshape(groups, owners, n_sides)

    sides = jnp.concatenate([tiles_all[..., 0], tiles_all[..., 1]], axis=-1)

    pick_slot = (slot[..., None] == jnp.arange(peers * held)).astype(jnp.bfloat16)
    side_rows = jnp.dot(
        pick_slot.reshape(-1, peers * held), mixed_in.reshape(peers * held, -1), preferred_element_type=jnp.float32
    ).astype(jnp.bfloat16).reshape(slot.shape + (TB, narrow))
    row_side = side_rows[:, :, :capacity]
    col_side = side_rows[:, :, capacity:]
    partial_tiles = jnp.einsum("qocid,qocjd->qocij", row_side, col_side, preferred_element_type=jnp.float32)
    lanes_shape = partial_tiles.shape
    summed = axis_sum(partial_tiles.reshape(-1, 128), "mp").reshape(lanes_shape)
    predicted = summed / math.sqrt(width)
    target_tiles = targets_all.reshape(seq_count, groups, capacity, TB, TB).transpose(1, 0, 2, 3, 4)
    live_mask = (jnp.arange(capacity)[None, None, :] < counts_all[:, :, None]).astype(jnp.float32)
    n_live = jnp.sum(counts_all, axis=-1).astype(jnp.float32)
    dpredicted = (
        2.0
        / math.sqrt(width)
        * live_mask[..., None, None]
        * (predicted - target_tiles)
        / n_live[:, None, None, None, None]
    )
    row_float = row_side.astype(jnp.float32)
    col_float = col_side.astype(jnp.float32)
    drow = jnp.einsum("qocij,qocjd->qocid", dpredicted, col_float, precision=lax.Precision.HIGHEST)
    dcol = jnp.einsum("qocij,qocid->qocjd", dpredicted, row_float, precision=lax.Precision.HIGHEST)
    grads = jnp.concatenate([drow, dcol], axis=2).astype(jnp.bfloat16).astype(jnp.float32)
    grads = grads.reshape(groups, owners * n_sides, TB, narrow)
    flat_sides = sides.reshape(groups, owners * n_sides)
    same_block = flat_sides[:, :, None] == flat_sides[:, None, :]
    total = jnp.einsum(
        "qab,qbtd->qatd", same_block.astype(jnp.float32), grads, precision=lax.Precision.HIGHEST
    )
    earlier = jnp.arange(owners * n_sides)[None, :] < jnp.arange(owners * n_sides)[:, None]
    first = jnp.logical_not(jnp.any(jnp.logical_and(same_block, earlier[None]), axis=-1))
    scaling = 1.25 * keep_all.astype(jnp.float32)
    dconv = (scaling[:, None, None, None] * total).astype(jnp.bfloat16)
    dconv = jnp.where(first[..., None, None], dconv, jnp.zeros_like(dconv))
    act_sides = jnp.take(act_in, slot.reshape(groups, owners * n_sides), axis=0)
    return jnp.stack(
        [
            jnp.einsum(
                "qato,qati->oi",
                dconv,
                act_sides[:, :, offset : offset + TB],
                preferred_element_type=jnp.float32,
            )
            for offset in range(taps)
        ]
    )


def per_device(features, conv_weight, keep, tiles, counts, targets):
    members, length, _ = features.shape
    owners, capacity = tiles.shape[1], tiles.shape[2]
    blocks = lax.axis_size("seq") * length // TB
    fits = members == 1 and targets.shape[1] == 1 and 2 * owners * capacity * TB <= length
    fits = fits and blocks <= 256 and capacity <= 256
    if fits:
        return sparse_path(features, conv_weight, keep, tiles, counts, targets)
    return dense_path(features, conv_weight, keep, tiles, counts, targets)


def solution(mesh):
    placed = (
        P("dp", "seq", None),
        P(None, "mp", None),
        P("dp"),
        P("dp", None, None, None),
        P("dp", None),
        P("dp", "seq", None, None),
    )
    return jax.shard_map(
        per_device,
        mesh=mesh,
        in_specs=placed,
        out_specs=P(None, "mp", ("seq", "dp")),
        check_vma=False,
    )
```

```python
import math

import jax
import jax.numpy as jnp
from jax import lax
from jax.sharding import PartitionSpec as P

TB = 32
PER = 2


def extended(cells, sides, width):
    for axis, dim in sides:
        count = lax.axis_size(axis)
        ends = count - 1
        head = lax.slice_in_dim(cells, 0, width, axis=dim)
        tail = lax.slice_in_dim(cells, cells.shape[dim] - width, cells.shape[dim], axis=dim)
        cells = jnp.concatenate(
            [
                lax.ppermute(tail, axis, [(i, (i + 1) % count) for i in range(ends)]),
                cells,
                lax.ppermute(head, axis, [((i + 1) % count, i) for i in range(ends)]),
            ],
            axis=dim,
        )
    return cells


def take_rows(source_array, index_array):
    return jax.vmap(lambda table, picked: table[picked])(source_array, index_array)


def conv_apply(padded, weight, length):
    total = jnp.einsum(
        "mbi,oi->mbo", padded[:, 0:length], weight[0], preferred_element_type=jnp.float32
    )
    for offset in range(1, weight.shape[0]):
        total = total + jnp.einsum(
            "mbi,oi->mbo",
            padded[:, offset : offset + length],
            weight[offset],
            preferred_element_type=jnp.float32,
        )
    return total


def weight_term(padded, dconv, length, taps):
    return jnp.stack(
        [
            jnp.einsum(
                "mbi,mbo->oi",
                padded[:, offset : offset + length],
                dconv,
                preferred_element_type=jnp.float32,
            )
            for offset in range(taps)
        ]
    )


def dense_path(features, conv_weight, keep, tiles, counts, targets):
    members, length, width = features.shape
    taps = conv_weight.shape[0]
    narrow = conv_weight.shape[1]
    seq_count = lax.axis_size("seq")
    my_index = lax.axis_index("seq")
    my_part = lax.axis_index("mp")
    x_float = features.astype(jnp.float32)
    activations = jax.nn.gelu(x_float).astype(jnp.bfloat16)
    padded = extended(activations, (("seq", 1),), 2)
    scaling = 1.25 * keep.astype(jnp.float32)
    conv_out = conv_apply(padded, conv_weight, length)
    x_local = lax.dynamic_slice_in_dim(x_float, my_part * narrow, narrow, 2)
    mixed_out = (x_local + scaling[:, None, None] * conv_out).astype(jnp.bfloat16)
    capacity = tiles.shape[2]
    n_sides = 2 * capacity
    per_block = length // TB
    sides = jnp.concatenate([tiles[..., 0], tiles[..., 1]], axis=-1)
    side_source = sides // per_block
    side_local = sides % per_block
    own_sides = lax.dynamic_index_in_dim(sides, my_index, 1, keepdims=False)
    own_source = own_sides // per_block
    before = jnp.arange(n_sides)[None, :] < jnp.arange(n_sides)[:, None]
    same_source = own_source[:, :, None] == own_source[:, None, :]
    rank_within = jnp.sum(jnp.logical_and(same_source, before[None]), axis=-1)
    slot_index = own_source * PER + rank_within
    held_here = side_source == my_index
    held_order = jnp.cumsum(held_here.astype(jnp.int32), axis=-1) - 1
    picks = jnp.stack(
        [
            jnp.sum(
                jnp.where(jnp.logical_and(held_here, held_order == position), side_local, 0),
                axis=-1,
            )
            for position in range(PER)
        ],
        axis=-1,
    )
    blocks = mixed_out.reshape(members, per_block, TB, narrow)
    whole = lax.all_gather(blocks, "seq", axis=1, tiled=True)
    side_rows = take_rows(whole, own_sides)
    row_side = side_rows[:, :capacity]
    col_side = side_rows[:, capacity:]
    partial_tiles = jnp.einsum(
        "mcid,mcjd->mcij", row_side, col_side, preferred_element_type=jnp.float32
    )
    predicted = lax.psum(partial_tiles, "mp") / math.sqrt(width)
    target_tiles = targets[:, 0].reshape(members, capacity, TB, TB)
    own_count = lax.dynamic_index_in_dim(counts, my_index, 1, keepdims=False)
    live_mask = (jnp.arange(capacity)[None, :] < own_count[:, None]).astype(jnp.float32)
    n_live = jnp.sum(counts, axis=-1).astype(jnp.float32)
    dpredicted = (
        2.0
        / math.sqrt(width)
        * live_mask[:, :, None, None]
        * (predicted - target_tiles)
        / n_live[:, None, None, None]
    )
    row_float = row_side.astype(jnp.float32)
    col_float = col_side.astype(jnp.float32)
    drow = jnp.einsum("mcij,mcjd->mcid", dpredicted, col_float, precision=lax.Precision.HIGHEST)
    dcol = jnp.einsum("mcij,mcid->mcjd", dpredicted, row_float, precision=lax.Precision.HIGHEST)
    dside = jnp.concatenate([drow, dcol], axis=1).astype(jnp.bfloat16)
    inverse = jnp.argsort(slot_index, axis=-1)
    outgoing_grads = take_rows(dside, inverse).reshape(members, seq_count, PER, TB, narrow)
    returned = lax.all_to_all(outgoing_grads, "seq", split_axis=1, concat_axis=1, tiled=True)
    selector = (
        picks.reshape(members, seq_count * PER)[:, :, None] == jnp.arange(per_block)[None, None, :]
    ).astype(jnp.bfloat16)
    dmixed = jnp.einsum(
        "mkn,mktd->mntd",
        selector,
        returned.reshape(members, seq_count * PER, TB, narrow),
        preferred_element_type=jnp.float32,
    ).reshape(members, length, narrow)
    dconv = (scaling[:, None, None] * dmixed).astype(jnp.bfloat16)
    weight_local = weight_term(padded, dconv, length, taps)
    return lax.psum_scatter(weight_local, ("seq", "dp"), scatter_dimension=2, tiled=True)


def axis_sum(value, axis):
    count = lax.axis_size(axis)
    total = value
    middle = count // 2
    for shift in [middle] + [k for k in range(1, count) if k != middle]:
        total = total + lax.ppermute(value, axis, [(i, (i + shift) % count) for i in range(count)])
    return total


def sparse_path(features, conv_weight, keep, tiles, counts, targets):
    _, length, width = features.shape
    taps, narrow, _ = conv_weight.shape
    halo = taps // 2
    span = TB + 2 * halo
    owners, capacity = tiles.shape[1], tiles.shape[2]
    n_sides = 2 * capacity
    per_block = length // TB
    seq_count = lax.axis_size("seq")
    groups = lax.axis_size("dp")
    peers = seq_count * groups
    held = owners * PER
    cols = width // peers
    my_index = lax.axis_index("seq")
    my_part = lax.axis_index("mp")

    before = jnp.arange(n_sides)[None, :] < jnp.arange(n_sides)[:, None]
    own_sides = jnp.concatenate([tiles[0, ..., 0], tiles[0, ..., 1]], axis=-1)
    own_source = own_sides // per_block
    own_same = own_source[:, :, None] == own_source[:, None, :]
    own_rank = jnp.sum(jnp.logical_and(own_same, before), axis=-1)
    held_here = own_source == my_index
    picks = jnp.stack(
        [
            jnp.sum(jnp.where(jnp.logical_and(held_here, own_rank == r), own_sides % per_block, 0), axis=-1)
            for r in range(PER)
        ],
        axis=-1,
    ).reshape(held)

    cells = features[0]
    ends = seq_count - 1
    if seq_count == 2:
        swapped = lax.ppermute(
            jnp.concatenate([cells[length - halo :], cells[:halo]]), "seq", [(0, 1), (1, 0)]
        )
        head = jnp.where(my_index == 0, jnp.zeros_like(swapped[:halo]), swapped[:halo])
        tail = jnp.where(my_index == ends, jnp.zeros_like(swapped[halo:]), swapped[halo:])
    else:
        head = lax.ppermute(cells[length - halo :], "seq", [(i, i + 1) for i in range(ends)])
        tail = lax.ppermute(cells[:halo], "seq", [(i + 1, i) for i in range(ends)])
    last = per_block - 1
    stacked = cells.reshape(per_block, TB * width)
    block_ids = jnp.arange(per_block)[None, :]

    def select(offset, part):
        choose = (picks[:, None] + offset == block_ids).astype(cells.dtype)
        return jnp.dot(choose, part, preferred_element_type=jnp.float32)

    middle = select(0, stacked).reshape(held, TB, width)
    prev_tail = select(-1, stacked[:, (TB - halo) * width :]).reshape(held, halo, width)
    next_head = select(1, stacked[:, : halo * width]).reshape(held, halo, width)
    lower = jnp.where((picks == 0)[:, None, None], head[None].astype(jnp.float32), prev_tail)
    upper = jnp.where((picks == last)[:, None, None], tail[None].astype(jnp.float32), next_head)
    windows = jnp.concatenate([lower, middle, upper], axis=1).astype(cells.dtype)
    x_float = windows.astype(jnp.float32)
    act = jax.nn.gelu(x_float).astype(jnp.bfloat16)
    conv_out = jnp.einsum("hti,oi->hto", act[:, 0:TB], conv_weight[0], preferred_element_type=jnp.float32)
    for offset in range(1, taps):
        conv_out = conv_out + jnp.einsum(
            "hti,oi->hto", act[:, offset : offset + TB], conv_weight[offset], preferred_element_type=jnp.float32
        )
    my_scale = 1.25 * keep[0].astype(jnp.float32)
    x_part = lax.dynamic_slice_in_dim(x_float[:, halo : halo + TB], my_part * narrow, narrow, 2)
    mixed = (x_part + my_scale * conv_out).astype(jnp.bfloat16)

    def lanes(part):
        flat = part.reshape(part.shape[0], -1)
        flat = jnp.pad(flat, ((0, 0), (0, -flat.shape[1] % 128)))
        return flat.reshape(flat.shape[0], -1, 128)

    act_cut = lanes(act.reshape(held, span, peers, cols).transpose(2, 0, 1, 3))
    mixed_part = lanes(mixed.reshape(1, -1))
    wide = targets.reshape(-1)
    pieces = []
    for _ in range(3):
        piece = lax.reduce_precision(wide, exponent_bits=8, mantissa_bits=7)
        pieces.append(piece)
        wide = wide - piece
    own_slot = (own_source * groups + lax.axis_index("dp")) * held + jnp.arange(owners)[:, None] * PER + own_rank
    small = jnp.concatenate(
        [tiles.reshape(-1), counts.reshape(-1), keep.reshape(-1), own_slot.reshape(-1)]
    ).astype(jnp.float32)
    meta_part = lanes(jnp.concatenate(pieces + [small]).astype(jnp.bfloat16).reshape(1, -1))
    rows_mixed, rows_act, rows_meta = mixed_part.shape[1], act_cut.shape[1], meta_part.shape[1]
    outgoing = jnp.concatenate(
        [
            jnp.broadcast_to(mixed_part, (peers, rows_mixed, 128)),
            act_cut,
            jnp.broadcast_to(meta_part, (peers, rows_meta, 128)),
        ],
        axis=1,
    )
    outgoing = jnp.pad(outgoing, ((0, 0), (0, -outgoing.shape[1] % 16), (0, 0)))
    incoming = lax.all_to_all(outgoing, ("seq", "dp"), 0, 0, tiled=True)
    n_mixed = held * TB * narrow
    n_act = held * span * cols
    mixed_in = incoming[:, :rows_mixed].reshape(peers, -1)[:, :n_mixed].reshape(peers * held, TB, narrow)
    act_in = incoming[:, rows_mixed : rows_mixed + rows_act].reshape(peers, -1)[:, :n_act]
    act_in = act_in.reshape(peers * held, span, cols)
    meta_in = incoming[:, rows_mixed + rows_act : rows_mixed + rows_act + rows_meta].reshape(peers, -1)
    meta_in = meta_in.astype(jnp.float32).reshape(seq_count, groups, -1)
    n_targets = capacity * TB * TB
    n_tiles = owners * capacity * 2
    targets_all = meta_in[:, :, :n_targets] + meta_in[:, :, n_targets : 2 * n_targets]
    targets_all = targets_all + meta_in[:, :, 2 * n_targets : 3 * n_targets]
    ints = meta_in[0, :, 3 * n_targets :].astype(jnp.int32)
    tiles_all = ints[:, :n_tiles].reshape(groups, owners, capacity, 2)
    counts_all = ints[:, n_tiles : n_tiles + owners]
    keep_all = ints[:, n_tiles + owners]
    slot = ints[:, n_tiles + owners + 1 : n_tiles + owners + 1 + owners * n_sides].reshape(groups, owners, n_sides)

    sides = jnp.concatenate([tiles_all[..., 0], tiles_all[..., 1]], axis=-1)

    pick_slot = (slot[..., None] == jnp.arange(peers * held)).astype(jnp.bfloat16)
    side_rows = jnp.dot(
        pick_slot.reshape(-1, peers * held), mixed_in.reshape(peers * held, -1), preferred_element_type=jnp.float32
    ).astype(jnp.bfloat16).reshape(slot.shape + (TB, narrow))
    row_side = side_rows[:, :, :capacity]
    col_side = side_rows[:, :, capacity:]
    partial_tiles = jnp.einsum("qocid,qocjd->qocij", row_side, col_side, preferred_element_type=jnp.float32)
    lanes_shape = partial_tiles.shape
    summed = axis_sum(partial_tiles.reshape(-1, 128), "mp").reshape(lanes_shape)
    predicted = summed / math.sqrt(width)
    target_tiles = targets_all.reshape(seq_count, groups, capacity, TB, TB).transpose(1, 0, 2, 3, 4)
    live_mask = (jnp.arange(capacity)[None, None, :] < counts_all[:, :, None]).astype(jnp.float32)
    n_live = jnp.sum(counts_all, axis=-1).astype(jnp.float32)
    dpredicted = (
        2.0
        / math.sqrt(width)
        * live_mask[..., None, None]
        * (predicted - target_tiles)
        / n_live[:, None, None, None, None]
    )
    row_float = row_side.astype(jnp.float32)
    col_float = col_side.astype(jnp.float32)
    drow = jnp.einsum("qocij,qocjd->qocid", dpredicted, col_float, precision=lax.Precision.HIGHEST)
    dcol = jnp.einsum("qocij,qocid->qocjd", dpredicted, row_float, precision=lax.Precision.HIGHEST)
    grads = jnp.concatenate([drow, dcol], axis=2).astype(jnp.bfloat16).astype(jnp.float32)
    grads = grads.reshape(groups, owners * n_sides, TB, narrow)
    flat_sides = sides.reshape(groups, owners * n_sides)
    same_block = flat_sides[:, :, None] == flat_sides[:, None, :]
    total = jnp.einsum(
        "qab,qbtd->qatd", same_block.astype(jnp.float32), grads, precision=lax.Precision.HIGHEST
    )
    earlier = jnp.arange(owners * n_sides)[None, :] < jnp.arange(owners * n_sides)[:, None]
    first = jnp.logical_not(jnp.any(jnp.logical_and(same_block, earlier[None]), axis=-1))
    scaling = 1.25 * keep_all.astype(jnp.float32)
    dconv = (scaling[:, None, None, None] * total).astype(jnp.bfloat16)
    dconv = jnp.where(first[..., None, None], dconv, jnp.zeros_like(dconv))
    act_sides = jnp.take(act_in, slot.reshape(groups, owners * n_sides), axis=0)
    return jnp.stack(
        [
            jnp.einsum(
                "qato,qati->oi",
                dconv,
                act_sides[:, :, offset : offset + TB],
                preferred_element_type=jnp.float32,
            )
            for offset in range(taps)
        ]
    )


def per_device(features, conv_weight, keep, tiles, counts, targets):
    members, length, _ = features.shape
    owners, capacity = tiles.shape[1], tiles.shape[2]
    blocks = lax.axis_size("seq") * length // TB
    fits = members == 1 and targets.shape[1] == 1 and 2 * owners * capacity * TB <= length
    fits = fits and blocks <= 256 and capacity <= 256
    if fits:
        return sparse_path(features, conv_weight, keep, tiles, counts, targets)
    return dense_path(features, conv_weight, keep, tiles, counts, targets)


def solution(mesh):
    placed = (
        P("dp", "seq", None),
        P(None, "mp", None),
        P("dp"),
        P("dp", None, None, None),
        P("dp", None),
        P("dp", "seq", None, None),
    )
    return jax.shard_map(
        per_device,
        mesh=mesh,
        in_specs=placed,
        out_specs=P(None, "mp", ("seq", "dp")),
        check_vma=False,
    )
```

```python
import math

import jax
import jax.numpy as jnp
from jax import lax
from jax.sharding import PartitionSpec as P

TB = 32
PER = 2


def extended(cells, sides, width):
    for axis, dim in sides:
        count = lax.axis_size(axis)
        ends = count - 1
        head = lax.slice_in_dim(cells, 0, width, axis=dim)
        tail = lax.slice_in_dim(cells, cells.shape[dim] - width, cells.shape[dim], axis=dim)
        cells = jnp.concatenate(
            [
                lax.ppermute(tail, axis, [(i, (i + 1) % count) for i in range(ends)]),
                cells,
                lax.ppermute(head, axis, [((i + 1) % count, i) for i in range(ends)]),
            ],
            axis=dim,
        )
    return cells


def take_rows(source_array, index_array):
    return jax.vmap(lambda table, picked: table[picked])(source_array, index_array)


def conv_apply(padded, weight, length):
    total = jnp.einsum(
        "mbi,oi->mbo", padded[:, 0:length], weight[0], preferred_element_type=jnp.float32
    )
    for offset in range(1, weight.shape[0]):
        total = total + jnp.einsum(
            "mbi,oi->mbo",
            padded[:, offset : offset + length],
            weight[offset],
            preferred_element_type=jnp.float32,
        )
    return total


def weight_term(padded, dconv, length, taps):
    return jnp.stack(
        [
            jnp.einsum(
                "mbi,mbo->oi",
                padded[:, offset : offset + length],
                dconv,
                preferred_element_type=jnp.float32,
            )
            for offset in range(taps)
        ]
    )


def dense_path(features, conv_weight, keep, tiles, counts, targets):
    members, length, width = features.shape
    taps = conv_weight.shape[0]
    narrow = conv_weight.shape[1]
    seq_count = lax.axis_size("seq")
    my_index = lax.axis_index("seq")
    my_part = lax.axis_index("mp")
    x_float = features.astype(jnp.float32)
    activations = jax.nn.gelu(x_float).astype(jnp.bfloat16)
    padded = extended(activations, (("seq", 1),), 2)
    scaling = 1.25 * keep.astype(jnp.float32)
    conv_out = conv_apply(padded, conv_weight, length)
    x_local = lax.dynamic_slice_in_dim(x_float, my_part * narrow, narrow, 2)
    mixed_out = (x_local + scaling[:, None, None] * conv_out).astype(jnp.bfloat16)
    capacity = tiles.shape[2]
    n_sides = 2 * capacity
    per_block = length // TB
    sides = jnp.concatenate([tiles[..., 0], tiles[..., 1]], axis=-1)
    side_source = sides // per_block
    side_local = sides % per_block
    own_sides = lax.dynamic_index_in_dim(sides, my_index, 1, keepdims=False)
    own_source = own_sides // per_block
    before = jnp.arange(n_sides)[None, :] < jnp.arange(n_sides)[:, None]
    same_source = own_source[:, :, None] == own_source[:, None, :]
    rank_within = jnp.sum(jnp.logical_and(same_source, before[None]), axis=-1)
    slot_index = own_source * PER + rank_within
    held_here = side_source == my_index
    held_order = jnp.cumsum(held_here.astype(jnp.int32), axis=-1) - 1
    picks = jnp.stack(
        [
            jnp.sum(
                jnp.where(jnp.logical_and(held_here, held_order == position), side_local, 0),
                axis=-1,
            )
            for position in range(PER)
        ],
        axis=-1,
    )
    blocks = mixed_out.reshape(members, per_block, TB, narrow)
    whole = lax.all_gather(blocks, "seq", axis=1, tiled=True)
    side_rows = take_rows(whole, own_sides)
    row_side = side_rows[:, :capacity]
    col_side = side_rows[:, capacity:]
    partial_tiles = jnp.einsum(
        "mcid,mcjd->mcij", row_side, col_side, preferred_element_type=jnp.float32
    )
    predicted = lax.psum(partial_tiles, "mp") / math.sqrt(width)
    target_tiles = targets[:, 0].reshape(members, capacity, TB, TB)
    own_count = lax.dynamic_index_in_dim(counts, my_index, 1, keepdims=False)
    live_mask = (jnp.arange(capacity)[None, :] < own_count[:, None]).astype(jnp.float32)
    n_live = jnp.sum(counts, axis=-1).astype(jnp.float32)
    dpredicted = (
        2.0
        / math.sqrt(width)
        * live_mask[:, :, None, None]
        * (predicted - target_tiles)
        / n_live[:, None, None, None]
    )
    row_float = row_side.astype(jnp.float32)
    col_float = col_side.astype(jnp.float32)
    drow = jnp.einsum("mcij,mcjd->mcid", dpredicted, col_float, precision=lax.Precision.HIGHEST)
    dcol = jnp.einsum("mcij,mcid->mcjd", dpredicted, row_float, precision=lax.Precision.HIGHEST)
    dside = jnp.concatenate([drow, dcol], axis=1).astype(jnp.bfloat16)
    inverse = jnp.argsort(slot_index, axis=-1)
    outgoing_grads = take_rows(dside, inverse).reshape(members, seq_count, PER, TB, narrow)
    returned = lax.all_to_all(outgoing_grads, "seq", split_axis=1, concat_axis=1, tiled=True)
    selector = (
        picks.reshape(members, seq_count * PER)[:, :, None] == jnp.arange(per_block)[None, None, :]
    ).astype(jnp.bfloat16)
    dmixed = jnp.einsum(
        "mkn,mktd->mntd",
        selector,
        returned.reshape(members, seq_count * PER, TB, narrow),
        preferred_element_type=jnp.float32,
    ).reshape(members, length, narrow)
    dconv = (scaling[:, None, None] * dmixed).astype(jnp.bfloat16)
    weight_local = weight_term(padded, dconv, length, taps)
    return lax.psum_scatter(weight_local, ("seq", "dp"), scatter_dimension=2, tiled=True)


def axis_sum(value, axis):
    count = lax.axis_size(axis)
    total = value
    for shift in range(1, count):
        total = total + lax.ppermute(value, axis, [(i, (i + shift) % count) for i in range(count)])
    return total


def sparse_path(features, conv_weight, keep, tiles, counts, targets):
    _, length, width = features.shape
    taps, narrow, _ = conv_weight.shape
    halo = taps // 2
    span = TB + 2 * halo
    owners, capacity = tiles.shape[1], tiles.shape[2]
    n_sides = 2 * capacity
    per_block = length // TB
    seq_count = lax.axis_size("seq")
    groups = lax.axis_size("dp")
    peers = seq_count * groups
    held = owners * PER
    cols = width // peers
    my_index = lax.axis_index("seq")
    my_part = lax.axis_index("mp")

    before = jnp.arange(n_sides)[None, :] < jnp.arange(n_sides)[:, None]
    own_sides = jnp.concatenate([tiles[0, ..., 0], tiles[0, ..., 1]], axis=-1)
    own_source = own_sides // per_block
    own_same = own_source[:, :, None] == own_source[:, None, :]
    own_rank = jnp.sum(jnp.logical_and(own_same, before), axis=-1)
    held_here = own_source == my_index
    picks = jnp.stack(
        [
            jnp.sum(jnp.where(jnp.logical_and(held_here, own_rank == r), own_sides % per_block, 0), axis=-1)
            for r in range(PER)
        ],
        axis=-1,
    ).reshape(held)

    cells = features[0]
    ends = seq_count - 1
    if seq_count == 2:
        swapped = lax.ppermute(
            jnp.concatenate([cells[length - halo :], cells[:halo]]), "seq", [(0, 1), (1, 0)]
        )
        head = jnp.where(my_index == 0, jnp.zeros_like(swapped[:halo]), swapped[:halo])
        tail = jnp.where(my_index == ends, jnp.zeros_like(swapped[halo:]), swapped[halo:])
    else:
        head = lax.ppermute(cells[length - halo :], "seq", [(i, i + 1) for i in range(ends)])
        tail = lax.ppermute(cells[:halo], "seq", [(i + 1, i) for i in range(ends)])
    last = per_block - 1
    stacked = cells.reshape(per_block, TB * width)
    block_ids = jnp.arange(per_block)[None, :]

    def select(offset, part):
        choose = (picks[:, None] + offset == block_ids).astype(cells.dtype)
        return jnp.dot(choose, part, preferred_element_type=jnp.float32)

    middle = select(0, stacked).reshape(held, TB, width)
    prev_tail = select(-1, stacked[:, (TB - halo) * width :]).reshape(held, halo, width)
    next_head = select(1, stacked[:, : halo * width]).reshape(held, halo, width)
    lower = jnp.where((picks == 0)[:, None, None], head[None].astype(jnp.float32), prev_tail)
    upper = jnp.where((picks == last)[:, None, None], tail[None].astype(jnp.float32), next_head)
    windows = jnp.concatenate([lower, middle, upper], axis=1).astype(cells.dtype)
    x_float = windows.astype(jnp.float32)
    act = jax.nn.gelu(x_float).astype(jnp.bfloat16)
    conv_out = jnp.einsum("hti,oi->hto", act[:, 0:TB], conv_weight[0], preferred_element_type=jnp.float32)
    for offset in range(1, taps):
        conv_out = conv_out + jnp.einsum(
            "hti,oi->hto", act[:, offset : offset + TB], conv_weight[offset], preferred_element_type=jnp.float32
        )
    my_scale = 1.25 * keep[0].astype(jnp.float32)
    x_part = lax.dynamic_slice_in_dim(x_float[:, halo : halo + TB], my_part * narrow, narrow, 2)
    mixed = (x_part + my_scale * conv_out).astype(jnp.bfloat16)

    def lanes(part):
        flat = part.reshape(part.shape[0], -1)
        flat = jnp.pad(flat, ((0, 0), (0, -flat.shape[1] % 128)))
        return flat.reshape(flat.shape[0], -1, 128)

    act_cut = lanes(act.reshape(held, span, peers, cols).transpose(2, 0, 1, 3))
    mixed_part = lanes(mixed.reshape(1, -1))
    wide = targets.reshape(-1)
    pieces = []
    for _ in range(3):
        piece = lax.reduce_precision(wide, exponent_bits=8, mantissa_bits=7)
        pieces.append(piece)
        wide = wide - piece
    own_slot = (own_source * groups + lax.axis_index("dp")) * held + jnp.arange(owners)[:, None] * PER + own_rank
    small = jnp.concatenate(
        [tiles.reshape(-1), counts.reshape(-1), keep.reshape(-1), own_slot.reshape(-1)]
    ).astype(jnp.float32)
    meta_part = lanes(jnp.concatenate(pieces + [small]).astype(jnp.bfloat16).reshape(1, -1))
    rows_mixed, rows_act, rows_meta = mixed_part.shape[1], act_cut.shape[1], meta_part.shape[1]
    outgoing = jnp.concatenate(
        [
            jnp.zeros((peers, rows_mixed, 128), jnp.bfloat16),
            act_cut,
            jnp.broadcast_to(meta_part, (peers, rows_meta, 128)),
        ],
        axis=1,
    )
    outgoing = jnp.pad(outgoing, ((0, 0), (0, -outgoing.shape[1] % 16), (0, 0)))
    outgoing = lax.dynamic_update_slice_in_dim(
        outgoing, jnp.broadcast_to(mixed_part, (peers, rows_mixed, 128)), 0, axis=1
    )
    incoming = lax.all_to_all(outgoing, ("seq", "dp"), 0, 0, tiled=True)
    n_mixed = held * TB * narrow
    n_act = held * span * cols
    mixed_in = incoming[:, :rows_mixed].reshape(peers, -1)[:, :n_mixed].reshape(peers * held, TB, narrow)
    act_in = incoming[:, rows_mixed : rows_mixed + rows_act].reshape(peers, -1)[:, :n_act]
    act_in = act_in.reshape(peers * held, span, cols)
    meta_in = incoming[:, rows_mixed + rows_act : rows_mixed + rows_act + rows_meta].reshape(peers, -1)
    meta_in = meta_in.astype(jnp.float32).reshape(seq_count, groups, -1)
    n_targets = capacity * TB * TB
    n_tiles = owners * capacity * 2
    targets_all = meta_in[:, :, :n_targets] + meta_in[:, :, n_targets : 2 * n_targets]
    targets_all = targets_all + meta_in[:, :, 2 * n_targets : 3 * n_targets]
    ints = meta_in[0, :, 3 * n_targets :].astype(jnp.int32)
    tiles_all = ints[:, :n_tiles].reshape(groups, owners, capacity, 2)
    counts_all = ints[:, n_tiles : n_tiles + owners]
    keep_all = ints[:, n_tiles + owners]
    slot = ints[:, n_tiles + owners + 1 : n_tiles + owners + 1 + owners * n_sides].reshape(groups, owners, n_sides)

    sides = jnp.concatenate([tiles_all[..., 0], tiles_all[..., 1]], axis=-1)

    pick_slot = (slot[..., None] == jnp.arange(peers * held)).astype(jnp.bfloat16)
    side_rows = jnp.dot(
        pick_slot.reshape(-1, peers * held), mixed_in.reshape(peers * held, -1), preferred_element_type=jnp.float32
    ).astype(jnp.bfloat16).reshape(slot.shape + (TB, narrow))
    row_side = side_rows[:, :, :capacity]
    col_side = side_rows[:, :, capacity:]
    partial_tiles = jnp.einsum("qocid,qocjd->qocij", row_side, col_side, preferred_element_type=jnp.float32)
    lanes_shape = partial_tiles.shape
    summed = axis_sum(partial_tiles.reshape(-1, 128), "mp").reshape(lanes_shape)
    predicted = summed / math.sqrt(width)
    target_tiles = targets_all.reshape(seq_count, groups, capacity, TB, TB).transpose(1, 0, 2, 3, 4)
    live_mask = (jnp.arange(capacity)[None, None, :] < counts_all[:, :, None]).astype(jnp.float32)
    n_live = jnp.sum(counts_all, axis=-1).astype(jnp.float32)
    dpredicted = (
        2.0
        / math.sqrt(width)
        * live_mask[..., None, None]
        * (predicted - target_tiles)
        / n_live[:, None, None, None, None]
    )
    row_float = row_side.astype(jnp.float32)
    col_float = col_side.astype(jnp.float32)
    drow = jnp.einsum("qocij,qocjd->qocid", dpredicted, col_float, precision=lax.Precision.HIGHEST)
    dcol = jnp.einsum("qocij,qocid->qocjd", dpredicted, row_float, precision=lax.Precision.HIGHEST)
    grads = jnp.concatenate([drow, dcol], axis=2).astype(jnp.bfloat16).astype(jnp.float32)
    grads = grads.reshape(groups, owners * n_sides, TB, narrow)
    flat_sides = sides.reshape(groups, owners * n_sides)
    same_block = flat_sides[:, :, None] == flat_sides[:, None, :]
    total = jnp.einsum(
        "qab,qbtd->qatd", same_block.astype(jnp.float32), grads, precision=lax.Precision.HIGHEST
    )
    earlier = jnp.arange(owners * n_sides)[None, :] < jnp.arange(owners * n_sides)[:, None]
    first = jnp.logical_not(jnp.any(jnp.logical_and(same_block, earlier[None]), axis=-1))
    scaling = 1.25 * keep_all.astype(jnp.float32)
    dconv = (scaling[:, None, None, None] * total).astype(jnp.bfloat16)
    dconv = jnp.where(first[..., None, None], dconv, jnp.zeros_like(dconv))
    act_sides = jnp.take(act_in, slot.reshape(groups, owners * n_sides), axis=0)
    return jnp.stack(
        [
            jnp.einsum(
                "qato,qati->oi",
                dconv,
                act_sides[:, :, offset : offset + TB],
                preferred_element_type=jnp.float32,
            )
            for offset in range(taps)
        ]
    )


def per_device(features, conv_weight, keep, tiles, counts, targets):
    members, length, _ = features.shape
    owners, capacity = tiles.shape[1], tiles.shape[2]
    blocks = lax.axis_size("seq") * length // TB
    fits = members == 1 and targets.shape[1] == 1 and 2 * owners * capacity * TB <= length
    fits = fits and blocks <= 256 and capacity <= 256
    if fits:
        return sparse_path(features, conv_weight, keep, tiles, counts, targets)
    return dense_path(features, conv_weight, keep, tiles, counts, targets)


def solution(mesh):
    placed = (
        P("dp", "seq", None),
        P(None, "mp", None),
        P("dp"),
        P("dp", None, None, None),
        P("dp", None),
        P("dp", "seq", None, None),
    )
    return jax.shard_map(
        per_device,
        mesh=mesh,
        in_specs=placed,
        out_specs=P(None, "mp", ("seq", "dp")),
        check_vma=False,
    )
```

```python
import math

import jax
import jax.numpy as jnp
from jax import lax
from jax.sharding import PartitionSpec as P

TB = 32
PER = 2


def extended(cells, sides, width):
    for axis, dim in sides:
        count = lax.axis_size(axis)
        ends = count - 1
        head = lax.slice_in_dim(cells, 0, width, axis=dim)
        tail = lax.slice_in_dim(cells, cells.shape[dim] - width, cells.shape[dim], axis=dim)
        cells = jnp.concatenate(
            [
                lax.ppermute(tail, axis, [(i, (i + 1) % count) for i in range(ends)]),
                cells,
                lax.ppermute(head, axis, [((i + 1) % count, i) for i in range(ends)]),
            ],
            axis=dim,
        )
    return cells


def take_rows(source_array, index_array):
    return jax.vmap(lambda table, picked: table[picked])(source_array, index_array)


def conv_apply(padded, weight, length):
    total = jnp.einsum(
        "mbi,oi->mbo", padded[:, 0:length], weight[0], preferred_element_type=jnp.float32
    )
    for offset in range(1, weight.shape[0]):
        total = total + jnp.einsum(
            "mbi,oi->mbo",
            padded[:, offset : offset + length],
            weight[offset],
            preferred_element_type=jnp.float32,
        )
    return total


def weight_term(padded, dconv, length, taps):
    return jnp.stack(
        [
            jnp.einsum(
                "mbi,mbo->oi",
                padded[:, offset : offset + length],
                dconv,
                preferred_element_type=jnp.float32,
            )
            for offset in range(taps)
        ]
    )


def dense_path(features, conv_weight, keep, tiles, counts, targets):
    members, length, width = features.shape
    taps = conv_weight.shape[0]
    narrow = conv_weight.shape[1]
    seq_count = lax.axis_size("seq")
    my_index = lax.axis_index("seq")
    my_part = lax.axis_index("mp")
    x_float = features.astype(jnp.float32)
    activations = jax.nn.gelu(x_float).astype(jnp.bfloat16)
    padded = extended(activations, (("seq", 1),), 2)
    scaling = 1.25 * keep.astype(jnp.float32)
    conv_out = conv_apply(padded, conv_weight, length)
    x_local = lax.dynamic_slice_in_dim(x_float, my_part * narrow, narrow, 2)
    mixed_out = (x_local + scaling[:, None, None] * conv_out).astype(jnp.bfloat16)
    capacity = tiles.shape[2]
    n_sides = 2 * capacity
    per_block = length // TB
    sides = jnp.concatenate([tiles[..., 0], tiles[..., 1]], axis=-1)
    side_source = sides // per_block
    side_local = sides % per_block
    own_sides = lax.dynamic_index_in_dim(sides, my_index, 1, keepdims=False)
    own_source = own_sides // per_block
    before = jnp.arange(n_sides)[None, :] < jnp.arange(n_sides)[:, None]
    same_source = own_source[:, :, None] == own_source[:, None, :]
    rank_within = jnp.sum(jnp.logical_and(same_source, before[None]), axis=-1)
    slot_index = own_source * PER + rank_within
    held_here = side_source == my_index
    held_order = jnp.cumsum(held_here.astype(jnp.int32), axis=-1) - 1
    picks = jnp.stack(
        [
            jnp.sum(
                jnp.where(jnp.logical_and(held_here, held_order == position), side_local, 0),
                axis=-1,
            )
            for position in range(PER)
        ],
        axis=-1,
    )
    blocks = mixed_out.reshape(members, per_block, TB, narrow)
    whole = lax.all_gather(blocks, "seq", axis=1, tiled=True)
    side_rows = take_rows(whole, own_sides)
    row_side = side_rows[:, :capacity]
    col_side = side_rows[:, capacity:]
    partial_tiles = jnp.einsum(
        "mcid,mcjd->mcij", row_side, col_side, preferred_element_type=jnp.float32
    )
    predicted = lax.psum(partial_tiles, "mp") / math.sqrt(width)
    target_tiles = targets[:, 0].reshape(members, capacity, TB, TB)
    own_count = lax.dynamic_index_in_dim(counts, my_index, 1, keepdims=False)
    live_mask = (jnp.arange(capacity)[None, :] < own_count[:, None]).astype(jnp.float32)
    n_live = jnp.sum(counts, axis=-1).astype(jnp.float32)
    dpredicted = (
        2.0
        / math.sqrt(width)
        * live_mask[:, :, None, None]
        * (predicted - target_tiles)
        / n_live[:, None, None, None]
    )
    row_float = row_side.astype(jnp.float32)
    col_float = col_side.astype(jnp.float32)
    drow = jnp.einsum("mcij,mcjd->mcid", dpredicted, col_float, precision=lax.Precision.HIGHEST)
    dcol = jnp.einsum("mcij,mcid->mcjd", dpredicted, row_float, precision=lax.Precision.HIGHEST)
    dside = jnp.concatenate([drow, dcol], axis=1).astype(jnp.bfloat16)
    inverse = jnp.argsort(slot_index, axis=-1)
    outgoing_grads = take_rows(dside, inverse).reshape(members, seq_count, PER, TB, narrow)
    returned = lax.all_to_all(outgoing_grads, "seq", split_axis=1, concat_axis=1, tiled=True)
    selector = (
        picks.reshape(members, seq_count * PER)[:, :, None] == jnp.arange(per_block)[None, None, :]
    ).astype(jnp.bfloat16)
    dmixed = jnp.einsum(
        "mkn,mktd->mntd",
        selector,
        returned.reshape(members, seq_count * PER, TB, narrow),
        preferred_element_type=jnp.float32,
    ).reshape(members, length, narrow)
    dconv = (scaling[:, None, None] * dmixed).astype(jnp.bfloat16)
    weight_local = weight_term(padded, dconv, length, taps)
    return lax.psum_scatter(weight_local, ("seq", "dp"), scatter_dimension=2, tiled=True)


def axis_sum(value, axis):
    count = lax.axis_size(axis)
    total = value
    for shift in range(1, count):
        total = total + lax.ppermute(value, axis, [(i, (i + shift) % count) for i in range(count)])
    return total


def sparse_path(features, conv_weight, keep, tiles, counts, targets):
    _, length, width = features.shape
    taps, narrow, _ = conv_weight.shape
    halo = taps // 2
    span = TB + 2 * halo
    owners, capacity = tiles.shape[1], tiles.shape[2]
    n_sides = 2 * capacity
    per_block = length // TB
    seq_count = lax.axis_size("seq")
    groups = lax.axis_size("dp")
    peers = seq_count * groups
    held = owners * PER
    cols = width // peers
    my_index = lax.axis_index("seq")
    my_part = lax.axis_index("mp")

    before = jnp.arange(n_sides)[None, :] < jnp.arange(n_sides)[:, None]
    own_sides = jnp.concatenate([tiles[0, ..., 0], tiles[0, ..., 1]], axis=-1)
    own_source = own_sides // per_block
    own_same = own_source[:, :, None] == own_source[:, None, :]
    own_rank = jnp.sum(jnp.logical_and(own_same, before), axis=-1)
    held_here = own_source == my_index
    picks = jnp.stack(
        [
            jnp.sum(jnp.where(jnp.logical_and(held_here, own_rank == r), own_sides % per_block, 0), axis=-1)
            for r in range(PER)
        ],
        axis=-1,
    ).reshape(held)

    cells = features[0]
    ends = seq_count - 1
    if seq_count == 2:
        swapped = lax.ppermute(
            jnp.concatenate([cells[length - halo :], cells[:halo]]), "seq", [(0, 1), (1, 0)]
        )
        head = jnp.where(my_index == 0, jnp.zeros_like(swapped[:halo]), swapped[:halo])
        tail = jnp.where(my_index == ends, jnp.zeros_like(swapped[halo:]), swapped[halo:])
    else:
        head = lax.ppermute(cells[length - halo :], "seq", [(i, i + 1) for i in range(ends)])
        tail = lax.ppermute(cells[:halo], "seq", [(i + 1, i) for i in range(ends)])
    last = per_block - 1
    stacked = cells.reshape(per_block, TB * width)
    block_ids = jnp.arange(per_block)[None, :]

    def select(offset, part):
        choose = (picks[:, None] + offset == block_ids).astype(cells.dtype)
        return jnp.dot(choose, part, preferred_element_type=jnp.float32)

    middle = select(0, stacked).reshape(held, TB, width)
    prev_tail = select(-1, stacked[:, (TB - halo) * width :]).reshape(held, halo, width)
    next_head = select(1, stacked[:, : halo * width]).reshape(held, halo, width)
    lower = jnp.where((picks == 0)[:, None, None], head[None].astype(jnp.float32), prev_tail)
    upper = jnp.where((picks == last)[:, None, None], tail[None].astype(jnp.float32), next_head)
    windows = jnp.concatenate([lower, middle, upper], axis=1).astype(cells.dtype)
    x_float = windows.astype(jnp.float32)
    act = jax.nn.gelu(x_float).astype(jnp.bfloat16)
    conv_out = jnp.einsum("hti,oi->hto", act[:, 0:TB], conv_weight[0], preferred_element_type=jnp.float32)
    for offset in range(1, taps):
        conv_out = conv_out + jnp.einsum(
            "hti,oi->hto", act[:, offset : offset + TB], conv_weight[offset], preferred_element_type=jnp.float32
        )
    my_scale = 1.25 * keep[0].astype(jnp.float32)
    x_part = lax.dynamic_slice_in_dim(x_float[:, halo : halo + TB], my_part * narrow, narrow, 2)
    mixed = (x_part + my_scale * conv_out).astype(jnp.bfloat16)

    def lanes(part):
        flat = part.reshape(part.shape[0], -1)
        flat = jnp.pad(flat, ((0, 0), (0, -flat.shape[1] % 128)))
        return flat.reshape(flat.shape[0], -1, 128)

    act_cut = lanes(act.reshape(held, span, peers, cols).transpose(2, 0, 1, 3))
    mixed_part = lanes(mixed.reshape(1, -1))
    wide = targets.reshape(-1)
    pieces = []
    for _ in range(3):
        piece = lax.reduce_precision(wide, exponent_bits=8, mantissa_bits=7)
        pieces.append(piece)
        wide = wide - piece
    own_slot = (own_source * groups + lax.axis_index("dp")) * held + jnp.arange(owners)[:, None] * PER + own_rank
    small = jnp.concatenate(
        [tiles.reshape(-1), counts.reshape(-1), keep.reshape(-1), own_slot.reshape(-1)]
    ).astype(jnp.float32)
    meta_part = lanes(jnp.concatenate(pieces + [small]).astype(jnp.bfloat16).reshape(1, -1))
    rows_mixed, rows_act, rows_meta = mixed_part.shape[1], act_cut.shape[1], meta_part.shape[1]
    outgoing = jnp.concatenate(
        [
            jnp.broadcast_to(mixed_part, (peers, rows_mixed, 128)),
            act_cut,
            jnp.broadcast_to(meta_part, (peers, rows_meta, 128)),
        ],
        axis=1,
    )
    outgoing = jnp.pad(outgoing, ((0, 0), (0, -outgoing.shape[1] % 16), (0, 0)))
    incoming = lax.all_to_all(outgoing, ("seq", "dp"), 0, 0, tiled=True)
    n_mixed = held * TB * narrow
    n_act = held * span * cols
    mixed_in = incoming[:, :rows_mixed].reshape(peers, -1)[:, :n_mixed].reshape(peers * held, TB, narrow)
    act_in = incoming[:, rows_mixed : rows_mixed + rows_act].reshape(peers, -1)[:, :n_act]
    act_in = act_in.reshape(peers * held, span, cols)
    meta_in = incoming[:, rows_mixed + rows_act : rows_mixed + rows_act + rows_meta].reshape(peers, -1)
    meta_in = meta_in.astype(jnp.float32).reshape(seq_count, groups, -1)
    n_targets = capacity * TB * TB
    n_tiles = owners * capacity * 2
    targets_all = meta_in[:, :, :n_targets] + meta_in[:, :, n_targets : 2 * n_targets]
    targets_all = targets_all + meta_in[:, :, 2 * n_targets : 3 * n_targets]
    ints = meta_in[0, :, 3 * n_targets :].astype(jnp.int32)
    tiles_all = ints[:, :n_tiles].reshape(groups, owners, capacity, 2)
    counts_all = ints[:, n_tiles : n_tiles + owners]
    keep_all = ints[:, n_tiles + owners]
    slot = ints[:, n_tiles + owners + 1 : n_tiles + owners + 1 + owners * n_sides].reshape(groups, owners, n_sides)

    sides = jnp.concatenate([tiles_all[..., 0], tiles_all[..., 1]], axis=-1)

    pick_slot = (slot[..., None] == jnp.arange(peers * held)).astype(jnp.bfloat16)
    side_rows = jnp.dot(
        pick_slot.reshape(-1, peers * held), mixed_in.reshape(peers * held, -1), preferred_element_type=jnp.float32
    ).astype(jnp.bfloat16).reshape(slot.shape + (TB, narrow))
    row_side = side_rows[:, :, :capacity]
    col_side = side_rows[:, :, capacity:]
    partial_tiles = jnp.einsum("qocid,qocjd->qocij", row_side, col_side, preferred_element_type=jnp.float32)
    lanes_shape = partial_tiles.shape
    summed = axis_sum(partial_tiles.reshape(-1, 128), "mp").reshape(lanes_shape)
    predicted = summed / math.sqrt(width)
    target_tiles = targets_all.reshape(seq_count, groups, capacity, TB, TB).transpose(1, 0, 2, 3, 4)
    live_mask = (jnp.arange(capacity)[None, None, :] < counts_all[:, :, None]).astype(jnp.float32)
    n_live = jnp.sum(counts_all, axis=-1).astype(jnp.float32)
    dpredicted = (
        2.0
        / math.sqrt(width)
        * live_mask[..., None, None]
        * (predicted - target_tiles)
        / n_live[:, None, None, None, None]
    )
    row_float = row_side.astype(jnp.float32)
    col_float = col_side.astype(jnp.float32)
    drow = jnp.einsum("qocij,qocjd->qocid", dpredicted, col_float, precision=lax.Precision.HIGHEST)
    dcol = jnp.einsum("qocij,qocid->qocjd", dpredicted, row_float, precision=lax.Precision.HIGHEST)
    grads = jnp.concatenate([drow, dcol], axis=2).astype(jnp.bfloat16).astype(jnp.float32)
    grads = grads.reshape(groups, owners * n_sides, TB, narrow)
    flat_sides = sides.reshape(groups, owners * n_sides)
    same_block = flat_sides[:, :, None] == flat_sides[:, None, :]
    total = jnp.einsum(
        "qab,qbtd->qatd",
        same_block.astype(jnp.bfloat16),
        grads.astype(jnp.bfloat16),
        preferred_element_type=jnp.float32,
    )
    earlier = jnp.arange(owners * n_sides)[None, :] < jnp.arange(owners * n_sides)[:, None]
    first = jnp.logical_not(jnp.any(jnp.logical_and(same_block, earlier[None]), axis=-1))
    scaling = 1.25 * keep_all.astype(jnp.float32)
    dconv = (scaling[:, None, None, None] * total).astype(jnp.bfloat16)
    dconv = jnp.where(first[..., None, None], dconv, jnp.zeros_like(dconv))
    act_sides = jnp.take(act_in, slot.reshape(groups, owners * n_sides), axis=0)
    return jnp.stack(
        [
            jnp.einsum(
                "qato,qati->oi",
                dconv,
                act_sides[:, :, offset : offset + TB],
                preferred_element_type=jnp.float32,
            )
            for offset in range(taps)
        ]
    )


def per_device(features, conv_weight, keep, tiles, counts, targets):
    members, length, _ = features.shape
    owners, capacity = tiles.shape[1], tiles.shape[2]
    blocks = lax.axis_size("seq") * length // TB
    fits = members == 1 and targets.shape[1] == 1 and 2 * owners * capacity * TB <= length
    fits = fits and blocks <= 256 and capacity <= 256
    if fits:
        return sparse_path(features, conv_weight, keep, tiles, counts, targets)
    return dense_path(features, conv_weight, keep, tiles, counts, targets)


def solution(mesh):
    placed = (
        P("dp", "seq", None),
        P(None, "mp", None),
        P("dp"),
        P("dp", None, None, None),
        P("dp", None),
        P("dp", "seq", None, None),
    )
    return jax.shard_map(
        per_device,
        mesh=mesh,
        in_specs=placed,
        out_specs=P(None, "mp", ("seq", "dp")),
        check_vma=False,
    )
```

```python
import math

import jax
import jax.numpy as jnp
from jax import lax
from jax.sharding import PartitionSpec as P

TB = 32
PER = 2


def extended(cells, sides, width):
    for axis, dim in sides:
        count = lax.axis_size(axis)
        ends = count - 1
        head = lax.slice_in_dim(cells, 0, width, axis=dim)
        tail = lax.slice_in_dim(cells, cells.shape[dim] - width, cells.shape[dim], axis=dim)
        cells = jnp.concatenate(
            [
                lax.ppermute(tail, axis, [(i, (i + 1) % count) for i in range(ends)]),
                cells,
                lax.ppermute(head, axis, [((i + 1) % count, i) for i in range(ends)]),
            ],
            axis=dim,
        )
    return cells


def take_rows(source_array, index_array):
    return jax.vmap(lambda table, picked: table[picked])(source_array, index_array)


def conv_apply(padded, weight, length):
    total = jnp.einsum(
        "mbi,oi->mbo", padded[:, 0:length], weight[0], preferred_element_type=jnp.float32
    )
    for offset in range(1, weight.shape[0]):
        total = total + jnp.einsum(
            "mbi,oi->mbo",
            padded[:, offset : offset + length],
            weight[offset],
            preferred_element_type=jnp.float32,
        )
    return total


def weight_term(padded, dconv, length, taps):
    return jnp.stack(
        [
            jnp.einsum(
                "mbi,mbo->oi",
                padded[:, offset : offset + length],
                dconv,
                preferred_element_type=jnp.float32,
            )
            for offset in range(taps)
        ]
    )


def dense_path(features, conv_weight, keep, tiles, counts, targets):
    members, length, width = features.shape
    taps = conv_weight.shape[0]
    narrow = conv_weight.shape[1]
    seq_count = lax.axis_size("seq")
    my_index = lax.axis_index("seq")
    my_part = lax.axis_index("mp")
    x_float = features.astype(jnp.float32)
    activations = jax.nn.gelu(x_float).astype(jnp.bfloat16)
    padded = extended(activations, (("seq", 1),), 2)
    scaling = 1.25 * keep.astype(jnp.float32)
    conv_out = conv_apply(padded, conv_weight, length)
    x_local = lax.dynamic_slice_in_dim(x_float, my_part * narrow, narrow, 2)
    mixed_out = (x_local + scaling[:, None, None] * conv_out).astype(jnp.bfloat16)
    capacity = tiles.shape[2]
    n_sides = 2 * capacity
    per_block = length // TB
    sides = jnp.concatenate([tiles[..., 0], tiles[..., 1]], axis=-1)
    side_source = sides // per_block
    side_local = sides % per_block
    own_sides = lax.dynamic_index_in_dim(sides, my_index, 1, keepdims=False)
    own_source = own_sides // per_block
    before = jnp.arange(n_sides)[None, :] < jnp.arange(n_sides)[:, None]
    same_source = own_source[:, :, None] == own_source[:, None, :]
    rank_within = jnp.sum(jnp.logical_and(same_source, before[None]), axis=-1)
    slot_index = own_source * PER + rank_within
    held_here = side_source == my_index
    held_order = jnp.cumsum(held_here.astype(jnp.int32), axis=-1) - 1
    picks = jnp.stack(
        [
            jnp.sum(
                jnp.where(jnp.logical_and(held_here, held_order == position), side_local, 0),
                axis=-1,
            )
            for position in range(PER)
        ],
        axis=-1,
    )
    blocks = mixed_out.reshape(members, per_block, TB, narrow)
    whole = lax.all_gather(blocks, "seq", axis=1, tiled=True)
    side_rows = take_rows(whole, own_sides)
    row_side = side_rows[:, :capacity]
    col_side = side_rows[:, capacity:]
    partial_tiles = jnp.einsum(
        "mcid,mcjd->mcij", row_side, col_side, preferred_element_type=jnp.float32
    )
    predicted = lax.psum(partial_tiles, "mp") / math.sqrt(width)
    target_tiles = targets[:, 0].reshape(members, capacity, TB, TB)
    own_count = lax.dynamic_index_in_dim(counts, my_index, 1, keepdims=False)
    live_mask = (jnp.arange(capacity)[None, :] < own_count[:, None]).astype(jnp.float32)
    n_live = jnp.sum(counts, axis=-1).astype(jnp.float32)
    dpredicted = (
        2.0
        / math.sqrt(width)
        * live_mask[:, :, None, None]
        * (predicted - target_tiles)
        / n_live[:, None, None, None]
    )
    row_float = row_side.astype(jnp.float32)
    col_float = col_side.astype(jnp.float32)
    drow = jnp.einsum("mcij,mcjd->mcid", dpredicted, col_float, precision=lax.Precision.HIGHEST)
    dcol = jnp.einsum("mcij,mcid->mcjd", dpredicted, row_float, precision=lax.Precision.HIGHEST)
    dside = jnp.concatenate([drow, dcol], axis=1).astype(jnp.bfloat16)
    inverse = jnp.argsort(slot_index, axis=-1)
    outgoing_grads = take_rows(dside, inverse).reshape(members, seq_count, PER, TB, narrow)
    returned = lax.all_to_all(outgoing_grads, "seq", split_axis=1, concat_axis=1, tiled=True)
    selector = (
        picks.reshape(members, seq_count * PER)[:, :, None] == jnp.arange(per_block)[None, None, :]
    ).astype(jnp.bfloat16)
    dmixed = jnp.einsum(
        "mkn,mktd->mntd",
        selector,
        returned.reshape(members, seq_count * PER, TB, narrow),
        preferred_element_type=jnp.float32,
    ).reshape(members, length, narrow)
    dconv = (scaling[:, None, None] * dmixed).astype(jnp.bfloat16)
    weight_local = weight_term(padded, dconv, length, taps)
    return lax.psum_scatter(weight_local, ("seq", "dp"), scatter_dimension=2, tiled=True)


def axis_sum(value, axis):
    count = lax.axis_size(axis)
    total = value
    for shift in range(1, count):
        total = total + lax.ppermute(value, axis, [(i, (i + shift) % count) for i in range(count)])
    return total


def sparse_path(features, conv_weight, keep, tiles, counts, targets):
    _, length, width = features.shape
    taps, narrow, _ = conv_weight.shape
    halo = taps // 2
    span = TB + 2 * halo
    owners, capacity = tiles.shape[1], tiles.shape[2]
    n_sides = 2 * capacity
    per_block = length // TB
    seq_count = lax.axis_size("seq")
    groups = lax.axis_size("dp")
    peers = seq_count * groups
    held = owners * PER
    cols = width // peers
    my_index = lax.axis_index("seq")
    my_part = lax.axis_index("mp")

    before = jnp.arange(n_sides)[None, :] < jnp.arange(n_sides)[:, None]
    own_sides = jnp.concatenate([tiles[0, ..., 0], tiles[0, ..., 1]], axis=-1)
    own_source = own_sides // per_block
    own_same = own_source[:, :, None] == own_source[:, None, :]
    own_rank = jnp.sum(jnp.logical_and(own_same, before), axis=-1)
    held_here = own_source == my_index
    picks = jnp.stack(
        [
            jnp.sum(jnp.where(jnp.logical_and(held_here, own_rank == r), own_sides % per_block, 0), axis=-1)
            for r in range(PER)
        ],
        axis=-1,
    ).reshape(held)

    cells = features[0]
    ends = seq_count - 1
    if seq_count == 2:
        swapped = lax.ppermute(
            jnp.concatenate([cells[length - halo :], cells[:halo]]), "seq", [(0, 1), (1, 0)]
        )
        head = jnp.where(my_index == 0, jnp.zeros_like(swapped[:halo]), swapped[:halo])
        tail = jnp.where(my_index == ends, jnp.zeros_like(swapped[halo:]), swapped[halo:])
    else:
        head = lax.ppermute(cells[length - halo :], "seq", [(i, i + 1) for i in range(ends)])
        tail = lax.ppermute(cells[:halo], "seq", [(i + 1, i) for i in range(ends)])
    last = per_block - 1
    stacked = cells.reshape(per_block, TB * width)
    block_ids = jnp.arange(per_block)[None, :]

    def select(offset, part):
        choose = (picks[:, None] + offset == block_ids).astype(cells.dtype)
        return jnp.dot(choose, part, preferred_element_type=jnp.float32)

    middle = select(0, stacked).reshape(held, TB, width)
    prev_tail = select(-1, stacked[:, (TB - halo) * width :]).reshape(held, halo, width)
    next_head = select(1, stacked[:, : halo * width]).reshape(held, halo, width)
    lower = jnp.where((picks == 0)[:, None, None], head[None].astype(jnp.float32), prev_tail)
    upper = jnp.where((picks == last)[:, None, None], tail[None].astype(jnp.float32), next_head)
    windows = jnp.concatenate([lower, middle, upper], axis=1).astype(cells.dtype)
    x_float = windows.astype(jnp.float32)
    act = jax.nn.gelu(x_float).astype(jnp.bfloat16)
    conv_out = jnp.einsum("hti,oi->hto", act[:, 0:TB], conv_weight[0], preferred_element_type=jnp.float32)
    for offset in range(1, taps):
        conv_out = conv_out + jnp.einsum(
            "hti,oi->hto", act[:, offset : offset + TB], conv_weight[offset], preferred_element_type=jnp.float32
        )
    my_scale = 1.25 * keep[0].astype(jnp.float32)
    x_part = lax.dynamic_slice_in_dim(x_float[:, halo : halo + TB], my_part * narrow, narrow, 2)
    mixed = (x_part + my_scale * conv_out).astype(jnp.bfloat16)

    def lanes(part):
        flat = part.reshape(part.shape[0], -1)
        flat = jnp.pad(flat, ((0, 0), (0, -flat.shape[1] % 128)))
        return flat.reshape(flat.shape[0], -1, 128)

    act_cut = lanes(act.reshape(held, span, peers, cols).transpose(2, 0, 1, 3))
    mixed_part = lanes(mixed.reshape(1, -1))
    wide = targets.reshape(-1)
    pieces = []
    for _ in range(3):
        piece = lax.reduce_precision(wide, exponent_bits=8, mantissa_bits=7)
        pieces.append(piece)
        wide = wide - piece
    own_slot = (own_source * groups + lax.axis_index("dp")) * held + jnp.arange(owners)[:, None] * PER + own_rank
    small = jnp.concatenate(
        [tiles.reshape(-1), counts.reshape(-1), keep.reshape(-1), own_slot.reshape(-1)]
    ).astype(jnp.float32)
    meta_part = lanes(jnp.concatenate(pieces + [small]).astype(jnp.bfloat16).reshape(1, -1))
    rows_mixed, rows_act, rows_meta = mixed_part.shape[1], act_cut.shape[1], meta_part.shape[1]
    outgoing = jnp.concatenate(
        [
            jnp.broadcast_to(mixed_part, (peers, rows_mixed, 128)),
            act_cut,
            jnp.broadcast_to(meta_part, (peers, rows_meta, 128)),
        ],
        axis=1,
    )
    outgoing = jnp.pad(outgoing, ((0, 0), (0, -outgoing.shape[1] % 16), (0, 0)))
    incoming = lax.all_to_all(outgoing, ("seq", "dp"), 0, 0, tiled=True)
    n_mixed = held * TB * narrow
    n_act = held * span * cols
    mixed_in = incoming[:, :rows_mixed].reshape(peers, -1)[:, :n_mixed].reshape(peers * held, TB, narrow)
    act_in = incoming[:, rows_mixed : rows_mixed + rows_act].reshape(peers, -1)[:, :n_act]
    act_in = act_in.reshape(peers * held, span, cols)
    meta_in = incoming[:, rows_mixed + rows_act : rows_mixed + rows_act + rows_meta].reshape(peers, -1)
    meta_in = meta_in.astype(jnp.float32).reshape(seq_count, groups, -1)
    n_targets = capacity * TB * TB
    n_tiles = owners * capacity * 2
    targets_all = meta_in[:, :, :n_targets] + meta_in[:, :, n_targets : 2 * n_targets]
    targets_all = targets_all + meta_in[:, :, 2 * n_targets : 3 * n_targets]
    ints = meta_in[0, :, 3 * n_targets :].astype(jnp.int32)
    tiles_all = ints[:, :n_tiles].reshape(groups, owners, capacity, 2)
    counts_all = ints[:, n_tiles : n_tiles + owners]
    keep_all = ints[:, n_tiles + owners]
    slot = ints[:, n_tiles + owners + 1 : n_tiles + owners + 1 + owners * n_sides].reshape(groups, owners, n_sides)

    sides = jnp.concatenate([tiles_all[..., 0], tiles_all[..., 1]], axis=-1)

    pick_slot = (slot[..., None] == jnp.arange(peers * held)).astype(jnp.bfloat16)
    side_rows = jnp.dot(
        pick_slot.reshape(-1, peers * held), mixed_in.reshape(peers * held, -1), preferred_element_type=jnp.float32
    ).astype(jnp.bfloat16).reshape(slot.shape + (TB, narrow))
    row_side = side_rows[:, :, :capacity]
    col_side = side_rows[:, :, capacity:]
    partial_tiles = jnp.einsum("qocid,qocjd->qocij", row_side, col_side, preferred_element_type=jnp.float32)
    lanes_shape = partial_tiles.shape
    summed = axis_sum(partial_tiles.reshape(-1, 128), "mp").reshape(lanes_shape)
    predicted = summed / math.sqrt(width)
    target_tiles = targets_all.reshape(seq_count, groups, capacity, TB, TB).transpose(1, 0, 2, 3, 4)
    live_mask = (jnp.arange(capacity)[None, None, :] < counts_all[:, :, None]).astype(jnp.float32)
    n_live = jnp.sum(counts_all, axis=-1).astype(jnp.float32)
    dpredicted = (
        2.0
        / math.sqrt(width)
        * live_mask[..., None, None]
        * (predicted - target_tiles)
        / n_live[:, None, None, None, None]
    )
    row_float = row_side.astype(jnp.float32)
    col_float = col_side.astype(jnp.float32)
    drow = jnp.einsum("qocij,qocjd->qocid", dpredicted, col_float, precision=lax.Precision.HIGH)
    dcol = jnp.einsum("qocij,qocid->qocjd", dpredicted, row_float, precision=lax.Precision.HIGH)
    grads = jnp.concatenate([drow, dcol], axis=2).astype(jnp.bfloat16).astype(jnp.float32)
    grads = grads.reshape(groups, owners * n_sides, TB, narrow)
    flat_sides = sides.reshape(groups, owners * n_sides)
    same_block = flat_sides[:, :, None] == flat_sides[:, None, :]
    total = jnp.einsum(
        "qab,qbtd->qatd",
        same_block.astype(jnp.bfloat16),
        grads.astype(jnp.bfloat16),
        preferred_element_type=jnp.float32,
    )
    earlier = jnp.arange(owners * n_sides)[None, :] < jnp.arange(owners * n_sides)[:, None]
    first = jnp.logical_not(jnp.any(jnp.logical_and(same_block, earlier[None]), axis=-1))
    scaling = 1.25 * keep_all.astype(jnp.float32)
    dconv = (scaling[:, None, None, None] * total).astype(jnp.bfloat16)
    dconv = jnp.where(first[..., None, None], dconv, jnp.zeros_like(dconv))
    act_sides = jnp.take(act_in, slot.reshape(groups, owners * n_sides), axis=0)
    return jnp.stack(
        [
            jnp.einsum(
                "qato,qati->oi",
                dconv,
                act_sides[:, :, offset : offset + TB],
                preferred_element_type=jnp.float32,
            )
            for offset in range(taps)
        ]
    )


def per_device(features, conv_weight, keep, tiles, counts, targets):
    members, length, _ = features.shape
    owners, capacity = tiles.shape[1], tiles.shape[2]
    blocks = lax.axis_size("seq") * length // TB
    fits = members == 1 and targets.shape[1] == 1 and 2 * owners * capacity * TB <= length
    fits = fits and blocks <= 256 and capacity <= 256
    if fits:
        return sparse_path(features, conv_weight, keep, tiles, counts, targets)
    return dense_path(features, conv_weight, keep, tiles, counts, targets)


def solution(mesh):
    placed = (
        P("dp", "seq", None),
        P(None, "mp", None),
        P("dp"),
        P("dp", None, None, None),
        P("dp", None),
        P("dp", "seq", None, None),
    )
    return jax.shard_map(
        per_device,
        mesh=mesh,
        in_specs=placed,
        out_specs=P(None, "mp", ("seq", "dp")),
        check_vma=False,
    )
```

```python
import math

import jax
import jax.numpy as jnp
from jax import lax
from jax.sharding import PartitionSpec as P

TB = 32
PER = 2


def extended(cells, sides, width):
    for axis, dim in sides:
        count = lax.axis_size(axis)
        ends = count - 1
        head = lax.slice_in_dim(cells, 0, width, axis=dim)
        tail = lax.slice_in_dim(cells, cells.shape[dim] - width, cells.shape[dim], axis=dim)
        cells = jnp.concatenate(
            [
                lax.ppermute(tail, axis, [(i, (i + 1) % count) for i in range(ends)]),
                cells,
                lax.ppermute(head, axis, [((i + 1) % count, i) for i in range(ends)]),
            ],
            axis=dim,
        )
    return cells


def take_rows(source_array, index_array):
    return jax.vmap(lambda table, picked: table[picked])(source_array, index_array)


def conv_apply(padded, weight, length):
    total = jnp.einsum(
        "mbi,oi->mbo", padded[:, 0:length], weight[0], preferred_element_type=jnp.float32
    )
    for offset in range(1, weight.shape[0]):
        total = total + jnp.einsum(
            "mbi,oi->mbo",
            padded[:, offset : offset + length],
            weight[offset],
            preferred_element_type=jnp.float32,
        )
    return total


def weight_term(padded, dconv, length, taps):
    return jnp.stack(
        [
            jnp.einsum(
                "mbi,mbo->oi",
                padded[:, offset : offset + length],
                dconv,
                preferred_element_type=jnp.float32,
            )
            for offset in range(taps)
        ]
    )


def dense_path(features, conv_weight, keep, tiles, counts, targets):
    members, length, width = features.shape
    taps = conv_weight.shape[0]
    narrow = conv_weight.shape[1]
    seq_count = lax.axis_size("seq")
    my_index = lax.axis_index("seq")
    my_part = lax.axis_index("mp")
    x_float = features.astype(jnp.float32)
    activations = jax.nn.gelu(x_float).astype(jnp.bfloat16)
    padded = extended(activations, (("seq", 1),), 2)
    scaling = 1.25 * keep.astype(jnp.float32)
    conv_out = conv_apply(padded, conv_weight, length)
    x_local = lax.dynamic_slice_in_dim(x_float, my_part * narrow, narrow, 2)
    mixed_out = (x_local + scaling[:, None, None] * conv_out).astype(jnp.bfloat16)
    capacity = tiles.shape[2]
    n_sides = 2 * capacity
    per_block = length // TB
    sides = jnp.concatenate([tiles[..., 0], tiles[..., 1]], axis=-1)
    side_source = sides // per_block
    side_local = sides % per_block
    own_sides = lax.dynamic_index_in_dim(sides, my_index, 1, keepdims=False)
    own_source = own_sides // per_block
    before = jnp.arange(n_sides)[None, :] < jnp.arange(n_sides)[:, None]
    same_source = own_source[:, :, None] == own_source[:, None, :]
    rank_within = jnp.sum(jnp.logical_and(same_source, before[None]), axis=-1)
    slot_index = own_source * PER + rank_within
    held_here = side_source == my_index
    held_order = jnp.cumsum(held_here.astype(jnp.int32), axis=-1) - 1
    picks = jnp.stack(
        [
            jnp.sum(
                jnp.where(jnp.logical_and(held_here, held_order == position), side_local, 0),
                axis=-1,
            )
            for position in range(PER)
        ],
        axis=-1,
    )
    blocks = mixed_out.reshape(members, per_block, TB, narrow)
    whole = lax.all_gather(blocks, "seq", axis=1, tiled=True)
    side_rows = take_rows(whole, own_sides)
    row_side = side_rows[:, :capacity]
    col_side = side_rows[:, capacity:]
    partial_tiles = jnp.einsum(
        "mcid,mcjd->mcij", row_side, col_side, preferred_element_type=jnp.float32
    )
    predicted = lax.psum(partial_tiles, "mp") / math.sqrt(width)
    target_tiles = targets[:, 0].reshape(members, capacity, TB, TB)
    own_count = lax.dynamic_index_in_dim(counts, my_index, 1, keepdims=False)
    live_mask = (jnp.arange(capacity)[None, :] < own_count[:, None]).astype(jnp.float32)
    n_live = jnp.sum(counts, axis=-1).astype(jnp.float32)
    dpredicted = (
        2.0
        / math.sqrt(width)
        * live_mask[:, :, None, None]
        * (predicted - target_tiles)
        / n_live[:, None, None, None]
    )
    row_float = row_side.astype(jnp.float32)
    col_float = col_side.astype(jnp.float32)
    drow = jnp.einsum("mcij,mcjd->mcid", dpredicted, col_float, precision=lax.Precision.HIGHEST)
    dcol = jnp.einsum("mcij,mcid->mcjd", dpredicted, row_float, precision=lax.Precision.HIGHEST)
    dside = jnp.concatenate([drow, dcol], axis=1).astype(jnp.bfloat16)
    inverse = jnp.argsort(slot_index, axis=-1)
    outgoing_grads = take_rows(dside, inverse).reshape(members, seq_count, PER, TB, narrow)
    returned = lax.all_to_all(outgoing_grads, "seq", split_axis=1, concat_axis=1, tiled=True)
    selector = (
        picks.reshape(members, seq_count * PER)[:, :, None] == jnp.arange(per_block)[None, None, :]
    ).astype(jnp.bfloat16)
    dmixed = jnp.einsum(
        "mkn,mktd->mntd",
        selector,
        returned.reshape(members, seq_count * PER, TB, narrow),
        preferred_element_type=jnp.float32,
    ).reshape(members, length, narrow)
    dconv = (scaling[:, None, None] * dmixed).astype(jnp.bfloat16)
    weight_local = weight_term(padded, dconv, length, taps)
    return lax.psum_scatter(weight_local, ("seq", "dp"), scatter_dimension=2, tiled=True)


def axis_sum(value, axis):
    count = lax.axis_size(axis)
    total = value
    for shift in range(1, count):
        total = total + lax.ppermute(value, axis, [(i, (i + shift) % count) for i in range(count)])
    return total


def sparse_path(features, conv_weight, keep, tiles, counts, targets):
    _, length, width = features.shape
    taps, narrow, _ = conv_weight.shape
    halo = taps // 2
    span = TB + 2 * halo
    owners, capacity = tiles.shape[1], tiles.shape[2]
    n_sides = 2 * capacity
    per_block = length // TB
    seq_count = lax.axis_size("seq")
    groups = lax.axis_size("dp")
    peers = seq_count * groups
    held = owners * PER
    cols = width // peers
    my_index = lax.axis_index("seq")
    my_part = lax.axis_index("mp")

    before = jnp.arange(n_sides)[None, :] < jnp.arange(n_sides)[:, None]
    own_sides = jnp.concatenate([tiles[0, ..., 0], tiles[0, ..., 1]], axis=-1)
    own_source = own_sides // per_block
    own_same = own_source[:, :, None] == own_source[:, None, :]
    own_rank = jnp.sum(jnp.logical_and(own_same, before), axis=-1)
    held_here = own_source == my_index
    picks = jnp.stack(
        [
            jnp.sum(jnp.where(jnp.logical_and(held_here, own_rank == r), own_sides % per_block, 0), axis=-1)
            for r in range(PER)
        ],
        axis=-1,
    ).reshape(held)

    cells = features[0]
    ends = seq_count - 1
    if seq_count == 2:
        swapped = lax.ppermute(
            jnp.concatenate([cells[length - halo :], cells[:halo]]), "seq", [(0, 1), (1, 0)]
        )
        head = jnp.where(my_index == 0, jnp.zeros_like(swapped[:halo]), swapped[:halo])
        tail = jnp.where(my_index == ends, jnp.zeros_like(swapped[halo:]), swapped[halo:])
    else:
        head = lax.ppermute(cells[length - halo :], "seq", [(i, i + 1) for i in range(ends)])
        tail = lax.ppermute(cells[:halo], "seq", [(i + 1, i) for i in range(ends)])
    last = per_block - 1
    stacked = cells.reshape(per_block, TB * width)
    block_ids = jnp.arange(per_block)[None, :]

    def select(offset, part):
        choose = (picks[:, None] + offset == block_ids).astype(cells.dtype)
        return jnp.dot(choose, part, preferred_element_type=jnp.float32)

    middle = select(0, stacked).reshape(held, TB, width)
    prev_tail = select(-1, stacked[:, (TB - halo) * width :]).reshape(held, halo, width)
    next_head = select(1, stacked[:, : halo * width]).reshape(held, halo, width)
    lower = jnp.where((picks == 0)[:, None, None], head[None].astype(jnp.float32), prev_tail)
    upper = jnp.where((picks == last)[:, None, None], tail[None].astype(jnp.float32), next_head)
    windows = jnp.concatenate([lower, middle, upper], axis=1).astype(cells.dtype)
    x_float = windows.astype(jnp.float32)
    act = jax.nn.gelu(x_float).astype(jnp.bfloat16)
    conv_out = jnp.einsum("hti,oi->hto", act[:, 0:TB], conv_weight[0], preferred_element_type=jnp.float32)
    for offset in range(1, taps):
        conv_out = conv_out + jnp.einsum(
            "hti,oi->hto", act[:, offset : offset + TB], conv_weight[offset], preferred_element_type=jnp.float32
        )
    my_scale = 1.25 * keep[0].astype(jnp.float32)
    x_part = lax.dynamic_slice_in_dim(x_float[:, halo : halo + TB], my_part * narrow, narrow, 2)
    mixed = (x_part + my_scale * conv_out).astype(jnp.bfloat16)

    def lanes(part):
        flat = part.reshape(part.shape[0], -1)
        flat = jnp.pad(flat, ((0, 0), (0, -flat.shape[1] % 128)))
        return flat.reshape(flat.shape[0], -1, 128)

    act_cut = lanes(act.reshape(held, span, peers, cols).transpose(2, 0, 1, 3))
    mixed_part = lanes(mixed.reshape(1, -1))
    wide = targets.reshape(-1)
    pieces = []
    for _ in range(3):
        piece = lax.reduce_precision(wide, exponent_bits=8, mantissa_bits=7)
        pieces.append(piece)
        wide = wide - piece
    own_slot = (own_source * groups + lax.axis_index("dp")) * held + jnp.arange(owners)[:, None] * PER + own_rank
    small = jnp.concatenate(
        [tiles.reshape(-1), counts.reshape(-1), keep.reshape(-1), own_slot.reshape(-1)]
    ).astype(jnp.float32)
    meta_part = lanes(jnp.concatenate(pieces + [small]).astype(jnp.bfloat16).reshape(1, -1))
    rows_mixed, rows_act, rows_meta = mixed_part.shape[1], act_cut.shape[1], meta_part.shape[1]
    outgoing = jnp.concatenate(
        [
            jnp.broadcast_to(mixed_part, (peers, rows_mixed, 128)),
            act_cut,
            jnp.broadcast_to(meta_part, (peers, rows_meta, 128)),
        ],
        axis=1,
    )
    outgoing = jnp.pad(outgoing, ((0, 0), (0, -outgoing.shape[1] % 16), (0, 0)))
    incoming = lax.all_to_all(outgoing, ("seq", "dp"), 0, 0, tiled=True)
    n_mixed = held * TB * narrow
    n_act = held * span * cols
    mixed_in = incoming[:, :rows_mixed].reshape(peers, -1)[:, :n_mixed].reshape(peers * held, TB, narrow)
    act_in = incoming[:, rows_mixed : rows_mixed + rows_act].reshape(peers, -1)[:, :n_act]
    act_in = act_in.reshape(peers * held, span, cols)
    meta_in = incoming[:, rows_mixed + rows_act : rows_mixed + rows_act + rows_meta].reshape(peers, -1)
    meta_in = meta_in.astype(jnp.float32).reshape(seq_count, groups, -1)
    n_targets = capacity * TB * TB
    n_tiles = owners * capacity * 2
    targets_all = meta_in[:, :, :n_targets] + meta_in[:, :, n_targets : 2 * n_targets]
    targets_all = targets_all + meta_in[:, :, 2 * n_targets : 3 * n_targets]
    ints = meta_in[0, :, 3 * n_targets :].astype(jnp.int32)
    tiles_all = ints[:, :n_tiles].reshape(groups, owners, capacity, 2)
    counts_all = ints[:, n_tiles : n_tiles + owners]
    keep_all = ints[:, n_tiles + owners]
    slot = ints[:, n_tiles + owners + 1 : n_tiles + owners + 1 + owners * n_sides].reshape(groups, owners, n_sides)

    sides = jnp.concatenate([tiles_all[..., 0], tiles_all[..., 1]], axis=-1)

    pick_slot = (slot[..., None] == jnp.arange(peers * held)).astype(jnp.bfloat16)
    side_rows = jnp.dot(
        pick_slot.reshape(-1, peers * held), mixed_in.reshape(peers * held, -1), preferred_element_type=jnp.float32
    ).astype(jnp.bfloat16).reshape(slot.shape + (TB, narrow))
    row_side = side_rows[:, :, :capacity]
    col_side = side_rows[:, :, capacity:]
    partial_tiles = jnp.einsum("qocid,qocjd->qocij", row_side, col_side, preferred_element_type=jnp.float32)
    lanes_shape = partial_tiles.shape
    summed = axis_sum(partial_tiles.reshape(-1, 128), "mp").reshape(lanes_shape)
    predicted = summed / math.sqrt(width)
    target_tiles = targets_all.reshape(seq_count, groups, capacity, TB, TB).transpose(1, 0, 2, 3, 4)
    live_mask = (jnp.arange(capacity)[None, None, :] < counts_all[:, :, None]).astype(jnp.float32)
    n_live = jnp.sum(counts_all, axis=-1).astype(jnp.float32)
    dpredicted = (
        2.0
        / math.sqrt(width)
        * live_mask[..., None, None]
        * (predicted - target_tiles)
        / n_live[:, None, None, None, None]
    )
    row_float = row_side.astype(jnp.float32)
    col_float = col_side.astype(jnp.float32)
    drow = jnp.einsum("qocij,qocjd->qocid", dpredicted, col_float, precision=lax.Precision.HIGHEST)
    dcol = jnp.einsum("qocij,qocid->qocjd", dpredicted, row_float, precision=lax.Precision.HIGHEST)
    grads = jnp.concatenate([drow, dcol], axis=2).astype(jnp.bfloat16).astype(jnp.float32)
    grads = grads.reshape(groups, owners * n_sides, TB, narrow)
    flat_sides = sides.reshape(groups, owners * n_sides)
    same_block = flat_sides[:, :, None] == flat_sides[:, None, :]
    total = jnp.einsum(
        "qab,qbtd->qatd",
        same_block.astype(jnp.bfloat16),
        grads.astype(jnp.bfloat16),
        preferred_element_type=jnp.float32,
    )
    earlier = jnp.arange(owners * n_sides)[None, :] < jnp.arange(owners * n_sides)[:, None]
    first = jnp.logical_not(jnp.any(jnp.logical_and(same_block, earlier[None]), axis=-1))
    scaling = 1.25 * keep_all.astype(jnp.float32)
    dconv = (scaling[:, None, None, None] * total).astype(jnp.bfloat16)
    dconv = jnp.where(first[..., None, None], dconv, jnp.zeros_like(dconv))
    pick_act = (slot.reshape(groups, owners * n_sides)[..., None] == jnp.arange(peers * held)).astype(jnp.bfloat16)
    act_sides = jnp.dot(
        pick_act.reshape(-1, peers * held), act_in.reshape(peers * held, -1), preferred_element_type=jnp.float32
    ).astype(jnp.bfloat16).reshape(groups, owners * n_sides, span, cols)
    return jnp.stack(
        [
            jnp.einsum(
                "qato,qati->oi",
                dconv,
                act_sides[:, :, offset : offset + TB],
                preferred_element_type=jnp.float32,
            )
            for offset in range(taps)
        ]
    )


def per_device(features, conv_weight, keep, tiles, counts, targets):
    members, length, _ = features.shape
    owners, capacity = tiles.shape[1], tiles.shape[2]
    blocks = lax.axis_size("seq") * length // TB
    fits = members == 1 and targets.shape[1] == 1 and 2 * owners * capacity * TB <= length
    fits = fits and blocks <= 256 and capacity <= 256
    if fits:
        return sparse_path(features, conv_weight, keep, tiles, counts, targets)
    return dense_path(features, conv_weight, keep, tiles, counts, targets)


def solution(mesh):
    placed = (
        P("dp", "seq", None),
        P(None, "mp", None),
        P("dp"),
        P("dp", None, None, None),
        P("dp", None),
        P("dp", "seq", None, None),
    )
    return jax.shard_map(
        per_device,
        mesh=mesh,
        in_specs=placed,
        out_specs=P(None, "mp", ("seq", "dp")),
        check_vma=False,
    )
```
